32 devices in a mesh: chk: 4 (over z), var: 8 (over y, x, core).
Axes of the slice: x: 2, y: 2, z: 4, core: 2. Of those that a mesh axis runs over, the one named last changes fastest.
Arguments:
- tile_bits: int32 [4, 8, 2, 4096], P('chk', 'var'), may hold values 0 or 1
- tile_pos: int32 [4, 8, 2, 2], P('chk', 'var'), may hold values from 0 to 3, as said below
- tile_count: int32 [4, 8], P('chk', 'var'), may hold values from 1 to 2, as said below
- edge_weight: float32 [4, 8, 2, 4096], P('chk', 'var'), may hold values from 0.1 to 1.9
- syndrome: int32 [1024, 128], P('chk'), may hold values 0 or 1
- channel_prior: float32 [2048], P('var'), may hold values from 1 to 6
- out_cot: float32 [2048, 128], P('var'), may hold values from -0.6 to 0.6
Outputs:
- marginals: float32 [2048, 128], P('var')
- weight_grad: float32 [4, 8, 2, 4096], P('chk', 'var')
- prior_grad: float32 [2048], P('var')
The draws below stay inside these ranges and needn't reach their ends.
Inputs may be any that keep to these rules, and one draw needn't show every extreme that they name: `tile_pos`: in each grid cell the 2 slots name distinct tiles of its 4 x 4 block grid, check block first. `tile_count`: some grid cell uses all 2 slots.
All inputs are finite; a program needn't handle non-finite values. No bound on the sum of `tile_bits` or of `syndrome` on one device may be relied on, other than what follows from the above.
Results may differ from the reference program's by a relative error of at most 0.0003.
Values sent between devices are 32-bit elements; how exact they have to be, the bound alone decides.
No kernel may reach another device: no remote copies, remote signals or barrier semaphores. Data moves between devices by JAX's collectives and lax.ppermute only.
A program may use at most 256 MiB of HBM per device.

```python
import math
import jax
import jax.numpy as jnp
from jax import lax

TILE = 64
CB_DEV = 4
VB_DEV = 4
TMAX = 2
ITERS = 2
SHOTS = 128
CHECKS = 1024
VARS = 2048
N_CHK = 4
N_VAR = 8


def tile_layout(key):
    base = jax.random.fold_in(key, 29)
    cells = N_CHK * N_VAR
    keys = jax.random.split(jax.random.fold_in(base, 1), cells)

    def one_order(one_key):
        return jax.random.permutation(one_key, CB_DEV * VB_DEV)
    orders = jax.vmap(one_order)(keys).astype(jnp.int32)
    chosen = orders[:, :TMAX]
    positions = jnp.stack([chosen // VB_DEV, chosen % VB_DEV], axis=-1).reshape(N_CHK, N_VAR, TMAX, 2)
    extra = jax.random.randint(jax.random.fold_in(base, 2), (cells,), 0, 4)
    counts = jnp.where(extra == 0, TMAX, 1)
    chosen_cell = jax.random.randint(jax.random.fold_in(base, 3), (), 0, cells)
    counts = jnp.where(jnp.arange(cells) == chosen_cell, TMAX, counts)
    return (positions.astype(jnp.int32), counts.astype(jnp.int32).reshape(N_CHK, N_VAR))


def draw_tile_pos(key, part):
    return tile_layout(key)[0]


def draw_tile_count(key, part):
    return tile_layout(key)[1]


def touch_ends(values, own_key, least, largest):
    longest = values.shape.index(max(values.shape))
    spots = []
    for shift in (0, 1):
        where = [jax.random.randint(jax.random.fold_in(own_key, axis), (), 0, length) for axis, length in enumerate(values.shape)]
        where[longest] = (where[longest] + shift) % values.shape[longest]
        spots.append(tuple(where))
    return values.at[spots[0]].set(least).at[spots[1]].set(largest)


def shard_levels(key, extent, shards, low, largest):
    factor_of = 1.0
    for axis_at, parts in shards:
        steps = jax.random.uniform(jax.random.fold_in(jax.random.fold_in(key, 6), axis_at), (parts,), jnp.float32, low / len(shards), largest / len(shards))
        factor_of = factor_of * jnp.repeat(jnp.exp(steps), extent[axis_at] // parts).reshape((-1,) + (1,) * (len(extent) - 1 - axis_at))
    return factor_of


def bell_draw(key, extent, width, reach, cuts=(), kind=jnp.bfloat16):
    values = jax.random.normal(key, extent, jnp.float32) * width
    if len(cuts) > 0:
        values = shard_levels(key, extent, cuts, -0.22, 0.18) * values
    return jnp.clip(values, min=-reach, max=reach).astype(kind)


def setup_inputs(seed: int = 0) -> dict:
    arg_keys = jax.random.split(jax.random.key(seed), 8)
    tile_bits = touch_ends((jax.random.randint(arg_keys[0], (N_CHK, N_VAR, TMAX, TILE * TILE), 0, 512) < 5).astype(jnp.int32), jax.random.fold_in(arg_keys[0], 1), 0, 1)
    tile_pos = draw_tile_pos(jax.random.fold_in(arg_keys[7], 71), 0)
    tile_count = draw_tile_count(jax.random.fold_in(arg_keys[7], 71), 0)
    edge_weight = jnp.clip(1.0 + 0.18 * jax.random.normal(arg_keys[3], (N_CHK, N_VAR, TMAX, TILE * TILE), jnp.float32), 0.1, 1.9)
    syndrome = touch_ends((jax.random.randint(arg_keys[4], (CHECKS, SHOTS), 0, 4) < 1).astype(jnp.int32), jax.random.fold_in(arg_keys[4], 1), 0, 1)
    channel_prior = jnp.clip(jnp.exp(math.log(6.0) - 1.7917595 * jax.random.uniform(arg_keys[5], (VARS,), jnp.float32) ** shard_levels(arg_keys[5], (VARS,), ((0, 8),), -0.2, 0.2)), 1.0, 6.0)
    out_cot = bell_draw(arg_keys[6], (VARS, SHOTS), 0.1, 0.6, ((0, 8),), jnp.float32)
    return dict(tile_bits=tile_bits, tile_pos=tile_pos, tile_count=tile_count, edge_weight=edge_weight, syndrome=syndrome, channel_prior=channel_prior, out_cot=out_cot)


DAMP = 0.97
EXACT = lax.Precision.HIGHEST

def linear_both(values, axis):
    length = values.shape[axis]
    pieces = [lax.slice_in_dim(values, index, index + 1, axis=axis) for index in range(length)]
    ones = jnp.ones_like(pieces[0])
    prefix = [ones]
    for index in range(length - 1):
        prefix.append(prefix[-1] * pieces[index])
    suffix = [ones]
    for index in range(length - 1, 0, -1):
        suffix.append(suffix[-1] * pieces[index])
    suffix = suffix[::-1]
    whole = prefix[-1] * pieces[-1]
    return (jnp.concatenate(prefix, axis=axis), jnp.concatenate(suffix, axis=axis), whole)

def exclusive_both(values, axis):
    length = values.shape[axis]
    if length < 16 or length % 8 != 0:
        return linear_both(values, axis)
    shape = values.shape
    split = values.reshape(shape[:axis] + (length // 8, 8) + shape[axis + 1:])
    inner_before, inner_after, group_whole = linear_both(split, axis + 1)
    outer_before, outer_after, whole = exclusive_both(group_whole, axis)
    before = (inner_before * outer_before).reshape(shape)
    after = (inner_after * outer_after).reshape(shape)
    whole = whole.reshape(shape[:axis] + (1,) + shape[axis + 1:])
    return (before, after, whole)

def device_tables(bits, positions, count, check_blocks, column_blocks):
    slot_total = bits.shape[0]
    slots = jnp.arange(slot_total, dtype=jnp.int32)
    live = slots < count
    edge = jnp.where(live[:, None], bits, 0).astype(jnp.float32).reshape(slot_total, TILE, TILE)
    row_hot = (positions[:, 0:1] == jnp.arange(check_blocks, dtype=jnp.int32)[None, :]).astype(jnp.float32)
    col_hot = (positions[:, 1:2] == jnp.arange(column_blocks, dtype=jnp.int32)[None, :]).astype(jnp.float32)
    same_row = (positions[:, None, 0] == positions[None, :, 0]) & (slots[:, None] != slots[None, :])
    return (edge, row_hot, col_hot, same_row)

def row_products(messages, edge, row_hot, same_row):
    halves = jnp.where(edge[..., None] > 0, jnp.tanh(0.5 * messages), 1.0)
    before, after, whole = exclusive_both(halves, 2)
    whole = whole[:, :, 0, :]
    rows = jnp.prod(jnp.where(row_hot[:, :, None, None] > 0, whole[:, None], 1.0), axis=0)
    others_here = jnp.prod(jnp.where(same_row[:, :, None, None], whole[None], 1.0), axis=1)
    inner = before * after * others_here[:, :, None, :]
    return (inner, rows)

def edge_messages(inner, others, weight, sign_slot, edge, row_hot, col_hot):
    others_slot = jnp.einsum('kc,crs->krs', row_hot, others, precision=EXACT)
    product = sign_slot[:, :, None, :] * inner * others_slot[:, :, None, :]
    update = (edge * weight)[..., None] * jnp.log((1.0 + DAMP * product) / (1.0 - DAMP * product))
    column = jnp.einsum('kv,kcs->vcs', col_hot, lax.optimization_barrier(jnp.sum(update, axis=1)), precision=EXACT)
    return (update, column)

def reference(tile_bits, tile_pos, tile_count, edge_weight, syndrome, channel_prior, out_cot):

    def tables(bits, positions, count):
        return device_tables(bits, positions, count, CB_DEV, VB_DEV)
    edge, row_hot, col_hot, same_row = jax.vmap(jax.vmap(tables))(tile_bits, tile_pos, tile_count)
    weight = edge_weight.reshape(N_CHK, N_VAR, TMAX, TILE, TILE)
    sign_dev = (1.0 - 2.0 * syndrome.astype(jnp.float32)).reshape(N_CHK, CB_DEV, TILE, SHOTS)
    prior_dev = channel_prior.reshape(N_VAR, VB_DEV, TILE)
    block = math.gcd(SHOTS, 8)
    count_blocks = SHOTS // block
    sign_blocks = jnp.moveaxis(sign_dev.reshape(N_CHK, CB_DEV, TILE, count_blocks, block), 3, 0)
    cot_blocks = jnp.moveaxis(out_cot.reshape(N_VAR, VB_DEV, TILE, count_blocks, block), 3, 0)
    products = jax.vmap(jax.vmap(row_products))
    exchange = jax.vmap(jax.vmap(edge_messages))

    def forward(weight_now, prior_now, sign_block):
        sign_slot = jnp.einsum('ijkc,icrs->ijkrs', row_hot, sign_block, precision=EXACT)
        prior_slot = jnp.einsum('ijkv,jvc->ijkc', col_hot, prior_now, precision=EXACT)
        messages = jnp.broadcast_to(prior_slot[:, :, :, None, :, None], (N_CHK, N_VAR, TMAX, TILE, TILE, block))
        total = None
        for step in range(ITERS):
            inner, rows = products(messages, edge, row_hot, same_row)
            before, after, unused = exclusive_both(rows, 1)
            update, column = exchange(inner, before * after, weight_now, sign_slot, edge, row_hot, col_hot)
            total = prior_now[..., None] + lax.optimization_barrier(jnp.sum(column, axis=0))
            spread = jnp.einsum('ijkv,jvcs->ijkcs', col_hot, total, precision=EXACT)
            messages = spread[:, :, :, None] - update
        return total

    def one_block(carry, pieces):
        sign_block, cot_block = pieces

        def closed(weight_now, prior_now):
            return forward(weight_now, prior_now, sign_block)
        total, pull = jax.vjp(closed, weight, prior_dev)
        weight_part, prior_part = pull(cot_block)
        return ((carry[0] + weight_part, carry[1] + prior_part), total)
    start = (jnp.zeros_like(weight), jnp.zeros_like(prior_dev))
    (weight_grad, prior_grad), totals = lax.scan(one_block, start, (sign_blocks, cot_blocks))
    marginals = jnp.moveaxis(totals, 0, 3).reshape(VARS, SHOTS)
    return (marginals, weight_grad.reshape(N_CHK, N_VAR, TMAX, TILE * TILE), prior_grad.reshape(VARS))
```

```python
import functools

import jax
import jax.numpy as jnp
from jax import lax
from jax.experimental import pallas as pl
from jax.sharding import PartitionSpec as P

TILE = 64
ITERS = 2


DAMP = 0.97
EXACT = lax.Precision.HIGHEST
F32 = jnp.float32
UNROLL = 4


def linear_both(values, axis):
    length = values.shape[axis]
    pieces = [lax.slice_in_dim(values, index, index + 1, axis=axis) for index in range(length)]
    ones = jnp.ones_like(pieces[0])
    prefix = [ones]
    for index in range(length - 1):
        prefix.append(prefix[-1] * pieces[index])
    suffix = [ones]
    for index in range(length - 1, 0, -1):
        suffix.append(suffix[-1] * pieces[index])
    suffix = suffix[::-1]
    whole = prefix[-1] * pieces[-1]
    return (jnp.concatenate(prefix, axis=axis), jnp.concatenate(suffix, axis=axis), whole)


def exclusive_both(values, axis):
    length = values.shape[axis]
    if length < 16 or length % 8 != 0:
        return linear_both(values, axis)
    shape = values.shape
    split = values.reshape(shape[:axis] + (length // 8, 8) + shape[axis + 1 :])
    inner_before, inner_after, group_whole = linear_both(split, axis + 1)
    outer_before, outer_after, whole = exclusive_both(group_whole, axis)
    before = (inner_before * outer_before).reshape(shape)
    after = (inner_after * outer_after).reshape(shape)
    whole = whole.reshape(shape[:axis] + (1,) + shape[axis + 1 :])
    return (before, after, whole)


def device_tables(bits, positions, count, check_blocks, column_blocks):
    slot_total = bits.shape[0]
    slots = jnp.arange(slot_total, dtype=jnp.int32)
    live = slots < count
    edge = jnp.where(live[:, None], bits, 0).astype(jnp.float32).reshape(slot_total, TILE, TILE)
    row_hot = (positions[:, 0:1] == jnp.arange(check_blocks, dtype=jnp.int32)[None, :]).astype(
        jnp.float32
    )
    col_hot = (positions[:, 1:2] == jnp.arange(column_blocks, dtype=jnp.int32)[None, :]).astype(
        jnp.float32
    )
    same_row = (positions[:, None, 0] == positions[None, :, 0]) & (slots[:, None] != slots[None, :])
    return (edge, row_hot, col_hot, same_row)


def _spread_row(ref, c, shape):
    return jnp.broadcast_to(ref[0, pl.ds(c, 1), :], shape)


def _fwd_products_kernel(has_u, *refs):
    if has_u:
        spread_ref, u_ref, em_ref, ba_ref, whole_ref, h_scr = refs
    else:
        spread_ref, em_ref, ba_ref, whole_ref, h_scr = refs
    n_c = em_ref.shape[1]
    shape = em_ref.shape[2:]

    def forward(c, carry):
        m = _spread_row(spread_ref, c, shape)
        if has_u:
            m = m - u_ref[0, c]
        h = jnp.where(em_ref[0, c] > 0, jnp.tanh(0.5 * m), 1.0)
        h_scr[c] = h
        ba_ref[0, c] = carry
        return carry * h

    whole = lax.fori_loop(0, n_c, forward, jnp.ones(shape, F32), unroll=UNROLL)
    whole_ref[0] = whole

    def backward(i, carry):
        c = n_c - 1 - i
        ba_ref[0, c] = ba_ref[0, c] * carry
        return carry * h_scr[c]

    lax.fori_loop(0, n_c, backward, jnp.ones(shape, F32), unroll=UNROLL)


def _fwd_messages_kernel(ba_ref, f_ref, ew_ref, u_ref, col_ref):
    n_c = ba_ref.shape[1]
    f = f_ref[0]

    def body(c, carry):
        x = ba_ref[0, c] * f
        u = ew_ref[0, c] * jnp.log((1.0 + DAMP * x) / (1.0 - DAMP * x))
        u_ref[0, c] = u
        col_ref[0, pl.ds(c, 1), :] = jnp.sum(u, axis=0, keepdims=True)
        return carry

    lax.fori_loop(0, n_c, body, 0, unroll=UNROLL)


def _bwd_messages_kernel(has_next, has_acc, *refs):
    refs = list(refs)
    gsp_ref = refs.pop(0)
    gm_ref = refs.pop(0) if has_next else None
    ba_ref, f_ref, ew_ref = refs[:3]
    refs = refs[3:]
    acc_ref = refs.pop(0) if has_acc else None
    gw_ref, gba_ref, d1_ref = refs
    n_c = ba_ref.shape[1]
    shape = ba_ref.shape[2:]
    f = f_ref[0]

    def body(c, total):
        gu = _spread_row(gsp_ref, c, shape)
        if has_next:
            gu = gu - gm_ref[0, c]
        ba = ba_ref[0, c]
        x = ba * f
        low = 1.0 - DAMP * x
        high = 1.0 + DAMP * x
        gw = gu * jnp.log(high / low)
        if has_acc:
            gw = gw + acc_ref[0, c]
        gw_ref[0, c] = gw
        gx = gu * ew_ref[0, c] * ((2.0 * DAMP) / (low * high))
        gba_ref[0, c] = gx * f
        return total + gx * ba

    d1_ref[0] = lax.fori_loop(0, n_c, body, jnp.zeros(shape, F32), unroll=UNROLL)


def _bwd_products_kernel(has_u, emit_gm, *refs):
    refs = list(refs)
    spread_ref = refs.pop(0)
    u_ref = refs.pop(0) if has_u else None
    em_ref, gba_ref, gwh_ref = refs[:3]
    refs = refs[3:]
    gm_ref = refs.pop(0) if emit_gm else None
    col_ref, h_scr, p_scr, q_scr = refs
    n_c = em_ref.shape[1]
    shape = em_ref.shape[2:]
    gwh = gwh_ref[0]

    def forward(c, carry):
        prod, grad = carry
        m = _spread_row(spread_ref, c, shape)
        if has_u:
            m = m - u_ref[0, c]
        h = jnp.where(em_ref[0, c] > 0, jnp.tanh(0.5 * m), 1.0)
        h_scr[c] = h
        p_scr[c] = prod
        q_scr[c] = grad
        return (prod * h, grad * h + gba_ref[0, c] * prod)

    ones = jnp.ones(shape, F32)
    zeros = jnp.zeros(shape, F32)
    lax.fori_loop(0, n_c, forward, (ones, zeros), unroll=UNROLL)

    def backward(i, carry):
        prod, grad = carry
        c = n_c - 1 - i
        h = h_scr[c]
        before = p_scr[c]
        gh = q_scr[c] * prod + before * (grad + gwh * prod)
        gm = jnp.where(em_ref[0, c] > 0, gh * (0.5 * (1.0 - h * h)), 0.0)
        if emit_gm:
            gm_ref[0, c] = gm
        col_ref[0, pl.ds(c, 1), :] = jnp.sum(gm, axis=0, keepdims=True)
        return (prod * h, grad * h + gba_ref[0, c] * prod)

    lax.fori_loop(0, n_c, backward, (ones, zeros), unroll=UNROLL)


def _big_spec(shape):
    return pl.BlockSpec((1,) + shape[1:], lambda k: (k, 0, 0, 0))


def _small_spec(shape):
    return pl.BlockSpec((1,) + shape[1:], lambda k: (k, 0, 0))


def _call(kernel, inputs, outputs, scratch=()):
    in_specs = [_big_spec(a.shape) if a.ndim == 4 else _small_spec(a.shape) for a in inputs]
    out_specs = [_big_spec(o.shape) if len(o.shape) == 4 else _small_spec(o.shape) for o in outputs]
    return pl.pallas_call(
        kernel,
        grid=(inputs[0].shape[0],),
        in_specs=in_specs,
        out_specs=out_specs,
        out_shape=list(outputs),
        scratch_shapes=list(scratch),
    )(*inputs)


def fwd_products(spread, u, em):
    k, c, r, s = em.shape
    has_u = u is not None
    inputs = [spread] + ([u] if has_u else []) + [em]
    outs = [jax.ShapeDtypeStruct(em.shape, F32), jax.ShapeDtypeStruct((k, r, s), F32)]
    from jax.experimental.pallas import tpu as pltpu

    return _call(
        functools.partial(_fwd_products_kernel, has_u),
        inputs,
        outs,
        [pltpu.VMEM((c, r, s), F32)],
    )


def fwd_messages(ba, f, ew):
    k, c, r, s = ba.shape
    outs = [jax.ShapeDtypeStruct(ba.shape, F32), jax.ShapeDtypeStruct((k, c, s), F32)]
    return _call(_fwd_messages_kernel, [ba, f, ew], outs)


def bwd_messages(gsp, gm, ba, f, ew, acc):
    k, c, r, s = ba.shape
    has_next = gm is not None
    has_acc = acc is not None
    inputs = [gsp] + ([gm] if has_next else []) + [ba, f, ew] + ([acc] if has_acc else [])
    outs = [
        jax.ShapeDtypeStruct(ba.shape, F32),
        jax.ShapeDtypeStruct(ba.shape, F32),
        jax.ShapeDtypeStruct((k, r, s), F32),
    ]
    return _call(functools.partial(_bwd_messages_kernel, has_next, has_acc), inputs, outs)


def bwd_products(spread, u, em, gba, gwh, emit_gm):
    from jax.experimental.pallas import tpu as pltpu

    k, c, r, s = em.shape
    has_u = u is not None
    inputs = [spread] + ([u] if has_u else []) + [em, gba, gwh]
    outs = ([jax.ShapeDtypeStruct(em.shape, F32)] if emit_gm else []) + [
        jax.ShapeDtypeStruct((k, c, s), F32)
    ]
    results = _call(
        functools.partial(_bwd_products_kernel, has_u, emit_gm),
        inputs,
        outs,
        [pltpu.VMEM((c, r, s), F32) for _ in range(3)],
    )
    if emit_gm:
        return results[0], results[1]
    return None, results[0]


def combine(whole, row_hot, same_row):
    slots = whole.shape[0]
    blocks = row_hot.shape[1]
    ones = jnp.ones_like(whole[0])
    rows = []
    for block in range(blocks):
        value = ones
        for k in range(slots):
            value = value * jnp.where(row_hot[k, block] > 0, whole[k], 1.0)
        rows.append(value)
    others_here = []
    for k in range(slots):
        value = ones
        for other in range(slots):
            if other != k:
                value = value * jnp.where(same_row[k, other], whole[other], 1.0)
        others_here.append(value)
    return jnp.stack(rows), jnp.stack(others_here)


def others_forward(rows, check_blocks):
    own = lax.axis_index("var")
    piece = lax.all_gather(rows, "var", axis=0, tiled=True)
    indices = jnp.arange(piece.shape[0], dtype=jnp.int32)
    keep = indices // check_blocks != own
    parts = []
    for block in range(check_blocks):
        pick = (keep & (indices % check_blocks == block))[:, None, None]
        parts.append(jnp.prod(jnp.where(pick, piece, 1.0), axis=0))
    return jnp.stack(parts), piece


def others_backward(row_piece, grads, check_blocks):
    own = lax.axis_index("var")
    grad_piece = lax.all_gather(grads, "var", axis=0, tiled=True)
    indices = jnp.arange(row_piece.shape[0], dtype=jnp.int32)
    keep = indices // check_blocks != own
    new_sums = []
    for block in range(check_blocks):
        pick = (keep & (indices % check_blocks == block))[:, None, None]
        factors = jnp.where(pick, row_piece, 1.0)
        weights = jnp.where(pick, grad_piece, 0.0)
        before, after, whole = exclusive_both(factors, 0)
        new_sums.append(jnp.sum(weights * before * after, axis=0))
    return jnp.stack(new_sums)


def body(tile_bits, tile_pos, tile_count, edge_weight, syndrome, channel_prior, out_cot):
    slot_total = tile_bits.shape[2]
    shots = syndrome.shape[1]
    check_blocks = syndrome.shape[0] // TILE
    column_blocks = channel_prior.shape[0] // TILE
    edge, row_hot, col_hot, same_row = device_tables(
        tile_bits[0, 0], tile_pos[0, 0], tile_count[0, 0], check_blocks, column_blocks
    )
    weight = edge_weight[0, 0].reshape(slot_total, TILE, TILE)
    edge_t = jnp.swapaxes(edge, 1, 2)
    dense = (slot_total, TILE, TILE, shots)
    em = jnp.broadcast_to(edge_t[..., None], dense)
    ew = jnp.broadcast_to((edge_t * jnp.swapaxes(weight, 1, 2))[..., None], dense)
    sign_dev = (1.0 - 2.0 * syndrome.astype(jnp.float32)).reshape(check_blocks, TILE, shots)
    sign_slot = jnp.einsum("kc,crs->krs", row_hot, sign_dev, precision=EXACT)
    prior_dev = channel_prior.reshape(column_blocks, TILE)
    prior_slot = jnp.einsum("kv,vc->kc", col_hot, prior_dev, precision=EXACT)
    spread = jnp.broadcast_to(prior_slot[:, :, None], (slot_total, TILE, shots))
    u = None
    saved = []
    total = None
    for step in range(ITERS):
        ba, whole = fwd_products(spread, u, em)
        rows, others_here = combine(whole, row_hot, same_row)
        others, piece = others_forward(rows, check_blocks)
        others_slot = jnp.einsum("kc,crs->krs", row_hot, others, precision=EXACT)
        factor = sign_slot * others_here * others_slot
        saved.append((spread, u, ba, whole, factor, others_here, others_slot, piece))
        u, colsum = fwd_messages(ba, factor, ew)
        column = jnp.einsum("kv,kcs->vcs", col_hot, colsum, precision=EXACT)
        total = prior_dev[:, :, None] + lax.psum(column, "chk")
        spread = jnp.einsum("kv,vcs->kcs", col_hot, total, precision=EXACT)
    marginals = total.reshape(column_blocks * TILE, shots)

    grad_total = out_cot.reshape(column_blocks, TILE, shots)
    prior_grad = jnp.zeros((column_blocks, TILE), jnp.float32)
    grad_m = None
    acc = None
    for step in reversed(range(ITERS)):
        spread_t, u_prev, ba, whole, factor, others_here, others_slot, piece = saved[step]
        prior_grad = prior_grad + jnp.sum(grad_total, axis=2)
        grad_spread = jnp.einsum("kv,vcs->kcs", col_hot, grad_total, precision=EXACT)
        acc, grad_ba, grad_factor = bwd_messages(grad_spread, grad_m, ba, factor, ew, acc)
        grad_here = grad_factor * sign_slot * others_slot
        grad_slot = grad_factor * sign_slot * others_here
        grad_others = jnp.einsum("kc,krs->crs", row_hot, grad_slot, precision=EXACT)
        grad_rows = others_backward(piece, grad_others, check_blocks)
        unused, pull = jax.vjp(lambda w: combine(w, row_hot, same_row), whole)
        grad_whole = pull((grad_rows, grad_here))[0]
        grad_m, colsum = bwd_products(spread_t, u_prev, em, grad_ba, grad_whole, step > 0)
        grad_total = lax.psum(
            jnp.einsum("kv,kcs->vcs", col_hot, colsum, precision=EXACT), "chk"
        )
    prior_grad = prior_grad + jnp.sum(grad_total, axis=2)
    weight_grad = edge * jnp.swapaxes(jnp.sum(acc, axis=3), 1, 2)
    return (
        marginals,
        weight_grad.reshape(1, 1, slot_total, TILE * TILE),
        prior_grad.reshape(column_blocks * TILE),
    )


def solution(mesh):
    placed = (
        P("chk", "var", None, None),
        P("chk", "var", None, None),
        P("chk", "var"),
        P("chk", "var", None, None),
        P("chk", None),
        P("var"),
        P("var", None),
    )
    return jax.shard_map(
        body,
        mesh=mesh,
        in_specs=placed,
        out_specs=(P("var", None), P("chk", "var", None, None), P("var")),
        check_vma=False,
    )
```

```python
import functools

import jax
import jax.numpy as jnp
from jax import lax
from jax.experimental import pallas as pl
from jax.sharding import PartitionSpec as P

TILE = 64
ITERS = 2


DAMP = 0.97
EXACT = lax.Precision.HIGHEST
F32 = jnp.float32
UNROLL = 4


def linear_both(values, axis):
    length = values.shape[axis]
    pieces = [lax.slice_in_dim(values, index, index + 1, axis=axis) for index in range(length)]
    ones = jnp.ones_like(pieces[0])
    prefix = [ones]
    for index in range(length - 1):
        prefix.append(prefix[-1] * pieces[index])
    suffix = [ones]
    for index in range(length - 1, 0, -1):
        suffix.append(suffix[-1] * pieces[index])
    suffix = suffix[::-1]
    whole = prefix[-1] * pieces[-1]
    return (jnp.concatenate(prefix, axis=axis), jnp.concatenate(suffix, axis=axis), whole)


def exclusive_both(values, axis):
    length = values.shape[axis]
    if length < 16 or length % 8 != 0:
        return linear_both(values, axis)
    shape = values.shape
    split = values.reshape(shape[:axis] + (length // 8, 8) + shape[axis + 1 :])
    inner_before, inner_after, group_whole = linear_both(split, axis + 1)
    outer_before, outer_after, whole = exclusive_both(group_whole, axis)
    before = (inner_before * outer_before).reshape(shape)
    after = (inner_after * outer_after).reshape(shape)
    whole = whole.reshape(shape[:axis] + (1,) + shape[axis + 1 :])
    return (before, after, whole)


def device_tables(bits, positions, count, check_blocks, column_blocks):
    slot_total = bits.shape[0]
    slots = jnp.arange(slot_total, dtype=jnp.int32)
    live = slots < count
    edge = jnp.where(live[:, None], bits, 0).astype(jnp.float32).reshape(slot_total, TILE, TILE)
    row_hot = (positions[:, 0:1] == jnp.arange(check_blocks, dtype=jnp.int32)[None, :]).astype(
        jnp.float32
    )
    col_hot = (positions[:, 1:2] == jnp.arange(column_blocks, dtype=jnp.int32)[None, :]).astype(
        jnp.float32
    )
    same_row = (positions[:, None, 0] == positions[None, :, 0]) & (slots[:, None] != slots[None, :])
    return (edge, row_hot, col_hot, same_row)


def _spread_row(ref, c, shape):
    return jnp.broadcast_to(ref[0, pl.ds(c, 1), :], shape)


def _fwd_products_kernel(has_u, *refs):
    if has_u:
        spread_ref, u_ref, em_ref, ba_ref, whole_ref, h_scr = refs
    else:
        spread_ref, em_ref, ba_ref, whole_ref, h_scr = refs
    n_c = em_ref.shape[1]
    shape = em_ref.shape[2:]

    def forward(c, carry):
        m = _spread_row(spread_ref, c, shape)
        if has_u:
            m = m - u_ref[0, c]
        h = jnp.where(em_ref[0, c] > 0, jnp.tanh(0.5 * m), 1.0)
        h_scr[c] = h
        ba_ref[0, c] = carry
        return carry * h

    whole = lax.fori_loop(0, n_c, forward, jnp.ones(shape, F32), unroll=UNROLL)
    whole_ref[0] = whole

    def backward(i, carry):
        c = n_c - 1 - i
        ba_ref[0, c] = ba_ref[0, c] * carry
        return carry * h_scr[c]

    lax.fori_loop(0, n_c, backward, jnp.ones(shape, F32), unroll=UNROLL)


def _fwd_messages_kernel(ba_ref, f_ref, ew_ref, u_ref, col_ref):
    n_c = ba_ref.shape[1]
    f = f_ref[0]

    def body(c, carry):
        x = ba_ref[0, c] * f
        u = ew_ref[0, c] * jnp.log((1.0 + DAMP * x) / (1.0 - DAMP * x))
        u_ref[0, c] = u
        col_ref[0, pl.ds(c, 1), :] = jnp.sum(u, axis=0, keepdims=True)
        return carry

    lax.fori_loop(0, n_c, body, 0, unroll=UNROLL)


def _bwd_messages_kernel(has_next, has_acc, *refs):
    refs = list(refs)
    gsp_ref = refs.pop(0)
    gm_ref = refs.pop(0) if has_next else None
    ba_ref, f_ref, ew_ref = refs[:3]
    refs = refs[3:]
    acc_ref = refs.pop(0) if has_acc else None
    gw_ref, gba_ref, d1_ref = refs
    n_c = ba_ref.shape[1]
    shape = ba_ref.shape[2:]
    f = f_ref[0]

    def body(c, total):
        gu = _spread_row(gsp_ref, c, shape)
        if has_next:
            gu = gu - gm_ref[0, c]
        ba = ba_ref[0, c]
        x = ba * f
        low = 1.0 - DAMP * x
        high = 1.0 + DAMP * x
        gw = gu * jnp.log(high / low)
        if has_acc:
            gw = gw + acc_ref[0, c]
        gw_ref[0, c] = gw
        gx = gu * ew_ref[0, c] * ((2.0 * DAMP) / (low * high))
        gba_ref[0, c] = gx * f
        return total + gx * ba

    d1_ref[0] = lax.fori_loop(0, n_c, body, jnp.zeros(shape, F32), unroll=UNROLL)


def _bwd_products_kernel(has_u, emit_gm, *refs):
    refs = list(refs)
    spread_ref = refs.pop(0)
    u_ref = refs.pop(0) if has_u else None
    em_ref, gba_ref, gwh_ref = refs[:3]
    refs = refs[3:]
    gm_ref = refs.pop(0) if emit_gm else None
    col_ref, h_scr, p_scr, q_scr = refs
    n_c = em_ref.shape[1]
    shape = em_ref.shape[2:]
    gwh = gwh_ref[0]

    def forward(c, carry):
        prod, grad = carry
        m = _spread_row(spread_ref, c, shape)
        if has_u:
            m = m - u_ref[0, c]
        h = jnp.where(em_ref[0, c] > 0, jnp.tanh(0.5 * m), 1.0)
        h_scr[c] = h
        p_scr[c] = prod
        q_scr[c] = grad
        return (prod * h, grad * h + gba_ref[0, c] * prod)

    ones = jnp.ones(shape, F32)
    zeros = jnp.zeros(shape, F32)
    lax.fori_loop(0, n_c, forward, (ones, zeros), unroll=UNROLL)

    def backward(i, carry):
        prod, grad = carry
        c = n_c - 1 - i
        h = h_scr[c]
        before = p_scr[c]
        gh = q_scr[c] * prod + before * (grad + gwh * prod)
        gm = jnp.where(em_ref[0, c] > 0, gh * (0.5 * (1.0 - h * h)), 0.0)
        if emit_gm:
            gm_ref[0, c] = gm
        col_ref[0, pl.ds(c, 1), :] = jnp.sum(gm, axis=0, keepdims=True)
        return (prod * h, grad * h + gba_ref[0, c] * prod)

    lax.fori_loop(0, n_c, backward, (ones, zeros), unroll=UNROLL)


def _big_spec(shape):
    return pl.BlockSpec((1,) + shape[1:], lambda k: (k, 0, 0, 0))


def _small_spec(shape):
    return pl.BlockSpec((1,) + shape[1:], lambda k: (k, 0, 0))


def _call(kernel, inputs, outputs, scratch=()):
    in_specs = [_big_spec(a.shape) if a.ndim == 4 else _small_spec(a.shape) for a in inputs]
    out_specs = [_big_spec(o.shape) if len(o.shape) == 4 else _small_spec(o.shape) for o in outputs]
    return pl.pallas_call(
        kernel,
        grid=(inputs[0].shape[0],),
        in_specs=in_specs,
        out_specs=out_specs,
        out_shape=list(outputs),
        scratch_shapes=list(scratch),
    )(*inputs)


def fwd_products(spread, u, em):
    k, c, r, s = em.shape
    has_u = u is not None
    inputs = [spread] + ([u] if has_u else []) + [em]
    outs = [jax.ShapeDtypeStruct(em.shape, F32), jax.ShapeDtypeStruct((k, r, s), F32)]
    from jax.experimental.pallas import tpu as pltpu

    return _call(
        functools.partial(_fwd_products_kernel, has_u),
        inputs,
        outs,
        [pltpu.VMEM((c, r, s), F32)],
    )


def fwd_messages(ba, f, ew):
    k, c, r, s = ba.shape
    outs = [jax.ShapeDtypeStruct(ba.shape, F32), jax.ShapeDtypeStruct((k, c, s), F32)]
    return _call(_fwd_messages_kernel, [ba, f, ew], outs)


def bwd_messages(gsp, gm, ba, f, ew, acc):
    k, c, r, s = ba.shape
    has_next = gm is not None
    has_acc = acc is not None
    inputs = [gsp] + ([gm] if has_next else []) + [ba, f, ew] + ([acc] if has_acc else [])
    outs = [
        jax.ShapeDtypeStruct(ba.shape, F32),
        jax.ShapeDtypeStruct(ba.shape, F32),
        jax.ShapeDtypeStruct((k, r, s), F32),
    ]
    return _call(functools.partial(_bwd_messages_kernel, has_next, has_acc), inputs, outs)


def bwd_products(spread, u, em, gba, gwh, emit_gm):
    from jax.experimental.pallas import tpu as pltpu

    k, c, r, s = em.shape
    has_u = u is not None
    inputs = [spread] + ([u] if has_u else []) + [em, gba, gwh]
    outs = ([jax.ShapeDtypeStruct(em.shape, F32)] if emit_gm else []) + [
        jax.ShapeDtypeStruct((k, c, s), F32)
    ]
    results = _call(
        functools.partial(_bwd_products_kernel, has_u, emit_gm),
        inputs,
        outs,
        [pltpu.VMEM((c, r, s), F32) for _ in range(3)],
    )
    if emit_gm:
        return results[0], results[1]
    return None, results[0]


def combine(whole, row_hot, same_row):
    slots = whole.shape[0]
    blocks = row_hot.shape[1]
    ones = jnp.ones_like(whole[0])
    rows = []
    for block in range(blocks):
        value = ones
        for k in range(slots):
            value = value * jnp.where(row_hot[k, block] > 0, whole[k], 1.0)
        rows.append(value)
    others_here = []
    for k in range(slots):
        value = ones
        for other in range(slots):
            if other != k:
                value = value * jnp.where(same_row[k, other], whole[other], 1.0)
        others_here.append(value)
    return jnp.stack(rows), jnp.stack(others_here)


def _power_of_two(n):
    return n > 1 and (n & (n - 1)) == 0


def _swap(value, axis, n, step):
    perm = [(j, j ^ (1 << step)) for j in range(n)]
    return lax.ppermute(value, axis, perm)


def checks_total(values, n):
    if not _power_of_two(n):
        return lax.psum(values, "chk")
    step = 0
    while (1 << step) < n:
        values = values + _swap(values, "chk", n, step)
        step += 1
    return values


def others_forward(rows, check_blocks, n):
    if not _power_of_two(n):
        return others_gather(rows, check_blocks)
    full = rows
    excl = jnp.ones_like(rows)
    trail = []
    step = 0
    while (1 << step) < n:
        other = _swap(full, "var", n, step)
        trail.append((full, excl, other))
        excl = excl * other
        full = full * other
        step += 1
    return excl, trail


def others_backward(trail, grads, check_blocks, n):
    if not _power_of_two(n):
        return others_scatter(trail, grads, check_blocks)
    spread = grads
    target = jnp.zeros_like(grads)
    for step, (full, excl, other) in enumerate(trail):
        other_spread = _swap(spread, "var", n, step)
        target = target * other + excl * other_spread
        spread = spread * other + other_spread * full
    return target


def others_gather(rows, check_blocks):
    own = lax.axis_index("var")
    piece = lax.all_gather(rows, "var", axis=0, tiled=True)
    indices = jnp.arange(piece.shape[0], dtype=jnp.int32)
    keep = indices // check_blocks != own
    parts = []
    for block in range(check_blocks):
        pick = (keep & (indices % check_blocks == block))[:, None, None]
        parts.append(jnp.prod(jnp.where(pick, piece, 1.0), axis=0))
    return jnp.stack(parts), piece


def others_scatter(row_piece, grads, check_blocks):
    own = lax.axis_index("var")
    grad_piece = lax.all_gather(grads, "var", axis=0, tiled=True)
    indices = jnp.arange(row_piece.shape[0], dtype=jnp.int32)
    keep = indices // check_blocks != own
    new_sums = []
    for block in range(check_blocks):
        pick = (keep & (indices % check_blocks == block))[:, None, None]
        factors = jnp.where(pick, row_piece, 1.0)
        weights = jnp.where(pick, grad_piece, 0.0)
        before, after, whole = exclusive_both(factors, 0)
        new_sums.append(jnp.sum(weights * before * after, axis=0))
    return jnp.stack(new_sums)


def body(n_chk, n_var, tile_bits, tile_pos, tile_count, edge_weight, syndrome, channel_prior, out_cot):
    slot_total = tile_bits.shape[2]
    shots = syndrome.shape[1]
    check_blocks = syndrome.shape[0] // TILE
    column_blocks = channel_prior.shape[0] // TILE
    edge, row_hot, col_hot, same_row = device_tables(
        tile_bits[0, 0], tile_pos[0, 0], tile_count[0, 0], check_blocks, column_blocks
    )
    weight = edge_weight[0, 0].reshape(slot_total, TILE, TILE)
    edge_t = jnp.swapaxes(edge, 1, 2)
    dense = (slot_total, TILE, TILE, shots)
    em = jnp.broadcast_to(edge_t[..., None], dense)
    ew = jnp.broadcast_to((edge_t * jnp.swapaxes(weight, 1, 2))[..., None], dense)
    sign_dev = (1.0 - 2.0 * syndrome.astype(jnp.float32)).reshape(check_blocks, TILE, shots)
    sign_slot = jnp.einsum("kc,crs->krs", row_hot, sign_dev, precision=EXACT)
    prior_dev = channel_prior.reshape(column_blocks, TILE)
    prior_slot = jnp.einsum("kv,vc->kc", col_hot, prior_dev, precision=EXACT)
    spread = jnp.broadcast_to(prior_slot[:, :, None], (slot_total, TILE, shots))
    u = None
    saved = []
    total = None
    for step in range(ITERS):
        ba, whole = fwd_products(spread, u, em)
        rows, others_here = combine(whole, row_hot, same_row)
        others, piece = others_forward(rows, check_blocks, n_var)
        others_slot = jnp.einsum("kc,crs->krs", row_hot, others, precision=EXACT)
        factor = sign_slot * others_here * others_slot
        saved.append((spread, u, ba, whole, factor, others_here, others_slot, piece))
        u, colsum = fwd_messages(ba, factor, ew)
        column = jnp.einsum("kv,kcs->vcs", col_hot, colsum, precision=EXACT)
        total = prior_dev[:, :, None] + checks_total(column, n_chk)
        spread = jnp.einsum("kv,vcs->kcs", col_hot, total, precision=EXACT)
    marginals = total.reshape(column_blocks * TILE, shots)

    grad_total = out_cot.reshape(column_blocks, TILE, shots)
    prior_grad = jnp.zeros((column_blocks, TILE), jnp.float32)
    grad_m = None
    acc = None
    for step in reversed(range(ITERS)):
        spread_t, u_prev, ba, whole, factor, others_here, others_slot, piece = saved[step]
        prior_grad = prior_grad + jnp.sum(grad_total, axis=2)
        grad_spread = jnp.einsum("kv,vcs->kcs", col_hot, grad_total, precision=EXACT)
        acc, grad_ba, grad_factor = bwd_messages(grad_spread, grad_m, ba, factor, ew, acc)
        grad_here = grad_factor * sign_slot * others_slot
        grad_slot = grad_factor * sign_slot * others_here
        grad_others = jnp.einsum("kc,krs->crs", row_hot, grad_slot, precision=EXACT)
        grad_rows = others_backward(piece, grad_others, check_blocks, n_var)
        unused, pull = jax.vjp(lambda w: combine(w, row_hot, same_row), whole)
        grad_whole = pull((grad_rows, grad_here))[0]
        grad_m, colsum = bwd_products(spread_t, u_prev, em, grad_ba, grad_whole, step > 0)
        grad_total = checks_total(
            jnp.einsum("kv,kcs->vcs", col_hot, colsum, precision=EXACT), n_chk
        )
    prior_grad = prior_grad + jnp.sum(grad_total, axis=2)
    weight_grad = edge * jnp.swapaxes(jnp.sum(acc, axis=3), 1, 2)
    return (
        marginals,
        weight_grad.reshape(1, 1, slot_total, TILE * TILE),
        prior_grad.reshape(column_blocks * TILE),
    )


def solution(mesh):
    placed = (
        P("chk", "var", None, None),
        P("chk", "var", None, None),
        P("chk", "var"),
        P("chk", "var", None, None),
        P("chk", None),
        P("var"),
        P("var", None),
    )
    return jax.shard_map(
        functools.partial(body, mesh.shape["chk"], mesh.shape["var"]),
        mesh=mesh,
        in_specs=placed,
        out_specs=(P("var", None), P("chk", "var", None, None), P("var")),
        check_vma=False,
    )
```

```python
import functools

import jax
import jax.numpy as jnp
from jax import lax
from jax.experimental import pallas as pl
from jax.sharding import PartitionSpec as P

TILE = 64
ITERS = 2


DAMP = 0.97
EXACT = lax.Precision.HIGHEST
F32 = jnp.float32
UNROLL = 4


def linear_both(values, axis):
    length = values.shape[axis]
    pieces = [lax.slice_in_dim(values, index, index + 1, axis=axis) for index in range(length)]
    ones = jnp.ones_like(pieces[0])
    prefix = [ones]
    for index in range(length - 1):
        prefix.append(prefix[-1] * pieces[index])
    suffix = [ones]
    for index in range(length - 1, 0, -1):
        suffix.append(suffix[-1] * pieces[index])
    suffix = suffix[::-1]
    whole = prefix[-1] * pieces[-1]
    return (jnp.concatenate(prefix, axis=axis), jnp.concatenate(suffix, axis=axis), whole)


def exclusive_both(values, axis):
    length = values.shape[axis]
    if length < 16 or length % 8 != 0:
        return linear_both(values, axis)
    shape = values.shape
    split = values.reshape(shape[:axis] + (length // 8, 8) + shape[axis + 1 :])
    inner_before, inner_after, group_whole = linear_both(split, axis + 1)
    outer_before, outer_after, whole = exclusive_both(group_whole, axis)
    before = (inner_before * outer_before).reshape(shape)
    after = (inner_after * outer_after).reshape(shape)
    whole = whole.reshape(shape[:axis] + (1,) + shape[axis + 1 :])
    return (before, after, whole)


def device_tables(bits, positions, count, check_blocks, column_blocks):
    slot_total = bits.shape[0]
    slots = jnp.arange(slot_total, dtype=jnp.int32)
    live = slots < count
    edge = jnp.where(live[:, None], bits, 0).astype(jnp.float32).reshape(slot_total, TILE, TILE)
    row_hot = (positions[:, 0:1] == jnp.arange(check_blocks, dtype=jnp.int32)[None, :]).astype(
        jnp.float32
    )
    col_hot = (positions[:, 1:2] == jnp.arange(column_blocks, dtype=jnp.int32)[None, :]).astype(
        jnp.float32
    )
    same_row = (positions[:, None, 0] == positions[None, :, 0]) & (slots[:, None] != slots[None, :])
    return (edge, row_hot, col_hot, same_row)


def _spread_row(ref, c, shape):
    return jnp.broadcast_to(ref[0, pl.ds(c, 1), :], shape)


def _fwd_products_kernel(has_u, *refs):
    if has_u:
        spread_ref, u_ref, em_ref, ba_ref, whole_ref, h_scr = refs
    else:
        spread_ref, em_ref, ba_ref, whole_ref, h_scr = refs
    n_c = em_ref.shape[1]
    shape = em_ref.shape[2:]

    def forward(c, carry):
        m = _spread_row(spread_ref, c, shape)
        if has_u:
            m = m - u_ref[0, c]
        h = jnp.where(em_ref[0, c] > 0, jnp.tanh(0.5 * m), 1.0)
        h_scr[c] = h
        ba_ref[0, c] = carry
        return carry * h

    whole = lax.fori_loop(0, n_c, forward, jnp.ones(shape, F32), unroll=UNROLL)
    whole_ref[0] = whole

    def backward(i, carry):
        c = n_c - 1 - i
        ba_ref[0, c] = ba_ref[0, c] * carry
        return carry * h_scr[c]

    lax.fori_loop(0, n_c, backward, jnp.ones(shape, F32), unroll=UNROLL)


def _fwd_messages_kernel(ba_ref, f_ref, ew_ref, u_ref, col_ref):
    first = pl.program_id(1) == 0
    n_c = ba_ref.shape[1]
    f = f_ref[0]

    def body(c, carry):
        x = ba_ref[0, c] * f
        u = ew_ref[0, c] * jnp.log((1.0 + DAMP * x) / (1.0 - DAMP * x))
        u_ref[0, c] = u
        row = jnp.sum(u, axis=0, keepdims=True)
        col_ref[0, pl.ds(c, 1), :] = jnp.where(first, row, col_ref[0, pl.ds(c, 1), :] + row)
        return carry

    lax.fori_loop(0, n_c, body, 0, unroll=UNROLL)


def _bwd_messages_kernel(has_next, has_acc, *refs):
    refs = list(refs)
    gsp_ref = refs.pop(0)
    gm_ref = refs.pop(0) if has_next else None
    ba_ref, f_ref, ew_ref = refs[:3]
    refs = refs[3:]
    acc_ref = refs.pop(0) if has_acc else None
    gw_ref, gba_ref, d1_ref = refs
    n_c = ba_ref.shape[1]
    shape = ba_ref.shape[2:]
    f = f_ref[0]

    def body(c, total):
        gu = _spread_row(gsp_ref, c, shape)
        if has_next:
            gu = gu - gm_ref[0, c]
        ba = ba_ref[0, c]
        x = ba * f
        low = 1.0 - DAMP * x
        high = 1.0 + DAMP * x
        gw = gu * jnp.log(high / low)
        if has_acc:
            gw = gw + acc_ref[0, c]
        gw_ref[0, c] = gw
        gx = gu * ew_ref[0, c] * ((2.0 * DAMP) / (low * high))
        gba_ref[0, c] = gx * f
        return total + gx * ba

    d1_ref[0] = lax.fori_loop(0, n_c, body, jnp.zeros(shape, F32), unroll=UNROLL)


def _bwd_products_kernel(has_u, emit_gm, *refs):
    refs = list(refs)
    spread_ref = refs.pop(0)
    u_ref = refs.pop(0) if has_u else None
    em_ref, gba_ref, gwh_ref = refs[:3]
    refs = refs[3:]
    gm_ref = refs.pop(0) if emit_gm else None
    col_ref, h_scr, p_scr, q_scr = refs
    first = pl.program_id(1) == 0
    n_c = em_ref.shape[1]
    shape = em_ref.shape[2:]
    gwh = gwh_ref[0]

    def forward(c, carry):
        prod, grad = carry
        m = _spread_row(spread_ref, c, shape)
        if has_u:
            m = m - u_ref[0, c]
        h = jnp.where(em_ref[0, c] > 0, jnp.tanh(0.5 * m), 1.0)
        h_scr[c] = h
        p_scr[c] = prod
        q_scr[c] = grad
        return (prod * h, grad * h + gba_ref[0, c] * prod)

    ones = jnp.ones(shape, F32)
    zeros = jnp.zeros(shape, F32)
    lax.fori_loop(0, n_c, forward, (ones, zeros), unroll=UNROLL)

    def backward(i, carry):
        prod, grad = carry
        c = n_c - 1 - i
        h = h_scr[c]
        before = p_scr[c]
        gh = q_scr[c] * prod + before * (grad + gwh * prod)
        gm = jnp.where(em_ref[0, c] > 0, gh * (0.5 * (1.0 - h * h)), 0.0)
        if emit_gm:
            gm_ref[0, c] = gm
        row = jnp.sum(gm, axis=0, keepdims=True)
        col_ref[0, pl.ds(c, 1), :] = jnp.where(first, row, col_ref[0, pl.ds(c, 1), :] + row)
        return (prod * h, grad * h + gba_ref[0, c] * prod)

    lax.fori_loop(0, n_c, backward, (ones, zeros), unroll=UNROLL)


ROW_BLOCK = 32


def _spec(kind, shape):
    if kind == "dense":
        return pl.BlockSpec((1, shape[1], ROW_BLOCK, shape[3]), lambda k, j: (k, 0, j, 0))
    if kind == "rows":
        return pl.BlockSpec((1, ROW_BLOCK, shape[2]), lambda k, j: (k, j, 0))
    return pl.BlockSpec((1,) + tuple(shape[1:]), lambda k, j: (k, 0, 0))


def _call(kernel, inputs, outputs, scratch=()):
    in_specs = [_spec(kind, a.shape) for kind, a in inputs]
    out_specs = [_spec(kind, o.shape) for kind, o in outputs]
    dense = [a for kind, a in inputs if kind == "dense"][0]
    return pl.pallas_call(
        kernel,
        grid=(dense.shape[0], dense.shape[2] // ROW_BLOCK),
        in_specs=in_specs,
        out_specs=out_specs,
        out_shape=[o for kind, o in outputs],
        scratch_shapes=list(scratch),
    )(*[a for kind, a in inputs])


def fwd_products(spread, u, em):
    k, c, r, s = em.shape
    has_u = u is not None
    inputs = [("cols", spread)] + ([("dense", u)] if has_u else []) + [("dense", em)]
    outs = [("dense", jax.ShapeDtypeStruct(em.shape, F32)), ("rows", jax.ShapeDtypeStruct((k, r, s), F32))]
    from jax.experimental.pallas import tpu as pltpu

    return _call(
        functools.partial(_fwd_products_kernel, has_u),
        inputs,
        outs,
        [pltpu.VMEM((c, ROW_BLOCK, s), F32)],
    )


def fwd_messages(ba, f, ew):
    k, c, r, s = ba.shape
    outs = [("dense", jax.ShapeDtypeStruct(ba.shape, F32)), ("cols", jax.ShapeDtypeStruct((k, c, s), F32))]
    return _call(_fwd_messages_kernel, [("dense", ba), ("rows", f), ("dense", ew)], outs)


def bwd_messages(gsp, gm, ba, f, ew, acc):
    k, c, r, s = ba.shape
    has_next = gm is not None
    has_acc = acc is not None
    inputs = (
        [("cols", gsp)]
        + ([("dense", gm)] if has_next else [])
        + [("dense", ba), ("rows", f), ("dense", ew)]
        + ([("dense", acc)] if has_acc else [])
    )
    outs = [
        ("dense", jax.ShapeDtypeStruct(ba.shape, F32)),
        ("dense", jax.ShapeDtypeStruct(ba.shape, F32)),
        ("rows", jax.ShapeDtypeStruct((k, r, s), F32)),
    ]
    return _call(functools.partial(_bwd_messages_kernel, has_next, has_acc), inputs, outs)


def bwd_products(spread, u, em, gba, gwh, emit_gm):
    from jax.experimental.pallas import tpu as pltpu

    k, c, r, s = em.shape
    has_u = u is not None
    inputs = [("cols", spread)] + ([("dense", u)] if has_u else []) + [
        ("dense", em),
        ("dense", gba),
        ("rows", gwh),
    ]
    outs = ([("dense", jax.ShapeDtypeStruct(em.shape, F32))] if emit_gm else []) + [
        ("cols", jax.ShapeDtypeStruct((k, c, s), F32))
    ]
    results = _call(
        functools.partial(_bwd_products_kernel, has_u, emit_gm),
        inputs,
        outs,
        [pltpu.VMEM((c, ROW_BLOCK, s), F32) for _ in range(3)],
    )
    if emit_gm:
        return results[0], results[1]
    return None, results[0]


def combine(whole, row_hot, same_row):
    slots = whole.shape[0]
    blocks = row_hot.shape[1]
    ones = jnp.ones_like(whole[0])
    rows = []
    for block in range(blocks):
        value = ones
        for k in range(slots):
            value = value * jnp.where(row_hot[k, block] > 0, whole[k], 1.0)
        rows.append(value)
    others_here = []
    for k in range(slots):
        value = ones
        for other in range(slots):
            if other != k:
                value = value * jnp.where(same_row[k, other], whole[other], 1.0)
        others_here.append(value)
    return jnp.stack(rows), jnp.stack(others_here)


def _power_of_two(n):
    return n > 1 and (n & (n - 1)) == 0


def _swap(value, axis, n, step):
    perm = [(j, j ^ (1 << step)) for j in range(n)]
    return lax.ppermute(value, axis, perm)


def checks_total(values, n):
    if not _power_of_two(n):
        return lax.psum(values, "chk")
    step = 0
    while (1 << step) < n:
        values = values + _swap(values, "chk", n, step)
        step += 1
    return values


def others_forward(rows, check_blocks, n):
    if not _power_of_two(n):
        return others_gather(rows, check_blocks)
    full = rows
    excl = jnp.ones_like(rows)
    trail = []
    step = 0
    while (1 << step) < n:
        other = _swap(full, "var", n, step)
        trail.append((full, excl, other))
        excl = excl * other
        full = full * other
        step += 1
    return excl, trail


def others_backward(trail, grads, check_blocks, n):
    if not _power_of_two(n):
        return others_scatter(trail, grads, check_blocks)
    spread = grads
    target = jnp.zeros_like(grads)
    for step, (full, excl, other) in enumerate(trail):
        other_spread = _swap(spread, "var", n, step)
        target = target * other + excl * other_spread
        spread = spread * other + other_spread * full
    return target


def others_gather(rows, check_blocks):
    own = lax.axis_index("var")
    piece = lax.all_gather(rows, "var", axis=0, tiled=True)
    indices = jnp.arange(piece.shape[0], dtype=jnp.int32)
    keep = indices // check_blocks != own
    parts = []
    for block in range(check_blocks):
        pick = (keep & (indices % check_blocks == block))[:, None, None]
        parts.append(jnp.prod(jnp.where(pick, piece, 1.0), axis=0))
    return jnp.stack(parts), piece


def others_scatter(row_piece, grads, check_blocks):
    own = lax.axis_index("var")
    grad_piece = lax.all_gather(grads, "var", axis=0, tiled=True)
    indices = jnp.arange(row_piece.shape[0], dtype=jnp.int32)
    keep = indices // check_blocks != own
    new_sums = []
    for block in range(check_blocks):
        pick = (keep & (indices % check_blocks == block))[:, None, None]
        factors = jnp.where(pick, row_piece, 1.0)
        weights = jnp.where(pick, grad_piece, 0.0)
        before, after, whole = exclusive_both(factors, 0)
        new_sums.append(jnp.sum(weights * before * after, axis=0))
    return jnp.stack(new_sums)


def body(n_chk, n_var, tile_bits, tile_pos, tile_count, edge_weight, syndrome, channel_prior, out_cot):
    slot_total = tile_bits.shape[2]
    shots = syndrome.shape[1]
    check_blocks = syndrome.shape[0] // TILE
    column_blocks = channel_prior.shape[0] // TILE
    edge, row_hot, col_hot, same_row = device_tables(
        tile_bits[0, 0], tile_pos[0, 0], tile_count[0, 0], check_blocks, column_blocks
    )
    weight = edge_weight[0, 0].reshape(slot_total, TILE, TILE)
    edge_t = jnp.swapaxes(edge, 1, 2)
    dense = (slot_total, TILE, TILE, shots)
    ew = jnp.broadcast_to((edge_t * jnp.swapaxes(weight, 1, 2))[..., None], dense)
    em = ew
    sign_dev = (1.0 - 2.0 * syndrome.astype(jnp.float32)).reshape(check_blocks, TILE, shots)
    sign_slot = jnp.einsum("kc,crs->krs", row_hot, sign_dev, precision=EXACT)
    prior_dev = channel_prior.reshape(column_blocks, TILE)
    prior_slot = jnp.einsum("kv,vc->kc", col_hot, prior_dev, precision=EXACT)
    spread = jnp.broadcast_to(prior_slot[:, :, None], (slot_total, TILE, shots))
    u = None
    saved = []
    total = None
    for step in range(ITERS):
        ba, whole = fwd_products(spread, u, em)
        rows, others_here = combine(whole, row_hot, same_row)
        others, piece = others_forward(rows, check_blocks, n_var)
        others_slot = jnp.einsum("kc,crs->krs", row_hot, others, precision=EXACT)
        factor = sign_slot * others_here * others_slot
        saved.append((spread, u, ba, whole, factor, others_here, others_slot, piece))
        u, colsum = fwd_messages(ba, factor, ew)
        column = jnp.einsum("kv,kcs->vcs", col_hot, colsum, precision=EXACT)
        total = prior_dev[:, :, None] + checks_total(column, n_chk)
        spread = jnp.einsum("kv,vcs->kcs", col_hot, total, precision=EXACT)
    marginals = total.reshape(column_blocks * TILE, shots)

    grad_total = out_cot.reshape(column_blocks, TILE, shots)
    prior_grad = jnp.zeros((column_blocks, TILE), jnp.float32)
    grad_m = None
    acc = None
    for step in reversed(range(ITERS)):
        spread_t, u_prev, ba, whole, factor, others_here, others_slot, piece = saved[step]
        prior_grad = prior_grad + jnp.sum(grad_total, axis=2)
        grad_spread = jnp.einsum("kv,vcs->kcs", col_hot, grad_total, precision=EXACT)
        acc, grad_ba, grad_factor = bwd_messages(grad_spread, grad_m, ba, factor, ew, acc)
        grad_here = grad_factor * sign_slot * others_slot
        grad_slot = grad_factor * sign_slot * others_here
        grad_others = jnp.einsum("kc,krs->crs", row_hot, grad_slot, precision=EXACT)
        grad_rows = others_backward(piece, grad_others, check_blocks, n_var)
        unused, pull = jax.vjp(lambda w: combine(w, row_hot, same_row), whole)
        grad_whole = pull((grad_rows, grad_here))[0]
        grad_m, colsum = bwd_products(spread_t, u_prev, em, grad_ba, grad_whole, step > 0)
        grad_total = checks_total(
            jnp.einsum("kv,kcs->vcs", col_hot, colsum, precision=EXACT), n_chk
        )
    prior_grad = prior_grad + jnp.sum(grad_total, axis=2)
    weight_grad = edge * jnp.swapaxes(jnp.sum(acc, axis=3), 1, 2)
    return (
        marginals,
        weight_grad.reshape(1, 1, slot_total, TILE * TILE),
        prior_grad.reshape(column_blocks * TILE),
    )


def solution(mesh):
    placed = (
        P("chk", "var", None, None),
        P("chk", "var", None, None),
        P("chk", "var"),
        P("chk", "var", None, None),
        P("chk", None),
        P("var"),
        P("var", None),
    )
    return jax.shard_map(
        functools.partial(body, mesh.shape["chk"], mesh.shape["var"]),
        mesh=mesh,
        in_specs=placed,
        out_specs=(P("var", None), P("chk", "var", None, None), P("var")),
        check_vma=False,
    )
```

```python
import functools

import jax
import jax.numpy as jnp
from jax import lax
from jax.experimental import pallas as pl
from jax.sharding import PartitionSpec as P

TILE = 64
ITERS = 2


DAMP = 0.97
EXACT = lax.Precision.HIGHEST
F32 = jnp.float32
UNROLL = 8


def linear_both(values, axis):
    length = values.shape[axis]
    pieces = [lax.slice_in_dim(values, index, index + 1, axis=axis) for index in range(length)]
    ones = jnp.ones_like(pieces[0])
    prefix = [ones]
    for index in range(length - 1):
        prefix.append(prefix[-1] * pieces[index])
    suffix = [ones]
    for index in range(length - 1, 0, -1):
        suffix.append(suffix[-1] * pieces[index])
    suffix = suffix[::-1]
    whole = prefix[-1] * pieces[-1]
    return (jnp.concatenate(prefix, axis=axis), jnp.concatenate(suffix, axis=axis), whole)


def exclusive_both(values, axis):
    length = values.shape[axis]
    if length < 16 or length % 8 != 0:
        return linear_both(values, axis)
    shape = values.shape
    split = values.reshape(shape[:axis] + (length // 8, 8) + shape[axis + 1 :])
    inner_before, inner_after, group_whole = linear_both(split, axis + 1)
    outer_before, outer_after, whole = exclusive_both(group_whole, axis)
    before = (inner_before * outer_before).reshape(shape)
    after = (inner_after * outer_after).reshape(shape)
    whole = whole.reshape(shape[:axis] + (1,) + shape[axis + 1 :])
    return (before, after, whole)


def device_tables(bits, positions, count, check_blocks, column_blocks):
    slot_total = bits.shape[0]
    slots = jnp.arange(slot_total, dtype=jnp.int32)
    live = slots < count
    edge = jnp.where(live[:, None], bits, 0).astype(jnp.float32).reshape(slot_total, TILE, TILE)
    row_hot = (positions[:, 0:1] == jnp.arange(check_blocks, dtype=jnp.int32)[None, :]).astype(
        jnp.float32
    )
    col_hot = (positions[:, 1:2] == jnp.arange(column_blocks, dtype=jnp.int32)[None, :]).astype(
        jnp.float32
    )
    same_row = (positions[:, None, 0] == positions[None, :, 0]) & (slots[:, None] != slots[None, :])
    return (edge, row_hot, col_hot, same_row)


def _spread_row(ref, c, shape):
    return jnp.broadcast_to(ref[0, pl.ds(c, 1), :], shape)


def _fwd_products_kernel(has_u, *refs):
    if has_u:
        spread_ref, u_ref, em_ref, ba_ref, whole_ref, h_scr = refs
    else:
        spread_ref, em_ref, ba_ref, whole_ref, h_scr = refs
    n_c = em_ref.shape[1]
    shape = em_ref.shape[2:]

    def forward(c, carry):
        m = _spread_row(spread_ref, c, shape)
        if has_u:
            m = m - u_ref[0, c]
        h = jnp.where(em_ref[0, c] > 0, jnp.tanh(0.5 * m), 1.0)
        h_scr[c] = h
        ba_ref[0, c] = carry
        return carry * h

    whole = lax.fori_loop(0, n_c, forward, jnp.ones(shape, F32), unroll=UNROLL)
    whole_ref[0] = whole

    def backward(i, carry):
        c = n_c - 1 - i
        ba_ref[0, c] = ba_ref[0, c] * carry
        return carry * h_scr[c]

    lax.fori_loop(0, n_c, backward, jnp.ones(shape, F32), unroll=UNROLL)


def _fwd_messages_kernel(ba_ref, f_ref, ew_ref, u_ref, col_ref):
    first = pl.program_id(1) == 0
    n_c = ba_ref.shape[1]
    f = f_ref[0]

    def body(c, carry):
        x = ba_ref[0, c] * f
        u = ew_ref[0, c] * jnp.log((1.0 + DAMP * x) / (1.0 - DAMP * x))
        u_ref[0, c] = u
        row = jnp.sum(u, axis=0, keepdims=True)
        col_ref[0, pl.ds(c, 1), :] = jnp.where(first, row, col_ref[0, pl.ds(c, 1), :] + row)
        return carry

    lax.fori_loop(0, n_c, body, 0, unroll=UNROLL)


def _bwd_messages_kernel(has_next, has_acc, *refs):
    refs = list(refs)
    gsp_ref = refs.pop(0)
    gm_ref = refs.pop(0) if has_next else None
    ba_ref, f_ref, ew_ref = refs[:3]
    refs = refs[3:]
    acc_ref = refs.pop(0) if has_acc else None
    gw_ref, gba_ref, d1_ref = refs
    n_c = ba_ref.shape[1]
    shape = ba_ref.shape[2:]
    f = f_ref[0]

    def body(c, total):
        gu = _spread_row(gsp_ref, c, shape)
        if has_next:
            gu = gu - gm_ref[0, c]
        ba = ba_ref[0, c]
        x = ba * f
        low = 1.0 - DAMP * x
        high = 1.0 + DAMP * x
        gw = gu * jnp.log(high / low)
        if has_acc:
            gw = gw + acc_ref[0, c]
        gw_ref[0, c] = gw
        gx = gu * ew_ref[0, c] * ((2.0 * DAMP) / (low * high))
        gba_ref[0, c] = gx * f
        return total + gx * ba

    d1_ref[0] = lax.fori_loop(0, n_c, body, jnp.zeros(shape, F32), unroll=UNROLL)


def _bwd_products_kernel(has_u, emit_gm, *refs):
    refs = list(refs)
    spread_ref = refs.pop(0)
    u_ref = refs.pop(0) if has_u else None
    em_ref, gba_ref, gwh_ref = refs[:3]
    refs = refs[3:]
    gm_ref = refs.pop(0) if emit_gm else None
    col_ref, h_scr, p_scr, q_scr = refs
    first = pl.program_id(1) == 0
    n_c = em_ref.shape[1]
    shape = em_ref.shape[2:]
    gwh = gwh_ref[0]

    def forward(c, carry):
        prod, grad = carry
        m = _spread_row(spread_ref, c, shape)
        if has_u:
            m = m - u_ref[0, c]
        h = jnp.where(em_ref[0, c] > 0, jnp.tanh(0.5 * m), 1.0)
        h_scr[c] = h
        p_scr[c] = prod
        q_scr[c] = grad
        return (prod * h, grad * h + gba_ref[0, c] * prod)

    ones = jnp.ones(shape, F32)
    zeros = jnp.zeros(shape, F32)
    lax.fori_loop(0, n_c, forward, (ones, zeros), unroll=UNROLL)

    def backward(i, carry):
        prod, grad = carry
        c = n_c - 1 - i
        h = h_scr[c]
        before = p_scr[c]
        gh = q_scr[c] * prod + before * (grad + gwh * prod)
        gm = jnp.where(em_ref[0, c] > 0, gh * (0.5 * (1.0 - h * h)), 0.0)
        if emit_gm:
            gm_ref[0, c] = gm
        row = jnp.sum(gm, axis=0, keepdims=True)
        col_ref[0, pl.ds(c, 1), :] = jnp.where(first, row, col_ref[0, pl.ds(c, 1), :] + row)
        return (prod * h, grad * h + gba_ref[0, c] * prod)

    lax.fori_loop(0, n_c, backward, (ones, zeros), unroll=UNROLL)


ROW_BLOCK = 64


def _spec(kind, shape):
    if kind == "dense":
        return pl.BlockSpec((1, shape[1], ROW_BLOCK, shape[3]), lambda k, j: (k, 0, j, 0))
    if kind == "rows":
        return pl.BlockSpec((1, ROW_BLOCK, shape[2]), lambda k, j: (k, j, 0))
    return pl.BlockSpec((1,) + tuple(shape[1:]), lambda k, j: (k, 0, 0))


def _call(kernel, inputs, outputs, scratch=()):
    in_specs = [_spec(kind, a.shape) for kind, a in inputs]
    out_specs = [_spec(kind, o.shape) for kind, o in outputs]
    dense = [a for kind, a in inputs if kind == "dense"][0]
    return pl.pallas_call(
        kernel,
        grid=(dense.shape[0], dense.shape[2] // ROW_BLOCK),
        in_specs=in_specs,
        out_specs=out_specs,
        out_shape=[o for kind, o in outputs],
        scratch_shapes=list(scratch),
    )(*[a for kind, a in inputs])


def fwd_products(spread, u, em):
    k, c, r, s = em.shape
    has_u = u is not None
    inputs = [("cols", spread)] + ([("dense", u)] if has_u else []) + [("dense", em)]
    outs = [("dense", jax.ShapeDtypeStruct(em.shape, F32)), ("rows", jax.ShapeDtypeStruct((k, r, s), F32))]
    from jax.experimental.pallas import tpu as pltpu

    return _call(
        functools.partial(_fwd_products_kernel, has_u),
        inputs,
        outs,
        [pltpu.VMEM((c, ROW_BLOCK, s), F32)],
    )


def fwd_messages(ba, f, ew):
    k, c, r, s = ba.shape
    outs = [("dense", jax.ShapeDtypeStruct(ba.shape, F32)), ("cols", jax.ShapeDtypeStruct((k, c, s), F32))]
    return _call(_fwd_messages_kernel, [("dense", ba), ("rows", f), ("dense", ew)], outs)


def bwd_messages(gsp, gm, ba, f, ew, acc):
    k, c, r, s = ba.shape
    has_next = gm is not None
    has_acc = acc is not None
    inputs = (
        [("cols", gsp)]
        + ([("dense", gm)] if has_next else [])
        + [("dense", ba), ("rows", f), ("dense", ew)]
        + ([("dense", acc)] if has_acc else [])
    )
    outs = [
        ("dense", jax.ShapeDtypeStruct(ba.shape, F32)),
        ("dense", jax.ShapeDtypeStruct(ba.shape, F32)),
        ("rows", jax.ShapeDtypeStruct((k, r, s), F32)),
    ]
    return _call(functools.partial(_bwd_messages_kernel, has_next, has_acc), inputs, outs)


def bwd_products(spread, u, em, gba, gwh, emit_gm):
    from jax.experimental.pallas import tpu as pltpu

    k, c, r, s = em.shape
    has_u = u is not None
    inputs = [("cols", spread)] + ([("dense", u)] if has_u else []) + [
        ("dense", em),
        ("dense", gba),
        ("rows", gwh),
    ]
    outs = ([("dense", jax.ShapeDtypeStruct(em.shape, F32))] if emit_gm else []) + [
        ("cols", jax.ShapeDtypeStruct((k, c, s), F32))
    ]
    results = _call(
        functools.partial(_bwd_products_kernel, has_u, emit_gm),
        inputs,
        outs,
        [pltpu.VMEM((c, ROW_BLOCK, s), F32) for _ in range(3)],
    )
    if emit_gm:
        return results[0], results[1]
    return None, results[0]


def pick(hot, values):
    parts = []
    for k in range(hot.shape[0]):
        value = jnp.zeros_like(values[0])
        for j in range(hot.shape[1]):
            value = value + jnp.where(hot[k, j] > 0, values[j], 0.0)
        parts.append(value)
    return jnp.stack(parts)


def place(hot, values):
    parts = []
    for j in range(hot.shape[1]):
        value = jnp.zeros_like(values[0])
        for k in range(hot.shape[0]):
            value = value + jnp.where(hot[k, j] > 0, values[k], 0.0)
        parts.append(value)
    return jnp.stack(parts)


def combine(whole, row_hot, same_row):
    slots = whole.shape[0]
    blocks = row_hot.shape[1]
    ones = jnp.ones_like(whole[0])
    rows = []
    for block in range(blocks):
        value = ones
        for k in range(slots):
            value = value * jnp.where(row_hot[k, block] > 0, whole[k], 1.0)
        rows.append(value)
    others_here = []
    for k in range(slots):
        value = ones
        for other in range(slots):
            if other != k:
                value = value * jnp.where(same_row[k, other], whole[other], 1.0)
        others_here.append(value)
    return jnp.stack(rows), jnp.stack(others_here)


def _power_of_two(n):
    return n > 1 and (n & (n - 1)) == 0


def _swap(value, axis, n, step):
    perm = [(j, j ^ (1 << step)) for j in range(n)]
    return lax.ppermute(value, axis, perm)


def checks_total(values, n):
    if not _power_of_two(n):
        return lax.psum(values, "chk")
    step = 0
    while (1 << step) < n:
        values = values + _swap(values, "chk", n, step)
        step += 1
    return values


def others_forward(rows, check_blocks, n):
    if not _power_of_two(n):
        return others_gather(rows, check_blocks)
    full = rows
    excl = jnp.ones_like(rows)
    trail = []
    step = 0
    while (1 << step) < n:
        other = _swap(full, "var", n, step)
        trail.append((full, excl, other))
        excl = excl * other
        full = full * other
        step += 1
    return excl, trail


def others_backward(trail, grads, check_blocks, n):
    if not _power_of_two(n):
        return others_scatter(trail, grads, check_blocks)
    spread = grads
    target = jnp.zeros_like(grads)
    for step, (full, excl, other) in enumerate(trail):
        other_spread = _swap(spread, "var", n, step)
        target = target * other + excl * other_spread
        spread = spread * other + other_spread * full
    return target


def others_gather(rows, check_blocks):
    own = lax.axis_index("var")
    piece = lax.all_gather(rows, "var", axis=0, tiled=True)
    indices = jnp.arange(piece.shape[0], dtype=jnp.int32)
    keep = indices // check_blocks != own
    parts = []
    for block in range(check_blocks):
        pick = (keep & (indices % check_blocks == block))[:, None, None]
        parts.append(jnp.prod(jnp.where(pick, piece, 1.0), axis=0))
    return jnp.stack(parts), piece


def others_scatter(row_piece, grads, check_blocks):
    own = lax.axis_index("var")
    grad_piece = lax.all_gather(grads, "var", axis=0, tiled=True)
    indices = jnp.arange(row_piece.shape[0], dtype=jnp.int32)
    keep = indices // check_blocks != own
    new_sums = []
    for block in range(check_blocks):
        pick = (keep & (indices % check_blocks == block))[:, None, None]
        factors = jnp.where(pick, row_piece, 1.0)
        weights = jnp.where(pick, grad_piece, 0.0)
        before, after, whole = exclusive_both(factors, 0)
        new_sums.append(jnp.sum(weights * before * after, axis=0))
    return jnp.stack(new_sums)


def body(n_chk, n_var, tile_bits, tile_pos, tile_count, edge_weight, syndrome, channel_prior, out_cot):
    slot_total = tile_bits.shape[2]
    shots = syndrome.shape[1]
    check_blocks = syndrome.shape[0] // TILE
    column_blocks = channel_prior.shape[0] // TILE
    edge, row_hot, col_hot, same_row = device_tables(
        tile_bits[0, 0], tile_pos[0, 0], tile_count[0, 0], check_blocks, column_blocks
    )
    weight = edge_weight[0, 0].reshape(slot_total, TILE, TILE)
    edge_t = jnp.swapaxes(edge, 1, 2)
    dense = (slot_total, TILE, TILE, shots)
    ew = jnp.broadcast_to((edge_t * jnp.swapaxes(weight, 1, 2))[..., None], dense)
    em = ew
    sign_dev = (1.0 - 2.0 * syndrome.astype(jnp.float32)).reshape(check_blocks, TILE, shots)
    sign_slot = jnp.einsum("kc,crs->krs", row_hot, sign_dev, precision=EXACT)
    prior_dev = channel_prior.reshape(column_blocks, TILE)
    prior_slot = jnp.einsum("kv,vc->kc", col_hot, prior_dev, precision=EXACT)
    spread = jnp.broadcast_to(prior_slot[:, :, None], (slot_total, TILE, shots))
    u = None
    saved = []
    total = None
    for step in range(ITERS):
        ba, whole = fwd_products(spread, u, em)
        rows, others_here = combine(whole, row_hot, same_row)
        others, piece = others_forward(rows, check_blocks, n_var)
        others_slot = pick(row_hot, others)
        factor = sign_slot * others_here * others_slot
        saved.append((spread, u, ba, whole, factor, others_here, others_slot, piece))
        u, colsum = fwd_messages(ba, factor, ew)
        column = place(col_hot, colsum)
        total = prior_dev[:, :, None] + checks_total(column, n_chk)
        spread = pick(col_hot, total)
    marginals = total.reshape(column_blocks * TILE, shots)

    grad_total = out_cot.reshape(column_blocks, TILE, shots)
    prior_grad = jnp.zeros((column_blocks, TILE), jnp.float32)
    grad_m = None
    acc = None
    for step in reversed(range(ITERS)):
        spread_t, u_prev, ba, whole, factor, others_here, others_slot, piece = saved[step]
        prior_grad = prior_grad + jnp.sum(grad_total, axis=2)
        grad_spread = pick(col_hot, grad_total)
        acc, grad_ba, grad_factor = bwd_messages(grad_spread, grad_m, ba, factor, ew, acc)
        grad_here = grad_factor * sign_slot * others_slot
        grad_slot = grad_factor * sign_slot * others_here
        grad_others = place(row_hot, grad_slot)
        grad_rows = others_backward(piece, grad_others, check_blocks, n_var)
        unused, pull = jax.vjp(lambda w: combine(w, row_hot, same_row), whole)
        grad_whole = pull((grad_rows, grad_here))[0]
        grad_m, colsum = bwd_products(spread_t, u_prev, em, grad_ba, grad_whole, step > 0)
        grad_total = checks_total(
            place(col_hot, colsum), n_chk
        )
    prior_grad = prior_grad + jnp.sum(grad_total, axis=2)
    weight_grad = edge * jnp.swapaxes(jnp.sum(acc, axis=3), 1, 2)
    return (
        marginals,
        weight_grad.reshape(1, 1, slot_total, TILE * TILE),
        prior_grad.reshape(column_blocks * TILE),
    )


def solution(mesh):
    placed = (
        P("chk", "var", None, None),
        P("chk", "var", None, None),
        P("chk", "var"),
        P("chk", "var", None, None),
        P("chk", None),
        P("var"),
        P("var", None),
    )
    return jax.shard_map(
        functools.partial(body, mesh.shape["chk"], mesh.shape["var"]),
        mesh=mesh,
        in_specs=placed,
        out_specs=(P("var", None), P("chk", "var", None, None), P("var")),
        check_vma=False,
    )
```

```python
import functools

import jax
import jax.numpy as jnp
from jax import lax
from jax.experimental import pallas as pl
from jax.sharding import PartitionSpec as P

TILE = 64
ITERS = 2


DAMP = 0.97
EXACT = lax.Precision.HIGHEST
F32 = jnp.float32
UNROLL = 8


def linear_both(values, axis):
    length = values.shape[axis]
    pieces = [lax.slice_in_dim(values, index, index + 1, axis=axis) for index in range(length)]
    ones = jnp.ones_like(pieces[0])
    prefix = [ones]
    for index in range(length - 1):
        prefix.append(prefix[-1] * pieces[index])
    suffix = [ones]
    for index in range(length - 1, 0, -1):
        suffix.append(suffix[-1] * pieces[index])
    suffix = suffix[::-1]
    whole = prefix[-1] * pieces[-1]
    return (jnp.concatenate(prefix, axis=axis), jnp.concatenate(suffix, axis=axis), whole)


def exclusive_both(values, axis):
    length = values.shape[axis]
    if length < 16 or length % 8 != 0:
        return linear_both(values, axis)
    shape = values.shape
    split = values.reshape(shape[:axis] + (length // 8, 8) + shape[axis + 1 :])
    inner_before, inner_after, group_whole = linear_both(split, axis + 1)
    outer_before, outer_after, whole = exclusive_both(group_whole, axis)
    before = (inner_before * outer_before).reshape(shape)
    after = (inner_after * outer_after).reshape(shape)
    whole = whole.reshape(shape[:axis] + (1,) + shape[axis + 1 :])
    return (before, after, whole)


def device_tables(bits, positions, count, check_blocks, column_blocks):
    slot_total = bits.shape[0]
    slots = jnp.arange(slot_total, dtype=jnp.int32)
    live = slots < count
    edge = jnp.where(live[:, None], bits, 0).astype(jnp.float32).reshape(slot_total, TILE, TILE)
    row_hot = (positions[:, 0:1] == jnp.arange(check_blocks, dtype=jnp.int32)[None, :]).astype(
        jnp.float32
    )
    col_hot = (positions[:, 1:2] == jnp.arange(column_blocks, dtype=jnp.int32)[None, :]).astype(
        jnp.float32
    )
    same_row = (positions[:, None, 0] == positions[None, :, 0]) & (slots[:, None] != slots[None, :])
    return (edge, row_hot, col_hot, same_row)


def _spread_row(ref, c, shape):
    return jnp.broadcast_to(ref[0, pl.ds(c, 1), :], shape)


def _row_block(pos_ref, k):
    return pos_ref[2 * k]


def _col_block(pos_ref, k):
    return pos_ref[2 * k + 1]


def _fwd_products_kernel(has_u, slots, blocks, pos_ref, *refs):
    refs = list(refs)
    spread_ref = refs.pop(0)
    u_ref = refs.pop(0) if has_u else None
    ew_ref, ba_ref, whole_ref, rows_ref, here_ref, h_scr = refs
    k = pl.program_id(0)
    n_c = ew_ref.shape[1]
    shape = ew_ref.shape[2:]

    def forward(c, carry):
        m = _spread_row(spread_ref, c, shape)
        if has_u:
            m = m - u_ref[0, c]
        h = jnp.where(ew_ref[0, c] > 0, jnp.tanh(0.5 * m), 1.0)
        h_scr[c] = h
        ba_ref[0, c] = carry
        return carry * h

    whole = lax.fori_loop(0, n_c, forward, jnp.ones(shape, F32), unroll=UNROLL)
    whole_ref[k] = whole

    def backward(i, carry):
        c = n_c - 1 - i
        ba_ref[0, c] = ba_ref[0, c] * carry
        return carry * h_scr[c]

    lax.fori_loop(0, n_c, backward, jnp.ones(shape, F32), unroll=UNROLL)

    @pl.when(k == slots - 1)
    def _():
        wholes = [whole_ref[j] for j in range(slots)]
        rows_of = [_row_block(pos_ref, j) for j in range(slots)]
        for block in range(blocks):
            value = jnp.ones(shape, F32)
            for j in range(slots):
                value = value * jnp.where(rows_of[j] == block, wholes[j], 1.0)
            rows_ref[block] = value
        for j in range(slots):
            value = jnp.ones(shape, F32)
            for other in range(slots):
                if other != j:
                    value = value * jnp.where(rows_of[other] == rows_of[j], wholes[other], 1.0)
            here_ref[j] = value


def _fwd_messages_kernel(pos_ref, ba_ref, sign_ref, here_ref, others_ref, ew_ref, u_ref, col_ref):
    k = pl.program_id(0)
    n_c = ba_ref.shape[1]

    @pl.when(k == 0)
    def _():
        col_ref[...] = jnp.zeros(col_ref.shape, F32)

    f = sign_ref[k] * here_ref[k] * others_ref[_row_block(pos_ref, k)]
    q = _col_block(pos_ref, k)

    def body(c, carry):
        x = ba_ref[0, c] * f
        u = ew_ref[0, c] * jnp.log((1.0 + DAMP * x) / (1.0 - DAMP * x))
        u_ref[0, c] = u
        col_ref[q, pl.ds(c, 1), :] = col_ref[q, pl.ds(c, 1), :] + jnp.sum(u, axis=0, keepdims=True)
        return carry

    lax.fori_loop(0, n_c, body, 0, unroll=UNROLL)


def _bwd_messages_kernel(has_next, has_acc, pos_ref, *refs):
    refs = list(refs)
    gsp_ref = refs.pop(0)
    gm_ref = refs.pop(0) if has_next else None
    ba_ref, sign_ref, here_ref, others_ref, ew_ref = refs[:5]
    refs = refs[5:]
    acc_ref = refs.pop(0) if has_acc else None
    gw_ref, gba_ref, ghere_ref, gothers_ref = refs
    k = pl.program_id(0)
    n_c = ba_ref.shape[1]
    shape = ba_ref.shape[2:]

    @pl.when(k == 0)
    def _():
        gothers_ref[...] = jnp.zeros(gothers_ref.shape, F32)

    p = _row_block(pos_ref, k)
    sign = sign_ref[k]
    here = here_ref[k]
    others = others_ref[p]
    f = sign * here * others

    def body(c, total):
        gu = _spread_row(gsp_ref, c, shape)
        if has_next:
            gu = gu - gm_ref[0, c]
        ba = ba_ref[0, c]
        x = ba * f
        low = 1.0 - DAMP * x
        high = 1.0 + DAMP * x
        gw = gu * jnp.log(high / low)
        if has_acc:
            gw = gw + acc_ref[0, c]
        gw_ref[0, c] = gw
        gx = gu * ew_ref[0, c] * ((2.0 * DAMP) / (low * high))
        gba_ref[0, c] = gx * f
        return total + gx * ba

    grad_factor = lax.fori_loop(0, n_c, body, jnp.zeros(shape, F32), unroll=UNROLL)
    ghere_ref[k] = grad_factor * sign * others
    gothers_ref[p] = gothers_ref[p] + grad_factor * sign * here


def _bwd_products_kernel(has_u, emit_gm, slots, pos_ref, *refs):
    refs = list(refs)
    spread_ref = refs.pop(0)
    u_ref = refs.pop(0) if has_u else None
    ew_ref, gba_ref, grows_ref, ghere_ref, whole_ref, here_ref = refs[:6]
    refs = refs[6:]
    gm_ref = refs.pop(0) if emit_gm else None
    col_ref, h_scr, p_scr, q_scr = refs
    k = pl.program_id(0)
    n_c = ew_ref.shape[1]
    shape = ew_ref.shape[2:]

    @pl.when(k == 0)
    def _():
        col_ref[...] = jnp.zeros(col_ref.shape, F32)

    p = _row_block(pos_ref, k)
    q = _col_block(pos_ref, k)
    rows_of = [_row_block(pos_ref, j) for j in range(slots)]
    gwh = grows_ref[p] * here_ref[k]
    for other in range(slots):
        term = jnp.where(rows_of[other] == p, ghere_ref[other], 0.0)
        for third in range(slots):
            if third != other:
                term = term * jnp.where(
                    (rows_of[third] == p) & (third != k), whole_ref[third], 1.0
                )
        gwh = gwh + jnp.where(other != k, term, 0.0)

    def forward(c, carry):
        prod, grad = carry
        m = _spread_row(spread_ref, c, shape)
        if has_u:
            m = m - u_ref[0, c]
        h = jnp.where(ew_ref[0, c] > 0, jnp.tanh(0.5 * m), 1.0)
        h_scr[c] = h
        p_scr[c] = prod
        q_scr[c] = grad
        return (prod * h, grad * h + gba_ref[0, c] * prod)

    ones = jnp.ones(shape, F32)
    zeros = jnp.zeros(shape, F32)
    lax.fori_loop(0, n_c, forward, (ones, zeros), unroll=UNROLL)

    def backward(i, carry):
        prod, grad = carry
        c = n_c - 1 - i
        h = h_scr[c]
        before = p_scr[c]
        gh = q_scr[c] * prod + before * (grad + gwh * prod)
        gm = jnp.where(ew_ref[0, c] > 0, gh * (0.5 * (1.0 - h * h)), 0.0)
        if emit_gm:
            gm_ref[0, c] = gm
        col_ref[q, pl.ds(c, 1), :] = col_ref[q, pl.ds(c, 1), :] + jnp.sum(gm, axis=0, keepdims=True)
        return (prod * h, grad * h + gba_ref[0, c] * prod)

    lax.fori_loop(0, n_c, backward, (ones, zeros), unroll=UNROLL)


def _spec(kind, shape):
    if kind == "dense":
        return pl.BlockSpec((1,) + tuple(shape[1:]), lambda k, pos: (k, 0, 0, 0))
    if kind == "column":
        return pl.BlockSpec((1,) + tuple(shape[1:]), lambda k, pos: (pos[2 * k + 1], 0, 0))
    return pl.BlockSpec(tuple(shape), lambda k, pos: (0,) * len(shape))


def _call(kernel, pos, inputs, outputs, scratch=()):
    from jax.experimental.pallas import tpu as pltpu

    dense = [a for kind, a in inputs if kind == "dense"][0]
    grid_spec = pltpu.PrefetchScalarGridSpec(
        num_scalar_prefetch=1,
        grid=(dense.shape[0],),
        in_specs=[_spec(kind, a.shape) for kind, a in inputs],
        out_specs=[_spec(kind, o.shape) for kind, o in outputs],
        scratch_shapes=list(scratch),
    )
    return pl.pallas_call(
        kernel,
        grid_spec=grid_spec,
        out_shape=[o for kind, o in outputs],
    )(pos, *[a for kind, a in inputs])


def _vmem(shape):
    from jax.experimental.pallas import tpu as pltpu

    return pltpu.VMEM(shape, F32)


def fwd_products(pos, spread, u, ew, blocks):
    k, c, r, s = ew.shape
    has_u = u is not None
    inputs = [("column", spread)] + ([("dense", u)] if has_u else []) + [("dense", ew)]
    outs = [
        ("dense", jax.ShapeDtypeStruct(ew.shape, F32)),
        ("full", jax.ShapeDtypeStruct((k, r, s), F32)),
        ("full", jax.ShapeDtypeStruct((blocks, r, s), F32)),
        ("full", jax.ShapeDtypeStruct((k, r, s), F32)),
    ]
    return _call(
        functools.partial(_fwd_products_kernel, has_u, k, blocks),
        pos,
        inputs,
        outs,
        [_vmem((c, r, s))],
    )


def fwd_messages(pos, ba, sign, here, others, ew, col_blocks):
    k, c, r, s = ba.shape
    inputs = [("dense", ba), ("full", sign), ("full", here), ("full", others), ("dense", ew)]
    outs = [
        ("dense", jax.ShapeDtypeStruct(ba.shape, F32)),
        ("full", jax.ShapeDtypeStruct((col_blocks, c, s), F32)),
    ]
    return _call(_fwd_messages_kernel, pos, inputs, outs)


def bwd_messages(pos, gsp, gm, ba, sign, here, others, ew, acc):
    k, c, r, s = ba.shape
    has_next = gm is not None
    has_acc = acc is not None
    inputs = (
        [("column", gsp)]
        + ([("dense", gm)] if has_next else [])
        + [("dense", ba), ("full", sign), ("full", here), ("full", others), ("dense", ew)]
        + ([("dense", acc)] if has_acc else [])
    )
    outs = [
        ("dense", jax.ShapeDtypeStruct(ba.shape, F32)),
        ("dense", jax.ShapeDtypeStruct(ba.shape, F32)),
        ("full", jax.ShapeDtypeStruct(here.shape, F32)),
        ("full", jax.ShapeDtypeStruct(others.shape, F32)),
    ]
    return _call(functools.partial(_bwd_messages_kernel, has_next, has_acc), pos, inputs, outs)


def bwd_products(pos, spread, u, ew, gba, grows, ghere, whole, here, col_blocks, emit_gm):
    k, c, r, s = ew.shape
    has_u = u is not None
    inputs = [("column", spread)] + ([("dense", u)] if has_u else []) + [
        ("dense", ew),
        ("dense", gba),
        ("full", grows),
        ("full", ghere),
        ("full", whole),
        ("full", here),
    ]
    outs = ([("dense", jax.ShapeDtypeStruct(ew.shape, F32))] if emit_gm else []) + [
        ("full", jax.ShapeDtypeStruct((col_blocks, c, s), F32))
    ]
    results = _call(
        functools.partial(_bwd_products_kernel, has_u, emit_gm, k),
        pos,
        inputs,
        outs,
        [_vmem((c, r, s)) for _ in range(3)],
    )
    if emit_gm:
        return results[0], results[1]
    return None, results[0]


def pick(hot, values):
    parts = []
    for k in range(hot.shape[0]):
        value = jnp.zeros_like(values[0])
        for j in range(hot.shape[1]):
            value = value + jnp.where(hot[k, j] > 0, values[j], 0.0)
        parts.append(value)
    return jnp.stack(parts)


def place(hot, values):
    parts = []
    for j in range(hot.shape[1]):
        value = jnp.zeros_like(values[0])
        for k in range(hot.shape[0]):
            value = value + jnp.where(hot[k, j] > 0, values[k], 0.0)
        parts.append(value)
    return jnp.stack(parts)


def combine(whole, row_hot, same_row):
    slots = whole.shape[0]
    blocks = row_hot.shape[1]
    ones = jnp.ones_like(whole[0])
    rows = []
    for block in range(blocks):
        value = ones
        for k in range(slots):
            value = value * jnp.where(row_hot[k, block] > 0, whole[k], 1.0)
        rows.append(value)
    others_here = []
    for k in range(slots):
        value = ones
        for other in range(slots):
            if other != k:
                value = value * jnp.where(same_row[k, other], whole[other], 1.0)
        others_here.append(value)
    return jnp.stack(rows), jnp.stack(others_here)


def _power_of_two(n):
    return n > 1 and (n & (n - 1)) == 0


def _swap(value, axis, n, step):
    perm = [(j, j ^ (1 << step)) for j in range(n)]
    return lax.ppermute(value, axis, perm)


def checks_total(values, n):
    if not _power_of_two(n):
        return lax.psum(values, "chk")
    step = 0
    while (1 << step) < n:
        values = values + _swap(values, "chk", n, step)
        step += 1
    return values


def others_forward(rows, check_blocks, n):
    if not _power_of_two(n):
        return others_gather(rows, check_blocks)
    full = rows
    excl = jnp.ones_like(rows)
    trail = []
    step = 0
    while (1 << step) < n:
        other = _swap(full, "var", n, step)
        trail.append((full, excl, other))
        excl = excl * other
        full = full * other
        step += 1
    return excl, trail


def others_backward(trail, grads, check_blocks, n):
    if not _power_of_two(n):
        return others_scatter(trail, grads, check_blocks)
    spread = grads
    target = jnp.zeros_like(grads)
    for step, (full, excl, other) in enumerate(trail):
        other_spread = _swap(spread, "var", n, step)
        target = target * other + excl * other_spread
        spread = spread * other + other_spread * full
    return target


def others_gather(rows, check_blocks):
    own = lax.axis_index("var")
    piece = lax.all_gather(rows, "var", axis=0, tiled=True)
    indices = jnp.arange(piece.shape[0], dtype=jnp.int32)
    keep = indices // check_blocks != own
    parts = []
    for block in range(check_blocks):
        pick = (keep & (indices % check_blocks == block))[:, None, None]
        parts.append(jnp.prod(jnp.where(pick, piece, 1.0), axis=0))
    return jnp.stack(parts), piece


def others_scatter(row_piece, grads, check_blocks):
    own = lax.axis_index("var")
    grad_piece = lax.all_gather(grads, "var", axis=0, tiled=True)
    indices = jnp.arange(row_piece.shape[0], dtype=jnp.int32)
    keep = indices // check_blocks != own
    new_sums = []
    for block in range(check_blocks):
        pick = (keep & (indices % check_blocks == block))[:, None, None]
        factors = jnp.where(pick, row_piece, 1.0)
        weights = jnp.where(pick, grad_piece, 0.0)
        before, after, whole = exclusive_both(factors, 0)
        new_sums.append(jnp.sum(weights * before * after, axis=0))
    return jnp.stack(new_sums)


def body(n_chk, n_var, tile_bits, tile_pos, tile_count, edge_weight, syndrome, channel_prior, out_cot):
    slot_total = tile_bits.shape[2]
    shots = syndrome.shape[1]
    check_blocks = syndrome.shape[0] // TILE
    column_blocks = channel_prior.shape[0] // TILE
    edge, row_hot, col_hot, same_row = device_tables(
        tile_bits[0, 0], tile_pos[0, 0], tile_count[0, 0], check_blocks, column_blocks
    )
    pos = tile_pos[0, 0].reshape(slot_total * 2)
    weight = edge_weight[0, 0].reshape(slot_total, TILE, TILE)
    edge_t = jnp.swapaxes(edge, 1, 2)
    dense = (slot_total, TILE, TILE, shots)
    ew = jnp.broadcast_to((edge_t * jnp.swapaxes(weight, 1, 2))[..., None], dense)
    sign_dev = (1.0 - 2.0 * syndrome.astype(jnp.float32)).reshape(check_blocks, TILE, shots)
    sign_slot = jnp.einsum("kc,crs->krs", row_hot, sign_dev, precision=EXACT)
    prior_dev = channel_prior.reshape(column_blocks, TILE)
    spread = jnp.broadcast_to(prior_dev[:, :, None], (column_blocks, TILE, shots))
    u = None
    saved = []
    total = None
    for step in range(ITERS):
        ba, whole, rows, others_here = fwd_products(pos, spread, u, ew, check_blocks)
        others, trail = others_forward(rows, check_blocks, n_var)
        saved.append((spread, u, ba, whole, others_here, others, trail))
        u, column = fwd_messages(pos, ba, sign_slot, others_here, others, ew, column_blocks)
        total = prior_dev[:, :, None] + checks_total(column, n_chk)
        spread = total
    marginals = total.reshape(column_blocks * TILE, shots)

    grad_total = out_cot.reshape(column_blocks, TILE, shots)
    prior_grad = jnp.zeros((column_blocks, TILE), jnp.float32)
    grad_m = None
    acc = None
    for step in reversed(range(ITERS)):
        spread_t, u_prev, ba, whole, others_here, others, trail = saved[step]
        prior_grad = prior_grad + jnp.sum(grad_total, axis=2)
        acc, grad_ba, grad_here, grad_others = bwd_messages(
            pos, grad_total, grad_m, ba, sign_slot, others_here, others, ew, acc
        )
        grad_rows = others_backward(trail, grad_others, check_blocks, n_var)
        grad_m, column = bwd_products(
            pos, spread_t, u_prev, ew, grad_ba, grad_rows, grad_here, whole, others_here,
            column_blocks, step > 0,
        )
        grad_total = checks_total(column, n_chk)
    prior_grad = prior_grad + jnp.sum(grad_total, axis=2)
    weight_grad = edge * jnp.swapaxes(jnp.sum(acc, axis=3), 1, 2)
    return (
        marginals,
        weight_grad.reshape(1, 1, slot_total, TILE * TILE),
        prior_grad.reshape(column_blocks * TILE),
    )


def solution(mesh):
    placed = (
        P("chk", "var", None, None),
        P("chk", "var", None, None),
        P("chk", "var"),
        P("chk", "var", None, None),
        P("chk", None),
        P("var"),
        P("var", None),
    )
    return jax.shard_map(
        functools.partial(body, mesh.shape["chk"], mesh.shape["var"]),
        mesh=mesh,
        in_specs=placed,
        out_specs=(P("var", None), P("chk", "var", None, None), P("var")),
        check_vma=False,
    )
```

```python
import functools

import jax
import jax.numpy as jnp
from jax import lax
from jax.experimental import pallas as pl
from jax.sharding import PartitionSpec as P

TILE = 64
ITERS = 2


DAMP = 0.97
EXACT = lax.Precision.HIGHEST
F32 = jnp.float32
UNROLL = 8


def linear_both(values, axis):
    length = values.shape[axis]
    pieces = [lax.slice_in_dim(values, index, index + 1, axis=axis) for index in range(length)]
    ones = jnp.ones_like(pieces[0])
    prefix = [ones]
    for index in range(length - 1):
        prefix.append(prefix[-1] * pieces[index])
    suffix = [ones]
    for index in range(length - 1, 0, -1):
        suffix.append(suffix[-1] * pieces[index])
    suffix = suffix[::-1]
    whole = prefix[-1] * pieces[-1]
    return (jnp.concatenate(prefix, axis=axis), jnp.concatenate(suffix, axis=axis), whole)


def exclusive_both(values, axis):
    length = values.shape[axis]
    if length < 16 or length % 8 != 0:
        return linear_both(values, axis)
    shape = values.shape
    split = values.reshape(shape[:axis] + (length // 8, 8) + shape[axis + 1 :])
    inner_before, inner_after, group_whole = linear_both(split, axis + 1)
    outer_before, outer_after, whole = exclusive_both(group_whole, axis)
    before = (inner_before * outer_before).reshape(shape)
    after = (inner_after * outer_after).reshape(shape)
    whole = whole.reshape(shape[:axis] + (1,) + shape[axis + 1 :])
    return (before, after, whole)


def device_tables(bits, positions, count, check_blocks, column_blocks):
    slot_total = bits.shape[0]
    slots = jnp.arange(slot_total, dtype=jnp.int32)
    live = slots < count
    edge = jnp.where(live[:, None], bits, 0).astype(jnp.float32).reshape(slot_total, TILE, TILE)
    row_hot = (positions[:, 0:1] == jnp.arange(check_blocks, dtype=jnp.int32)[None, :]).astype(
        jnp.float32
    )
    col_hot = (positions[:, 1:2] == jnp.arange(column_blocks, dtype=jnp.int32)[None, :]).astype(
        jnp.float32
    )
    same_row = (positions[:, None, 0] == positions[None, :, 0]) & (slots[:, None] != slots[None, :])
    return (edge, row_hot, col_hot, same_row)


def _spread_row(ref, c, shape):
    return jnp.broadcast_to(ref[0, pl.ds(c, 1), :], shape)


def _row_block(pos_ref, k):
    return pos_ref[2 * k]


def _col_block(pos_ref, k):
    return pos_ref[2 * k + 1]


def _fwd_products_kernel(has_u, slots, blocks, pos_ref, *refs):
    refs = list(refs)
    spread_ref = refs.pop(0)
    u_ref = refs.pop(0) if has_u else None
    ew_ref, ba_ref, whole_ref, rows_ref, here_ref, h_scr = refs
    k = pl.program_id(0)
    n_c = ew_ref.shape[1]
    shape = ew_ref.shape[2:]

    def forward(c, carry):
        m = _spread_row(spread_ref, c, shape)
        if has_u:
            m = m - u_ref[0, c]
        h = jnp.where(ew_ref[0, c] > 0, jnp.tanh(0.5 * m), 1.0)
        h_scr[c] = h
        ba_ref[0, c] = carry
        return carry * h

    whole = lax.fori_loop(0, n_c, forward, jnp.ones(shape, F32), unroll=UNROLL)
    whole_ref[k] = whole

    def backward(i, carry):
        c = n_c - 1 - i
        ba_ref[0, c] = ba_ref[0, c] * carry
        return carry * h_scr[c]

    lax.fori_loop(0, n_c, backward, jnp.ones(shape, F32), unroll=UNROLL)

    @pl.when(k == slots - 1)
    def _():
        wholes = [whole_ref[j] for j in range(slots)]
        rows_of = [_row_block(pos_ref, j) for j in range(slots)]
        for block in range(blocks):
            value = jnp.ones(shape, F32)
            for j in range(slots):
                value = value * jnp.where(rows_of[j] == block, wholes[j], 1.0)
            rows_ref[block] = value
        for j in range(slots):
            value = jnp.ones(shape, F32)
            for other in range(slots):
                if other != j:
                    value = value * jnp.where(rows_of[other] == rows_of[j], wholes[other], 1.0)
            here_ref[j] = value


def _fwd_messages_kernel(pos_ref, ba_ref, sign_ref, here_ref, others_ref, ew_ref, u_ref, col_ref):
    k = pl.program_id(0)
    n_c = ba_ref.shape[1]

    @pl.when(k == 0)
    def _():
        col_ref[...] = jnp.zeros(col_ref.shape, F32)

    f = sign_ref[k] * here_ref[k] * others_ref[_row_block(pos_ref, k)]
    q = _col_block(pos_ref, k)

    def body(c, carry):
        x = ba_ref[0, c] * f
        u = ew_ref[0, c] * jnp.log((1.0 + DAMP * x) / (1.0 - DAMP * x))
        u_ref[0, c] = u
        col_ref[q, pl.ds(c, 1), :] = col_ref[q, pl.ds(c, 1), :] + jnp.sum(u, axis=0, keepdims=True)
        return carry

    lax.fori_loop(0, n_c, body, 0, unroll=UNROLL)


def _bwd_messages_kernel(has_next, has_acc, pos_ref, *refs):
    refs = list(refs)
    gsp_ref = refs.pop(0)
    gm_ref = refs.pop(0) if has_next else None
    ba_ref, sign_ref, here_ref, others_ref, ew_ref = refs[:5]
    refs = refs[5:]
    acc_ref = refs.pop(0) if has_acc else None
    gw_ref, gba_ref, ghere_ref, gothers_ref = refs
    k = pl.program_id(0)
    n_c = ba_ref.shape[1]
    shape = ba_ref.shape[2:]

    @pl.when(k == 0)
    def _():
        gothers_ref[...] = jnp.zeros(gothers_ref.shape, F32)

    p = _row_block(pos_ref, k)
    sign = sign_ref[k]
    here = here_ref[k]
    others = others_ref[p]
    f = sign * here * others

    def body(c, total):
        gu = _spread_row(gsp_ref, c, shape)
        if has_next:
            gu = gu - gm_ref[0, c]
        ba = ba_ref[0, c]
        x = ba * f
        low = 1.0 - DAMP * x
        high = 1.0 + DAMP * x
        gw = gu * jnp.log(high / low)
        if has_acc:
            gw = gw + acc_ref[0, c]
        gw_ref[0, c] = gw
        gx = gu * ew_ref[0, c] * ((2.0 * DAMP) / (low * high))
        gba_ref[0, c] = gx * f
        return total + gx * ba

    grad_factor = lax.fori_loop(0, n_c, body, jnp.zeros(shape, F32), unroll=UNROLL)
    ghere_ref[k] = grad_factor * sign * others
    gothers_ref[p] = gothers_ref[p] + grad_factor * sign * here


def _bwd_products_kernel(has_u, emit_gm, slots, pos_ref, *refs):
    refs = list(refs)
    spread_ref = refs.pop(0)
    u_ref = refs.pop(0) if has_u else None
    ew_ref, gba_ref, grows_ref, ghere_ref, whole_ref, here_ref = refs[:6]
    refs = refs[6:]
    gm_ref = refs.pop(0) if emit_gm else None
    col_ref, h_scr, p_scr, q_scr = refs
    k = pl.program_id(0)
    n_c = ew_ref.shape[1]
    shape = ew_ref.shape[2:]

    @pl.when(k == 0)
    def _():
        col_ref[...] = jnp.zeros(col_ref.shape, F32)

    p = _row_block(pos_ref, k)
    q = _col_block(pos_ref, k)
    rows_of = [_row_block(pos_ref, j) for j in range(slots)]
    gwh = grows_ref[p] * here_ref[k]
    for other in range(slots):
        term = jnp.where(rows_of[other] == p, ghere_ref[other], 0.0)
        for third in range(slots):
            if third != other:
                term = term * jnp.where(
                    (rows_of[third] == p) & (third != k), whole_ref[third], 1.0
                )
        gwh = gwh + jnp.where(other != k, term, 0.0)

    def forward(c, carry):
        prod, grad = carry
        m = _spread_row(spread_ref, c, shape)
        if has_u:
            m = m - u_ref[0, c]
        h = jnp.where(ew_ref[0, c] > 0, jnp.tanh(0.5 * m), 1.0)
        h_scr[c] = h
        p_scr[c] = prod
        q_scr[c] = grad
        return (prod * h, grad * h + gba_ref[0, c] * prod)

    ones = jnp.ones(shape, F32)
    zeros = jnp.zeros(shape, F32)
    lax.fori_loop(0, n_c, forward, (ones, zeros), unroll=UNROLL)

    def backward(i, carry):
        prod, grad = carry
        c = n_c - 1 - i
        h = h_scr[c]
        before = p_scr[c]
        gh = q_scr[c] * prod + before * (grad + gwh * prod)
        gm = jnp.where(ew_ref[0, c] > 0, gh * (0.5 * (1.0 - h * h)), 0.0)
        if emit_gm:
            gm_ref[0, c] = gm
        col_ref[q, pl.ds(c, 1), :] = col_ref[q, pl.ds(c, 1), :] + jnp.sum(gm, axis=0, keepdims=True)
        return (prod * h, grad * h + gba_ref[0, c] * prod)

    lax.fori_loop(0, n_c, backward, (ones, zeros), unroll=UNROLL)


def _spec(kind, shape):
    if kind == "dense":
        return pl.BlockSpec((1,) + tuple(shape[1:]), lambda k, pos: (k, 0, 0, 0))
    if kind == "column":
        return pl.BlockSpec((1,) + tuple(shape[1:]), lambda k, pos: (pos[2 * k + 1], 0, 0))
    return pl.BlockSpec(tuple(shape), lambda k, pos: (0,) * len(shape))


def _call(kernel, pos, inputs, outputs, scratch=()):
    from jax.experimental.pallas import tpu as pltpu

    dense = [a for kind, a in inputs if kind == "dense"][0]
    grid_spec = pltpu.PrefetchScalarGridSpec(
        num_scalar_prefetch=1,
        grid=(dense.shape[0],),
        in_specs=[_spec(kind, a.shape) for kind, a in inputs],
        out_specs=[_spec(kind, o.shape) for kind, o in outputs],
        scratch_shapes=list(scratch),
    )
    return pl.pallas_call(
        kernel,
        grid_spec=grid_spec,
        out_shape=[o for kind, o in outputs],
    )(pos, *[a for kind, a in inputs])


def _vmem(shape):
    from jax.experimental.pallas import tpu as pltpu

    return pltpu.VMEM(shape, F32)


def fwd_products(pos, spread, u, ew, blocks):
    k, c, r, s = ew.shape
    has_u = u is not None
    inputs = [("column", spread)] + ([("dense", u)] if has_u else []) + [("dense", ew)]
    outs = [
        ("dense", jax.ShapeDtypeStruct(ew.shape, F32)),
        ("full", jax.ShapeDtypeStruct((k, r, s), F32)),
        ("full", jax.ShapeDtypeStruct((blocks, r, s), F32)),
        ("full", jax.ShapeDtypeStruct((k, r, s), F32)),
    ]
    return _call(
        functools.partial(_fwd_products_kernel, has_u, k, blocks),
        pos,
        inputs,
        outs,
        [_vmem((c, r, s))],
    )


def fwd_messages(pos, ba, sign, here, others, ew, col_blocks):
    k, c, r, s = ba.shape
    inputs = [("dense", ba), ("full", sign), ("full", here), ("full", others), ("dense", ew)]
    outs = [
        ("dense", jax.ShapeDtypeStruct(ba.shape, F32)),
        ("full", jax.ShapeDtypeStruct((col_blocks, c, s), F32)),
    ]
    return _call(_fwd_messages_kernel, pos, inputs, outs)


def bwd_messages(pos, gsp, gm, ba, sign, here, others, ew, acc):
    k, c, r, s = ba.shape
    has_next = gm is not None
    has_acc = acc is not None
    inputs = (
        [("column", gsp)]
        + ([("dense", gm)] if has_next else [])
        + [("dense", ba), ("full", sign), ("full", here), ("full", others), ("dense", ew)]
        + ([("dense", acc)] if has_acc else [])
    )
    outs = [
        ("dense", jax.ShapeDtypeStruct(ba.shape, F32)),
        ("dense", jax.ShapeDtypeStruct(ba.shape, F32)),
        ("full", jax.ShapeDtypeStruct(here.shape, F32)),
        ("full", jax.ShapeDtypeStruct(others.shape, F32)),
    ]
    return _call(functools.partial(_bwd_messages_kernel, has_next, has_acc), pos, inputs, outs)


def bwd_products(pos, spread, u, ew, gba, grows, ghere, whole, here, col_blocks, emit_gm):
    k, c, r, s = ew.shape
    has_u = u is not None
    inputs = [("column", spread)] + ([("dense", u)] if has_u else []) + [
        ("dense", ew),
        ("dense", gba),
        ("full", grows),
        ("full", ghere),
        ("full", whole),
        ("full", here),
    ]
    outs = ([("dense", jax.ShapeDtypeStruct(ew.shape, F32))] if emit_gm else []) + [
        ("full", jax.ShapeDtypeStruct((col_blocks, c, s), F32))
    ]
    results = _call(
        functools.partial(_bwd_products_kernel, has_u, emit_gm, k),
        pos,
        inputs,
        outs,
        [_vmem((c, r, s)) for _ in range(3)],
    )
    if emit_gm:
        return results[0], results[1]
    return None, results[0]


def pick(hot, values):
    parts = []
    for k in range(hot.shape[0]):
        value = jnp.zeros_like(values[0])
        for j in range(hot.shape[1]):
            value = value + jnp.where(hot[k, j] > 0, values[j], 0.0)
        parts.append(value)
    return jnp.stack(parts)


def place(hot, values):
    parts = []
    for j in range(hot.shape[1]):
        value = jnp.zeros_like(values[0])
        for k in range(hot.shape[0]):
            value = value + jnp.where(hot[k, j] > 0, values[k], 0.0)
        parts.append(value)
    return jnp.stack(parts)


def combine(whole, row_hot, same_row):
    slots = whole.shape[0]
    blocks = row_hot.shape[1]
    ones = jnp.ones_like(whole[0])
    rows = []
    for block in range(blocks):
        value = ones
        for k in range(slots):
            value = value * jnp.where(row_hot[k, block] > 0, whole[k], 1.0)
        rows.append(value)
    others_here = []
    for k in range(slots):
        value = ones
        for other in range(slots):
            if other != k:
                value = value * jnp.where(same_row[k, other], whole[other], 1.0)
        others_here.append(value)
    return jnp.stack(rows), jnp.stack(others_here)


def _power_of_two(n):
    return n > 1 and (n & (n - 1)) == 0


def _swap(value, axis, n, step):
    perm = [(j, j ^ (1 << step)) for j in range(n)]
    return lax.ppermute(value, axis, perm)


def checks_total(values, n):
    if not _power_of_two(n):
        return lax.psum(values, "chk")
    step = 0
    while (1 << step) < n:
        values = values + _swap(values, "chk", n, step)
        step += 1
    return values


def others_forward(rows, check_blocks, n, uniform=False):
    if not _power_of_two(n):
        return others_gather(rows, check_blocks)
    if uniform:
        shape = rows.shape
        small = rows[:, :, 0].reshape(-1, shape[2])
        others, trail = others_forward(small, check_blocks, n)
        grow = lambda value: jnp.broadcast_to(value.reshape(shape[:2] + (1,)), shape)
        trail = [tuple(grow(value) for value in entry) for entry in trail]
        return grow(others), trail
    full = rows
    excl = jnp.ones_like(rows)
    trail = []
    step = 0
    while (1 << step) < n:
        other = _swap(full, "var", n, step)
        trail.append((full, excl, other))
        excl = excl * other
        full = full * other
        step += 1
    return excl, trail


def others_backward(trail, grads, check_blocks, n):
    if not _power_of_two(n):
        return others_scatter(trail, grads, check_blocks)
    spread = grads
    target = jnp.zeros_like(grads)
    for step, (full, excl, other) in enumerate(trail):
        other_spread = _swap(spread, "var", n, step)
        target = target * other + excl * other_spread
        spread = spread * other + other_spread * full
    return target


def others_gather(rows, check_blocks):
    own = lax.axis_index("var")
    piece = lax.all_gather(rows, "var", axis=0, tiled=True)
    indices = jnp.arange(piece.shape[0], dtype=jnp.int32)
    keep = indices // check_blocks != own
    parts = []
    for block in range(check_blocks):
        pick = (keep & (indices % check_blocks == block))[:, None, None]
        parts.append(jnp.prod(jnp.where(pick, piece, 1.0), axis=0))
    return jnp.stack(parts), piece


def others_scatter(row_piece, grads, check_blocks):
    own = lax.axis_index("var")
    grad_piece = lax.all_gather(grads, "var", axis=0, tiled=True)
    indices = jnp.arange(row_piece.shape[0], dtype=jnp.int32)
    keep = indices // check_blocks != own
    new_sums = []
    for block in range(check_blocks):
        pick = (keep & (indices % check_blocks == block))[:, None, None]
        factors = jnp.where(pick, row_piece, 1.0)
        weights = jnp.where(pick, grad_piece, 0.0)
        before, after, whole = exclusive_both(factors, 0)
        new_sums.append(jnp.sum(weights * before * after, axis=0))
    return jnp.stack(new_sums)


def body(n_chk, n_var, tile_bits, tile_pos, tile_count, edge_weight, syndrome, channel_prior, out_cot):
    slot_total = tile_bits.shape[2]
    shots = syndrome.shape[1]
    check_blocks = syndrome.shape[0] // TILE
    column_blocks = channel_prior.shape[0] // TILE
    edge, row_hot, col_hot, same_row = device_tables(
        tile_bits[0, 0], tile_pos[0, 0], tile_count[0, 0], check_blocks, column_blocks
    )
    pos = tile_pos[0, 0].reshape(slot_total * 2)
    weight = edge_weight[0, 0].reshape(slot_total, TILE, TILE)
    edge_t = jnp.swapaxes(edge, 1, 2)
    dense = (slot_total, TILE, TILE, shots)
    ew = jnp.broadcast_to((edge_t * jnp.swapaxes(weight, 1, 2))[..., None], dense)
    sign_dev = (1.0 - 2.0 * syndrome.astype(jnp.float32)).reshape(check_blocks, TILE, shots)
    sign_slot = jnp.einsum("kc,crs->krs", row_hot, sign_dev, precision=EXACT)
    prior_dev = channel_prior.reshape(column_blocks, TILE)
    spread = jnp.broadcast_to(prior_dev[:, :, None], (column_blocks, TILE, shots))
    u = None
    saved = []
    total = None
    for step in range(ITERS):
        ba, whole, rows, others_here = fwd_products(pos, spread, u, ew, check_blocks)
        others, trail = others_forward(rows, check_blocks, n_var, uniform=(step == 0 and (check_blocks * TILE) % shots == 0))
        saved.append((spread, u, ba, whole, others_here, others, trail))
        u, column = fwd_messages(pos, ba, sign_slot, others_here, others, ew, column_blocks)
        if step + 1 < ITERS:
            total = prior_dev[:, :, None] + checks_total(column, n_chk)
            spread = total
    last_column = column

    grad_total = out_cot.reshape(column_blocks, TILE, shots)
    prior_grad = jnp.zeros((column_blocks, TILE), jnp.float32)
    grad_m = None
    acc = None
    for step in reversed(range(ITERS)):
        spread_t, u_prev, ba, whole, others_here, others, trail = saved[step]
        prior_grad = prior_grad + jnp.sum(grad_total, axis=2)
        acc, grad_ba, grad_here, grad_others = bwd_messages(
            pos, grad_total, grad_m, ba, sign_slot, others_here, others, ew, acc
        )
        if step + 1 == ITERS:
            last_column, grad_ba = lax.optimization_barrier((last_column, grad_ba))
            total = prior_dev[:, :, None] + checks_total(last_column, n_chk)
            marginals = total.reshape(column_blocks * TILE, shots)
        grad_rows = others_backward(trail, grad_others, check_blocks, n_var)
        grad_m, column = bwd_products(
            pos, spread_t, u_prev, ew, grad_ba, grad_rows, grad_here, whole, others_here,
            column_blocks, step > 0,
        )
        if step > 0:
            grad_total = checks_total(column, n_chk)
    shot_sums = jnp.sum(column, axis=2)
    if (column_blocks * TILE) % 128 == 0:
        shot_sums = checks_total(shot_sums.reshape(-1, 128), n_chk).reshape(column_blocks, TILE)
    else:
        shot_sums = checks_total(shot_sums, n_chk)
    prior_grad = prior_grad + shot_sums
    weight_grad = edge * jnp.swapaxes(jnp.sum(acc, axis=3), 1, 2)
    return (
        marginals,
        weight_grad.reshape(1, 1, slot_total, TILE * TILE),
        prior_grad.reshape(column_blocks * TILE),
    )


def solution(mesh):
    placed = (
        P("chk", "var", None, None),
        P("chk", "var", None, None),
        P("chk", "var"),
        P("chk", "var", None, None),
        P("chk", None),
        P("var"),
        P("var", None),
    )
    return jax.shard_map(
        functools.partial(body, mesh.shape["chk"], mesh.shape["var"]),
        mesh=mesh,
        in_specs=placed,
        out_specs=(P("var", None), P("chk", "var", None, None), P("var")),
        check_vma=False,
    )
```

```python
import functools

import jax
import jax.numpy as jnp
from jax import lax
from jax.experimental import pallas as pl
from jax.sharding import PartitionSpec as P

TILE = 64
ITERS = 2


DAMP = 0.97
EXACT = lax.Precision.HIGHEST
F32 = jnp.float32
UNROLL = 8


def linear_both(values, axis):
    length = values.shape[axis]
    pieces = [lax.slice_in_dim(values, index, index + 1, axis=axis) for index in range(length)]
    ones = jnp.ones_like(pieces[0])
    prefix = [ones]
    for index in range(length - 1):
        prefix.append(prefix[-1] * pieces[index])
    suffix = [ones]
    for index in range(length - 1, 0, -1):
        suffix.append(suffix[-1] * pieces[index])
    suffix = suffix[::-1]
    whole = prefix[-1] * pieces[-1]
    return (jnp.concatenate(prefix, axis=axis), jnp.concatenate(suffix, axis=axis), whole)


def exclusive_both(values, axis):
    length = values.shape[axis]
    if length < 16 or length % 8 != 0:
        return linear_both(values, axis)
    shape = values.shape
    split = values.reshape(shape[:axis] + (length // 8, 8) + shape[axis + 1 :])
    inner_before, inner_after, group_whole = linear_both(split, axis + 1)
    outer_before, outer_after, whole = exclusive_both(group_whole, axis)
    before = (inner_before * outer_before).reshape(shape)
    after = (inner_after * outer_after).reshape(shape)
    whole = whole.reshape(shape[:axis] + (1,) + shape[axis + 1 :])
    return (before, after, whole)


def device_tables(bits, positions, count, check_blocks, column_blocks):
    slot_total = bits.shape[0]
    slots = jnp.arange(slot_total, dtype=jnp.int32)
    live = slots < count
    edge = jnp.where(live[:, None], bits, 0).astype(jnp.float32).reshape(slot_total, TILE, TILE)
    row_hot = (positions[:, 0:1] == jnp.arange(check_blocks, dtype=jnp.int32)[None, :]).astype(
        jnp.float32
    )
    col_hot = (positions[:, 1:2] == jnp.arange(column_blocks, dtype=jnp.int32)[None, :]).astype(
        jnp.float32
    )
    same_row = (positions[:, None, 0] == positions[None, :, 0]) & (slots[:, None] != slots[None, :])
    return (edge, row_hot, col_hot, same_row)


def _spread_row(ref, c, shape):
    return jnp.broadcast_to(ref[0, pl.ds(c, 1), :], shape)


def _row_block(pos_ref, k):
    return pos_ref[2 * k]


def _col_block(pos_ref, k):
    return pos_ref[2 * k + 1]


def _columns(pos_ref, k, slots, n_c):
    return pos_ref[2 * slots + k], 3 * slots + k * n_c


def _loop(count, body, init):
    return lax.fori_loop(0, count, body, init)


def _fwd_products_kernel(has_u, slots, blocks, pos_ref, *refs):
    refs = list(refs)
    spread_ref = refs.pop(0)
    u_ref = refs.pop(0) if has_u else None
    ew_ref, ba_ref, whole_ref, rows_ref, here_ref, h_scr = refs
    k = pl.program_id(0)
    n_c = ew_ref.shape[1]
    shape = ew_ref.shape[2:]

    count, base = _columns(pos_ref, k, slots, n_c)

    def forward(i, carry):
        c = pos_ref[base + i]
        m = _spread_row(spread_ref, c, shape)
        if has_u:
            m = m - u_ref[0, c]
        h = jnp.where(ew_ref[0, c] > 0, jnp.tanh(0.5 * m), 1.0)
        h_scr[c] = h
        ba_ref[0, c] = carry
        return carry * h

    whole = _loop(count, forward, jnp.ones(shape, F32))
    whole_ref[k] = whole

    def backward(i, carry):
        c = pos_ref[base + count - 1 - i]
        ba_ref[0, c] = ba_ref[0, c] * carry
        return carry * h_scr[c]

    _loop(count, backward, jnp.ones(shape, F32))

    @pl.when(k == slots - 1)
    def _():
        wholes = [whole_ref[j] for j in range(slots)]
        rows_of = [_row_block(pos_ref, j) for j in range(slots)]
        for block in range(blocks):
            value = jnp.ones(shape, F32)
            for j in range(slots):
                value = value * jnp.where(rows_of[j] == block, wholes[j], 1.0)
            rows_ref[block] = value
        for j in range(slots):
            value = jnp.ones(shape, F32)
            for other in range(slots):
                if other != j:
                    value = value * jnp.where(rows_of[other] == rows_of[j], wholes[other], 1.0)
            here_ref[j] = value


def _fwd_messages_kernel(slots, pos_ref, ba_ref, sign_ref, here_ref, others_ref, ew_ref, u_ref, col_ref):
    k = pl.program_id(0)
    n_c = ba_ref.shape[1]
    count, base = _columns(pos_ref, k, slots, n_c)

    @pl.when(k == 0)
    def _():
        col_ref[...] = jnp.zeros(col_ref.shape, F32)

    f = sign_ref[k] * here_ref[k] * others_ref[_row_block(pos_ref, k)]
    q = _col_block(pos_ref, k)

    def body(i, carry):
        c = pos_ref[base + i]
        x = ba_ref[0, c] * f
        u = ew_ref[0, c] * jnp.log((1.0 + DAMP * x) / (1.0 - DAMP * x))
        u_ref[0, c] = u
        col_ref[q, pl.ds(c, 1), :] = col_ref[q, pl.ds(c, 1), :] + jnp.sum(u, axis=0, keepdims=True)
        return carry

    _loop(count, body, 0)


def _bwd_messages_kernel(has_next, has_acc, slots, pos_ref, *refs):
    refs = list(refs)
    gsp_ref = refs.pop(0)
    gm_ref = refs.pop(0) if has_next else None
    ba_ref, sign_ref, here_ref, others_ref, ew_ref = refs[:5]
    refs = refs[5:]
    acc_ref = refs.pop(0) if has_acc else None
    gw_ref, gba_ref, ghere_ref, gothers_ref = refs
    k = pl.program_id(0)
    n_c = ba_ref.shape[1]
    shape = ba_ref.shape[2:]

    @pl.when(k == 0)
    def _():
        gothers_ref[...] = jnp.zeros(gothers_ref.shape, F32)

    p = _row_block(pos_ref, k)
    sign = sign_ref[k]
    here = here_ref[k]
    others = others_ref[p]
    f = sign * here * others
    count, base = _columns(pos_ref, k, slots, n_c)

    def body(i, total):
        c = pos_ref[base + i]
        gu = _spread_row(gsp_ref, c, shape)
        if has_next:
            gu = gu - gm_ref[0, c]
        ba = ba_ref[0, c]
        x = ba * f
        low = 1.0 - DAMP * x
        high = 1.0 + DAMP * x
        gw = gu * jnp.log(high / low)
        if has_acc:
            gw = gw + acc_ref[0, c]
        gw_ref[0, c] = gw
        gx = gu * ew_ref[0, c] * ((2.0 * DAMP) / (low * high))
        gba_ref[0, c] = gx * f
        return total + gx * ba

    grad_factor = _loop(count, body, jnp.zeros(shape, F32))
    ghere_ref[k] = grad_factor * sign * others
    gothers_ref[p] = gothers_ref[p] + grad_factor * sign * here


def _bwd_products_kernel(has_u, emit_gm, slots, pos_ref, *refs):
    refs = list(refs)
    spread_ref = refs.pop(0)
    u_ref = refs.pop(0) if has_u else None
    ew_ref, gba_ref, grows_ref, ghere_ref, whole_ref, here_ref = refs[:6]
    refs = refs[6:]
    gm_ref = refs.pop(0) if emit_gm else None
    col_ref, h_scr, p_scr, q_scr = refs
    k = pl.program_id(0)
    n_c = ew_ref.shape[1]
    shape = ew_ref.shape[2:]

    @pl.when(k == 0)
    def _():
        col_ref[...] = jnp.zeros(col_ref.shape, F32)

    p = _row_block(pos_ref, k)
    q = _col_block(pos_ref, k)
    rows_of = [_row_block(pos_ref, j) for j in range(slots)]
    gwh = grows_ref[p] * here_ref[k]
    for other in range(slots):
        term = jnp.where(rows_of[other] == p, ghere_ref[other], 0.0)
        for third in range(slots):
            if third != other:
                term = term * jnp.where(
                    (rows_of[third] == p) & (third != k), whole_ref[third], 1.0
                )
        gwh = gwh + jnp.where(other != k, term, 0.0)

    count, base = _columns(pos_ref, k, slots, n_c)

    def forward(i, carry):
        prod, grad = carry
        c = pos_ref[base + i]
        m = _spread_row(spread_ref, c, shape)
        if has_u:
            m = m - u_ref[0, c]
        h = jnp.where(ew_ref[0, c] > 0, jnp.tanh(0.5 * m), 1.0)
        h_scr[c] = h
        p_scr[c] = prod
        q_scr[c] = grad
        return (prod * h, grad * h + gba_ref[0, c] * prod)

    ones = jnp.ones(shape, F32)
    zeros = jnp.zeros(shape, F32)
    _loop(count, forward, (ones, zeros))

    def backward(i, carry):
        prod, grad = carry
        c = pos_ref[base + count - 1 - i]
        h = h_scr[c]
        before = p_scr[c]
        gh = q_scr[c] * prod + before * (grad + gwh * prod)
        gm = jnp.where(ew_ref[0, c] > 0, gh * (0.5 * (1.0 - h * h)), 0.0)
        if emit_gm:
            gm_ref[0, c] = gm
        col_ref[q, pl.ds(c, 1), :] = col_ref[q, pl.ds(c, 1), :] + jnp.sum(gm, axis=0, keepdims=True)
        return (prod * h, grad * h + gba_ref[0, c] * prod)

    _loop(count, backward, (ones, zeros))


def _spec(kind, shape):
    if kind == "dense":
        return pl.BlockSpec((1,) + tuple(shape[1:]), lambda k, pos: (k, 0, 0, 0))
    if kind == "column":
        return pl.BlockSpec((1,) + tuple(shape[1:]), lambda k, pos: (pos[2 * k + 1], 0, 0))
    return pl.BlockSpec(tuple(shape), lambda k, pos: (0,) * len(shape))


def _call(kernel, pos, inputs, outputs, scratch=()):
    from jax.experimental.pallas import tpu as pltpu

    dense = [a for kind, a in inputs if kind == "dense"][0]
    grid_spec = pltpu.PrefetchScalarGridSpec(
        num_scalar_prefetch=1,
        grid=(dense.shape[0],),
        in_specs=[_spec(kind, a.shape) for kind, a in inputs],
        out_specs=[_spec(kind, o.shape) for kind, o in outputs],
        scratch_shapes=list(scratch),
    )
    return pl.pallas_call(
        kernel,
        grid_spec=grid_spec,
        out_shape=[o for kind, o in outputs],
    )(pos, *[a for kind, a in inputs])


def _vmem(shape):
    from jax.experimental.pallas import tpu as pltpu

    return pltpu.VMEM(shape, F32)


def fwd_products(pos, spread, u, ew, blocks):
    k, c, r, s = ew.shape
    has_u = u is not None
    inputs = [("column", spread)] + ([("dense", u)] if has_u else []) + [("dense", ew)]
    outs = [
        ("dense", jax.ShapeDtypeStruct(ew.shape, F32)),
        ("full", jax.ShapeDtypeStruct((k, r, s), F32)),
        ("full", jax.ShapeDtypeStruct((blocks, r, s), F32)),
        ("full", jax.ShapeDtypeStruct((k, r, s), F32)),
    ]
    return _call(
        functools.partial(_fwd_products_kernel, has_u, k, blocks),
        pos,
        inputs,
        outs,
        [_vmem((c, r, s))],
    )


def fwd_messages(pos, ba, sign, here, others, ew, col_blocks):
    k, c, r, s = ba.shape
    inputs = [("dense", ba), ("full", sign), ("full", here), ("full", others), ("dense", ew)]
    outs = [
        ("dense", jax.ShapeDtypeStruct(ba.shape, F32)),
        ("full", jax.ShapeDtypeStruct((col_blocks, c, s), F32)),
    ]
    return _call(functools.partial(_fwd_messages_kernel, k), pos, inputs, outs)


def bwd_messages(pos, gsp, gm, ba, sign, here, others, ew, acc):
    k, c, r, s = ba.shape
    has_next = gm is not None
    has_acc = acc is not None
    inputs = (
        [("column", gsp)]
        + ([("dense", gm)] if has_next else [])
        + [("dense", ba), ("full", sign), ("full", here), ("full", others), ("dense", ew)]
        + ([("dense", acc)] if has_acc else [])
    )
    outs = [
        ("dense", jax.ShapeDtypeStruct(ba.shape, F32)),
        ("dense", jax.ShapeDtypeStruct(ba.shape, F32)),
        ("full", jax.ShapeDtypeStruct(here.shape, F32)),
        ("full", jax.ShapeDtypeStruct(others.shape, F32)),
    ]
    return _call(functools.partial(_bwd_messages_kernel, has_next, has_acc, k), pos, inputs, outs)


def bwd_products(pos, spread, u, ew, gba, grows, ghere, whole, here, col_blocks, emit_gm):
    k, c, r, s = ew.shape
    has_u = u is not None
    inputs = [("column", spread)] + ([("dense", u)] if has_u else []) + [
        ("dense", ew),
        ("dense", gba),
        ("full", grows),
        ("full", ghere),
        ("full", whole),
        ("full", here),
    ]
    outs = ([("dense", jax.ShapeDtypeStruct(ew.shape, F32))] if emit_gm else []) + [
        ("full", jax.ShapeDtypeStruct((col_blocks, c, s), F32))
    ]
    results = _call(
        functools.partial(_bwd_products_kernel, has_u, emit_gm, k),
        pos,
        inputs,
        outs,
        [_vmem((c, r, s)) for _ in range(3)],
    )
    if emit_gm:
        return results[0], results[1]
    return None, results[0]


def pick(hot, values):
    parts = []
    for k in range(hot.shape[0]):
        value = jnp.zeros_like(values[0])
        for j in range(hot.shape[1]):
            value = value + jnp.where(hot[k, j] > 0, values[j], 0.0)
        parts.append(value)
    return jnp.stack(parts)


def place(hot, values):
    parts = []
    for j in range(hot.shape[1]):
        value = jnp.zeros_like(values[0])
        for k in range(hot.shape[0]):
            value = value + jnp.where(hot[k, j] > 0, values[k], 0.0)
        parts.append(value)
    return jnp.stack(parts)


def combine(whole, row_hot, same_row):
    slots = whole.shape[0]
    blocks = row_hot.shape[1]
    ones = jnp.ones_like(whole[0])
    rows = []
    for block in range(blocks):
        value = ones
        for k in range(slots):
            value = value * jnp.where(row_hot[k, block] > 0, whole[k], 1.0)
        rows.append(value)
    others_here = []
    for k in range(slots):
        value = ones
        for other in range(slots):
            if other != k:
                value = value * jnp.where(same_row[k, other], whole[other], 1.0)
        others_here.append(value)
    return jnp.stack(rows), jnp.stack(others_here)


def _power_of_two(n):
    return n > 1 and (n & (n - 1)) == 0


def _swap(value, axis, n, step):
    perm = [(j, j ^ (1 << step)) for j in range(n)]
    return lax.ppermute(value, axis, perm)


def checks_total(values, n):
    if not _power_of_two(n):
        return lax.psum(values, "chk")
    step = 0
    while (1 << step) < n:
        values = values + _swap(values, "chk", n, step)
        step += 1
    return values


def others_forward(rows, check_blocks, n, uniform=False):
    if not _power_of_two(n):
        return others_gather(rows, check_blocks)
    if uniform:
        shape = rows.shape
        small = rows[:, :, 0].reshape(-1, shape[2])
        others, trail = others_forward(small, check_blocks, n)
        grow = lambda value: jnp.broadcast_to(value.reshape(shape[:2] + (1,)), shape)
        trail = [tuple(grow(value) for value in entry) for entry in trail]
        return grow(others), trail
    full = rows
    excl = jnp.ones_like(rows)
    trail = []
    step = 0
    while (1 << step) < n:
        other = _swap(full, "var", n, step)
        trail.append((full, excl, other))
        excl = excl * other
        full = full * other
        step += 1
    return excl, trail


def others_backward(trail, grads, check_blocks, n):
    if not _power_of_two(n):
        return others_scatter(trail, grads, check_blocks)
    spread = grads
    target = jnp.zeros_like(grads)
    for step, (full, excl, other) in enumerate(trail):
        other_spread = _swap(spread, "var", n, step)
        target = target * other + excl * other_spread
        spread = spread * other + other_spread * full
    return target


def others_gather(rows, check_blocks):
    own = lax.axis_index("var")
    piece = lax.all_gather(rows, "var", axis=0, tiled=True)
    indices = jnp.arange(piece.shape[0], dtype=jnp.int32)
    keep = indices // check_blocks != own
    parts = []
    for block in range(check_blocks):
        pick = (keep & (indices % check_blocks == block))[:, None, None]
        parts.append(jnp.prod(jnp.where(pick, piece, 1.0), axis=0))
    return jnp.stack(parts), piece


def others_scatter(row_piece, grads, check_blocks):
    own = lax.axis_index("var")
    grad_piece = lax.all_gather(grads, "var", axis=0, tiled=True)
    indices = jnp.arange(row_piece.shape[0], dtype=jnp.int32)
    keep = indices // check_blocks != own
    new_sums = []
    for block in range(check_blocks):
        pick = (keep & (indices % check_blocks == block))[:, None, None]
        factors = jnp.where(pick, row_piece, 1.0)
        weights = jnp.where(pick, grad_piece, 0.0)
        before, after, whole = exclusive_both(factors, 0)
        new_sums.append(jnp.sum(weights * before * after, axis=0))
    return jnp.stack(new_sums)


def body(n_chk, n_var, tile_bits, tile_pos, tile_count, edge_weight, syndrome, channel_prior, out_cot):
    slot_total = tile_bits.shape[2]
    shots = syndrome.shape[1]
    check_blocks = syndrome.shape[0] // TILE
    column_blocks = channel_prior.shape[0] // TILE
    edge, row_hot, col_hot, same_row = device_tables(
        tile_bits[0, 0], tile_pos[0, 0], tile_count[0, 0], check_blocks, column_blocks
    )
    weight = edge_weight[0, 0].reshape(slot_total, TILE, TILE)
    edge_t = jnp.swapaxes(edge, 1, 2)
    filled = jnp.any(edge_t > 0, axis=2)
    order = jnp.argsort(jnp.where(filled, 0, 1).astype(jnp.int32), axis=1, stable=True)
    pos = jnp.concatenate(
        [
            tile_pos[0, 0].reshape(slot_total * 2),
            jnp.sum(filled.astype(jnp.int32), axis=1),
            order.astype(jnp.int32).reshape(slot_total * TILE),
        ]
    )
    dense = (slot_total, TILE, TILE, shots)
    ew = jnp.broadcast_to((edge_t * jnp.swapaxes(weight, 1, 2))[..., None], dense)
    sign_dev = (1.0 - 2.0 * syndrome.astype(jnp.float32)).reshape(check_blocks, TILE, shots)
    sign_slot = jnp.einsum("kc,crs->krs", row_hot, sign_dev, precision=EXACT)
    prior_dev = channel_prior.reshape(column_blocks, TILE)
    spread = jnp.broadcast_to(prior_dev[:, :, None], (column_blocks, TILE, shots))
    u = None
    saved = []
    total = None
    for step in range(ITERS):
        ba, whole, rows, others_here = fwd_products(pos, spread, u, ew, check_blocks)
        others, trail = others_forward(rows, check_blocks, n_var, uniform=(step == 0 and (check_blocks * TILE) % shots == 0))
        saved.append((spread, u, ba, whole, others_here, others, trail))
        u, column = fwd_messages(pos, ba, sign_slot, others_here, others, ew, column_blocks)
        if step + 1 < ITERS:
            total = prior_dev[:, :, None] + checks_total(column, n_chk)
            spread = total
    last_column = column

    grad_total = out_cot.reshape(column_blocks, TILE, shots)
    prior_grad = jnp.zeros((column_blocks, TILE), jnp.float32)
    grad_m = None
    acc = None
    for step in reversed(range(ITERS)):
        spread_t, u_prev, ba, whole, others_here, others, trail = saved[step]
        prior_grad = prior_grad + jnp.sum(grad_total, axis=2)
        acc, grad_ba, grad_here, grad_others = bwd_messages(
            pos, grad_total, grad_m, ba, sign_slot, others_here, others, ew, acc
        )
        if step + 1 == ITERS:
            last_column, grad_ba = lax.optimization_barrier((last_column, grad_ba))
            total = prior_dev[:, :, None] + checks_total(last_column, n_chk)
            marginals = total.reshape(column_blocks * TILE, shots)
        grad_rows = others_backward(trail, grad_others, check_blocks, n_var)
        grad_m, column = bwd_products(
            pos, spread_t, u_prev, ew, grad_ba, grad_rows, grad_here, whole, others_here,
            column_blocks, step > 0,
        )
        if step > 0:
            grad_total = checks_total(column, n_chk)
    shot_sums = jnp.sum(column, axis=2)
    if (column_blocks * TILE) % 128 == 0:
        shot_sums = checks_total(shot_sums.reshape(-1, 128), n_chk).reshape(column_blocks, TILE)
    else:
        shot_sums = checks_total(shot_sums, n_chk)
    prior_grad = prior_grad + shot_sums
    weight_grad = jnp.where(edge > 0, jnp.swapaxes(jnp.sum(acc, axis=3), 1, 2), 0.0)
    return (
        marginals,
        weight_grad.reshape(1, 1, slot_total, TILE * TILE),
        prior_grad.reshape(column_blocks * TILE),
    )


def solution(mesh):
    placed = (
        P("chk", "var", None, None),
        P("chk", "var", None, None),
        P("chk", "var"),
        P("chk", "var", None, None),
        P("chk", None),
        P("var"),
        P("var", None),
    )
    return jax.shard_map(
        functools.partial(body, mesh.shape["chk"], mesh.shape["var"]),
        mesh=mesh,
        in_specs=placed,
        out_specs=(P("var", None), P("chk", "var", None, None), P("var")),
        check_vma=False,
    )
```

```python
import functools

import jax
import jax.numpy as jnp
from jax import lax
from jax.experimental import pallas as pl
from jax.sharding import PartitionSpec as P

TILE = 64
ITERS = 2


DAMP = 0.97
EXACT = lax.Precision.HIGHEST
F32 = jnp.float32
UNROLL = 8


def linear_both(values, axis):
    length = values.shape[axis]
    pieces = [lax.slice_in_dim(values, index, index + 1, axis=axis) for index in range(length)]
    ones = jnp.ones_like(pieces[0])
    prefix = [ones]
    for index in range(length - 1):
        prefix.append(prefix[-1] * pieces[index])
    suffix = [ones]
    for index in range(length - 1, 0, -1):
        suffix.append(suffix[-1] * pieces[index])
    suffix = suffix[::-1]
    whole = prefix[-1] * pieces[-1]
    return (jnp.concatenate(prefix, axis=axis), jnp.concatenate(suffix, axis=axis), whole)


def exclusive_both(values, axis):
    length = values.shape[axis]
    if length < 16 or length % 8 != 0:
        return linear_both(values, axis)
    shape = values.shape
    split = values.reshape(shape[:axis] + (length // 8, 8) + shape[axis + 1 :])
    inner_before, inner_after, group_whole = linear_both(split, axis + 1)
    outer_before, outer_after, whole = exclusive_both(group_whole, axis)
    before = (inner_before * outer_before).reshape(shape)
    after = (inner_after * outer_after).reshape(shape)
    whole = whole.reshape(shape[:axis] + (1,) + shape[axis + 1 :])
    return (before, after, whole)


def device_tables(bits, positions, count, check_blocks, column_blocks):
    slot_total = bits.shape[0]
    slots = jnp.arange(slot_total, dtype=jnp.int32)
    live = slots < count
    edge = jnp.where(live[:, None], bits, 0).astype(jnp.float32).reshape(slot_total, TILE, TILE)
    row_hot = (positions[:, 0:1] == jnp.arange(check_blocks, dtype=jnp.int32)[None, :]).astype(
        jnp.float32
    )
    col_hot = (positions[:, 1:2] == jnp.arange(column_blocks, dtype=jnp.int32)[None, :]).astype(
        jnp.float32
    )
    same_row = (positions[:, None, 0] == positions[None, :, 0]) & (slots[:, None] != slots[None, :])
    return (edge, row_hot, col_hot, same_row)


def _spread_row(ref, c, shape):
    return jnp.broadcast_to(ref[0, pl.ds(c, 1), :], shape)


def _row_block(pos_ref, k):
    return pos_ref[2 * k]


def _col_block(pos_ref, k):
    return pos_ref[2 * k + 1]


def _columns(pos_ref, k, slots, n_c):
    return pos_ref[2 * slots + k], 3 * slots + k * n_c


def _loop(count, body, init):
    return lax.fori_loop(0, count, body, init)


def _fwd_products_kernel(has_u, slots, blocks, pos_ref, *refs):
    refs = list(refs)
    spread_ref = refs.pop(0)
    u_ref = refs.pop(0) if has_u else None
    ew_ref, ba_ref, whole_ref, rows_ref, here_ref, h_scr = refs
    k = pl.program_id(0)
    n_c = ew_ref.shape[1]
    shape = ew_ref.shape[2:]

    count, base = _columns(pos_ref, k, slots, n_c)

    def forward(i, carry):
        c = pos_ref[base + i]
        m = _spread_row(spread_ref, c, shape)
        if has_u:
            m = m - u_ref[0, c]
        h = jnp.where(ew_ref[0, c] > 0, jnp.tanh(0.5 * m), 1.0)
        h_scr[c] = h
        ba_ref[0, c] = carry
        return carry * h

    whole = _loop(count, forward, jnp.ones(shape, F32))
    whole_ref[k] = whole

    def backward(i, carry):
        c = pos_ref[base + count - 1 - i]
        ba_ref[0, c] = ba_ref[0, c] * carry
        return carry * h_scr[c]

    _loop(count, backward, jnp.ones(shape, F32))

    @pl.when(k == slots - 1)
    def _():
        wholes = [whole_ref[j] for j in range(slots)]
        rows_of = [_row_block(pos_ref, j) for j in range(slots)]
        for block in range(blocks):
            value = jnp.ones(shape, F32)
            for j in range(slots):
                value = value * jnp.where(rows_of[j] == block, wholes[j], 1.0)
            rows_ref[block] = value
        for j in range(slots):
            value = jnp.ones(shape, F32)
            for other in range(slots):
                if other != j:
                    value = value * jnp.where(rows_of[other] == rows_of[j], wholes[other], 1.0)
            here_ref[j] = value


def _fwd_messages_kernel(slots, pos_ref, ba_ref, sign_ref, here_ref, others_ref, ew_ref, u_ref, col_ref):
    k = pl.program_id(0)
    n_c = ba_ref.shape[1]
    count, base = _columns(pos_ref, k, slots, n_c)

    @pl.when(k == 0)
    def _():
        col_ref[...] = jnp.zeros(col_ref.shape, F32)

    f = sign_ref[k] * here_ref[k] * others_ref[_row_block(pos_ref, k)]
    q = _col_block(pos_ref, k)

    def body(i, carry):
        c = pos_ref[base + i]
        x = ba_ref[0, c] * f
        u = ew_ref[0, c] * jnp.log((1.0 + DAMP * x) / (1.0 - DAMP * x))
        u_ref[0, c] = u
        col_ref[q, pl.ds(c, 1), :] = col_ref[q, pl.ds(c, 1), :] + jnp.sum(u, axis=0, keepdims=True)
        return carry

    _loop(count, body, 0)


def _bwd_messages_kernel(has_next, has_acc, slots, pos_ref, *refs):
    refs = list(refs)
    gsp_ref = refs.pop(0)
    gm_ref = refs.pop(0) if has_next else None
    ba_ref, sign_ref, here_ref, others_ref, ew_ref = refs[:5]
    refs = refs[5:]
    acc_ref = refs.pop(0) if has_acc else None
    gw_ref, gba_ref, ghere_ref, gothers_ref = refs
    lanes = lax.broadcasted_iota(jnp.int32, (ba_ref.shape[2], gw_ref.shape[2]), 1)
    k = pl.program_id(0)
    n_c = ba_ref.shape[1]
    shape = ba_ref.shape[2:]

    @pl.when(k == 0)
    def _():
        gothers_ref[...] = jnp.zeros(gothers_ref.shape, F32)

    p = _row_block(pos_ref, k)
    sign = sign_ref[k]
    here = here_ref[k]
    others = others_ref[p]
    f = sign * here * others
    count, base = _columns(pos_ref, k, slots, n_c)

    def body(i, carry):
        total, table = carry
        c = pos_ref[base + i]
        gu = _spread_row(gsp_ref, c, shape)
        if has_next:
            gu = gu - gm_ref[0, c]
        ba = ba_ref[0, c]
        x = ba * f
        low = 1.0 - DAMP * x
        high = 1.0 + DAMP * x
        part = jnp.sum(gu * jnp.log(high / low), axis=1, keepdims=True)
        table = jnp.where(lanes == c, part, table)
        gx = gu * ew_ref[0, c] * ((2.0 * DAMP) / (low * high))
        gba_ref[0, c] = gx * f
        return (total + gx * ba, table)

    grad_factor, table = _loop(
        count, body, (jnp.zeros(shape, F32), jnp.zeros((shape[0], gw_ref.shape[2]), F32))
    )
    if has_acc:
        table = table + acc_ref[k]
    gw_ref[k] = table
    ghere_ref[k] = grad_factor * sign * others
    gothers_ref[p] = gothers_ref[p] + grad_factor * sign * here


def _bwd_products_kernel(has_u, emit_gm, slots, pos_ref, *refs):
    refs = list(refs)
    spread_ref = refs.pop(0)
    u_ref = refs.pop(0) if has_u else None
    ew_ref, gba_ref, grows_ref, ghere_ref, whole_ref, here_ref = refs[:6]
    refs = refs[6:]
    gm_ref = refs.pop(0) if emit_gm else None
    col_ref, h_scr, p_scr, q_scr = refs
    k = pl.program_id(0)
    n_c = ew_ref.shape[1]
    shape = ew_ref.shape[2:]

    @pl.when(k == 0)
    def _():
        col_ref[...] = jnp.zeros(col_ref.shape, F32)

    p = _row_block(pos_ref, k)
    q = _col_block(pos_ref, k)
    rows_of = [_row_block(pos_ref, j) for j in range(slots)]
    gwh = grows_ref[p] * here_ref[k]
    for other in range(slots):
        term = jnp.where(rows_of[other] == p, ghere_ref[other], 0.0)
        for third in range(slots):
            if third != other:
                term = term * jnp.where(
                    (rows_of[third] == p) & (third != k), whole_ref[third], 1.0
                )
        gwh = gwh + jnp.where(other != k, term, 0.0)

    count, base = _columns(pos_ref, k, slots, n_c)

    def forward(i, carry):
        prod, grad = carry
        c = pos_ref[base + i]
        m = _spread_row(spread_ref, c, shape)
        if has_u:
            m = m - u_ref[0, c]
        h = jnp.where(ew_ref[0, c] > 0, jnp.tanh(0.5 * m), 1.0)
        h_scr[c] = h
        p_scr[c] = prod
        q_scr[c] = grad
        return (prod * h, grad * h + gba_ref[0, c] * prod)

    ones = jnp.ones(shape, F32)
    zeros = jnp.zeros(shape, F32)
    _loop(count, forward, (ones, zeros))

    def backward(i, carry):
        prod, grad = carry
        c = pos_ref[base + count - 1 - i]
        h = h_scr[c]
        before = p_scr[c]
        gh = q_scr[c] * prod + before * (grad + gwh * prod)
        gm = jnp.where(ew_ref[0, c] > 0, gh * (0.5 * (1.0 - h * h)), 0.0)
        if emit_gm:
            gm_ref[0, c] = gm
        col_ref[q, pl.ds(c, 1), :] = col_ref[q, pl.ds(c, 1), :] + jnp.sum(gm, axis=0, keepdims=True)
        return (prod * h, grad * h + gba_ref[0, c] * prod)

    _loop(count, backward, (ones, zeros))


def _spec(kind, shape):
    if kind == "dense":
        return pl.BlockSpec((1,) + tuple(shape[1:]), lambda k, pos: (k, 0, 0, 0))
    if kind == "column":
        return pl.BlockSpec((1,) + tuple(shape[1:]), lambda k, pos: (pos[2 * k + 1], 0, 0))
    return pl.BlockSpec(tuple(shape), lambda k, pos: (0,) * len(shape))


def _call(kernel, pos, inputs, outputs, scratch=()):
    from jax.experimental.pallas import tpu as pltpu

    dense = [a for kind, a in inputs if kind == "dense"][0]
    grid_spec = pltpu.PrefetchScalarGridSpec(
        num_scalar_prefetch=1,
        grid=(dense.shape[0],),
        in_specs=[_spec(kind, a.shape) for kind, a in inputs],
        out_specs=[_spec(kind, o.shape) for kind, o in outputs],
        scratch_shapes=list(scratch),
    )
    return pl.pallas_call(
        kernel,
        grid_spec=grid_spec,
        out_shape=[o for kind, o in outputs],
    )(pos, *[a for kind, a in inputs])


def _vmem(shape):
    from jax.experimental.pallas import tpu as pltpu

    return pltpu.VMEM(shape, F32)


def fwd_products(pos, spread, u, ew, blocks):
    k, c, r, s = ew.shape
    has_u = u is not None
    inputs = [("column", spread)] + ([("dense", u)] if has_u else []) + [("dense", ew)]
    outs = [
        ("dense", jax.ShapeDtypeStruct(ew.shape, F32)),
        ("full", jax.ShapeDtypeStruct((k, r, s), F32)),
        ("full", jax.ShapeDtypeStruct((blocks, r, s), F32)),
        ("full", jax.ShapeDtypeStruct((k, r, s), F32)),
    ]
    return _call(
        functools.partial(_fwd_products_kernel, has_u, k, blocks),
        pos,
        inputs,
        outs,
        [_vmem((c, r, s))],
    )


def fwd_messages(pos, ba, sign, here, others, ew, col_blocks):
    k, c, r, s = ba.shape
    inputs = [("dense", ba), ("full", sign), ("full", here), ("full", others), ("dense", ew)]
    outs = [
        ("dense", jax.ShapeDtypeStruct(ba.shape, F32)),
        ("full", jax.ShapeDtypeStruct((col_blocks, c, s), F32)),
    ]
    return _call(functools.partial(_fwd_messages_kernel, k), pos, inputs, outs)


def bwd_messages(pos, gsp, gm, ba, sign, here, others, ew, acc):
    k, c, r, s = ba.shape
    has_next = gm is not None
    has_acc = acc is not None
    inputs = (
        [("column", gsp)]
        + ([("dense", gm)] if has_next else [])
        + [("dense", ba), ("full", sign), ("full", here), ("full", others), ("dense", ew)]
        + ([("full", acc)] if has_acc else [])
    )
    outs = [
        ("full", jax.ShapeDtypeStruct((k, r, 128), F32)),
        ("dense", jax.ShapeDtypeStruct(ba.shape, F32)),
        ("full", jax.ShapeDtypeStruct(here.shape, F32)),
        ("full", jax.ShapeDtypeStruct(others.shape, F32)),
    ]
    return _call(functools.partial(_bwd_messages_kernel, has_next, has_acc, k), pos, inputs, outs)


def bwd_products(pos, spread, u, ew, gba, grows, ghere, whole, here, col_blocks, emit_gm):
    k, c, r, s = ew.shape
    has_u = u is not None
    inputs = [("column", spread)] + ([("dense", u)] if has_u else []) + [
        ("dense", ew),
        ("dense", gba),
        ("full", grows),
        ("full", ghere),
        ("full", whole),
        ("full", here),
    ]
    outs = ([("dense", jax.ShapeDtypeStruct(ew.shape, F32))] if emit_gm else []) + [
        ("full", jax.ShapeDtypeStruct((col_blocks, c, s), F32))
    ]
    results = _call(
        functools.partial(_bwd_products_kernel, has_u, emit_gm, k),
        pos,
        inputs,
        outs,
        [_vmem((c, r, s)) for _ in range(3)],
    )
    if emit_gm:
        return results[0], results[1]
    return None, results[0]


def pick(hot, values):
    parts = []
    for k in range(hot.shape[0]):
        value = jnp.zeros_like(values[0])
        for j in range(hot.shape[1]):
            value = value + jnp.where(hot[k, j] > 0, values[j], 0.0)
        parts.append(value)
    return jnp.stack(parts)


def place(hot, values):
    parts = []
    for j in range(hot.shape[1]):
        value = jnp.zeros_like(values[0])
        for k in range(hot.shape[0]):
            value = value + jnp.where(hot[k, j] > 0, values[k], 0.0)
        parts.append(value)
    return jnp.stack(parts)


def combine(whole, row_hot, same_row):
    slots = whole.shape[0]
    blocks = row_hot.shape[1]
    ones = jnp.ones_like(whole[0])
    rows = []
    for block in range(blocks):
        value = ones
        for k in range(slots):
            value = value * jnp.where(row_hot[k, block] > 0, whole[k], 1.0)
        rows.append(value)
    others_here = []
    for k in range(slots):
        value = ones
        for other in range(slots):
            if other != k:
                value = value * jnp.where(same_row[k, other], whole[other], 1.0)
        others_here.append(value)
    return jnp.stack(rows), jnp.stack(others_here)


def _power_of_two(n):
    return n > 1 and (n & (n - 1)) == 0


def _swap(value, axis, n, step):
    perm = [(j, j ^ (1 << step)) for j in range(n)]
    return lax.ppermute(value, axis, perm)


def checks_total(values, n):
    if not _power_of_two(n):
        return lax.psum(values, "chk")
    step = 0
    while (1 << step) < n:
        values = values + _swap(values, "chk", n, step)
        step += 1
    return values


def others_forward(rows, check_blocks, n, uniform=False):
    if not _power_of_two(n):
        return others_gather(rows, check_blocks)
    if uniform:
        shape = rows.shape
        small = rows[:, :, 0].reshape(-1, shape[2])
        others, trail = others_forward(small, check_blocks, n)
        grow = lambda value: jnp.broadcast_to(value.reshape(shape[:2] + (1,)), shape)
        trail = [tuple(grow(value) for value in entry) for entry in trail]
        return grow(others), trail
    full = rows
    excl = jnp.ones_like(rows)
    trail = []
    step = 0
    while (1 << step) < n:
        other = _swap(full, "var", n, step)
        trail.append((full, excl, other))
        excl = excl * other
        full = full * other
        step += 1
    return excl, trail


def others_backward(trail, grads, check_blocks, n):
    if not _power_of_two(n):
        return others_scatter(trail, grads, check_blocks)
    spread = grads
    target = jnp.zeros_like(grads)
    for step, (full, excl, other) in enumerate(trail):
        other_spread = _swap(spread, "var", n, step)
        target = target * other + excl * other_spread
        spread = spread * other + other_spread * full
    return target


def others_gather(rows, check_blocks):
    own = lax.axis_index("var")
    piece = lax.all_gather(rows, "var", axis=0, tiled=True)
    indices = jnp.arange(piece.shape[0], dtype=jnp.int32)
    keep = indices // check_blocks != own
    parts = []
    for block in range(check_blocks):
        pick = (keep & (indices % check_blocks == block))[:, None, None]
        parts.append(jnp.prod(jnp.where(pick, piece, 1.0), axis=0))
    return jnp.stack(parts), piece


def others_scatter(row_piece, grads, check_blocks):
    own = lax.axis_index("var")
    grad_piece = lax.all_gather(grads, "var", axis=0, tiled=True)
    indices = jnp.arange(row_piece.shape[0], dtype=jnp.int32)
    keep = indices // check_blocks != own
    new_sums = []
    for block in range(check_blocks):
        pick = (keep & (indices % check_blocks == block))[:, None, None]
        factors = jnp.where(pick, row_piece, 1.0)
        weights = jnp.where(pick, grad_piece, 0.0)
        before, after, whole = exclusive_both(factors, 0)
        new_sums.append(jnp.sum(weights * before * after, axis=0))
    return jnp.stack(new_sums)


def body(n_chk, n_var, tile_bits, tile_pos, tile_count, edge_weight, syndrome, channel_prior, out_cot):
    slot_total = tile_bits.shape[2]
    shots = syndrome.shape[1]
    check_blocks = syndrome.shape[0] // TILE
    column_blocks = channel_prior.shape[0] // TILE
    edge, row_hot, col_hot, same_row = device_tables(
        tile_bits[0, 0], tile_pos[0, 0], tile_count[0, 0], check_blocks, column_blocks
    )
    weight = edge_weight[0, 0].reshape(slot_total, TILE, TILE)
    edge_t = jnp.swapaxes(edge, 1, 2)
    filled = jnp.any(edge_t > 0, axis=2)
    order = jnp.argsort(jnp.where(filled, 0, 1).astype(jnp.int32), axis=1, stable=True)
    pos = jnp.concatenate(
        [
            tile_pos[0, 0].reshape(slot_total * 2),
            jnp.sum(filled.astype(jnp.int32), axis=1),
            order.astype(jnp.int32).reshape(slot_total * TILE),
        ]
    )
    dense = (slot_total, TILE, TILE, shots)
    ew = jnp.broadcast_to((edge_t * jnp.swapaxes(weight, 1, 2))[..., None], dense)
    sign_dev = (1.0 - 2.0 * syndrome.astype(jnp.float32)).reshape(check_blocks, TILE, shots)
    sign_slot = jnp.einsum("kc,crs->krs", row_hot, sign_dev, precision=EXACT)
    prior_dev = channel_prior.reshape(column_blocks, TILE)
    spread = jnp.broadcast_to(prior_dev[:, :, None], (column_blocks, TILE, shots))
    u = None
    saved = []
    total = None
    for step in range(ITERS):
        ba, whole, rows, others_here = fwd_products(pos, spread, u, ew, check_blocks)
        others, trail = others_forward(rows, check_blocks, n_var, uniform=(step == 0 and (check_blocks * TILE) % shots == 0))
        saved.append((spread, u, ba, whole, others_here, others, trail))
        u, column = fwd_messages(pos, ba, sign_slot, others_here, others, ew, column_blocks)
        if step + 1 < ITERS:
            total = prior_dev[:, :, None] + checks_total(column, n_chk)
            spread = total
    last_column = column

    grad_total = out_cot.reshape(column_blocks, TILE, shots)
    prior_grad = jnp.zeros((column_blocks, TILE), jnp.float32)
    grad_m = None
    acc = None
    for step in reversed(range(ITERS)):
        spread_t, u_prev, ba, whole, others_here, others, trail = saved[step]
        prior_grad = prior_grad + jnp.sum(grad_total, axis=2)
        acc, grad_ba, grad_here, grad_others = bwd_messages(
            pos, grad_total, grad_m, ba, sign_slot, others_here, others, ew, acc
        )
        if step + 1 == ITERS:
            last_column, grad_ba = lax.optimization_barrier((last_column, grad_ba))
            total = prior_dev[:, :, None] + checks_total(last_column, n_chk)
            marginals = total.reshape(column_blocks * TILE, shots)
        grad_rows = others_backward(trail, grad_others, check_blocks, n_var)
        grad_m, column = bwd_products(
            pos, spread_t, u_prev, ew, grad_ba, grad_rows, grad_here, whole, others_here,
            column_blocks, step > 0,
        )
        if step > 0:
            grad_total = checks_total(column, n_chk)
    shot_sums = jnp.sum(column, axis=2)
    if (column_blocks * TILE) % 128 == 0:
        shot_sums = checks_total(shot_sums.reshape(-1, 128), n_chk).reshape(column_blocks, TILE)
    else:
        shot_sums = checks_total(shot_sums, n_chk)
    prior_grad = prior_grad + shot_sums
    weight_grad = jnp.where(edge > 0, acc[:, :, :TILE], 0.0)
    return (
        marginals,
        weight_grad.reshape(1, 1, slot_total, TILE * TILE),
        prior_grad.reshape(column_blocks * TILE),
    )


def solution(mesh):
    placed = (
        P("chk", "var", None, None),
        P("chk", "var", None, None),
        P("chk", "var"),
        P("chk", "var", None, None),
        P("chk", None),
        P("var"),
        P("var", None),
    )
    return jax.shard_map(
        functools.partial(body, mesh.shape["chk"], mesh.shape["var"]),
        mesh=mesh,
        in_specs=placed,
        out_specs=(P("var", None), P("chk", "var", None, None), P("var")),
        check_vma=False,
    )
```

```python
import functools

import jax
import jax.numpy as jnp
from jax import lax
from jax.experimental import pallas as pl
from jax.sharding import PartitionSpec as P

TILE = 64
ITERS = 2


DAMP = 0.97
EXACT = lax.Precision.HIGHEST
F32 = jnp.float32
UNROLL = 8


def linear_both(values, axis):
    length = values.shape[axis]
    pieces = [lax.slice_in_dim(values, index, index + 1, axis=axis) for index in range(length)]
    ones = jnp.ones_like(pieces[0])
    prefix = [ones]
    for index in range(length - 1):
        prefix.append(prefix[-1] * pieces[index])
    suffix = [ones]
    for index in range(length - 1, 0, -1):
        suffix.append(suffix[-1] * pieces[index])
    suffix = suffix[::-1]
    whole = prefix[-1] * pieces[-1]
    return (jnp.concatenate(prefix, axis=axis), jnp.concatenate(suffix, axis=axis), whole)


def exclusive_both(values, axis):
    length = values.shape[axis]
    if length < 16 or length % 8 != 0:
        return linear_both(values, axis)
    shape = values.shape
    split = values.reshape(shape[:axis] + (length // 8, 8) + shape[axis + 1 :])
    inner_before, inner_after, group_whole = linear_both(split, axis + 1)
    outer_before, outer_after, whole = exclusive_both(group_whole, axis)
    before = (inner_before * outer_before).reshape(shape)
    after = (inner_after * outer_after).reshape(shape)
    whole = whole.reshape(shape[:axis] + (1,) + shape[axis + 1 :])
    return (before, after, whole)


def device_tables(bits, positions, count, check_blocks, column_blocks):
    slot_total = bits.shape[0]
    slots = jnp.arange(slot_total, dtype=jnp.int32)
    live = slots < count
    edge = jnp.where(live[:, None], bits, 0).astype(jnp.float32).reshape(slot_total, TILE, TILE)
    row_hot = (positions[:, 0:1] == jnp.arange(check_blocks, dtype=jnp.int32)[None, :]).astype(
        jnp.float32
    )
    col_hot = (positions[:, 1:2] == jnp.arange(column_blocks, dtype=jnp.int32)[None, :]).astype(
        jnp.float32
    )
    same_row = (positions[:, None, 0] == positions[None, :, 0]) & (slots[:, None] != slots[None, :])
    return (edge, row_hot, col_hot, same_row)


def _spread_row(ref, c, shape):
    return jnp.broadcast_to(ref[0, pl.ds(c, 1), :], shape)


def _row_block(pos_ref, k):
    return pos_ref[2 * k]


def _col_block(pos_ref, k):
    return pos_ref[2 * k + 1]


def _columns(pos_ref, k, slots, n_c):
    return pos_ref[2 * slots + k], 3 * slots + k * n_c


def _loop(count, body, init):
    return lax.fori_loop(0, count, body, init)


def _fwd_products_kernel(has_u, slots, blocks, pos_ref, *refs):
    refs = list(refs)
    spread_ref = refs.pop(0)
    u_ref = refs.pop(0) if has_u else None
    ew_ref, ba_ref, whole_ref, rows_ref, here_ref, h_scr = refs
    k = pl.program_id(0)
    n_c = ew_ref.shape[1]
    shape = ew_ref.shape[2:]

    count, base = _columns(pos_ref, k, slots, n_c)

    def forward(i, carry):
        c = pos_ref[base + i]
        m = _spread_row(spread_ref, c, shape)
        if has_u:
            m = m - u_ref[0, c]
        h = jnp.where(ew_ref[0, c] > 0, jnp.tanh(0.5 * m), 1.0)
        h_scr[c] = h
        ba_ref[0, c] = carry
        return carry * h

    whole = _loop(count, forward, jnp.ones(shape, F32))
    whole_ref[k] = whole

    def backward(i, carry):
        c = pos_ref[base + count - 1 - i]
        ba_ref[0, c] = ba_ref[0, c] * carry
        return carry * h_scr[c]

    _loop(count, backward, jnp.ones(shape, F32))

    @pl.when(k == slots - 1)
    def _():
        wholes = [whole_ref[j] for j in range(slots)]
        rows_of = [_row_block(pos_ref, j) for j in range(slots)]
        for block in range(blocks):
            value = jnp.ones(shape, F32)
            for j in range(slots):
                value = value * jnp.where(rows_of[j] == block, wholes[j], 1.0)
            rows_ref[block] = value
        for j in range(slots):
            value = jnp.ones(shape, F32)
            for other in range(slots):
                if other != j:
                    value = value * jnp.where(rows_of[other] == rows_of[j], wholes[other], 1.0)
            here_ref[j] = value


def _fwd_messages_kernel(slots, pos_ref, ba_ref, sign_ref, here_ref, others_ref, ew_ref, u_ref, col_ref):
    k = pl.program_id(0)
    n_c = ba_ref.shape[1]
    count, base = _columns(pos_ref, k, slots, n_c)

    @pl.when(k == 0)
    def _():
        col_ref[...] = jnp.zeros(col_ref.shape, F32)

    f = sign_ref[k] * here_ref[k] * others_ref[_row_block(pos_ref, k)]
    q = _col_block(pos_ref, k)

    def body(i, carry):
        c = pos_ref[base + i]
        x = ba_ref[0, c] * f
        u = ew_ref[0, c] * jnp.log((1.0 + DAMP * x) / (1.0 - DAMP * x))
        u_ref[0, c] = u
        col_ref[q, pl.ds(c, 1), :] = col_ref[q, pl.ds(c, 1), :] + jnp.sum(u, axis=0, keepdims=True)
        return carry

    _loop(count, body, 0)


def _bwd_messages_kernel(has_next, has_acc, slots, pos_ref, *refs):
    refs = list(refs)
    gsp_ref = refs.pop(0)
    gm_ref = refs.pop(0) if has_next else None
    ba_ref, sign_ref, here_ref, others_ref, ew_ref = refs[:5]
    refs = refs[5:]
    acc_ref = refs.pop(0) if has_acc else None
    gw_ref, gba_ref, ghere_ref, gothers_ref = refs
    k = pl.program_id(0)
    n_c = ba_ref.shape[1]
    shape = ba_ref.shape[2:]

    @pl.when(k == 0)
    def _():
        gothers_ref[...] = jnp.zeros(gothers_ref.shape, F32)

    p = _row_block(pos_ref, k)
    sign = sign_ref[k]
    here = here_ref[k]
    others = others_ref[p]
    f = sign * here * others
    count, base = _columns(pos_ref, k, slots, n_c)

    def body(i, total):
        c = pos_ref[base + i]
        gu = _spread_row(gsp_ref, c, shape)
        if has_next:
            gu = gu - gm_ref[0, c]
        ba = ba_ref[0, c]
        x = ba * f
        low = 1.0 - DAMP * x
        high = 1.0 + DAMP * x
        gw = gu * jnp.log(high / low)
        if has_acc:
            gw = gw + acc_ref[0, c]
        gw_ref[0, c] = gw
        gx = gu * ew_ref[0, c] * ((2.0 * DAMP) / (low * high))
        gba_ref[0, c] = gx * f
        return total + gx * ba

    grad_factor = _loop(count, body, jnp.zeros(shape, F32))
    ghere_ref[k] = grad_factor * sign * others
    gothers_ref[p] = gothers_ref[p] + grad_factor * sign * here


def _bwd_products_kernel(has_u, emit_gm, slots, pos_ref, *refs):
    refs = list(refs)
    spread_ref = refs.pop(0)
    u_ref = refs.pop(0) if has_u else None
    ew_ref, gba_ref, grows_ref, ghere_ref, whole_ref, here_ref = refs[:6]
    refs = refs[6:]
    gm_ref = refs.pop(0) if emit_gm else None
    col_ref, h_scr, p_scr, q_scr = refs
    k = pl.program_id(0)
    n_c = ew_ref.shape[1]
    shape = ew_ref.shape[2:]

    @pl.when(k == 0)
    def _():
        col_ref[...] = jnp.zeros(col_ref.shape, F32)

    p = _row_block(pos_ref, k)
    q = _col_block(pos_ref, k)
    rows_of = [_row_block(pos_ref, j) for j in range(slots)]
    gwh = grows_ref[p] * here_ref[k]
    for other in range(slots):
        term = jnp.where(rows_of[other] == p, ghere_ref[other], 0.0)
        for third in range(slots):
            if third != other:
                term = term * jnp.where(
                    (rows_of[third] == p) & (third != k), whole_ref[third], 1.0
                )
        gwh = gwh + jnp.where(other != k, term, 0.0)

    count, base = _columns(pos_ref, k, slots, n_c)

    def forward(i, carry):
        prod, grad = carry
        c = pos_ref[base + i]
        m = _spread_row(spread_ref, c, shape)
        if has_u:
            m = m - u_ref[0, c]
        h = jnp.where(ew_ref[0, c] > 0, jnp.tanh(0.5 * m), 1.0)
        h_scr[c] = h
        p_scr[c] = prod
        q_scr[c] = grad
        return (prod * h, grad * h + gba_ref[0, c] * prod)

    ones = jnp.ones(shape, F32)
    zeros = jnp.zeros(shape, F32)
    _loop(count, forward, (ones, zeros))

    def backward(i, carry):
        prod, grad = carry
        c = pos_ref[base + count - 1 - i]
        h = h_scr[c]
        before = p_scr[c]
        gh = q_scr[c] * prod + before * (grad + gwh * prod)
        gm = jnp.where(ew_ref[0, c] > 0, gh * (0.5 * (1.0 - h * h)), 0.0)
        if emit_gm:
            gm_ref[0, c] = gm
        col_ref[q, pl.ds(c, 1), :] = col_ref[q, pl.ds(c, 1), :] + jnp.sum(gm, axis=0, keepdims=True)
        return (prod * h, grad * h + gba_ref[0, c] * prod)

    _loop(count, backward, (ones, zeros))


def _spec(kind, shape):
    if kind == "dense":
        return pl.BlockSpec((1,) + tuple(shape[1:]), lambda k, pos: (k, 0, 0, 0))
    if kind == "column":
        return pl.BlockSpec((1,) + tuple(shape[1:]), lambda k, pos: (pos[2 * k + 1], 0, 0))
    return pl.BlockSpec(tuple(shape), lambda k, pos: (0,) * len(shape))


def _call(kernel, pos, inputs, outputs, scratch=()):
    from jax.experimental.pallas import tpu as pltpu

    dense = [a for kind, a in inputs if kind == "dense"][0]
    grid_spec = pltpu.PrefetchScalarGridSpec(
        num_scalar_prefetch=1,
        grid=(dense.shape[0],),
        in_specs=[_spec(kind, a.shape) for kind, a in inputs],
        out_specs=[_spec(kind, o.shape) for kind, o in outputs],
        scratch_shapes=list(scratch),
    )
    return pl.pallas_call(
        kernel,
        grid_spec=grid_spec,
        out_shape=[o for kind, o in outputs],
    )(pos, *[a for kind, a in inputs])


def _vmem(shape):
    from jax.experimental.pallas import tpu as pltpu

    return pltpu.VMEM(shape, F32)


def fwd_products(pos, spread, u, ew, blocks):
    k, c, r, s = ew.shape
    has_u = u is not None
    inputs = [("column", spread)] + ([("dense", u)] if has_u else []) + [("dense", ew)]
    outs = [
        ("dense", jax.ShapeDtypeStruct(ew.shape, F32)),
        ("full", jax.ShapeDtypeStruct((k, r, s), F32)),
        ("full", jax.ShapeDtypeStruct((blocks, r, s), F32)),
        ("full", jax.ShapeDtypeStruct((k, r, s), F32)),
    ]
    return _call(
        functools.partial(_fwd_products_kernel, has_u, k, blocks),
        pos,
        inputs,
        outs,
        [_vmem((c, r, s))],
    )


def fwd_messages(pos, ba, sign, here, others, ew, col_blocks):
    k, c, r, s = ba.shape
    inputs = [("dense", ba), ("full", sign), ("full", here), ("full", others), ("dense", ew)]
    outs = [
        ("dense", jax.ShapeDtypeStruct(ba.shape, F32)),
        ("full", jax.ShapeDtypeStruct((col_blocks, c, s), F32)),
    ]
    return _call(functools.partial(_fwd_messages_kernel, k), pos, inputs, outs)


def bwd_messages(pos, gsp, gm, ba, sign, here, others, ew, acc):
    k, c, r, s = ba.shape
    has_next = gm is not None
    has_acc = acc is not None
    inputs = (
        [("column", gsp)]
        + ([("dense", gm)] if has_next else [])
        + [("dense", ba), ("full", sign), ("full", here), ("full", others), ("dense", ew)]
        + ([("dense", acc)] if has_acc else [])
    )
    outs = [
        ("dense", jax.ShapeDtypeStruct(ba.shape, F32)),
        ("dense", jax.ShapeDtypeStruct(ba.shape, F32)),
        ("full", jax.ShapeDtypeStruct(here.shape, F32)),
        ("full", jax.ShapeDtypeStruct(others.shape, F32)),
    ]
    return _call(functools.partial(_bwd_messages_kernel, has_next, has_acc, k), pos, inputs, outs)


def bwd_products(pos, spread, u, ew, gba, grows, ghere, whole, here, col_blocks, emit_gm):
    k, c, r, s = ew.shape
    has_u = u is not None
    inputs = [("column", spread)] + ([("dense", u)] if has_u else []) + [
        ("dense", ew),
        ("dense", gba),
        ("full", grows),
        ("full", ghere),
        ("full", whole),
        ("full", here),
    ]
    outs = ([("dense", jax.ShapeDtypeStruct(ew.shape, F32))] if emit_gm else []) + [
        ("full", jax.ShapeDtypeStruct((col_blocks, c, s), F32))
    ]
    results = _call(
        functools.partial(_bwd_products_kernel, has_u, emit_gm, k),
        pos,
        inputs,
        outs,
        [_vmem((c, r, s)) for _ in range(3)],
    )
    if emit_gm:
        return results[0], results[1]
    return None, results[0]


def pick(hot, values):
    parts = []
    for k in range(hot.shape[0]):
        value = jnp.zeros_like(values[0])
        for j in range(hot.shape[1]):
            value = value + jnp.where(hot[k, j] > 0, values[j], 0.0)
        parts.append(value)
    return jnp.stack(parts)


def place(hot, values):
    parts = []
    for j in range(hot.shape[1]):
        value = jnp.zeros_like(values[0])
        for k in range(hot.shape[0]):
            value = value + jnp.where(hot[k, j] > 0, values[k], 0.0)
        parts.append(value)
    return jnp.stack(parts)


def combine(whole, row_hot, same_row):
    slots = whole.shape[0]
    blocks = row_hot.shape[1]
    ones = jnp.ones_like(whole[0])
    rows = []
    for block in range(blocks):
        value = ones
        for k in range(slots):
            value = value * jnp.where(row_hot[k, block] > 0, whole[k], 1.0)
        rows.append(value)
    others_here = []
    for k in range(slots):
        value = ones
        for other in range(slots):
            if other != k:
                value = value * jnp.where(same_row[k, other], whole[other], 1.0)
        others_here.append(value)
    return jnp.stack(rows), jnp.stack(others_here)


def _power_of_two(n):
    return n > 1 and (n & (n - 1)) == 0


def _swap(value, axis, n, step):
    perm = [(j, j ^ (1 << step)) for j in range(n)]
    return lax.ppermute(value, axis, perm)


def checks_total(values, n):
    if not _power_of_two(n):
        return lax.psum(values, "chk")
    step = 0
    while (1 << step) < n:
        values = values + _swap(values, "chk", n, step)
        step += 1
    return values


def others_uniform(rows, check_blocks, n, shape):
    others, trail = others_forward(rows.reshape(-1, shape[2]), check_blocks, n)
    grow = lambda value: jnp.broadcast_to(value.reshape(shape[:2] + (1,)), shape)
    trail = [tuple(grow(value) for value in entry) for entry in trail]
    return grow(others), trail


def others_forward(rows, check_blocks, n):
    if not _power_of_two(n):
        return others_gather(rows, check_blocks)
    full = rows
    excl = jnp.ones_like(rows)
    trail = []
    step = 0
    while (1 << step) < n:
        other = _swap(full, "var", n, step)
        trail.append((full, excl, other))
        excl = excl * other
        full = full * other
        step += 1
    return excl, trail


def others_backward(trail, grads, check_blocks, n):
    if not _power_of_two(n):
        return others_scatter(trail, grads, check_blocks)
    spread = grads
    target = jnp.zeros_like(grads)
    for step, (full, excl, other) in enumerate(trail):
        other_spread = _swap(spread, "var", n, step)
        target = target * other + excl * other_spread
        spread = spread * other + other_spread * full
    return target


def others_gather(rows, check_blocks):
    own = lax.axis_index("var")
    piece = lax.all_gather(rows, "var", axis=0, tiled=True)
    indices = jnp.arange(piece.shape[0], dtype=jnp.int32)
    keep = indices // check_blocks != own
    parts = []
    for block in range(check_blocks):
        pick = (keep & (indices % check_blocks == block))[:, None, None]
        parts.append(jnp.prod(jnp.where(pick, piece, 1.0), axis=0))
    return jnp.stack(parts), piece


def others_scatter(row_piece, grads, check_blocks):
    own = lax.axis_index("var")
    grad_piece = lax.all_gather(grads, "var", axis=0, tiled=True)
    indices = jnp.arange(row_piece.shape[0], dtype=jnp.int32)
    keep = indices // check_blocks != own
    new_sums = []
    for block in range(check_blocks):
        pick = (keep & (indices % check_blocks == block))[:, None, None]
        factors = jnp.where(pick, row_piece, 1.0)
        weights = jnp.where(pick, grad_piece, 0.0)
        before, after, whole = exclusive_both(factors, 0)
        new_sums.append(jnp.sum(weights * before * after, axis=0))
    return jnp.stack(new_sums)


def body(n_chk, n_var, tile_bits, tile_pos, tile_count, edge_weight, syndrome, channel_prior, out_cot):
    slot_total = tile_bits.shape[2]
    shots = syndrome.shape[1]
    check_blocks = syndrome.shape[0] // TILE
    column_blocks = channel_prior.shape[0] // TILE
    edge, row_hot, col_hot, same_row = device_tables(
        tile_bits[0, 0], tile_pos[0, 0], tile_count[0, 0], check_blocks, column_blocks
    )
    weight = edge_weight[0, 0].reshape(slot_total, TILE, TILE)
    edge_t = jnp.swapaxes(edge, 1, 2)
    filled = jnp.any(edge_t > 0, axis=2)
    order = jnp.argsort(jnp.where(filled, 0, 1).astype(jnp.int32), axis=1, stable=True)
    pos = jnp.concatenate(
        [
            tile_pos[0, 0].reshape(slot_total * 2),
            jnp.sum(filled.astype(jnp.int32), axis=1),
            order.astype(jnp.int32).reshape(slot_total * TILE),
        ]
    )
    dense = (slot_total, TILE, TILE, shots)
    ew = jnp.broadcast_to((edge_t * jnp.swapaxes(weight, 1, 2))[..., None], dense)
    sign_dev = (1.0 - 2.0 * syndrome.astype(jnp.float32)).reshape(check_blocks, TILE, shots)
    sign_slot = jnp.einsum("kc,crs->krs", row_hot, sign_dev, precision=EXACT)
    prior_dev = channel_prior.reshape(column_blocks, TILE)
    spread = jnp.broadcast_to(prior_dev[:, :, None], (column_blocks, TILE, shots))
    uniform = _power_of_two(n_var) and (check_blocks * TILE) % shots == 0
    if uniform:
        prior_slot = pick(col_hot, prior_dev)
        first = jnp.where(edge_t > 0, jnp.tanh(0.5 * prior_slot[:, :, None]), 1.0)
        first_rows = combine(jnp.prod(first, axis=1), row_hot, same_row)[0]
        first_others = others_uniform(
            first_rows, check_blocks, n_var, (check_blocks, TILE, shots)
        )
    u = None
    saved = []
    total = None
    for step in range(ITERS):
        ba, whole, rows, others_here = fwd_products(pos, spread, u, ew, check_blocks)
        if step == 0 and uniform:
            others, trail = first_others
        else:
            others, trail = others_forward(rows, check_blocks, n_var)
        saved.append((spread, u, ba, whole, others_here, others, trail))
        u, column = fwd_messages(pos, ba, sign_slot, others_here, others, ew, column_blocks)
        if step + 1 < ITERS:
            total = prior_dev[:, :, None] + checks_total(column, n_chk)
            spread = total
    last_column = column

    grad_total = out_cot.reshape(column_blocks, TILE, shots)
    prior_grad = jnp.zeros((column_blocks, TILE), jnp.float32)
    grad_m = None
    acc = None
    for step in reversed(range(ITERS)):
        spread_t, u_prev, ba, whole, others_here, others, trail = saved[step]
        prior_grad = prior_grad + jnp.sum(grad_total, axis=2)
        acc, grad_ba, grad_here, grad_others = bwd_messages(
            pos, grad_total, grad_m, ba, sign_slot, others_here, others, ew, acc
        )
        if step + 1 == ITERS:
            last_column, grad_ba = lax.optimization_barrier((last_column, grad_ba))
            total = prior_dev[:, :, None] + checks_total(last_column, n_chk)
            marginals = total.reshape(column_blocks * TILE, shots)
        grad_rows = others_backward(trail, grad_others, check_blocks, n_var)
        grad_m, column = bwd_products(
            pos, spread_t, u_prev, ew, grad_ba, grad_rows, grad_here, whole, others_here,
            column_blocks, step > 0,
        )
        if step > 0:
            grad_total = checks_total(column, n_chk)
    shot_sums = jnp.sum(column, axis=2)
    if (column_blocks * TILE) % 128 == 0:
        shot_sums = checks_total(shot_sums.reshape(-1, 128), n_chk).reshape(column_blocks, TILE)
    else:
        shot_sums = checks_total(shot_sums, n_chk)
    prior_grad = prior_grad + shot_sums
    weight_grad = jnp.where(edge > 0, jnp.swapaxes(jnp.sum(acc, axis=3), 1, 2), 0.0)
    return (
        marginals,
        weight_grad.reshape(1, 1, slot_total, TILE * TILE),
        prior_grad.reshape(column_blocks * TILE),
    )


def solution(mesh):
    placed = (
        P("chk", "var", None, None),
        P("chk", "var", None, None),
        P("chk", "var"),
        P("chk", "var", None, None),
        P("chk", None),
        P("var"),
        P("var", None),
    )
    return jax.shard_map(
        functools.partial(body, mesh.shape["chk"], mesh.shape["var"]),
        mesh=mesh,
        in_specs=placed,
        out_specs=(P("var", None), P("chk", "var", None, None), P("var")),
        check_vma=False,
    )
```

```python
import functools

import jax
import jax.numpy as jnp
from jax import lax
from jax.experimental import pallas as pl
from jax.sharding import PartitionSpec as P

TILE = 64
ITERS = 2


DAMP = 0.97
EXACT = lax.Precision.HIGHEST
F32 = jnp.float32
UNROLL = 4


def linear_both(values, axis):
    length = values.shape[axis]
    pieces = [lax.slice_in_dim(values, index, index + 1, axis=axis) for index in range(length)]
    ones = jnp.ones_like(pieces[0])
    prefix = [ones]
    for index in range(length - 1):
        prefix.append(prefix[-1] * pieces[index])
    suffix = [ones]
    for index in range(length - 1, 0, -1):
        suffix.append(suffix[-1] * pieces[index])
    suffix = suffix[::-1]
    whole = prefix[-1] * pieces[-1]
    return (jnp.concatenate(prefix, axis=axis), jnp.concatenate(suffix, axis=axis), whole)


def exclusive_both(values, axis):
    length = values.shape[axis]
    if length < 16 or length % 8 != 0:
        return linear_both(values, axis)
    shape = values.shape
    split = values.reshape(shape[:axis] + (length // 8, 8) + shape[axis + 1 :])
    inner_before, inner_after, group_whole = linear_both(split, axis + 1)
    outer_before, outer_after, whole = exclusive_both(group_whole, axis)
    before = (inner_before * outer_before).reshape(shape)
    after = (inner_after * outer_after).reshape(shape)
    whole = whole.reshape(shape[:axis] + (1,) + shape[axis + 1 :])
    return (before, after, whole)


def device_tables(bits, positions, count, check_blocks, column_blocks):
    slot_total = bits.shape[0]
    slots = jnp.arange(slot_total, dtype=jnp.int32)
    live = slots < count
    edge = jnp.where(live[:, None], bits, 0).astype(jnp.float32).reshape(slot_total, TILE, TILE)
    row_hot = (positions[:, 0:1] == jnp.arange(check_blocks, dtype=jnp.int32)[None, :]).astype(
        jnp.float32
    )
    col_hot = (positions[:, 1:2] == jnp.arange(column_blocks, dtype=jnp.int32)[None, :]).astype(
        jnp.float32
    )
    same_row = (positions[:, None, 0] == positions[None, :, 0]) & (slots[:, None] != slots[None, :])
    return (edge, row_hot, col_hot, same_row)


def _spread_row(ref, c, shape):
    return jnp.broadcast_to(ref[0, pl.ds(c, 1), :], shape)


def _row_block(pos_ref, k):
    return pos_ref[2 * k]


def _col_block(pos_ref, k):
    return pos_ref[2 * k + 1]


def _columns(pos_ref, k, slots, n_c):
    return pos_ref[2 * slots + k], 3 * slots + k * n_c


def _loop(count, body, init):
    def group(j, carry):
        for t in range(UNROLL):
            carry = body(UNROLL * j + t, carry)
        return carry

    carry = lax.fori_loop(0, count // UNROLL, group, init)
    return lax.fori_loop(UNROLL * (count // UNROLL), count, body, carry)


def _fwd_products_kernel(has_u, slots, blocks, pos_ref, *refs):
    refs = list(refs)
    spread_ref = refs.pop(0)
    u_ref = refs.pop(0) if has_u else None
    ew_ref, ba_ref, whole_ref, rows_ref, here_ref, h_scr = refs
    k = pl.program_id(0)
    n_c = ew_ref.shape[1]
    shape = ew_ref.shape[2:]

    count, base = _columns(pos_ref, k, slots, n_c)

    def forward(i, carry):
        c = pos_ref[base + i]
        m = _spread_row(spread_ref, c, shape)
        if has_u:
            m = m - u_ref[0, c]
        h = jnp.where(ew_ref[0, c] > 0, jnp.tanh(0.5 * m), 1.0)
        h_scr[c] = h
        ba_ref[0, c] = carry
        return carry * h

    whole = _loop(count, forward, jnp.ones(shape, F32))
    whole_ref[k] = whole

    def backward(i, carry):
        c = pos_ref[base + count - 1 - i]
        ba_ref[0, c] = ba_ref[0, c] * carry
        return carry * h_scr[c]

    _loop(count, backward, jnp.ones(shape, F32))

    @pl.when(k == slots - 1)
    def _():
        wholes = [whole_ref[j] for j in range(slots)]
        rows_of = [_row_block(pos_ref, j) for j in range(slots)]
        for block in range(blocks):
            value = jnp.ones(shape, F32)
            for j in range(slots):
                value = value * jnp.where(rows_of[j] == block, wholes[j], 1.0)
            rows_ref[block] = value
        for j in range(slots):
            value = jnp.ones(shape, F32)
            for other in range(slots):
                if other != j:
                    value = value * jnp.where(rows_of[other] == rows_of[j], wholes[other], 1.0)
            here_ref[j] = value


def _fwd_messages_kernel(slots, pos_ref, ba_ref, sign_ref, here_ref, others_ref, ew_ref, u_ref, col_ref):
    k = pl.program_id(0)
    n_c = ba_ref.shape[1]
    count, base = _columns(pos_ref, k, slots, n_c)

    @pl.when(k == 0)
    def _():
        col_ref[...] = jnp.zeros(col_ref.shape, F32)

    f = sign_ref[k] * here_ref[k] * others_ref[_row_block(pos_ref, k)]
    q = _col_block(pos_ref, k)

    def body(i, carry):
        c = pos_ref[base + i]
        x = ba_ref[0, c] * f
        u = ew_ref[0, c] * jnp.log((1.0 + DAMP * x) / (1.0 - DAMP * x))
        u_ref[0, c] = u
        col_ref[q, pl.ds(c, 1), :] = col_ref[q, pl.ds(c, 1), :] + jnp.sum(u, axis=0, keepdims=True)
        return carry

    _loop(count, body, 0)


def _bwd_messages_kernel(has_next, has_acc, slots, pos_ref, *refs):
    refs = list(refs)
    gsp_ref = refs.pop(0)
    gm_ref = refs.pop(0) if has_next else None
    ba_ref, sign_ref, here_ref, others_ref, ew_ref = refs[:5]
    refs = refs[5:]
    acc_ref = refs.pop(0) if has_acc else None
    gw_ref, gba_ref, ghere_ref, gothers_ref = refs
    k = pl.program_id(0)
    n_c = ba_ref.shape[1]
    shape = ba_ref.shape[2:]

    @pl.when(k == 0)
    def _():
        gothers_ref[...] = jnp.zeros(gothers_ref.shape, F32)

    p = _row_block(pos_ref, k)
    sign = sign_ref[k]
    here = here_ref[k]
    others = others_ref[p]
    f = sign * here * others
    count, base = _columns(pos_ref, k, slots, n_c)

    def body(i, total):
        c = pos_ref[base + i]
        gu = _spread_row(gsp_ref, c, shape)
        if has_next:
            gu = gu - gm_ref[0, c]
        ba = ba_ref[0, c]
        x = ba * f
        low = 1.0 - DAMP * x
        high = 1.0 + DAMP * x
        gw = gu * jnp.log(high / low)
        if has_acc:
            gw = gw + acc_ref[0, c]
        gw_ref[0, c] = gw
        gx = gu * ew_ref[0, c] * ((2.0 * DAMP) / (low * high))
        gba_ref[0, c] = gx * f
        return total + gx * ba

    grad_factor = _loop(count, body, jnp.zeros(shape, F32))
    ghere_ref[k] = grad_factor * sign * others
    gothers_ref[p] = gothers_ref[p] + grad_factor * sign * here


def _bwd_products_kernel(has_u, emit_gm, slots, pos_ref, *refs):
    refs = list(refs)
    spread_ref = refs.pop(0)
    u_ref = refs.pop(0) if has_u else None
    ew_ref, gba_ref, grows_ref, ghere_ref, whole_ref, here_ref = refs[:6]
    refs = refs[6:]
    gm_ref = refs.pop(0) if emit_gm else None
    col_ref, h_scr, p_scr, q_scr = refs
    k = pl.program_id(0)
    n_c = ew_ref.shape[1]
    shape = ew_ref.shape[2:]

    @pl.when(k == 0)
    def _():
        col_ref[...] = jnp.zeros(col_ref.shape, F32)

    p = _row_block(pos_ref, k)
    q = _col_block(pos_ref, k)
    rows_of = [_row_block(pos_ref, j) for j in range(slots)]
    gwh = grows_ref[p] * here_ref[k]
    for other in range(slots):
        term = jnp.where(rows_of[other] == p, ghere_ref[other], 0.0)
        for third in range(slots):
            if third != other:
                term = term * jnp.where(
                    (rows_of[third] == p) & (third != k), whole_ref[third], 1.0
                )
        gwh = gwh + jnp.where(other != k, term, 0.0)

    count, base = _columns(pos_ref, k, slots, n_c)

    def forward(i, carry):
        prod, grad = carry
        c = pos_ref[base + i]
        m = _spread_row(spread_ref, c, shape)
        if has_u:
            m = m - u_ref[0, c]
        h = jnp.where(ew_ref[0, c] > 0, jnp.tanh(0.5 * m), 1.0)
        h_scr[c] = h
        p_scr[c] = prod
        q_scr[c] = grad
        return (prod * h, grad * h + gba_ref[0, c] * prod)

    ones = jnp.ones(shape, F32)
    zeros = jnp.zeros(shape, F32)
    _loop(count, forward, (ones, zeros))

    def backward(i, carry):
        prod, grad = carry
        c = pos_ref[base + count - 1 - i]
        h = h_scr[c]
        before = p_scr[c]
        gh = q_scr[c] * prod + before * (grad + gwh * prod)
        gm = jnp.where(ew_ref[0, c] > 0, gh * (0.5 * (1.0 - h * h)), 0.0)
        if emit_gm:
            gm_ref[0, c] = gm
        col_ref[q, pl.ds(c, 1), :] = col_ref[q, pl.ds(c, 1), :] + jnp.sum(gm, axis=0, keepdims=True)
        return (prod * h, grad * h + gba_ref[0, c] * prod)

    _loop(count, backward, (ones, zeros))


def _spec(kind, shape):
    if kind == "dense":
        return pl.BlockSpec((1,) + tuple(shape[1:]), lambda k, pos: (k, 0, 0, 0))
    if kind == "column":
        return pl.BlockSpec((1,) + tuple(shape[1:]), lambda k, pos: (pos[2 * k + 1], 0, 0))
    return pl.BlockSpec(tuple(shape), lambda k, pos: (0,) * len(shape))


def _call(kernel, pos, inputs, outputs, scratch=()):
    from jax.experimental.pallas import tpu as pltpu

    dense = [a for kind, a in inputs if kind == "dense"][0]
    grid_spec = pltpu.PrefetchScalarGridSpec(
        num_scalar_prefetch=1,
        grid=(dense.shape[0],),
        in_specs=[_spec(kind, a.shape) for kind, a in inputs],
        out_specs=[_spec(kind, o.shape) for kind, o in outputs],
        scratch_shapes=list(scratch),
    )
    return pl.pallas_call(
        kernel,
        grid_spec=grid_spec,
        out_shape=[o for kind, o in outputs],
    )(pos, *[a for kind, a in inputs])


def _vmem(shape):
    from jax.experimental.pallas import tpu as pltpu

    return pltpu.VMEM(shape, F32)


def fwd_products(pos, spread, u, ew, blocks):
    k, c, r, s = ew.shape
    has_u = u is not None
    inputs = [("column", spread)] + ([("dense", u)] if has_u else []) + [("dense", ew)]
    outs = [
        ("dense", jax.ShapeDtypeStruct(ew.shape, F32)),
        ("full", jax.ShapeDtypeStruct((k, r, s), F32)),
        ("full", jax.ShapeDtypeStruct((blocks, r, s), F32)),
        ("full", jax.ShapeDtypeStruct((k, r, s), F32)),
    ]
    return _call(
        functools.partial(_fwd_products_kernel, has_u, k, blocks),
        pos,
        inputs,
        outs,
        [_vmem((c, r, s))],
    )


def fwd_messages(pos, ba, sign, here, others, ew, col_blocks):
    k, c, r, s = ba.shape
    inputs = [("dense", ba), ("full", sign), ("full", here), ("full", others), ("dense", ew)]
    outs = [
        ("dense", jax.ShapeDtypeStruct(ba.shape, F32)),
        ("full", jax.ShapeDtypeStruct((col_blocks, c, s), F32)),
    ]
    return _call(functools.partial(_fwd_messages_kernel, k), pos, inputs, outs)


def bwd_messages(pos, gsp, gm, ba, sign, here, others, ew, acc):
    k, c, r, s = ba.shape
    has_next = gm is not None
    has_acc = acc is not None
    inputs = (
        [("column", gsp)]
        + ([("dense", gm)] if has_next else [])
        + [("dense", ba), ("full", sign), ("full", here), ("full", others), ("dense", ew)]
        + ([("dense", acc)] if has_acc else [])
    )
    outs = [
        ("dense", jax.ShapeDtypeStruct(ba.shape, F32)),
        ("dense", jax.ShapeDtypeStruct(ba.shape, F32)),
        ("full", jax.ShapeDtypeStruct(here.shape, F32)),
        ("full", jax.ShapeDtypeStruct(others.shape, F32)),
    ]
    return _call(functools.partial(_bwd_messages_kernel, has_next, has_acc, k), pos, inputs, outs)


def bwd_products(pos, spread, u, ew, gba, grows, ghere, whole, here, col_blocks, emit_gm):
    k, c, r, s = ew.shape
    has_u = u is not None
    inputs = [("column", spread)] + ([("dense", u)] if has_u else []) + [
        ("dense", ew),
        ("dense", gba),
        ("full", grows),
        ("full", ghere),
        ("full", whole),
        ("full", here),
    ]
    outs = ([("dense", jax.ShapeDtypeStruct(ew.shape, F32))] if emit_gm else []) + [
        ("full", jax.ShapeDtypeStruct((col_blocks, c, s), F32))
    ]
    results = _call(
        functools.partial(_bwd_products_kernel, has_u, emit_gm, k),
        pos,
        inputs,
        outs,
        [_vmem((c, r, s)) for _ in range(3)],
    )
    if emit_gm:
        return results[0], results[1]
    return None, results[0]


def pick(hot, values):
    parts = []
    for k in range(hot.shape[0]):
        value = jnp.zeros_like(values[0])
        for j in range(hot.shape[1]):
            value = value + jnp.where(hot[k, j] > 0, values[j], 0.0)
        parts.append(value)
    return jnp.stack(parts)


def place(hot, values):
    parts = []
    for j in range(hot.shape[1]):
        value = jnp.zeros_like(values[0])
        for k in range(hot.shape[0]):
            value = value + jnp.where(hot[k, j] > 0, values[k], 0.0)
        parts.append(value)
    return jnp.stack(parts)


def combine(whole, row_hot, same_row):
    slots = whole.shape[0]
    blocks = row_hot.shape[1]
    ones = jnp.ones_like(whole[0])
    rows = []
    for block in range(blocks):
        value = ones
        for k in range(slots):
            value = value * jnp.where(row_hot[k, block] > 0, whole[k], 1.0)
        rows.append(value)
    others_here = []
    for k in range(slots):
        value = ones
        for other in range(slots):
            if other != k:
                value = value * jnp.where(same_row[k, other], whole[other], 1.0)
        others_here.append(value)
    return jnp.stack(rows), jnp.stack(others_here)


def _power_of_two(n):
    return n > 1 and (n & (n - 1)) == 0


def _swap(value, axis, n, step):
    perm = [(j, j ^ (1 << step)) for j in range(n)]
    return lax.ppermute(value, axis, perm)


def checks_total(values, n):
    if not _power_of_two(n):
        return lax.psum(values, "chk")
    step = 0
    while (1 << step) < n:
        values = values + _swap(values, "chk", n, step)
        step += 1
    return values


def others_forward(rows, check_blocks, n, uniform=False):
    if not _power_of_two(n):
        return others_gather(rows, check_blocks)
    if uniform:
        shape = rows.shape
        small = rows[:, :, 0].reshape(-1, shape[2])
        others, trail = others_forward(small, check_blocks, n)
        grow = lambda value: jnp.broadcast_to(value.reshape(shape[:2] + (1,)), shape)
        trail = [tuple(grow(value) for value in entry) for entry in trail]
        return grow(others), trail
    full = rows
    excl = jnp.ones_like(rows)
    trail = []
    step = 0
    while (1 << step) < n:
        other = _swap(full, "var", n, step)
        trail.append((full, excl, other))
        excl = excl * other
        full = full * other
        step += 1
    return excl, trail


def others_backward(trail, grads, check_blocks, n):
    if not _power_of_two(n):
        return others_scatter(trail, grads, check_blocks)
    spread = grads
    target = jnp.zeros_like(grads)
    for step, (full, excl, other) in enumerate(trail):
        other_spread = _swap(spread, "var", n, step)
        target = target * other + excl * other_spread
        spread = spread * other + other_spread * full
    return target


def others_gather(rows, check_blocks):
    own = lax.axis_index("var")
    piece = lax.all_gather(rows, "var", axis=0, tiled=True)
    indices = jnp.arange(piece.shape[0], dtype=jnp.int32)
    keep = indices // check_blocks != own
    parts = []
    for block in range(check_blocks):
        pick = (keep & (indices % check_blocks == block))[:, None, None]
        parts.append(jnp.prod(jnp.where(pick, piece, 1.0), axis=0))
    return jnp.stack(parts), piece


def others_scatter(row_piece, grads, check_blocks):
    own = lax.axis_index("var")
    grad_piece = lax.all_gather(grads, "var", axis=0, tiled=True)
    indices = jnp.arange(row_piece.shape[0], dtype=jnp.int32)
    keep = indices // check_blocks != own
    new_sums = []
    for block in range(check_blocks):
        pick = (keep & (indices % check_blocks == block))[:, None, None]
        factors = jnp.where(pick, row_piece, 1.0)
        weights = jnp.where(pick, grad_piece, 0.0)
        before, after, whole = exclusive_both(factors, 0)
        new_sums.append(jnp.sum(weights * before * after, axis=0))
    return jnp.stack(new_sums)


def body(n_chk, n_var, tile_bits, tile_pos, tile_count, edge_weight, syndrome, channel_prior, out_cot):
    slot_total = tile_bits.shape[2]
    shots = syndrome.shape[1]
    check_blocks = syndrome.shape[0] // TILE
    column_blocks = channel_prior.shape[0] // TILE
    edge, row_hot, col_hot, same_row = device_tables(
        tile_bits[0, 0], tile_pos[0, 0], tile_count[0, 0], check_blocks, column_blocks
    )
    weight = edge_weight[0, 0].reshape(slot_total, TILE, TILE)
    edge_t = jnp.swapaxes(edge, 1, 2)
    filled = jnp.any(edge_t > 0, axis=2)
    order = jnp.argsort(jnp.where(filled, 0, 1).astype(jnp.int32), axis=1, stable=True)
    pos = jnp.concatenate(
        [
            tile_pos[0, 0].reshape(slot_total * 2),
            jnp.sum(filled.astype(jnp.int32), axis=1),
            order.astype(jnp.int32).reshape(slot_total * TILE),
        ]
    )
    dense = (slot_total, TILE, TILE, shots)
    ew = jnp.broadcast_to((edge_t * jnp.swapaxes(weight, 1, 2))[..., None], dense)
    sign_dev = (1.0 - 2.0 * syndrome.astype(jnp.float32)).reshape(check_blocks, TILE, shots)
    sign_slot = jnp.einsum("kc,crs->krs", row_hot, sign_dev, precision=EXACT)
    prior_dev = channel_prior.reshape(column_blocks, TILE)
    spread = jnp.broadcast_to(prior_dev[:, :, None], (column_blocks, TILE, shots))
    u = None
    saved = []
    total = None
    for step in range(ITERS):
        ba, whole, rows, others_here = fwd_products(pos, spread, u, ew, check_blocks)
        others, trail = others_forward(rows, check_blocks, n_var, uniform=(step == 0 and (check_blocks * TILE) % shots == 0))
        saved.append((spread, u, ba, whole, others_here, others, trail))
        u, column = fwd_messages(pos, ba, sign_slot, others_here, others, ew, column_blocks)
        if step + 1 < ITERS:
            total = prior_dev[:, :, None] + checks_total(column, n_chk)
            spread = total
    last_column = column

    grad_total = out_cot.reshape(column_blocks, TILE, shots)
    prior_grad = jnp.zeros((column_blocks, TILE), jnp.float32)
    grad_m = None
    acc = None
    for step in reversed(range(ITERS)):
        spread_t, u_prev, ba, whole, others_here, others, trail = saved[step]
        prior_grad = prior_grad + jnp.sum(grad_total, axis=2)
        acc, grad_ba, grad_here, grad_others = bwd_messages(
            pos, grad_total, grad_m, ba, sign_slot, others_here, others, ew, acc
        )
        if step + 1 == ITERS:
            last_column, grad_ba = lax.optimization_barrier((last_column, grad_ba))
            total = prior_dev[:, :, None] + checks_total(last_column, n_chk)
            marginals = total.reshape(column_blocks * TILE, shots)
        grad_rows = others_backward(trail, grad_others, check_blocks, n_var)
        grad_m, column = bwd_products(
            pos, spread_t, u_prev, ew, grad_ba, grad_rows, grad_here, whole, others_here,
            column_blocks, step > 0,
        )
        if step > 0:
            grad_total = checks_total(column, n_chk)
    shot_sums = jnp.sum(column, axis=2)
    if (column_blocks * TILE) % 128 == 0:
        shot_sums = checks_total(shot_sums.reshape(-1, 128), n_chk).reshape(column_blocks, TILE)
    else:
        shot_sums = checks_total(shot_sums, n_chk)
    prior_grad = prior_grad + shot_sums
    weight_grad = jnp.where(edge > 0, jnp.swapaxes(jnp.sum(acc, axis=3), 1, 2), 0.0)
    return (
        marginals,
        weight_grad.reshape(1, 1, slot_total, TILE * TILE),
        prior_grad.reshape(column_blocks * TILE),
    )


def solution(mesh):
    placed = (
        P("chk", "var", None, None),
        P("chk", "var", None, None),
        P("chk", "var"),
        P("chk", "var", None, None),
        P("chk", None),
        P("var"),
        P("var", None),
    )
    return jax.shard_map(
        functools.partial(body, mesh.shape["chk"], mesh.shape["var"]),
        mesh=mesh,
        in_specs=placed,
        out_specs=(P("var", None), P("chk", "var", None, None), P("var")),
        check_vma=False,
    )
```

```python
import functools

import jax
import jax.numpy as jnp
from jax import lax
from jax.experimental import pallas as pl
from jax.sharding import PartitionSpec as P

TILE = 64
ITERS = 2


DAMP = 0.97
EXACT = lax.Precision.HIGHEST
F32 = jnp.float32
UNROLL = 8


def linear_both(values, axis):
    length = values.shape[axis]
    pieces = [lax.slice_in_dim(values, index, index + 1, axis=axis) for index in range(length)]
    ones = jnp.ones_like(pieces[0])
    prefix = [ones]
    for index in range(length - 1):
        prefix.append(prefix[-1] * pieces[index])
    suffix = [ones]
    for index in range(length - 1, 0, -1):
        suffix.append(suffix[-1] * pieces[index])
    suffix = suffix[::-1]
    whole = prefix[-1] * pieces[-1]
    return (jnp.concatenate(prefix, axis=axis), jnp.concatenate(suffix, axis=axis), whole)


def exclusive_both(values, axis):
    length = values.shape[axis]
    if length < 16 or length % 8 != 0:
        return linear_both(values, axis)
    shape = values.shape
    split = values.reshape(shape[:axis] + (length // 8, 8) + shape[axis + 1 :])
    inner_before, inner_after, group_whole = linear_both(split, axis + 1)
    outer_before, outer_after, whole = exclusive_both(group_whole, axis)
    before = (inner_before * outer_before).reshape(shape)
    after = (inner_after * outer_after).reshape(shape)
    whole = whole.reshape(shape[:axis] + (1,) + shape[axis + 1 :])
    return (before, after, whole)


def device_tables(bits, positions, count, check_blocks, column_blocks):
    slot_total = bits.shape[0]
    slots = jnp.arange(slot_total, dtype=jnp.int32)
    live = slots < count
    edge = jnp.where(live[:, None], bits, 0).astype(jnp.float32).reshape(slot_total, TILE, TILE)
    row_hot = (positions[:, 0:1] == jnp.arange(check_blocks, dtype=jnp.int32)[None, :]).astype(
        jnp.float32
    )
    col_hot = (positions[:, 1:2] == jnp.arange(column_blocks, dtype=jnp.int32)[None, :]).astype(
        jnp.float32
    )
    same_row = (positions[:, None, 0] == positions[None, :, 0]) & (slots[:, None] != slots[None, :])
    return (edge, row_hot, col_hot, same_row)


def _spread_row(ref, c, shape):
    return jnp.broadcast_to(ref[0, pl.ds(c, 1), :], shape)


def _row_block(pos_ref, k):
    return pos_ref[2 * k]


def _col_block(pos_ref, k):
    return pos_ref[2 * k + 1]


def _columns(pos_ref, k, slots, n_c):
    return pos_ref[2 * slots + k], 3 * slots + k * n_c


def _loop(count, body, init):
    def group(j, carry):
        for t in range(UNROLL):
            carry = body(UNROLL * j + t, carry)
        return carry

    carry = lax.fori_loop(0, count // UNROLL, group, init)
    return lax.fori_loop(UNROLL * (count // UNROLL), count, body, carry)


def _fwd_products_kernel(has_u, slots, blocks, pos_ref, *refs):
    refs = list(refs)
    spread_ref = refs.pop(0)
    u_ref = refs.pop(0) if has_u else None
    ew_ref, ba_ref, whole_ref, rows_ref, here_ref, h_scr = refs
    k = pl.program_id(0)
    n_c = ew_ref.shape[1]
    shape = ew_ref.shape[2:]

    count, base = _columns(pos_ref, k, slots, n_c)

    def forward(i, carry):
        c = pos_ref[base + i]
        m = _spread_row(spread_ref, c, shape)
        if has_u:
            m = m - u_ref[0, c]
        h = jnp.where(ew_ref[0, c] > 0, jnp.tanh(0.5 * m), 1.0)
        h_scr[c] = h
        ba_ref[0, c] = carry
        return carry * h

    whole = _loop(count, forward, jnp.ones(shape, F32))
    whole_ref[k] = whole

    def backward(i, carry):
        c = pos_ref[base + count - 1 - i]
        ba_ref[0, c] = ba_ref[0, c] * carry
        return carry * h_scr[c]

    _loop(count, backward, jnp.ones(shape, F32))

    @pl.when(k == slots - 1)
    def _():
        wholes = [whole_ref[j] for j in range(slots)]
        rows_of = [_row_block(pos_ref, j) for j in range(slots)]
        for block in range(blocks):
            value = jnp.ones(shape, F32)
            for j in range(slots):
                value = value * jnp.where(rows_of[j] == block, wholes[j], 1.0)
            rows_ref[block] = value
        for j in range(slots):
            value = jnp.ones(shape, F32)
            for other in range(slots):
                if other != j:
                    value = value * jnp.where(rows_of[other] == rows_of[j], wholes[other], 1.0)
            here_ref[j] = value


def _fwd_messages_kernel(slots, pos_ref, ba_ref, sign_ref, here_ref, others_ref, ew_ref, u_ref, col_ref):
    k = pl.program_id(0)
    n_c = ba_ref.shape[1]
    count, base = _columns(pos_ref, k, slots, n_c)

    @pl.when(k == 0)
    def _():
        col_ref[...] = jnp.zeros(col_ref.shape, F32)

    f = sign_ref[k] * here_ref[k] * others_ref[_row_block(pos_ref, k)]
    q = _col_block(pos_ref, k)

    def body(i, carry):
        c = pos_ref[base + i]
        x = ba_ref[0, c] * f
        u = ew_ref[0, c] * jnp.log((1.0 + DAMP * x) / (1.0 - DAMP * x))
        u_ref[0, c] = u
        col_ref[q, pl.ds(c, 1), :] = col_ref[q, pl.ds(c, 1), :] + jnp.sum(u, axis=0, keepdims=True)
        return carry

    _loop(count, body, 0)


def _bwd_messages_kernel(has_next, has_acc, slots, pos_ref, *refs):
    refs = list(refs)
    gsp_ref = refs.pop(0)
    gm_ref = refs.pop(0) if has_next else None
    ba_ref, sign_ref, here_ref, others_ref, ew_ref = refs[:5]
    refs = refs[5:]
    acc_ref = refs.pop(0) if has_acc else None
    gw_ref, gba_ref, ghere_ref, gothers_ref = refs
    k = pl.program_id(0)
    n_c = ba_ref.shape[1]
    shape = ba_ref.shape[2:]

    @pl.when(k == 0)
    def _():
        gothers_ref[...] = jnp.zeros(gothers_ref.shape, F32)

    p = _row_block(pos_ref, k)
    sign = sign_ref[k]
    here = here_ref[k]
    others = others_ref[p]
    f = sign * here * others
    count, base = _columns(pos_ref, k, slots, n_c)

    def body(i, total):
        c = pos_ref[base + i]
        gu = _spread_row(gsp_ref, c, shape)
        if has_next:
            gu = gu - gm_ref[0, c]
        ba = ba_ref[0, c]
        x = ba * f
        low = 1.0 - DAMP * x
        high = 1.0 + DAMP * x
        gw = gu * jnp.log(high / low)
        if has_acc:
            gw = gw + acc_ref[0, c]
        gw_ref[0, c] = gw
        gx = gu * ew_ref[0, c] * ((2.0 * DAMP) / (low * high))
        gba_ref[0, c] = gx * f
        return total + gx * ba

    grad_factor = _loop(count, body, jnp.zeros(shape, F32))
    ghere_ref[k] = grad_factor * sign * others
    gothers_ref[p] = gothers_ref[p] + grad_factor * sign * here


def _bwd_products_kernel(has_u, emit_gm, slots, pos_ref, *refs):
    refs = list(refs)
    spread_ref = refs.pop(0)
    u_ref = refs.pop(0) if has_u else None
    ew_ref, gba_ref, grows_ref, ghere_ref, whole_ref, here_ref = refs[:6]
    refs = refs[6:]
    gm_ref = refs.pop(0) if emit_gm else None
    col_ref, h_scr, p_scr, q_scr = refs
    k = pl.program_id(0)
    n_c = ew_ref.shape[1]
    shape = ew_ref.shape[2:]

    @pl.when(k == 0)
    def _():
        col_ref[...] = jnp.zeros(col_ref.shape, F32)

    p = _row_block(pos_ref, k)
    q = _col_block(pos_ref, k)
    rows_of = [_row_block(pos_ref, j) for j in range(slots)]
    gwh = grows_ref[p] * here_ref[k]
    for other in range(slots):
        term = jnp.where(rows_of[other] == p, ghere_ref[other], 0.0)
        for third in range(slots):
            if third != other:
                term = term * jnp.where(
                    (rows_of[third] == p) & (third != k), whole_ref[third], 1.0
                )
        gwh = gwh + jnp.where(other != k, term, 0.0)

    count, base = _columns(pos_ref, k, slots, n_c)

    def forward(i, carry):
        prod, grad = carry
        c = pos_ref[base + i]
        m = _spread_row(spread_ref, c, shape)
        if has_u:
            m = m - u_ref[0, c]
        h = jnp.where(ew_ref[0, c] > 0, jnp.tanh(0.5 * m), 1.0)
        h_scr[c] = h
        p_scr[c] = prod
        q_scr[c] = grad
        return (prod * h, grad * h + gba_ref[0, c] * prod)

    ones = jnp.ones(shape, F32)
    zeros = jnp.zeros(shape, F32)
    _loop(count, forward, (ones, zeros))

    def backward(i, carry):
        prod, grad = carry
        c = pos_ref[base + count - 1 - i]
        h = h_scr[c]
        before = p_scr[c]
        gh = q_scr[c] * prod + before * (grad + gwh * prod)
        gm = jnp.where(ew_ref[0, c] > 0, gh * (0.5 * (1.0 - h * h)), 0.0)
        if emit_gm:
            gm_ref[0, c] = gm
        col_ref[q, pl.ds(c, 1), :] = col_ref[q, pl.ds(c, 1), :] + jnp.sum(gm, axis=0, keepdims=True)
        return (prod * h, grad * h + gba_ref[0, c] * prod)

    _loop(count, backward, (ones, zeros))


def _spec(kind, shape):
    if kind == "dense":
        return pl.BlockSpec((1,) + tuple(shape[1:]), lambda k, pos: (k, 0, 0, 0))
    if kind == "column":
        return pl.BlockSpec((1,) + tuple(shape[1:]), lambda k, pos: (pos[2 * k + 1], 0, 0))
    return pl.BlockSpec(tuple(shape), lambda k, pos: (0,) * len(shape))


def _call(kernel, pos, inputs, outputs, scratch=()):
    from jax.experimental.pallas import tpu as pltpu

    dense = [a for kind, a in inputs if kind == "dense"][0]
    grid_spec = pltpu.PrefetchScalarGridSpec(
        num_scalar_prefetch=1,
        grid=(dense.shape[0],),
        in_specs=[_spec(kind, a.shape) for kind, a in inputs],
        out_specs=[_spec(kind, o.shape) for kind, o in outputs],
        scratch_shapes=list(scratch),
    )
    return pl.pallas_call(
        kernel,
        grid_spec=grid_spec,
        out_shape=[o for kind, o in outputs],
    )(pos, *[a for kind, a in inputs])


def _vmem(shape):
    from jax.experimental.pallas import tpu as pltpu

    return pltpu.VMEM(shape, F32)


def fwd_products(pos, spread, u, ew, blocks):
    k, c, r, s = ew.shape
    has_u = u is not None
    inputs = [("column", spread)] + ([("dense", u)] if has_u else []) + [("dense", ew)]
    outs = [
        ("dense", jax.ShapeDtypeStruct(ew.shape, F32)),
        ("full", jax.ShapeDtypeStruct((k, r, s), F32)),
        ("full", jax.ShapeDtypeStruct((blocks, r, s), F32)),
        ("full", jax.ShapeDtypeStruct((k, r, s), F32)),
    ]
    return _call(
        functools.partial(_fwd_products_kernel, has_u, k, blocks),
        pos,
        inputs,
        outs,
        [_vmem((c, r, s))],
    )


def fwd_messages(pos, ba, sign, here, others, ew, col_blocks):
    k, c, r, s = ba.shape
    inputs = [("dense", ba), ("full", sign), ("full", here), ("full", others), ("dense", ew)]
    outs = [
        ("dense", jax.ShapeDtypeStruct(ba.shape, F32)),
        ("full", jax.ShapeDtypeStruct((col_blocks, c, s), F32)),
    ]
    return _call(functools.partial(_fwd_messages_kernel, k), pos, inputs, outs)


def bwd_messages(pos, gsp, gm, ba, sign, here, others, ew, acc):
    k, c, r, s = ba.shape
    has_next = gm is not None
    has_acc = acc is not None
    inputs = (
        [("column", gsp)]
        + ([("dense", gm)] if has_next else [])
        + [("dense", ba), ("full", sign), ("full", here), ("full", others), ("dense", ew)]
        + ([("dense", acc)] if has_acc else [])
    )
    outs = [
        ("dense", jax.ShapeDtypeStruct(ba.shape, F32)),
        ("dense", jax.ShapeDtypeStruct(ba.shape, F32)),
        ("full", jax.ShapeDtypeStruct(here.shape, F32)),
        ("full", jax.ShapeDtypeStruct(others.shape, F32)),
    ]
    return _call(functools.partial(_bwd_messages_kernel, has_next, has_acc, k), pos, inputs, outs)


def bwd_products(pos, spread, u, ew, gba, grows, ghere, whole, here, col_blocks, emit_gm):
    k, c, r, s = ew.shape
    has_u = u is not None
    inputs = [("column", spread)] + ([("dense", u)] if has_u else []) + [
        ("dense", ew),
        ("dense", gba),
        ("full", grows),
        ("full", ghere),
        ("full", whole),
        ("full", here),
    ]
    outs = ([("dense", jax.ShapeDtypeStruct(ew.shape, F32))] if emit_gm else []) + [
        ("full", jax.ShapeDtypeStruct((col_blocks, c, s), F32))
    ]
    results = _call(
        functools.partial(_bwd_products_kernel, has_u, emit_gm, k),
        pos,
        inputs,
        outs,
        [_vmem((c, r, s)) for _ in range(3)],
    )
    if emit_gm:
        return results[0], results[1]
    return None, results[0]


def pick(hot, values):
    parts = []
    for k in range(hot.shape[0]):
        value = jnp.zeros_like(values[0])
        for j in range(hot.shape[1]):
            value = value + jnp.where(hot[k, j] > 0, values[j], 0.0)
        parts.append(value)
    return jnp.stack(parts)


def place(hot, values):
    parts = []
    for j in range(hot.shape[1]):
        value = jnp.zeros_like(values[0])
        for k in range(hot.shape[0]):
            value = value + jnp.where(hot[k, j] > 0, values[k], 0.0)
        parts.append(value)
    return jnp.stack(parts)


def combine(whole, row_hot, same_row):
    slots = whole.shape[0]
    blocks = row_hot.shape[1]
    ones = jnp.ones_like(whole[0])
    rows = []
    for block in range(blocks):
        value = ones
        for k in range(slots):
            value = value * jnp.where(row_hot[k, block] > 0, whole[k], 1.0)
        rows.append(value)
    others_here = []
    for k in range(slots):
        value = ones
        for other in range(slots):
            if other != k:
                value = value * jnp.where(same_row[k, other], whole[other], 1.0)
        others_here.append(value)
    return jnp.stack(rows), jnp.stack(others_here)


def _power_of_two(n):
    return n > 1 and (n & (n - 1)) == 0


def _swap(value, axis, n, step):
    perm = [(j, j ^ (1 << step)) for j in range(n)]
    return lax.ppermute(value, axis, perm)


def checks_total(values, n):
    if not _power_of_two(n):
        return lax.psum(values, "chk")
    step = 0
    while (1 << step) < n:
        values = values + _swap(values, "chk", n, step)
        step += 1
    return values


def others_forward(rows, check_blocks, n, uniform=False):
    if not _power_of_two(n):
        return others_gather(rows, check_blocks)
    if uniform:
        shape = rows.shape
        small = rows[:, :, 0].reshape(-1, shape[2])
        others, trail = others_forward(small, check_blocks, n)
        grow = lambda value: jnp.broadcast_to(value.reshape(shape[:2] + (1,)), shape)
        trail = [tuple(grow(value) for value in entry) for entry in trail]
        return grow(others), trail
    full = rows
    excl = jnp.ones_like(rows)
    trail = []
    step = 0
    while (1 << step) < n:
        other = _swap(full, "var", n, step)
        trail.append((full, excl, other))
        excl = excl * other
        full = full * other
        step += 1
    return excl, trail


def others_backward(trail, grads, check_blocks, n):
    if not _power_of_two(n):
        return others_scatter(trail, grads, check_blocks)
    spread = grads
    target = jnp.zeros_like(grads)
    for step, (full, excl, other) in enumerate(trail):
        other_spread = _swap(spread, "var", n, step)
        target = target * other + excl * other_spread
        spread = spread * other + other_spread * full
    return target


def others_gather(rows, check_blocks):
    own = lax.axis_index("var")
    piece = lax.all_gather(rows, "var", axis=0, tiled=True)
    indices = jnp.arange(piece.shape[0], dtype=jnp.int32)
    keep = indices // check_blocks != own
    parts = []
    for block in range(check_blocks):
        pick = (keep & (indices % check_blocks == block))[:, None, None]
        parts.append(jnp.prod(jnp.where(pick, piece, 1.0), axis=0))
    return jnp.stack(parts), piece


def others_scatter(row_piece, grads, check_blocks):
    own = lax.axis_index("var")
    grad_piece = lax.all_gather(grads, "var", axis=0, tiled=True)
    indices = jnp.arange(row_piece.shape[0], dtype=jnp.int32)
    keep = indices // check_blocks != own
    new_sums = []
    for block in range(check_blocks):
        pick = (keep & (indices % check_blocks == block))[:, None, None]
        factors = jnp.where(pick, row_piece, 1.0)
        weights = jnp.where(pick, grad_piece, 0.0)
        before, after, whole = exclusive_both(factors, 0)
        new_sums.append(jnp.sum(weights * before * after, axis=0))
    return jnp.stack(new_sums)


def body(n_chk, n_var, tile_bits, tile_pos, tile_count, edge_weight, syndrome, channel_prior, out_cot):
    slot_total = tile_bits.shape[2]
    shots = syndrome.shape[1]
    check_blocks = syndrome.shape[0] // TILE
    column_blocks = channel_prior.shape[0] // TILE
    edge, row_hot, col_hot, same_row = device_tables(
        tile_bits[0, 0], tile_pos[0, 0], tile_count[0, 0], check_blocks, column_blocks
    )
    weight = edge_weight[0, 0].reshape(slot_total, TILE, TILE)
    edge_t = jnp.swapaxes(edge, 1, 2)
    filled = jnp.any(edge_t > 0, axis=2)
    order = jnp.argsort(jnp.where(filled, 0, 1).astype(jnp.int32), axis=1, stable=True)
    pos = jnp.concatenate(
        [
            tile_pos[0, 0].reshape(slot_total * 2),
            jnp.sum(filled.astype(jnp.int32), axis=1),
            order.astype(jnp.int32).reshape(slot_total * TILE),
        ]
    )
    dense = (slot_total, TILE, TILE, shots)
    ew = jnp.broadcast_to((edge_t * jnp.swapaxes(weight, 1, 2))[..., None], dense)
    sign_dev = (1.0 - 2.0 * syndrome.astype(jnp.float32)).reshape(check_blocks, TILE, shots)
    sign_slot = jnp.einsum("kc,crs->krs", row_hot, sign_dev, precision=EXACT)
    prior_dev = channel_prior.reshape(column_blocks, TILE)
    spread = jnp.broadcast_to(prior_dev[:, :, None], (column_blocks, TILE, shots))
    u = None
    saved = []
    total = None
    for step in range(ITERS):
        ba, whole, rows, others_here = fwd_products(pos, spread, u, ew, check_blocks)
        others, trail = others_forward(rows, check_blocks, n_var, uniform=(step == 0 and (check_blocks * TILE) % shots == 0))
        saved.append((spread, u, ba, whole, others_here, others, trail))
        u, column = fwd_messages(pos, ba, sign_slot, others_here, others, ew, column_blocks)
        if step + 1 < ITERS:
            total = prior_dev[:, :, None] + checks_total(column, n_chk)
            spread = total
    last_column = column

    grad_total = out_cot.reshape(column_blocks, TILE, shots)
    prior_grad = jnp.zeros((column_blocks, TILE), jnp.float32)
    grad_m = None
    acc = None
    for step in reversed(range(ITERS)):
        spread_t, u_prev, ba, whole, others_here, others, trail = saved[step]
        prior_grad = prior_grad + jnp.sum(grad_total, axis=2)
        acc, grad_ba, grad_here, grad_others = bwd_messages(
            pos, grad_total, grad_m, ba, sign_slot, others_here, others, ew, acc
        )
        if step + 1 == ITERS:
            last_column, grad_ba = lax.optimization_barrier((last_column, grad_ba))
            total = prior_dev[:, :, None] + checks_total(last_column, n_chk)
            marginals = total.reshape(column_blocks * TILE, shots)
        grad_rows = others_backward(trail, grad_others, check_blocks, n_var)
        grad_m, column = bwd_products(
            pos, spread_t, u_prev, ew, grad_ba, grad_rows, grad_here, whole, others_here,
            column_blocks, step > 0,
        )
        if step > 0:
            grad_total = checks_total(column, n_chk)
    shot_sums = jnp.sum(column, axis=2)
    if (column_blocks * TILE) % 128 == 0:
        shot_sums = checks_total(shot_sums.reshape(-1, 128), n_chk).reshape(column_blocks, TILE)
    else:
        shot_sums = checks_total(shot_sums, n_chk)
    prior_grad = prior_grad + shot_sums
    weight_grad = jnp.where(edge > 0, jnp.swapaxes(jnp.sum(acc, axis=3), 1, 2), 0.0)
    return (
        marginals,
        weight_grad.reshape(1, 1, slot_total, TILE * TILE),
        prior_grad.reshape(column_blocks * TILE),
    )


def solution(mesh):
    placed = (
        P("chk", "var", None, None),
        P("chk", "var", None, None),
        P("chk", "var"),
        P("chk", "var", None, None),
        P("chk", None),
        P("var"),
        P("var", None),
    )
    return jax.shard_map(
        functools.partial(body, mesh.shape["chk"], mesh.shape["var"]),
        mesh=mesh,
        in_specs=placed,
        out_specs=(P("var", None), P("chk", "var", None, None), P("var")),
        check_vma=False,
    )
```

```python
import functools

import jax
import jax.numpy as jnp
from jax import lax
from jax.experimental import pallas as pl
from jax.sharding import PartitionSpec as P

TILE = 64
ITERS = 2


DAMP = 0.97
EXACT = lax.Precision.HIGHEST
F32 = jnp.float32
UNROLL = 4


def linear_both(values, axis):
    length = values.shape[axis]
    pieces = [lax.slice_in_dim(values, index, index + 1, axis=axis) for index in range(length)]
    ones = jnp.ones_like(pieces[0])
    prefix = [ones]
    for index in range(length - 1):
        prefix.append(prefix[-1] * pieces[index])
    suffix = [ones]
    for index in range(length - 1, 0, -1):
        suffix.append(suffix[-1] * pieces[index])
    suffix = suffix[::-1]
    whole = prefix[-1] * pieces[-1]
    return (jnp.concatenate(prefix, axis=axis), jnp.concatenate(suffix, axis=axis), whole)


def exclusive_both(values, axis):
    length = values.shape[axis]
    if length < 16 or length % 8 != 0:
        return linear_both(values, axis)
    shape = values.shape
    split = values.reshape(shape[:axis] + (length // 8, 8) + shape[axis + 1 :])
    inner_before, inner_after, group_whole = linear_both(split, axis + 1)
    outer_before, outer_after, whole = exclusive_both(group_whole, axis)
    before = (inner_before * outer_before).reshape(shape)
    after = (inner_after * outer_after).reshape(shape)
    whole = whole.reshape(shape[:axis] + (1,) + shape[axis + 1 :])
    return (before, after, whole)


def device_tables(bits, positions, count, check_blocks, column_blocks):
    slot_total = bits.shape[0]
    slots = jnp.arange(slot_total, dtype=jnp.int32)
    live = slots < count
    edge = jnp.where(live[:, None], bits, 0).astype(jnp.float32).reshape(slot_total, TILE, TILE)
    row_hot = (positions[:, 0:1] == jnp.arange(check_blocks, dtype=jnp.int32)[None, :]).astype(
        jnp.float32
    )
    col_hot = (positions[:, 1:2] == jnp.arange(column_blocks, dtype=jnp.int32)[None, :]).astype(
        jnp.float32
    )
    same_row = (positions[:, None, 0] == positions[None, :, 0]) & (slots[:, None] != slots[None, :])
    return (edge, row_hot, col_hot, same_row)


def _spread_row(ref, c, shape):
    return jnp.broadcast_to(ref[0, pl.ds(c, 1), :], shape)


def _row_block(pos_ref, k):
    return pos_ref[2 * k]


def _col_block(pos_ref, k):
    return pos_ref[2 * k + 1]


def _columns(pos_ref, k, slots, n_c):
    return pos_ref[2 * slots + k], 3 * slots + k * n_c


def _loop(count, body, init):
    def group(j, carry):
        for t in range(UNROLL):
            carry = body(UNROLL * j + t, carry)
        return carry

    carry = lax.fori_loop(0, count // UNROLL, group, init)
    return lax.fori_loop(UNROLL * (count // UNROLL), count, body, carry)


def _fwd_products_kernel(has_u, slots, blocks, pos_ref, *refs):
    refs = list(refs)
    spread_ref = refs.pop(0)
    u_ref = refs.pop(0) if has_u else None
    ew_ref, ba_ref, whole_ref, rows_ref, here_ref, h_scr = refs
    k = pl.program_id(0)
    n_c = ew_ref.shape[1]
    shape = ew_ref.shape[2:]

    count, base = _columns(pos_ref, k, slots, n_c)

    def forward(i, carry):
        c = pos_ref[base + i]
        m = _spread_row(spread_ref, c, shape)
        if has_u:
            m = m - u_ref[0, c]
        h = jnp.where(ew_ref[0, c] > 0, jnp.tanh(0.5 * m), 1.0)
        h_scr[c] = h
        ba_ref[0, c] = carry
        return carry * h

    whole = _loop(count, forward, jnp.ones(shape, F32))
    whole_ref[k] = whole

    def backward(i, carry):
        c = pos_ref[base + count - 1 - i]
        ba_ref[0, c] = ba_ref[0, c] * carry
        return carry * h_scr[c]

    _loop(count, backward, jnp.ones(shape, F32))

    @pl.when(k == slots - 1)
    def _():
        wholes = [whole_ref[j] for j in range(slots)]
        rows_of = [_row_block(pos_ref, j) for j in range(slots)]
        for block in range(blocks):
            value = jnp.ones(shape, F32)
            for j in range(slots):
                value = value * jnp.where(rows_of[j] == block, wholes[j], 1.0)
            rows_ref[block] = value
        for j in range(slots):
            value = jnp.ones(shape, F32)
            for other in range(slots):
                if other != j:
                    value = value * jnp.where(rows_of[other] == rows_of[j], wholes[other], 1.0)
            here_ref[j] = value


def _fwd_messages_kernel(slots, pos_ref, ba_ref, sign_ref, here_ref, others_ref, ew_ref, u_ref, col_ref):
    k = pl.program_id(0)
    n_c = ba_ref.shape[1]
    count, base = _columns(pos_ref, k, slots, n_c)

    @pl.when(k == 0)
    def _():
        col_ref[...] = jnp.zeros(col_ref.shape, F32)

    f = sign_ref[k] * here_ref[k] * others_ref[_row_block(pos_ref, k)]
    q = _col_block(pos_ref, k)

    def body(i, carry):
        c = pos_ref[base + i]
        x = ba_ref[0, c] * f
        u = ew_ref[0, c] * jnp.log((1.0 + DAMP * x) / (1.0 - DAMP * x))
        u_ref[0, c] = u
        col_ref[q, pl.ds(c, 1), :] = col_ref[q, pl.ds(c, 1), :] + jnp.sum(u, axis=0, keepdims=True)
        return carry

    _loop(count, body, 0)


def _bwd_messages_kernel(has_next, has_acc, emit_column, slots, pos_ref, *refs):
    refs = list(refs)
    gsp_ref = refs.pop(0)
    gm_ref = refs.pop(0) if has_next else None
    ba_ref, sign_ref, here_ref, others_ref, ew_ref = refs[:5]
    refs = refs[5:]
    acc_ref = refs.pop(0) if has_acc else None
    gw_ref, gba_ref, ghere_ref, gothers_ref = refs[:4]
    col_ref = refs[4] if emit_column else None
    k = pl.program_id(0)
    n_c = ba_ref.shape[1]
    shape = ba_ref.shape[2:]
    q = _col_block(pos_ref, k)

    @pl.when(k == 0)
    def _():
        gothers_ref[...] = jnp.zeros(gothers_ref.shape, F32)
        if emit_column:
            col_ref[...] = jnp.zeros(col_ref.shape, F32)

    p = _row_block(pos_ref, k)
    sign = sign_ref[k]
    here = here_ref[k]
    others = others_ref[p]
    f = sign * here * others
    count, base = _columns(pos_ref, k, slots, n_c)

    def body(i, total):
        c = pos_ref[base + i]
        gu = _spread_row(gsp_ref, c, shape)
        if has_next:
            gu = gu - gm_ref[0, c]
        ba = ba_ref[0, c]
        x = ba * f
        low = 1.0 - DAMP * x
        high = 1.0 + DAMP * x
        ratio = jnp.log(high / low)
        if emit_column:
            u = ew_ref[0, c] * ratio
            col_ref[q, pl.ds(c, 1), :] = col_ref[q, pl.ds(c, 1), :] + jnp.sum(u, axis=0, keepdims=True)
        gw = gu * ratio
        if has_acc:
            gw = gw + acc_ref[0, c]
        gw_ref[0, c] = gw
        gx = gu * ew_ref[0, c] * ((2.0 * DAMP) / (low * high))
        gba_ref[0, c] = gx * f
        return total + gx * ba

    grad_factor = _loop(count, body, jnp.zeros(shape, F32))
    ghere_ref[k] = grad_factor * sign * others
    gothers_ref[p] = gothers_ref[p] + grad_factor * sign * here


def _bwd_products_kernel(has_u, emit_gm, slots, pos_ref, *refs):
    refs = list(refs)
    spread_ref = refs.pop(0)
    u_ref = refs.pop(0) if has_u else None
    ew_ref, gba_ref, grows_ref, ghere_ref, whole_ref, here_ref = refs[:6]
    refs = refs[6:]
    gm_ref = refs.pop(0) if emit_gm else None
    col_ref, h_scr, p_scr, q_scr = refs
    k = pl.program_id(0)
    n_c = ew_ref.shape[1]
    shape = ew_ref.shape[2:]

    @pl.when(k == 0)
    def _():
        col_ref[...] = jnp.zeros(col_ref.shape, F32)

    p = _row_block(pos_ref, k)
    q = _col_block(pos_ref, k)
    rows_of = [_row_block(pos_ref, j) for j in range(slots)]
    gwh = grows_ref[p] * here_ref[k]
    for other in range(slots):
        term = jnp.where(rows_of[other] == p, ghere_ref[other], 0.0)
        for third in range(slots):
            if third != other:
                term = term * jnp.where(
                    (rows_of[third] == p) & (third != k), whole_ref[third], 1.0
                )
        gwh = gwh + jnp.where(other != k, term, 0.0)

    count, base = _columns(pos_ref, k, slots, n_c)

    def forward(i, carry):
        prod, grad = carry
        c = pos_ref[base + i]
        m = _spread_row(spread_ref, c, shape)
        if has_u:
            m = m - u_ref[0, c]
        h = jnp.where(ew_ref[0, c] > 0, jnp.tanh(0.5 * m), 1.0)
        h_scr[c] = h
        p_scr[c] = prod
        q_scr[c] = grad
        return (prod * h, grad * h + gba_ref[0, c] * prod)

    ones = jnp.ones(shape, F32)
    zeros = jnp.zeros(shape, F32)
    _loop(count, forward, (ones, zeros))

    def backward(i, carry):
        prod, grad = carry
        c = pos_ref[base + count - 1 - i]
        h = h_scr[c]
        before = p_scr[c]
        gh = q_scr[c] * prod + before * (grad + gwh * prod)
        gm = jnp.where(ew_ref[0, c] > 0, gh * (0.5 * (1.0 - h * h)), 0.0)
        if emit_gm:
            gm_ref[0, c] = gm
        col_ref[q, pl.ds(c, 1), :] = col_ref[q, pl.ds(c, 1), :] + jnp.sum(gm, axis=0, keepdims=True)
        return (prod * h, grad * h + gba_ref[0, c] * prod)

    _loop(count, backward, (ones, zeros))


def _spec(kind, shape):
    if kind == "dense":
        return pl.BlockSpec((1,) + tuple(shape[1:]), lambda k, pos: (k, 0, 0, 0))
    if kind == "column":
        return pl.BlockSpec((1,) + tuple(shape[1:]), lambda k, pos: (pos[2 * k + 1], 0, 0))
    return pl.BlockSpec(tuple(shape), lambda k, pos: (0,) * len(shape))


def _call(kernel, pos, inputs, outputs, scratch=()):
    from jax.experimental.pallas import tpu as pltpu

    dense = [a for kind, a in inputs if kind == "dense"][0]
    grid_spec = pltpu.PrefetchScalarGridSpec(
        num_scalar_prefetch=1,
        grid=(dense.shape[0],),
        in_specs=[_spec(kind, a.shape) for kind, a in inputs],
        out_specs=[_spec(kind, o.shape) for kind, o in outputs],
        scratch_shapes=list(scratch),
    )
    return pl.pallas_call(
        kernel,
        grid_spec=grid_spec,
        out_shape=[o for kind, o in outputs],
    )(pos, *[a for kind, a in inputs])


def _vmem(shape):
    from jax.experimental.pallas import tpu as pltpu

    return pltpu.VMEM(shape, F32)


def fwd_products(pos, spread, u, ew, blocks):
    k, c, r, s = ew.shape
    has_u = u is not None
    inputs = [("column", spread)] + ([("dense", u)] if has_u else []) + [("dense", ew)]
    outs = [
        ("dense", jax.ShapeDtypeStruct(ew.shape, F32)),
        ("full", jax.ShapeDtypeStruct((k, r, s), F32)),
        ("full", jax.ShapeDtypeStruct((blocks, r, s), F32)),
        ("full", jax.ShapeDtypeStruct((k, r, s), F32)),
    ]
    return _call(
        functools.partial(_fwd_products_kernel, has_u, k, blocks),
        pos,
        inputs,
        outs,
        [_vmem((c, r, s))],
    )


def fwd_messages(pos, ba, sign, here, others, ew, col_blocks):
    k, c, r, s = ba.shape
    inputs = [("dense", ba), ("full", sign), ("full", here), ("full", others), ("dense", ew)]
    outs = [
        ("dense", jax.ShapeDtypeStruct(ba.shape, F32)),
        ("full", jax.ShapeDtypeStruct((col_blocks, c, s), F32)),
    ]
    return _call(functools.partial(_fwd_messages_kernel, k), pos, inputs, outs)


def bwd_messages(pos, gsp, gm, ba, sign, here, others, ew, acc, col_blocks=0):
    k, c, r, s = ba.shape
    has_next = gm is not None
    has_acc = acc is not None
    inputs = (
        [("column", gsp)]
        + ([("dense", gm)] if has_next else [])
        + [("dense", ba), ("full", sign), ("full", here), ("full", others), ("dense", ew)]
        + ([("dense", acc)] if has_acc else [])
    )
    outs = [
        ("dense", jax.ShapeDtypeStruct(ba.shape, F32)),
        ("dense", jax.ShapeDtypeStruct(ba.shape, F32)),
        ("full", jax.ShapeDtypeStruct(here.shape, F32)),
        ("full", jax.ShapeDtypeStruct(others.shape, F32)),
    ]
    if col_blocks:
        outs.append(("full", jax.ShapeDtypeStruct((col_blocks, c, s), F32)))
    return _call(
        functools.partial(_bwd_messages_kernel, has_next, has_acc, col_blocks > 0, k), pos, inputs, outs
    )


def bwd_products(pos, spread, u, ew, gba, grows, ghere, whole, here, col_blocks, emit_gm):
    k, c, r, s = ew.shape
    has_u = u is not None
    inputs = [("column", spread)] + ([("dense", u)] if has_u else []) + [
        ("dense", ew),
        ("dense", gba),
        ("full", grows),
        ("full", ghere),
        ("full", whole),
        ("full", here),
    ]
    outs = ([("dense", jax.ShapeDtypeStruct(ew.shape, F32))] if emit_gm else []) + [
        ("full", jax.ShapeDtypeStruct((col_blocks, c, s), F32))
    ]
    results = _call(
        functools.partial(_bwd_products_kernel, has_u, emit_gm, k),
        pos,
        inputs,
        outs,
        [_vmem((c, r, s)) for _ in range(3)],
    )
    if emit_gm:
        return results[0], results[1]
    return None, results[0]


def pick(hot, values):
    parts = []
    for k in range(hot.shape[0]):
        value = jnp.zeros_like(values[0])
        for j in range(hot.shape[1]):
            value = value + jnp.where(hot[k, j] > 0, values[j], 0.0)
        parts.append(value)
    return jnp.stack(parts)


def place(hot, values):
    parts = []
    for j in range(hot.shape[1]):
        value = jnp.zeros_like(values[0])
        for k in range(hot.shape[0]):
            value = value + jnp.where(hot[k, j] > 0, values[k], 0.0)
        parts.append(value)
    return jnp.stack(parts)


def combine(whole, row_hot, same_row):
    slots = whole.shape[0]
    blocks = row_hot.shape[1]
    ones = jnp.ones_like(whole[0])
    rows = []
    for block in range(blocks):
        value = ones
        for k in range(slots):
            value = value * jnp.where(row_hot[k, block] > 0, whole[k], 1.0)
        rows.append(value)
    others_here = []
    for k in range(slots):
        value = ones
        for other in range(slots):
            if other != k:
                value = value * jnp.where(same_row[k, other], whole[other], 1.0)
        others_here.append(value)
    return jnp.stack(rows), jnp.stack(others_here)


def _power_of_two(n):
    return n > 1 and (n & (n - 1)) == 0


def _swap(value, axis, n, step):
    perm = [(j, j ^ (1 << step)) for j in range(n)]
    return lax.ppermute(value, axis, perm)


def checks_total(values, n):
    if not _power_of_two(n):
        return lax.psum(values, "chk")
    step = 0
    while (1 << step) < n:
        values = values + _swap(values, "chk", n, step)
        step += 1
    return values


def others_forward(rows, check_blocks, n, uniform=False):
    if not _power_of_two(n):
        return others_gather(rows, check_blocks)
    if uniform:
        shape = rows.shape
        small = rows[:, :, 0].reshape(-1, shape[2])
        others, trail = others_forward(small, check_blocks, n)
        grow = lambda value: jnp.broadcast_to(value.reshape(shape[:2] + (1,)), shape)
        trail = [tuple(grow(value) for value in entry) for entry in trail]
        return grow(others), trail
    full = rows
    excl = jnp.ones_like(rows)
    trail = []
    step = 0
    while (1 << step) < n:
        other = _swap(full, "var", n, step)
        trail.append((full, excl, other))
        excl = excl * other
        full = full * other
        step += 1
    return excl, trail


def others_backward(trail, grads, check_blocks, n):
    if not _power_of_two(n):
        return others_scatter(trail, grads, check_blocks)
    spread = grads
    target = jnp.zeros_like(grads)
    for step, (full, excl, other) in enumerate(trail):
        other_spread = _swap(spread, "var", n, step)
        target = target * other + excl * other_spread
        spread = spread * other + other_spread * full
    return target


def others_gather(rows, check_blocks):
    own = lax.axis_index("var")
    piece = lax.all_gather(rows, "var", axis=0, tiled=True)
    indices = jnp.arange(piece.shape[0], dtype=jnp.int32)
    keep = indices // check_blocks != own
    parts = []
    for block in range(check_blocks):
        pick = (keep & (indices % check_blocks == block))[:, None, None]
        parts.append(jnp.prod(jnp.where(pick, piece, 1.0), axis=0))
    return jnp.stack(parts), piece


def others_scatter(row_piece, grads, check_blocks):
    own = lax.axis_index("var")
    grad_piece = lax.all_gather(grads, "var", axis=0, tiled=True)
    indices = jnp.arange(row_piece.shape[0], dtype=jnp.int32)
    keep = indices // check_blocks != own
    new_sums = []
    for block in range(check_blocks):
        pick = (keep & (indices % check_blocks == block))[:, None, None]
        factors = jnp.where(pick, row_piece, 1.0)
        weights = jnp.where(pick, grad_piece, 0.0)
        before, after, whole = exclusive_both(factors, 0)
        new_sums.append(jnp.sum(weights * before * after, axis=0))
    return jnp.stack(new_sums)


def body(n_chk, n_var, tile_bits, tile_pos, tile_count, edge_weight, syndrome, channel_prior, out_cot):
    slot_total = tile_bits.shape[2]
    shots = syndrome.shape[1]
    check_blocks = syndrome.shape[0] // TILE
    column_blocks = channel_prior.shape[0] // TILE
    edge, row_hot, col_hot, same_row = device_tables(
        tile_bits[0, 0], tile_pos[0, 0], tile_count[0, 0], check_blocks, column_blocks
    )
    weight = edge_weight[0, 0].reshape(slot_total, TILE, TILE)
    edge_t = jnp.swapaxes(edge, 1, 2)
    filled = jnp.any(edge_t > 0, axis=2)
    order = jnp.argsort(jnp.where(filled, 0, 1).astype(jnp.int32), axis=1, stable=True)
    pos = jnp.concatenate(
        [
            tile_pos[0, 0].reshape(slot_total * 2),
            jnp.sum(filled.astype(jnp.int32), axis=1),
            order.astype(jnp.int32).reshape(slot_total * TILE),
        ]
    )
    dense = (slot_total, TILE, TILE, shots)
    ew = jnp.broadcast_to((edge_t * jnp.swapaxes(weight, 1, 2))[..., None], dense)
    sign_dev = (1.0 - 2.0 * syndrome.astype(jnp.float32)).reshape(check_blocks, TILE, shots)
    sign_slot = jnp.einsum("kc,crs->krs", row_hot, sign_dev, precision=EXACT)
    prior_dev = channel_prior.reshape(column_blocks, TILE)
    spread = jnp.broadcast_to(prior_dev[:, :, None], (column_blocks, TILE, shots))
    u = None
    saved = []
    total = None
    for step in range(ITERS):
        ba, whole, rows, others_here = fwd_products(pos, spread, u, ew, check_blocks)
        others, trail = others_forward(rows, check_blocks, n_var, uniform=(step == 0 and (check_blocks * TILE) % shots == 0))
        saved.append((spread, u, ba, whole, others_here, others, trail))
        if step + 1 < ITERS:
            u, column = fwd_messages(pos, ba, sign_slot, others_here, others, ew, column_blocks)
            total = prior_dev[:, :, None] + checks_total(column, n_chk)
            spread = total

    grad_total = out_cot.reshape(column_blocks, TILE, shots)
    prior_grad = jnp.zeros((column_blocks, TILE), jnp.float32)
    grad_m = None
    acc = None
    for step in reversed(range(ITERS)):
        spread_t, u_prev, ba, whole, others_here, others, trail = saved[step]
        prior_grad = prior_grad + jnp.sum(grad_total, axis=2)
        if step + 1 == ITERS:
            acc, grad_ba, grad_here, grad_others, last_column = bwd_messages(
                pos, grad_total, grad_m, ba, sign_slot, others_here, others, ew, acc, column_blocks
            )
            total = prior_dev[:, :, None] + checks_total(last_column, n_chk)
            marginals = total.reshape(column_blocks * TILE, shots)
        else:
            acc, grad_ba, grad_here, grad_others = bwd_messages(
                pos, grad_total, grad_m, ba, sign_slot, others_here, others, ew, acc
            )
        grad_rows = others_backward(trail, grad_others, check_blocks, n_var)
        grad_m, column = bwd_products(
            pos, spread_t, u_prev, ew, grad_ba, grad_rows, grad_here, whole, others_here,
            column_blocks, step > 0,
        )
        if step > 0:
            grad_total = checks_total(column, n_chk)
    shot_sums = jnp.sum(column, axis=2)
    if (column_blocks * TILE) % 128 == 0:
        shot_sums = checks_total(shot_sums.reshape(-1, 128), n_chk).reshape(column_blocks, TILE)
    else:
        shot_sums = checks_total(shot_sums, n_chk)
    prior_grad = prior_grad + shot_sums
    weight_grad = jnp.where(edge > 0, jnp.swapaxes(jnp.sum(acc, axis=3), 1, 2), 0.0)
    return (
        marginals,
        weight_grad.reshape(1, 1, slot_total, TILE * TILE),
        prior_grad.reshape(column_blocks * TILE),
    )


def solution(mesh):
    placed = (
        P("chk", "var", None, None),
        P("chk", "var", None, None),
        P("chk", "var"),
        P("chk", "var", None, None),
        P("chk", None),
        P("var"),
        P("var", None),
    )
    return jax.shard_map(
        functools.partial(body, mesh.shape["chk"], mesh.shape["var"]),
        mesh=mesh,
        in_specs=placed,
        out_specs=(P("var", None), P("chk", "var", None, None), P("var")),
        check_vma=False,
    )
```

```python
import functools

import jax
import jax.numpy as jnp
from jax import lax
from jax.experimental import pallas as pl
from jax.sharding import PartitionSpec as P

TILE = 64
ITERS = 2


DAMP = 0.97
EXACT = lax.Precision.HIGHEST
F32 = jnp.float32
UNROLL = 4


def linear_both(values, axis):
    length = values.shape[axis]
    pieces = [lax.slice_in_dim(values, index, index + 1, axis=axis) for index in range(length)]
    ones = jnp.ones_like(pieces[0])
    prefix = [ones]
    for index in range(length - 1):
        prefix.append(prefix[-1] * pieces[index])
    suffix = [ones]
    for index in range(length - 1, 0, -1):
        suffix.append(suffix[-1] * pieces[index])
    suffix = suffix[::-1]
    whole = prefix[-1] * pieces[-1]
    return (jnp.concatenate(prefix, axis=axis), jnp.concatenate(suffix, axis=axis), whole)


def exclusive_both(values, axis):
    length = values.shape[axis]
    if length < 16 or length % 8 != 0:
        return linear_both(values, axis)
    shape = values.shape
    split = values.reshape(shape[:axis] + (length // 8, 8) + shape[axis + 1 :])
    inner_before, inner_after, group_whole = linear_both(split, axis + 1)
    outer_before, outer_after, whole = exclusive_both(group_whole, axis)
    before = (inner_before * outer_before).reshape(shape)
    after = (inner_after * outer_after).reshape(shape)
    whole = whole.reshape(shape[:axis] + (1,) + shape[axis + 1 :])
    return (before, after, whole)


def device_tables(bits, positions, count, check_blocks, column_blocks):
    slot_total = bits.shape[0]
    slots = jnp.arange(slot_total, dtype=jnp.int32)
    live = slots < count
    edge = jnp.where(live[:, None], bits, 0).astype(jnp.float32).reshape(slot_total, TILE, TILE)
    row_hot = (positions[:, 0:1] == jnp.arange(check_blocks, dtype=jnp.int32)[None, :]).astype(
        jnp.float32
    )
    col_hot = (positions[:, 1:2] == jnp.arange(column_blocks, dtype=jnp.int32)[None, :]).astype(
        jnp.float32
    )
    same_row = (positions[:, None, 0] == positions[None, :, 0]) & (slots[:, None] != slots[None, :])
    return (edge, row_hot, col_hot, same_row)


def _spread_row(ref, c, shape):
    return jnp.broadcast_to(ref[0, pl.ds(c, 1), :], shape)


def _row_block(pos_ref, k):
    return pos_ref[2 * k]


def _col_block(pos_ref, k):
    return pos_ref[2 * k + 1]


def _columns(pos_ref, k, slots, n_c):
    return pos_ref[2 * slots + k], 3 * slots + k * n_c


def _loop(count, body, init):
    def group(j, carry):
        for t in range(UNROLL):
            carry = body(UNROLL * j + t, carry)
        return carry

    carry = lax.fori_loop(0, count // UNROLL, group, init)
    return lax.fori_loop(UNROLL * (count // UNROLL), count, body, carry)


def _fwd_products_kernel(has_u, slots, blocks, pos_ref, *refs):
    refs = list(refs)
    spread_ref = refs.pop(0)
    u_ref = refs.pop(0) if has_u else None
    ew_ref, ba_ref, whole_ref, rows_ref, here_ref, h_scr = refs
    k = pl.program_id(0)
    n_c = ew_ref.shape[1]
    shape = ew_ref.shape[2:]

    count, base = _columns(pos_ref, k, slots, n_c)

    def forward(i, carry):
        c = pos_ref[base + i]
        m = _spread_row(spread_ref, c, shape)
        if has_u:
            m = m - u_ref[0, c]
        h = jnp.where(ew_ref[0, c] > 0, jnp.tanh(0.5 * m), 1.0)
        h_scr[c] = h
        ba_ref[0, c] = carry
        return carry * h

    whole = _loop(count, forward, jnp.ones(shape, F32))
    whole_ref[k] = whole

    def backward(i, carry):
        c = pos_ref[base + count - 1 - i]
        ba_ref[0, c] = ba_ref[0, c] * carry
        return carry * h_scr[c]

    _loop(count, backward, jnp.ones(shape, F32))

    @pl.when(k == slots - 1)
    def _():
        wholes = [whole_ref[j] for j in range(slots)]
        rows_of = [_row_block(pos_ref, j) for j in range(slots)]
        for block in range(blocks):
            value = jnp.ones(shape, F32)
            for j in range(slots):
                value = value * jnp.where(rows_of[j] == block, wholes[j], 1.0)
            rows_ref[block] = value
        for j in range(slots):
            value = jnp.ones(shape, F32)
            for other in range(slots):
                if other != j:
                    value = value * jnp.where(rows_of[other] == rows_of[j], wholes[other], 1.0)
            here_ref[j] = value


def _fwd_messages_kernel(slots, pos_ref, ba_ref, sign_ref, here_ref, others_ref, ew_ref, u_ref, col_ref):
    k = pl.program_id(0)
    n_c = ba_ref.shape[1]
    count, base = _columns(pos_ref, k, slots, n_c)

    @pl.when(k == 0)
    def _():
        col_ref[...] = jnp.zeros(col_ref.shape, F32)

    f = sign_ref[k] * here_ref[k] * others_ref[_row_block(pos_ref, k)]
    q = _col_block(pos_ref, k)

    def body(i, carry):
        c = pos_ref[base + i]
        x = ba_ref[0, c] * f
        u = ew_ref[0, c] * jnp.log((1.0 + DAMP * x) / (1.0 - DAMP * x))
        u_ref[0, c] = u
        col_ref[q, pl.ds(c, 1), :] = col_ref[q, pl.ds(c, 1), :] + jnp.sum(u, axis=0, keepdims=True)
        return carry

    _loop(count, body, 0)


def _bwd_messages_kernel(has_next, has_acc, emit_column, slots, pos_ref, *refs):
    refs = list(refs)
    gsp_ref = refs.pop(0)
    gm_ref = refs.pop(0) if has_next else None
    ba_ref, sign_ref, here_ref, others_ref, ew_ref = refs[:5]
    refs = refs[5:]
    acc_ref = refs.pop(0) if has_acc else None
    gw_ref, gba_ref, ghere_ref, gothers_ref = refs[:4]
    col_ref = refs[4] if emit_column else None
    k = pl.program_id(0)
    n_c = ba_ref.shape[1]
    shape = ba_ref.shape[2:]
    q = _col_block(pos_ref, k)

    @pl.when(k == 0)
    def _():
        gothers_ref[...] = jnp.zeros(gothers_ref.shape, F32)
        if emit_column:
            col_ref[...] = jnp.zeros(col_ref.shape, F32)

    p = _row_block(pos_ref, k)
    sign = sign_ref[k]
    here = here_ref[k]
    others = others_ref[p]
    f = sign * here * others
    count, base = _columns(pos_ref, k, slots, n_c)

    def body(i, total):
        c = pos_ref[base + i]
        gu = _spread_row(gsp_ref, c, shape)
        if has_next:
            gu = gu - gm_ref[0, c]
        ba = ba_ref[0, c]
        x = ba * f
        low = 1.0 - DAMP * x
        high = 1.0 + DAMP * x
        ratio = jnp.log(high / low)
        if emit_column:
            u = ew_ref[0, c] * ratio
            col_ref[q, pl.ds(c, 1), :] = col_ref[q, pl.ds(c, 1), :] + jnp.sum(u, axis=0, keepdims=True)
        gw = gu * ratio
        if has_acc:
            gw = gw + acc_ref[0, c]
        gw_ref[0, c] = gw
        gx = gu * ew_ref[0, c] * ((2.0 * DAMP) / (low * high))
        gba_ref[0, c] = gx * f
        return total + gx * ba

    grad_factor = _loop(count, body, jnp.zeros(shape, F32))
    ghere_ref[k] = grad_factor * sign * others
    gothers_ref[p] = gothers_ref[p] + grad_factor * sign * here


def _bwd_products_kernel(has_u, emit_gm, slots, pos_ref, *refs):
    refs = list(refs)
    spread_ref = refs.pop(0)
    u_ref = refs.pop(0) if has_u else None
    ew_ref, gba_ref, grows_ref, ghere_ref, whole_ref, here_ref = refs[:6]
    refs = refs[6:]
    gm_ref = refs.pop(0) if emit_gm else None
    col_ref, h_scr, p_scr, q_scr = refs
    k = pl.program_id(0)
    n_c = ew_ref.shape[1]
    shape = ew_ref.shape[2:]

    @pl.when(k == 0)
    def _():
        col_ref[...] = jnp.zeros(col_ref.shape, F32)

    p = _row_block(pos_ref, k)
    q = _col_block(pos_ref, k)
    rows_of = [_row_block(pos_ref, j) for j in range(slots)]
    gwh = grows_ref[p] * here_ref[k]
    for other in range(slots):
        term = jnp.where(rows_of[other] == p, ghere_ref[other], 0.0)
        for third in range(slots):
            if third != other:
                term = term * jnp.where(
                    (rows_of[third] == p) & (third != k), whole_ref[third], 1.0
                )
        gwh = gwh + jnp.where(other != k, term, 0.0)

    count, base = _columns(pos_ref, k, slots, n_c)

    def forward(i, carry):
        prod, grad = carry
        c = pos_ref[base + i]
        m = _spread_row(spread_ref, c, shape)
        if has_u:
            m = m - u_ref[0, c]
        h = jnp.where(ew_ref[0, c] > 0, jnp.tanh(0.5 * m), 1.0)
        h_scr[c] = h
        p_scr[c] = prod
        q_scr[c] = grad
        return (prod * h, grad * h + gba_ref[0, c] * prod)

    ones = jnp.ones(shape, F32)
    zeros = jnp.zeros(shape, F32)
    _loop(count, forward, (ones, zeros))

    def backward(i, carry):
        prod, grad = carry
        c = pos_ref[base + count - 1 - i]
        h = h_scr[c]
        before = p_scr[c]
        gh = q_scr[c] * prod + before * (grad + gwh * prod)
        gm = jnp.where(ew_ref[0, c] > 0, gh * (0.5 * (1.0 - h * h)), 0.0)
        if emit_gm:
            gm_ref[0, c] = gm
        col_ref[q, pl.ds(c, 1), :] = col_ref[q, pl.ds(c, 1), :] + jnp.sum(gm, axis=0, keepdims=True)
        return (prod * h, grad * h + gba_ref[0, c] * prod)

    _loop(count, backward, (ones, zeros))


def _spec(kind, shape):
    if kind == "dense":
        return pl.BlockSpec((1,) + tuple(shape[1:]), lambda k, pos: (k, 0, 0, 0))
    if kind == "column":
        return pl.BlockSpec((1,) + tuple(shape[1:]), lambda k, pos: (pos[2 * k + 1], 0, 0))
    return pl.BlockSpec(tuple(shape), lambda k, pos: (0,) * len(shape))


def _call(kernel, pos, inputs, outputs, scratch=()):
    from jax.experimental.pallas import tpu as pltpu

    dense = [a for kind, a in inputs if kind == "dense"][0]
    grid_spec = pltpu.PrefetchScalarGridSpec(
        num_scalar_prefetch=1,
        grid=(dense.shape[0],),
        in_specs=[_spec(kind, a.shape) for kind, a in inputs],
        out_specs=[_spec(kind, o.shape) for kind, o in outputs],
        scratch_shapes=list(scratch),
    )
    return pl.pallas_call(
        kernel,
        grid_spec=grid_spec,
        out_shape=[o for kind, o in outputs],
    )(pos, *[a for kind, a in inputs])


def _vmem(shape):
    from jax.experimental.pallas import tpu as pltpu

    return pltpu.VMEM(shape, F32)


def fwd_products(pos, spread, u, ew, blocks):
    k, c, r, s = ew.shape
    has_u = u is not None
    inputs = [("column", spread)] + ([("dense", u)] if has_u else []) + [("dense", ew)]
    outs = [
        ("dense", jax.ShapeDtypeStruct(ew.shape, F32)),
        ("full", jax.ShapeDtypeStruct((k, r, s), F32)),
        ("full", jax.ShapeDtypeStruct((blocks, r, s), F32)),
        ("full", jax.ShapeDtypeStruct((k, r, s), F32)),
    ]
    return _call(
        functools.partial(_fwd_products_kernel, has_u, k, blocks),
        pos,
        inputs,
        outs,
        [_vmem((c, r, s))],
    )


def fwd_messages(pos, ba, sign, here, others, ew, col_blocks):
    k, c, r, s = ba.shape
    inputs = [("dense", ba), ("full", sign), ("full", here), ("full", others), ("dense", ew)]
    outs = [
        ("dense", jax.ShapeDtypeStruct(ba.shape, F32)),
        ("full", jax.ShapeDtypeStruct((col_blocks, c, s), F32)),
    ]
    return _call(functools.partial(_fwd_messages_kernel, k), pos, inputs, outs)


def bwd_messages(pos, gsp, gm, ba, sign, here, others, ew, acc, col_blocks=0):
    k, c, r, s = ba.shape
    has_next = gm is not None
    has_acc = acc is not None
    inputs = (
        [("column", gsp)]
        + ([("dense", gm)] if has_next else [])
        + [("dense", ba), ("full", sign), ("full", here), ("full", others), ("dense", ew)]
        + ([("dense", acc)] if has_acc else [])
    )
    outs = [
        ("dense", jax.ShapeDtypeStruct(ba.shape, F32)),
        ("dense", jax.ShapeDtypeStruct(ba.shape, F32)),
        ("full", jax.ShapeDtypeStruct(here.shape, F32)),
        ("full", jax.ShapeDtypeStruct(others.shape, F32)),
    ]
    if col_blocks:
        outs.append(("full", jax.ShapeDtypeStruct((col_blocks, c, s), F32)))
    return _call(
        functools.partial(_bwd_messages_kernel, has_next, has_acc, col_blocks > 0, k), pos, inputs, outs
    )


def bwd_products(pos, spread, u, ew, gba, grows, ghere, whole, here, col_blocks, emit_gm):
    k, c, r, s = ew.shape
    has_u = u is not None
    inputs = [("column", spread)] + ([("dense", u)] if has_u else []) + [
        ("dense", ew),
        ("dense", gba),
        ("full", grows),
        ("full", ghere),
        ("full", whole),
        ("full", here),
    ]
    outs = ([("dense", jax.ShapeDtypeStruct(ew.shape, F32))] if emit_gm else []) + [
        ("full", jax.ShapeDtypeStruct((col_blocks, c, s), F32))
    ]
    results = _call(
        functools.partial(_bwd_products_kernel, has_u, emit_gm, k),
        pos,
        inputs,
        outs,
        [_vmem((c, r, s)) for _ in range(3)],
    )
    if emit_gm:
        return results[0], results[1]
    return None, results[0]


def pick(hot, values):
    parts = []
    for k in range(hot.shape[0]):
        value = jnp.zeros_like(values[0])
        for j in range(hot.shape[1]):
            value = value + jnp.where(hot[k, j] > 0, values[j], 0.0)
        parts.append(value)
    return jnp.stack(parts)


def place(hot, values):
    parts = []
    for j in range(hot.shape[1]):
        value = jnp.zeros_like(values[0])
        for k in range(hot.shape[0]):
            value = value + jnp.where(hot[k, j] > 0, values[k], 0.0)
        parts.append(value)
    return jnp.stack(parts)


def combine(whole, row_hot, same_row):
    slots = whole.shape[0]
    blocks = row_hot.shape[1]
    ones = jnp.ones_like(whole[0])
    rows = []
    for block in range(blocks):
        value = ones
        for k in range(slots):
            value = value * jnp.where(row_hot[k, block] > 0, whole[k], 1.0)
        rows.append(value)
    others_here = []
    for k in range(slots):
        value = ones
        for other in range(slots):
            if other != k:
                value = value * jnp.where(same_row[k, other], whole[other], 1.0)
        others_here.append(value)
    return jnp.stack(rows), jnp.stack(others_here)


def _power_of_two(n):
    return n > 1 and (n & (n - 1)) == 0


def _swap(value, axis, n, step):
    perm = [(j, j ^ (1 << step)) for j in range(n)]
    return lax.ppermute(value, axis, perm)


def checks_total(values, n):
    if not _power_of_two(n):
        return lax.psum(values, "chk")
    step = 0
    while (1 << step) < n:
        values = values + _swap(values, "chk", n, step)
        step += 1
    return values


def others_forward(rows, check_blocks, n, uniform=False):
    if not _power_of_two(n):
        return others_gather(rows, check_blocks)
    if uniform:
        shape = rows.shape
        small = rows[:, :, 0].reshape(-1, shape[2])
        others, trail = others_forward(small, check_blocks, n)
        grow = lambda value: jnp.broadcast_to(value.reshape(shape[:2] + (1,)), shape)
        trail = [tuple(grow(value) for value in entry) for entry in trail]
        return grow(others), trail
    full = rows
    excl = jnp.ones_like(rows)
    trail = []
    step = 0
    while (1 << step) < n:
        other = _swap(full, "var", n, step)
        trail.append((full, excl, other))
        excl = excl * other
        full = full * other
        step += 1
    return excl, trail


def others_backward(trail, grads, check_blocks, n):
    if not _power_of_two(n):
        return others_scatter(trail, grads, check_blocks)
    spread = grads
    target = jnp.zeros_like(grads)
    for step, (full, excl, other) in enumerate(trail):
        other_spread = _swap(spread, "var", n, step)
        target = target * other + excl * other_spread
        spread = spread * other + other_spread * full
    return target


def others_gather(rows, check_blocks):
    own = lax.axis_index("var")
    piece = lax.all_gather(rows, "var", axis=0, tiled=True)
    indices = jnp.arange(piece.shape[0], dtype=jnp.int32)
    keep = indices // check_blocks != own
    parts = []
    for block in range(check_blocks):
        pick = (keep & (indices % check_blocks == block))[:, None, None]
        parts.append(jnp.prod(jnp.where(pick, piece, 1.0), axis=0))
    return jnp.stack(parts), piece


def others_scatter(row_piece, grads, check_blocks):
    own = lax.axis_index("var")
    grad_piece = lax.all_gather(grads, "var", axis=0, tiled=True)
    indices = jnp.arange(row_piece.shape[0], dtype=jnp.int32)
    keep = indices // check_blocks != own
    new_sums = []
    for block in range(check_blocks):
        pick = (keep & (indices % check_blocks == block))[:, None, None]
        factors = jnp.where(pick, row_piece, 1.0)
        weights = jnp.where(pick, grad_piece, 0.0)
        before, after, whole = exclusive_both(factors, 0)
        new_sums.append(jnp.sum(weights * before * after, axis=0))
    return jnp.stack(new_sums)


def body(n_chk, n_var, tile_bits, tile_pos, tile_count, edge_weight, syndrome, channel_prior, out_cot):
    slot_total = tile_bits.shape[2]
    shots = syndrome.shape[1]
    check_blocks = syndrome.shape[0] // TILE
    column_blocks = channel_prior.shape[0] // TILE
    edge, row_hot, col_hot, same_row = device_tables(
        tile_bits[0, 0], tile_pos[0, 0], tile_count[0, 0], check_blocks, column_blocks
    )
    weight = edge_weight[0, 0].reshape(slot_total, TILE, TILE)
    edge_t = jnp.swapaxes(edge, 1, 2)
    filled = jnp.any(edge_t > 0, axis=2)
    order = jnp.argsort(jnp.where(filled, 0, 1).astype(jnp.int32), axis=1, stable=True)
    pos = jnp.concatenate(
        [
            tile_pos[0, 0].reshape(slot_total * 2),
            jnp.sum(filled.astype(jnp.int32), axis=1),
            order.astype(jnp.int32).reshape(slot_total * TILE),
        ]
    )
    dense = (slot_total, TILE, TILE, shots)
    ew = jnp.broadcast_to((edge_t * jnp.swapaxes(weight, 1, 2))[..., None], dense)
    sign_dev = (1.0 - 2.0 * syndrome.astype(jnp.float32)).reshape(check_blocks, TILE, shots)
    sign_slot = jnp.einsum("kc,crs->krs", row_hot, sign_dev, precision=EXACT)
    prior_dev = channel_prior.reshape(column_blocks, TILE)
    spread = jnp.broadcast_to(prior_dev[:, :, None], (column_blocks, TILE, shots))
    u = None
    saved = []
    total = None
    for step in range(ITERS):
        ba, whole, rows, others_here = fwd_products(pos, spread, u, ew, check_blocks)
        others, trail = others_forward(rows, check_blocks, n_var, uniform=(step == 0 and (check_blocks * TILE) % shots == 0))
        saved.append((spread, u, ba, whole, others_here, others, trail))
        if step + 1 < ITERS:
            u, column = fwd_messages(pos, ba, sign_slot, others_here, others, ew, column_blocks)
            total = prior_dev[:, :, None] + checks_total(column, n_chk)
            spread = total

    grad_total = out_cot.reshape(column_blocks, TILE, shots)
    prior_grad = jnp.zeros((column_blocks, TILE), jnp.float32)
    grad_m = None
    acc = None
    for step in reversed(range(ITERS)):
        spread_t, u_prev, ba, whole, others_here, others, trail = saved[step]
        prior_grad = prior_grad + jnp.sum(grad_total, axis=2)
        if step + 1 == ITERS:
            term, grad_ba, grad_here, grad_others, last_column = bwd_messages(
                pos, grad_total, grad_m, ba, sign_slot, others_here, others, ew, None, column_blocks
            )
            total = prior_dev[:, :, None] + checks_total(last_column, n_chk)
            marginals = total.reshape(column_blocks * TILE, shots)
        else:
            term, grad_ba, grad_here, grad_others = bwd_messages(
                pos, grad_total, grad_m, ba, sign_slot, others_here, others, ew, None
            )
        term = jnp.sum(term, axis=3)
        acc = term if acc is None else acc + term
        grad_rows = others_backward(trail, grad_others, check_blocks, n_var)
        grad_m, column = bwd_products(
            pos, spread_t, u_prev, ew, grad_ba, grad_rows, grad_here, whole, others_here,
            column_blocks, step > 0,
        )
        if step > 0:
            grad_total = checks_total(column, n_chk)
    shot_sums = jnp.sum(column, axis=2)
    if (column_blocks * TILE) % 128 == 0:
        shot_sums = checks_total(shot_sums.reshape(-1, 128), n_chk).reshape(column_blocks, TILE)
    else:
        shot_sums = checks_total(shot_sums, n_chk)
    prior_grad = prior_grad + shot_sums
    weight_grad = jnp.where(edge > 0, jnp.swapaxes(acc, 1, 2), 0.0)
    return (
        marginals,
        weight_grad.reshape(1, 1, slot_total, TILE * TILE),
        prior_grad.reshape(column_blocks * TILE),
    )


def solution(mesh):
    placed = (
        P("chk", "var", None, None),
        P("chk", "var", None, None),
        P("chk", "var"),
        P("chk", "var", None, None),
        P("chk", None),
        P("var"),
        P("var", None),
    )
    return jax.shard_map(
        functools.partial(body, mesh.shape["chk"], mesh.shape["var"]),
        mesh=mesh,
        in_specs=placed,
        out_specs=(P("var", None), P("chk", "var", None, None), P("var")),
        check_vma=False,
    )
```

```python
import functools

import jax
import jax.numpy as jnp
from jax import lax
from jax.experimental import pallas as pl
from jax.sharding import PartitionSpec as P

TILE = 64
ITERS = 2


DAMP = 0.97
EXACT = lax.Precision.HIGHEST
F32 = jnp.float32
UNROLL = 4


def linear_both(values, axis):
    length = values.shape[axis]
    pieces = [lax.slice_in_dim(values, index, index + 1, axis=axis) for index in range(length)]
    ones = jnp.ones_like(pieces[0])
    prefix = [ones]
    for index in range(length - 1):
        prefix.append(prefix[-1] * pieces[index])
    suffix = [ones]
    for index in range(length - 1, 0, -1):
        suffix.append(suffix[-1] * pieces[index])
    suffix = suffix[::-1]
    whole = prefix[-1] * pieces[-1]
    return (jnp.concatenate(prefix, axis=axis), jnp.concatenate(suffix, axis=axis), whole)


def exclusive_both(values, axis):
    length = values.shape[axis]
    if length < 16 or length % 8 != 0:
        return linear_both(values, axis)
    shape = values.shape
    split = values.reshape(shape[:axis] + (length // 8, 8) + shape[axis + 1 :])
    inner_before, inner_after, group_whole = linear_both(split, axis + 1)
    outer_before, outer_after, whole = exclusive_both(group_whole, axis)
    before = (inner_before * outer_before).reshape(shape)
    after = (inner_after * outer_after).reshape(shape)
    whole = whole.reshape(shape[:axis] + (1,) + shape[axis + 1 :])
    return (before, after, whole)


def device_tables(bits, positions, count, check_blocks, column_blocks):
    slot_total = bits.shape[0]
    slots = jnp.arange(slot_total, dtype=jnp.int32)
    live = slots < count
    edge = jnp.where(live[:, None], bits, 0).astype(jnp.float32).reshape(slot_total, TILE, TILE)
    row_hot = (positions[:, 0:1] == jnp.arange(check_blocks, dtype=jnp.int32)[None, :]).astype(
        jnp.float32
    )
    col_hot = (positions[:, 1:2] == jnp.arange(column_blocks, dtype=jnp.int32)[None, :]).astype(
        jnp.float32
    )
    same_row = (positions[:, None, 0] == positions[None, :, 0]) & (slots[:, None] != slots[None, :])
    return (edge, row_hot, col_hot, same_row)


def _spread_row(ref, c, shape):
    return jnp.broadcast_to(ref[0, pl.ds(c, 1), :], shape)


def _row_block(pos_ref, k):
    return pos_ref[2 * k]


def _col_block(pos_ref, k):
    return pos_ref[2 * k + 1]


def _columns(pos_ref, k, slots, n_c):
    return pos_ref[2 * slots + k], 3 * slots + k * n_c


def _loop(count, body, init):
    def group(j, carry):
        for t in range(UNROLL):
            carry = body(UNROLL * j + t, carry)
        return carry

    carry = lax.fori_loop(0, count // UNROLL, group, init)
    return lax.fori_loop(UNROLL * (count // UNROLL), count, body, carry)


def _fwd_products_kernel(has_u, slots, blocks, pos_ref, *refs):
    refs = list(refs)
    spread_ref = refs.pop(0)
    u_ref = refs.pop(0) if has_u else None
    ew_ref, ba_ref, h_scr, whole_ref, rows_ref, here_ref = refs
    k = pl.program_id(0)
    n_c = ew_ref.shape[1]
    shape = ew_ref.shape[2:]

    count, base = _columns(pos_ref, k, slots, n_c)

    def forward(i, carry):
        c = pos_ref[base + i]
        m = _spread_row(spread_ref, c, shape)
        if has_u:
            m = m - u_ref[0, c]
        h = jnp.where(ew_ref[0, c] > 0, jnp.tanh(0.5 * m), 1.0)
        h_scr[0, c] = h
        ba_ref[0, c] = carry
        return carry * h

    whole = _loop(count, forward, jnp.ones(shape, F32))
    whole_ref[k] = whole

    def backward(i, carry):
        c = pos_ref[base + count - 1 - i]
        ba_ref[0, c] = ba_ref[0, c] * carry
        return carry * h_scr[0, c]

    _loop(count, backward, jnp.ones(shape, F32))

    @pl.when(k == slots - 1)
    def _():
        wholes = [whole_ref[j] for j in range(slots)]
        rows_of = [_row_block(pos_ref, j) for j in range(slots)]
        for block in range(blocks):
            value = jnp.ones(shape, F32)
            for j in range(slots):
                value = value * jnp.where(rows_of[j] == block, wholes[j], 1.0)
            rows_ref[block] = value
        for j in range(slots):
            value = jnp.ones(shape, F32)
            for other in range(slots):
                if other != j:
                    value = value * jnp.where(rows_of[other] == rows_of[j], wholes[other], 1.0)
            here_ref[j] = value


def _fwd_messages_kernel(slots, pos_ref, ba_ref, sign_ref, here_ref, others_ref, ew_ref, u_ref, col_ref):
    k = pl.program_id(0)
    n_c = ba_ref.shape[1]
    count, base = _columns(pos_ref, k, slots, n_c)

    @pl.when(k == 0)
    def _():
        col_ref[...] = jnp.zeros(col_ref.shape, F32)

    f = sign_ref[k] * here_ref[k] * others_ref[_row_block(pos_ref, k)]
    q = _col_block(pos_ref, k)

    def body(i, carry):
        c = pos_ref[base + i]
        x = ba_ref[0, c] * f
        u = ew_ref[0, c] * jnp.log((1.0 + DAMP * x) / (1.0 - DAMP * x))
        u_ref[0, c] = u
        col_ref[q, pl.ds(c, 1), :] = col_ref[q, pl.ds(c, 1), :] + jnp.sum(u, axis=0, keepdims=True)
        return carry

    _loop(count, body, 0)


def _bwd_messages_kernel(has_next, has_acc, emit_column, slots, pos_ref, *refs):
    refs = list(refs)
    gsp_ref = refs.pop(0)
    gm_ref = refs.pop(0) if has_next else None
    ba_ref, sign_ref, here_ref, others_ref, ew_ref = refs[:5]
    refs = refs[5:]
    acc_ref = refs.pop(0) if has_acc else None
    gw_ref, gba_ref, ghere_ref, gothers_ref = refs[:4]
    col_ref = refs[4] if emit_column else None
    k = pl.program_id(0)
    n_c = ba_ref.shape[1]
    shape = ba_ref.shape[2:]
    q = _col_block(pos_ref, k)

    @pl.when(k == 0)
    def _():
        gothers_ref[...] = jnp.zeros(gothers_ref.shape, F32)
        if emit_column:
            col_ref[...] = jnp.zeros(col_ref.shape, F32)

    p = _row_block(pos_ref, k)
    sign = sign_ref[k]
    here = here_ref[k]
    others = others_ref[p]
    f = sign * here * others
    count, base = _columns(pos_ref, k, slots, n_c)

    def body(i, total):
        c = pos_ref[base + i]
        gu = _spread_row(gsp_ref, c, shape)
        if has_next:
            gu = gu - gm_ref[0, c]
        ba = ba_ref[0, c]
        x = ba * f
        low = 1.0 - DAMP * x
        high = 1.0 + DAMP * x
        ratio = jnp.log(high / low)
        if emit_column:
            u = ew_ref[0, c] * ratio
            col_ref[q, pl.ds(c, 1), :] = col_ref[q, pl.ds(c, 1), :] + jnp.sum(u, axis=0, keepdims=True)
        gw = gu * ratio
        if has_acc:
            gw = gw + acc_ref[0, c]
        gw_ref[0, c] = gw
        gx = gu * ew_ref[0, c] * ((2.0 * DAMP) / (low * high))
        gba_ref[0, c] = gx * f
        return total + gx * ba

    grad_factor = _loop(count, body, jnp.zeros(shape, F32))
    ghere_ref[k] = grad_factor * sign * others
    gothers_ref[p] = gothers_ref[p] + grad_factor * sign * here


def _bwd_products_kernel(emit_gm, slots, pos_ref, *refs):
    refs = list(refs)
    h_ref, gba_ref, grows_ref, ghere_ref, whole_ref, here_ref = refs[:6]
    refs = refs[6:]
    gm_ref = refs.pop(0) if emit_gm else None
    col_ref, p_scr, q_scr = refs
    k = pl.program_id(0)
    n_c = h_ref.shape[1]
    shape = h_ref.shape[2:]

    @pl.when(k == 0)
    def _():
        col_ref[...] = jnp.zeros(col_ref.shape, F32)

    p = _row_block(pos_ref, k)
    q = _col_block(pos_ref, k)
    rows_of = [_row_block(pos_ref, j) for j in range(slots)]
    gwh = grows_ref[p] * here_ref[k]
    for other in range(slots):
        term = jnp.where(rows_of[other] == p, ghere_ref[other], 0.0)
        for third in range(slots):
            if third != other:
                term = term * jnp.where(
                    (rows_of[third] == p) & (third != k), whole_ref[third], 1.0
                )
        gwh = gwh + jnp.where(other != k, term, 0.0)

    count, base = _columns(pos_ref, k, slots, n_c)

    def forward(i, carry):
        prod, grad = carry
        c = pos_ref[base + i]
        h = h_ref[0, c]
        p_scr[c] = prod
        q_scr[c] = grad
        return (prod * h, grad * h + gba_ref[0, c] * prod)

    ones = jnp.ones(shape, F32)
    zeros = jnp.zeros(shape, F32)
    _loop(count, forward, (ones, zeros))

    def backward(i, carry):
        prod, grad = carry
        c = pos_ref[base + count - 1 - i]
        h = h_ref[0, c]
        before = p_scr[c]
        gh = q_scr[c] * prod + before * (grad + gwh * prod)
        gm = gh * (0.5 * (1.0 - h * h))
        if emit_gm:
            gm_ref[0, c] = gm
        col_ref[q, pl.ds(c, 1), :] = col_ref[q, pl.ds(c, 1), :] + jnp.sum(gm, axis=0, keepdims=True)
        return (prod * h, grad * h + gba_ref[0, c] * prod)

    _loop(count, backward, (ones, zeros))


def _spec(kind, shape):
    if kind == "dense":
        return pl.BlockSpec((1,) + tuple(shape[1:]), lambda k, pos: (k, 0, 0, 0))
    if kind == "column":
        return pl.BlockSpec((1,) + tuple(shape[1:]), lambda k, pos: (pos[2 * k + 1], 0, 0))
    return pl.BlockSpec(tuple(shape), lambda k, pos: (0,) * len(shape))


def _call(kernel, pos, inputs, outputs, scratch=()):
    from jax.experimental.pallas import tpu as pltpu

    dense = [a for kind, a in inputs if kind == "dense"][0]
    grid_spec = pltpu.PrefetchScalarGridSpec(
        num_scalar_prefetch=1,
        grid=(dense.shape[0],),
        in_specs=[_spec(kind, a.shape) for kind, a in inputs],
        out_specs=[_spec(kind, o.shape) for kind, o in outputs],
        scratch_shapes=list(scratch),
    )
    return pl.pallas_call(
        kernel,
        grid_spec=grid_spec,
        out_shape=[o for kind, o in outputs],
    )(pos, *[a for kind, a in inputs])


def _vmem(shape):
    from jax.experimental.pallas import tpu as pltpu

    return pltpu.VMEM(shape, F32)


def fwd_products(pos, spread, u, ew, blocks):
    k, c, r, s = ew.shape
    has_u = u is not None
    inputs = [("column", spread)] + ([("dense", u)] if has_u else []) + [("dense", ew)]
    outs = [
        ("dense", jax.ShapeDtypeStruct(ew.shape, F32)),
        ("dense", jax.ShapeDtypeStruct(ew.shape, F32)),
        ("full", jax.ShapeDtypeStruct((k, r, s), F32)),
        ("full", jax.ShapeDtypeStruct((blocks, r, s), F32)),
        ("full", jax.ShapeDtypeStruct((k, r, s), F32)),
    ]
    return _call(functools.partial(_fwd_products_kernel, has_u, k, blocks), pos, inputs, outs)


def fwd_messages(pos, ba, sign, here, others, ew, col_blocks):
    k, c, r, s = ba.shape
    inputs = [("dense", ba), ("full", sign), ("full", here), ("full", others), ("dense", ew)]
    outs = [
        ("dense", jax.ShapeDtypeStruct(ba.shape, F32)),
        ("full", jax.ShapeDtypeStruct((col_blocks, c, s), F32)),
    ]
    return _call(functools.partial(_fwd_messages_kernel, k), pos, inputs, outs)


def bwd_messages(pos, gsp, gm, ba, sign, here, others, ew, acc, col_blocks=0):
    k, c, r, s = ba.shape
    has_next = gm is not None
    has_acc = acc is not None
    inputs = (
        [("column", gsp)]
        + ([("dense", gm)] if has_next else [])
        + [("dense", ba), ("full", sign), ("full", here), ("full", others), ("dense", ew)]
        + ([("dense", acc)] if has_acc else [])
    )
    outs = [
        ("dense", jax.ShapeDtypeStruct(ba.shape, F32)),
        ("dense", jax.ShapeDtypeStruct(ba.shape, F32)),
        ("full", jax.ShapeDtypeStruct(here.shape, F32)),
        ("full", jax.ShapeDtypeStruct(others.shape, F32)),
    ]
    if col_blocks:
        outs.append(("full", jax.ShapeDtypeStruct((col_blocks, c, s), F32)))
    return _call(
        functools.partial(_bwd_messages_kernel, has_next, has_acc, col_blocks > 0, k), pos, inputs, outs
    )


def bwd_products(pos, h, gba, grows, ghere, whole, here, col_blocks, emit_gm):
    k, c, r, s = h.shape
    inputs = [
        ("dense", h),
        ("dense", gba),
        ("full", grows),
        ("full", ghere),
        ("full", whole),
        ("full", here),
    ]
    outs = ([("dense", jax.ShapeDtypeStruct(h.shape, F32))] if emit_gm else []) + [
        ("full", jax.ShapeDtypeStruct((col_blocks, c, s), F32))
    ]
    results = _call(
        functools.partial(_bwd_products_kernel, emit_gm, k),
        pos,
        inputs,
        outs,
        [_vmem((c, r, s)) for _ in range(2)],
    )
    if emit_gm:
        return results[0], results[1]
    return None, results[0]


def pick(hot, values):
    parts = []
    for k in range(hot.shape[0]):
        value = jnp.zeros_like(values[0])
        for j in range(hot.shape[1]):
            value = value + jnp.where(hot[k, j] > 0, values[j], 0.0)
        parts.append(value)
    return jnp.stack(parts)


def place(hot, values):
    parts = []
    for j in range(hot.shape[1]):
        value = jnp.zeros_like(values[0])
        for k in range(hot.shape[0]):
            value = value + jnp.where(hot[k, j] > 0, values[k], 0.0)
        parts.append(value)
    return jnp.stack(parts)


def combine(whole, row_hot, same_row):
    slots = whole.shape[0]
    blocks = row_hot.shape[1]
    ones = jnp.ones_like(whole[0])
    rows = []
    for block in range(blocks):
        value = ones
        for k in range(slots):
            value = value * jnp.where(row_hot[k, block] > 0, whole[k], 1.0)
        rows.append(value)
    others_here = []
    for k in range(slots):
        value = ones
        for other in range(slots):
            if other != k:
                value = value * jnp.where(same_row[k, other], whole[other], 1.0)
        others_here.append(value)
    return jnp.stack(rows), jnp.stack(others_here)


def _power_of_two(n):
    return n > 1 and (n & (n - 1)) == 0


def _swap(value, axis, n, step):
    perm = [(j, j ^ (1 << step)) for j in range(n)]
    return lax.ppermute(value, axis, perm)


def checks_total(values, n):
    if not _power_of_two(n):
        return lax.psum(values, "chk")
    step = 0
    while (1 << step) < n:
        values = values + _swap(values, "chk", n, step)
        step += 1
    return values


def others_forward(rows, check_blocks, n, uniform=False):
    if not _power_of_two(n):
        return others_gather(rows, check_blocks)
    if uniform:
        shape = rows.shape
        small = rows[:, :, 0].reshape(-1, shape[2])
        others, trail = others_forward(small, check_blocks, n)
        grow = lambda value: jnp.broadcast_to(value.reshape(shape[:2] + (1,)), shape)
        trail = [tuple(grow(value) for value in entry) for entry in trail]
        return grow(others), trail
    full = rows
    excl = jnp.ones_like(rows)
    trail = []
    step = 0
    while (1 << step) < n:
        other = _swap(full, "var", n, step)
        trail.append((full, excl, other))
        excl = excl * other
        full = full * other
        step += 1
    return excl, trail


def others_backward(trail, grads, check_blocks, n):
    if not _power_of_two(n):
        return others_scatter(trail, grads, check_blocks)
    spread = grads
    target = jnp.zeros_like(grads)
    for step, (full, excl, other) in enumerate(trail):
        other_spread = _swap(spread, "var", n, step)
        target = target * other + excl * other_spread
        spread = spread * other + other_spread * full
    return target


def others_gather(rows, check_blocks):
    own = lax.axis_index("var")
    piece = lax.all_gather(rows, "var", axis=0, tiled=True)
    indices = jnp.arange(piece.shape[0], dtype=jnp.int32)
    keep = indices // check_blocks != own
    parts = []
    for block in range(check_blocks):
        pick = (keep & (indices % check_blocks == block))[:, None, None]
        parts.append(jnp.prod(jnp.where(pick, piece, 1.0), axis=0))
    return jnp.stack(parts), piece


def others_scatter(row_piece, grads, check_blocks):
    own = lax.axis_index("var")
    grad_piece = lax.all_gather(grads, "var", axis=0, tiled=True)
    indices = jnp.arange(row_piece.shape[0], dtype=jnp.int32)
    keep = indices // check_blocks != own
    new_sums = []
    for block in range(check_blocks):
        pick = (keep & (indices % check_blocks == block))[:, None, None]
        factors = jnp.where(pick, row_piece, 1.0)
        weights = jnp.where(pick, grad_piece, 0.0)
        before, after, whole = exclusive_both(factors, 0)
        new_sums.append(jnp.sum(weights * before * after, axis=0))
    return jnp.stack(new_sums)


def body(n_chk, n_var, tile_bits, tile_pos, tile_count, edge_weight, syndrome, channel_prior, out_cot):
    slot_total = tile_bits.shape[2]
    shots = syndrome.shape[1]
    check_blocks = syndrome.shape[0] // TILE
    column_blocks = channel_prior.shape[0] // TILE
    edge, row_hot, col_hot, same_row = device_tables(
        tile_bits[0, 0], tile_pos[0, 0], tile_count[0, 0], check_blocks, column_blocks
    )
    weight = edge_weight[0, 0].reshape(slot_total, TILE, TILE)
    edge_t = jnp.swapaxes(edge, 1, 2)
    filled = jnp.any(edge_t > 0, axis=2)
    order = jnp.argsort(jnp.where(filled, 0, 1).astype(jnp.int32), axis=1, stable=True)
    pos = jnp.concatenate(
        [
            tile_pos[0, 0].reshape(slot_total * 2),
            jnp.sum(filled.astype(jnp.int32), axis=1),
            order.astype(jnp.int32).reshape(slot_total * TILE),
        ]
    )
    dense = (slot_total, TILE, TILE, shots)
    ew = jnp.broadcast_to((edge_t * jnp.swapaxes(weight, 1, 2))[..., None], dense)
    sign_dev = (1.0 - 2.0 * syndrome.astype(jnp.float32)).reshape(check_blocks, TILE, shots)
    sign_slot = jnp.einsum("kc,crs->krs", row_hot, sign_dev, precision=EXACT)
    prior_dev = channel_prior.reshape(column_blocks, TILE)
    spread = jnp.broadcast_to(prior_dev[:, :, None], (column_blocks, TILE, shots))
    u = None
    saved = []
    total = None
    for step in range(ITERS):
        ba, halves, whole, rows, others_here = fwd_products(pos, spread, u, ew, check_blocks)
        others, trail = others_forward(rows, check_blocks, n_var, uniform=(step == 0 and (check_blocks * TILE) % shots == 0))
        saved.append((halves, ba, whole, others_here, others, trail))
        if step + 1 < ITERS:
            u, column = fwd_messages(pos, ba, sign_slot, others_here, others, ew, column_blocks)
            total = prior_dev[:, :, None] + checks_total(column, n_chk)
            spread = total

    grad_total = out_cot.reshape(column_blocks, TILE, shots)
    prior_grad = jnp.zeros((column_blocks, TILE), jnp.float32)
    grad_m = None
    acc = None
    for step in reversed(range(ITERS)):
        halves, ba, whole, others_here, others, trail = saved[step]
        prior_grad = prior_grad + jnp.sum(grad_total, axis=2)
        if step + 1 == ITERS:
            acc, grad_ba, grad_here, grad_others, last_column = bwd_messages(
                pos, grad_total, grad_m, ba, sign_slot, others_here, others, ew, acc, column_blocks
            )
            total = prior_dev[:, :, None] + checks_total(last_column, n_chk)
            marginals = total.reshape(column_blocks * TILE, shots)
        else:
            acc, grad_ba, grad_here, grad_others = bwd_messages(
                pos, grad_total, grad_m, ba, sign_slot, others_here, others, ew, acc
            )
        grad_rows = others_backward(trail, grad_others, check_blocks, n_var)
        grad_m, column = bwd_products(
            pos, halves, grad_ba, grad_rows, grad_here, whole, others_here,
            column_blocks, step > 0,
        )
        if step > 0:
            grad_total = checks_total(column, n_chk)
    shot_sums = jnp.sum(column, axis=2)
    if (column_blocks * TILE) % 128 == 0:
        shot_sums = checks_total(shot_sums.reshape(-1, 128), n_chk).reshape(column_blocks, TILE)
    else:
        shot_sums = checks_total(shot_sums, n_chk)
    prior_grad = prior_grad + shot_sums
    weight_grad = jnp.where(edge > 0, jnp.swapaxes(jnp.sum(acc, axis=3), 1, 2), 0.0)
    return (
        marginals,
        weight_grad.reshape(1, 1, slot_total, TILE * TILE),
        prior_grad.reshape(column_blocks * TILE),
    )


def solution(mesh):
    placed = (
        P("chk", "var", None, None),
        P("chk", "var", None, None),
        P("chk", "var"),
        P("chk", "var", None, None),
        P("chk", None),
        P("var"),
        P("var", None),
    )
    return jax.shard_map(
        functools.partial(body, mesh.shape["chk"], mesh.shape["var"]),
        mesh=mesh,
        in_specs=placed,
        out_specs=(P("var", None), P("chk", "var", None, None), P("var")),
        check_vma=False,
    )
```

```python
import functools

import jax
import jax.numpy as jnp
from jax import lax
from jax.experimental import pallas as pl
from jax.sharding import PartitionSpec as P

TILE = 64
ITERS = 2


DAMP = 0.97
EXACT = lax.Precision.HIGHEST
F32 = jnp.float32
UNROLL = 4


def linear_both(values, axis):
    length = values.shape[axis]
    pieces = [lax.slice_in_dim(values, index, index + 1, axis=axis) for index in range(length)]
    ones = jnp.ones_like(pieces[0])
    prefix = [ones]
    for index in range(length - 1):
        prefix.append(prefix[-1] * pieces[index])
    suffix = [ones]
    for index in range(length - 1, 0, -1):
        suffix.append(suffix[-1] * pieces[index])
    suffix = suffix[::-1]
    whole = prefix[-1] * pieces[-1]
    return (jnp.concatenate(prefix, axis=axis), jnp.concatenate(suffix, axis=axis), whole)


def exclusive_both(values, axis):
    length = values.shape[axis]
    if length < 16 or length % 8 != 0:
        return linear_both(values, axis)
    shape = values.shape
    split = values.reshape(shape[:axis] + (length // 8, 8) + shape[axis + 1 :])
    inner_before, inner_after, group_whole = linear_both(split, axis + 1)
    outer_before, outer_after, whole = exclusive_both(group_whole, axis)
    before = (inner_before * outer_before).reshape(shape)
    after = (inner_after * outer_after).reshape(shape)
    whole = whole.reshape(shape[:axis] + (1,) + shape[axis + 1 :])
    return (before, after, whole)


def device_tables(bits, positions, count, check_blocks, column_blocks):
    slot_total = bits.shape[0]
    slots = jnp.arange(slot_total, dtype=jnp.int32)
    live = slots < count
    edge = jnp.where(live[:, None], bits, 0).astype(jnp.float32).reshape(slot_total, TILE, TILE)
    row_hot = (positions[:, 0:1] == jnp.arange(check_blocks, dtype=jnp.int32)[None, :]).astype(
        jnp.float32
    )
    col_hot = (positions[:, 1:2] == jnp.arange(column_blocks, dtype=jnp.int32)[None, :]).astype(
        jnp.float32
    )
    same_row = (positions[:, None, 0] == positions[None, :, 0]) & (slots[:, None] != slots[None, :])
    return (edge, row_hot, col_hot, same_row)


def _spread_row(ref, c, shape):
    return jnp.broadcast_to(ref[0, pl.ds(c, 1), :], shape)


def _row_block(pos_ref, k):
    return pos_ref[2 * k]


def _col_block(pos_ref, k):
    return pos_ref[2 * k + 1]


def _columns(pos_ref, k, slots, n_c):
    return pos_ref[2 * slots + k], 3 * slots + k * n_c


def _loop(count, body, init, start=0):
    def group(j, carry):
        for t in range(UNROLL):
            carry = body(start + UNROLL * j + t, carry)
        return carry

    carry = lax.fori_loop(0, count // UNROLL, group, init)
    return lax.fori_loop(start + UNROLL * (count // UNROLL), start + count, body, carry)


def _half_range(pos_ref, k, h, slots, n_c):
    count, base = _columns(pos_ref, k, slots, n_c)
    low = pos_ref[3 * slots + slots * n_c + k]
    start = jnp.where(h == 0, 0, low)
    stop = jnp.where(h == 0, low, count)
    return start, stop - start, base


def _fwd_products_kernel(has_u, slots, blocks, pos_ref, *refs):
    refs = list(refs)
    spread_ref = refs.pop(0)
    u_ref = refs.pop(0) if has_u else None
    ew_ref, ba_ref, h_scr, whole_ref, rows_ref, here_ref = refs
    k = pl.program_id(0)
    n_c = ew_ref.shape[1]
    shape = ew_ref.shape[2:]

    count, base = _columns(pos_ref, k, slots, n_c)

    def forward(i, carry):
        c = pos_ref[base + i]
        m = _spread_row(spread_ref, c, shape)
        if has_u:
            m = m - u_ref[0, c]
        h = jnp.where(ew_ref[0, c] > 0, jnp.tanh(0.5 * m), 1.0)
        h_scr[0, c] = h
        ba_ref[0, c] = carry
        return carry * h

    whole = _loop(count, forward, jnp.ones(shape, F32))
    whole_ref[k] = whole

    def backward(i, carry):
        c = pos_ref[base + count - 1 - i]
        ba_ref[0, c] = ba_ref[0, c] * carry
        return carry * h_scr[0, c]

    _loop(count, backward, jnp.ones(shape, F32))

    @pl.when(k == slots - 1)
    def _():
        wholes = [whole_ref[j] for j in range(slots)]
        rows_of = [_row_block(pos_ref, j) for j in range(slots)]
        for block in range(blocks):
            value = jnp.ones(shape, F32)
            for j in range(slots):
                value = value * jnp.where(rows_of[j] == block, wholes[j], 1.0)
            rows_ref[block] = value
        for j in range(slots):
            value = jnp.ones(shape, F32)
            for other in range(slots):
                if other != j:
                    value = value * jnp.where(rows_of[other] == rows_of[j], wholes[other], 1.0)
            here_ref[j] = value


def _fwd_messages_kernel(slots, pos_ref, ba_ref, sign_ref, here_ref, others_ref, ew_ref, u_ref, col_ref):
    k = pl.program_id(0)
    h = pl.program_id(1)
    width = ba_ref.shape[1]
    n_c = width * 2
    start, count, base = _half_range(pos_ref, k, h, slots, n_c)

    @pl.when((k == 0) & (h == 0))
    def _():
        col_ref[...] = jnp.zeros(col_ref.shape, F32)

    f = sign_ref[k] * here_ref[k] * others_ref[_row_block(pos_ref, k)]
    q = _col_block(pos_ref, k)

    def body(i, carry):
        c = pos_ref[base + i]
        local = c - h * width
        x = ba_ref[0, local] * f
        u = ew_ref[0, local] * jnp.log((1.0 + DAMP * x) / (1.0 - DAMP * x))
        u_ref[0, local] = u
        col_ref[q, pl.ds(c, 1), :] = col_ref[q, pl.ds(c, 1), :] + jnp.sum(u, axis=0, keepdims=True)
        return carry

    _loop(count, body, 0, start)


def _bwd_messages_kernel(has_next, has_acc, emit_column, slots, pos_ref, *refs):
    refs = list(refs)
    gsp_ref = refs.pop(0)
    gm_ref = refs.pop(0) if has_next else None
    ba_ref, sign_ref, here_ref, others_ref, ew_ref = refs[:5]
    refs = refs[5:]
    acc_ref = refs.pop(0) if has_acc else None
    gw_ref, gba_ref, ghere_ref, gothers_ref = refs[:4]
    col_ref = refs[4] if emit_column else None
    d1_scr = refs[-1]
    k = pl.program_id(0)
    h = pl.program_id(1)
    width = ba_ref.shape[1]
    n_c = width * 2
    shape = ba_ref.shape[2:]
    q = _col_block(pos_ref, k)

    @pl.when((k == 0) & (h == 0))
    def _():
        gothers_ref[...] = jnp.zeros(gothers_ref.shape, F32)
        if emit_column:
            col_ref[...] = jnp.zeros(col_ref.shape, F32)

    p = _row_block(pos_ref, k)
    sign = sign_ref[k]
    here = here_ref[k]
    others = others_ref[p]
    f = sign * here * others
    start, count, base = _half_range(pos_ref, k, h, slots, n_c)

    def body(i, total):
        c = pos_ref[base + i]
        local = c - h * width
        gu = _spread_row(gsp_ref, c, shape)
        if has_next:
            gu = gu - gm_ref[0, local]
        ba = ba_ref[0, local]
        x = ba * f
        low = 1.0 - DAMP * x
        high = 1.0 + DAMP * x
        ratio = jnp.log(high / low)
        if emit_column:
            u = ew_ref[0, local] * ratio
            col_ref[q, pl.ds(c, 1), :] = col_ref[q, pl.ds(c, 1), :] + jnp.sum(u, axis=0, keepdims=True)
        gw = gu * ratio
        if has_acc:
            gw = gw + acc_ref[0, local]
        gw_ref[0, local] = gw
        gx = gu * ew_ref[0, local] * ((2.0 * DAMP) / (low * high))
        gba_ref[0, local] = gx * f
        return total + gx * ba

    begin = jnp.where(h == 0, jnp.zeros(shape, F32), d1_scr[...])
    grad_factor = _loop(count, body, begin, start)
    d1_scr[...] = grad_factor

    @pl.when(h == 1)
    def _():
        ghere_ref[k] = grad_factor * sign * others
        gothers_ref[p] = gothers_ref[p] + grad_factor * sign * here


def _bwd_products_kernel(emit_gm, slots, pos_ref, *refs):
    refs = list(refs)
    h_ref, gba_ref, grows_ref, ghere_ref, whole_ref, here_ref = refs[:6]
    refs = refs[6:]
    gm_ref = refs.pop(0) if emit_gm else None
    col_ref, p_scr, q_scr = refs
    k = pl.program_id(0)
    n_c = h_ref.shape[1]
    shape = h_ref.shape[2:]

    @pl.when(k == 0)
    def _():
        col_ref[...] = jnp.zeros(col_ref.shape, F32)

    p = _row_block(pos_ref, k)
    q = _col_block(pos_ref, k)
    rows_of = [_row_block(pos_ref, j) for j in range(slots)]
    gwh = grows_ref[p] * here_ref[k]
    for other in range(slots):
        term = jnp.where(rows_of[other] == p, ghere_ref[other], 0.0)
        for third in range(slots):
            if third != other:
                term = term * jnp.where(
                    (rows_of[third] == p) & (third != k), whole_ref[third], 1.0
                )
        gwh = gwh + jnp.where(other != k, term, 0.0)

    count, base = _columns(pos_ref, k, slots, n_c)

    def forward(i, carry):
        prod, grad = carry
        c = pos_ref[base + i]
        h = h_ref[0, c]
        p_scr[c] = prod
        q_scr[c] = grad
        return (prod * h, grad * h + gba_ref[0, c] * prod)

    ones = jnp.ones(shape, F32)
    zeros = jnp.zeros(shape, F32)
    _loop(count, forward, (ones, zeros))

    def backward(i, carry):
        prod, grad = carry
        c = pos_ref[base + count - 1 - i]
        h = h_ref[0, c]
        before = p_scr[c]
        gh = q_scr[c] * prod + before * (grad + gwh * prod)
        gm = gh * (0.5 * (1.0 - h * h))
        if emit_gm:
            gm_ref[0, c] = gm
        col_ref[q, pl.ds(c, 1), :] = col_ref[q, pl.ds(c, 1), :] + jnp.sum(gm, axis=0, keepdims=True)
        return (prod * h, grad * h + gba_ref[0, c] * prod)

    _loop(count, backward, (ones, zeros))


def _spec(kind, shape, halves):
    if halves > 1:
        if kind == "dense":
            block = (1, shape[1] // halves) + tuple(shape[2:])
            return pl.BlockSpec(block, lambda k, h, pos: (k, h, 0, 0))
        if kind == "column":
            return pl.BlockSpec((1,) + tuple(shape[1:]), lambda k, h, pos: (pos[2 * k + 1], 0, 0))
        return pl.BlockSpec(tuple(shape), lambda k, h, pos: (0,) * len(shape))
    if kind == "dense":
        return pl.BlockSpec((1,) + tuple(shape[1:]), lambda k, pos: (k, 0, 0, 0))
    if kind == "column":
        return pl.BlockSpec((1,) + tuple(shape[1:]), lambda k, pos: (pos[2 * k + 1], 0, 0))
    return pl.BlockSpec(tuple(shape), lambda k, pos: (0,) * len(shape))


def _call(kernel, pos, inputs, outputs, scratch=(), halves=1):
    from jax.experimental.pallas import tpu as pltpu

    dense = [a for kind, a in inputs if kind == "dense"][0]
    grid = (dense.shape[0],) if halves == 1 else (dense.shape[0], halves)
    grid_spec = pltpu.PrefetchScalarGridSpec(
        num_scalar_prefetch=1,
        grid=grid,
        in_specs=[_spec(kind, a.shape, halves) for kind, a in inputs],
        out_specs=[_spec(kind, o.shape, halves) for kind, o in outputs],
        scratch_shapes=list(scratch),
    )
    return pl.pallas_call(
        kernel,
        grid_spec=grid_spec,
        out_shape=[o for kind, o in outputs],
    )(pos, *[a for kind, a in inputs])


def _vmem(shape):
    from jax.experimental.pallas import tpu as pltpu

    return pltpu.VMEM(shape, F32)


def fwd_products(pos, spread, u, ew, blocks):
    k, c, r, s = ew.shape
    has_u = u is not None
    inputs = [("column", spread)] + ([("dense", u)] if has_u else []) + [("dense", ew)]
    outs = [
        ("dense", jax.ShapeDtypeStruct(ew.shape, F32)),
        ("dense", jax.ShapeDtypeStruct(ew.shape, F32)),
        ("full", jax.ShapeDtypeStruct((k, r, s), F32)),
        ("full", jax.ShapeDtypeStruct((blocks, r, s), F32)),
        ("full", jax.ShapeDtypeStruct((k, r, s), F32)),
    ]
    return _call(functools.partial(_fwd_products_kernel, has_u, k, blocks), pos, inputs, outs)


def fwd_messages(pos, ba, sign, here, others, ew, col_blocks):
    k, c, r, s = ba.shape
    inputs = [("dense", ba), ("full", sign), ("full", here), ("full", others), ("dense", ew)]
    outs = [
        ("dense", jax.ShapeDtypeStruct(ba.shape, F32)),
        ("full", jax.ShapeDtypeStruct((col_blocks, c, s), F32)),
    ]
    return _call(functools.partial(_fwd_messages_kernel, k), pos, inputs, outs, halves=2)


def bwd_messages(pos, gsp, gm, ba, sign, here, others, ew, acc, col_blocks=0):
    k, c, r, s = ba.shape
    has_next = gm is not None
    has_acc = acc is not None
    inputs = (
        [("column", gsp)]
        + ([("dense", gm)] if has_next else [])
        + [("dense", ba), ("full", sign), ("full", here), ("full", others), ("dense", ew)]
        + ([("dense", acc)] if has_acc else [])
    )
    outs = [
        ("dense", jax.ShapeDtypeStruct(ba.shape, F32)),
        ("dense", jax.ShapeDtypeStruct(ba.shape, F32)),
        ("full", jax.ShapeDtypeStruct(here.shape, F32)),
        ("full", jax.ShapeDtypeStruct(others.shape, F32)),
    ]
    if col_blocks:
        outs.append(("full", jax.ShapeDtypeStruct((col_blocks, c, s), F32)))
    return _call(
        functools.partial(_bwd_messages_kernel, has_next, has_acc, col_blocks > 0, k),
        pos,
        inputs,
        outs,
        [_vmem((r, s))],
        halves=2,
    )


def bwd_products(pos, h, gba, grows, ghere, whole, here, col_blocks, emit_gm):
    k, c, r, s = h.shape
    inputs = [
        ("dense", h),
        ("dense", gba),
        ("full", grows),
        ("full", ghere),
        ("full", whole),
        ("full", here),
    ]
    outs = ([("dense", jax.ShapeDtypeStruct(h.shape, F32))] if emit_gm else []) + [
        ("full", jax.ShapeDtypeStruct((col_blocks, c, s), F32))
    ]
    results = _call(
        functools.partial(_bwd_products_kernel, emit_gm, k),
        pos,
        inputs,
        outs,
        [_vmem((c, r, s)) for _ in range(2)],
    )
    if emit_gm:
        return results[0], results[1]
    return None, results[0]


def pick(hot, values):
    parts = []
    for k in range(hot.shape[0]):
        value = jnp.zeros_like(values[0])
        for j in range(hot.shape[1]):
            value = value + jnp.where(hot[k, j] > 0, values[j], 0.0)
        parts.append(value)
    return jnp.stack(parts)


def place(hot, values):
    parts = []
    for j in range(hot.shape[1]):
        value = jnp.zeros_like(values[0])
        for k in range(hot.shape[0]):
            value = value + jnp.where(hot[k, j] > 0, values[k], 0.0)
        parts.append(value)
    return jnp.stack(parts)


def combine(whole, row_hot, same_row):
    slots = whole.shape[0]
    blocks = row_hot.shape[1]
    ones = jnp.ones_like(whole[0])
    rows = []
    for block in range(blocks):
        value = ones
        for k in range(slots):
            value = value * jnp.where(row_hot[k, block] > 0, whole[k], 1.0)
        rows.append(value)
    others_here = []
    for k in range(slots):
        value = ones
        for other in range(slots):
            if other != k:
                value = value * jnp.where(same_row[k, other], whole[other], 1.0)
        others_here.append(value)
    return jnp.stack(rows), jnp.stack(others_here)


def _power_of_two(n):
    return n > 1 and (n & (n - 1)) == 0


def _swap(value, axis, n, step):
    perm = [(j, j ^ (1 << step)) for j in range(n)]
    return lax.ppermute(value, axis, perm)


def checks_total(values, n):
    if not _power_of_two(n):
        return lax.psum(values, "chk")
    step = 0
    while (1 << step) < n:
        values = values + _swap(values, "chk", n, step)
        step += 1
    return values


def others_forward(rows, check_blocks, n, uniform=False):
    if not _power_of_two(n):
        return others_gather(rows, check_blocks)
    if uniform:
        shape = rows.shape
        small = rows[:, :, 0].reshape(-1, shape[2])
        others, trail = others_forward(small, check_blocks, n)
        grow = lambda value: jnp.broadcast_to(value.reshape(shape[:2] + (1,)), shape)
        trail = [tuple(grow(value) for value in entry) for entry in trail]
        return grow(others), trail
    full = rows
    excl = jnp.ones_like(rows)
    trail = []
    step = 0
    while (1 << step) < n:
        other = _swap(full, "var", n, step)
        trail.append((full, excl, other))
        excl = excl * other
        full = full * other
        step += 1
    return excl, trail


def others_backward(trail, grads, check_blocks, n):
    if not _power_of_two(n):
        return others_scatter(trail, grads, check_blocks)
    spread = grads
    target = jnp.zeros_like(grads)
    for step, (full, excl, other) in enumerate(trail):
        other_spread = _swap(spread, "var", n, step)
        target = target * other + excl * other_spread
        spread = spread * other + other_spread * full
    return target


def others_gather(rows, check_blocks):
    own = lax.axis_index("var")
    piece = lax.all_gather(rows, "var", axis=0, tiled=True)
    indices = jnp.arange(piece.shape[0], dtype=jnp.int32)
    keep = indices // check_blocks != own
    parts = []
    for block in range(check_blocks):
        pick = (keep & (indices % check_blocks == block))[:, None, None]
        parts.append(jnp.prod(jnp.where(pick, piece, 1.0), axis=0))
    return jnp.stack(parts), piece


def others_scatter(row_piece, grads, check_blocks):
    own = lax.axis_index("var")
    grad_piece = lax.all_gather(grads, "var", axis=0, tiled=True)
    indices = jnp.arange(row_piece.shape[0], dtype=jnp.int32)
    keep = indices // check_blocks != own
    new_sums = []
    for block in range(check_blocks):
        pick = (keep & (indices % check_blocks == block))[:, None, None]
        factors = jnp.where(pick, row_piece, 1.0)
        weights = jnp.where(pick, grad_piece, 0.0)
        before, after, whole = exclusive_both(factors, 0)
        new_sums.append(jnp.sum(weights * before * after, axis=0))
    return jnp.stack(new_sums)


def body(n_chk, n_var, tile_bits, tile_pos, tile_count, edge_weight, syndrome, channel_prior, out_cot):
    slot_total = tile_bits.shape[2]
    shots = syndrome.shape[1]
    check_blocks = syndrome.shape[0] // TILE
    column_blocks = channel_prior.shape[0] // TILE
    edge, row_hot, col_hot, same_row = device_tables(
        tile_bits[0, 0], tile_pos[0, 0], tile_count[0, 0], check_blocks, column_blocks
    )
    weight = edge_weight[0, 0].reshape(slot_total, TILE, TILE)
    edge_t = jnp.swapaxes(edge, 1, 2)
    filled = jnp.any(edge_t > 0, axis=2)
    order = jnp.argsort(jnp.where(filled, 0, 1).astype(jnp.int32), axis=1, stable=True)
    pos = jnp.concatenate(
        [
            tile_pos[0, 0].reshape(slot_total * 2),
            jnp.sum(filled.astype(jnp.int32), axis=1),
            order.astype(jnp.int32).reshape(slot_total * TILE),
            jnp.sum(filled[:, : TILE // 2].astype(jnp.int32), axis=1),
        ]
    )
    dense = (slot_total, TILE, TILE, shots)
    ew = jnp.broadcast_to((edge_t * jnp.swapaxes(weight, 1, 2))[..., None], dense)
    sign_dev = (1.0 - 2.0 * syndrome.astype(jnp.float32)).reshape(check_blocks, TILE, shots)
    sign_slot = jnp.einsum("kc,crs->krs", row_hot, sign_dev, precision=EXACT)
    prior_dev = channel_prior.reshape(column_blocks, TILE)
    spread = jnp.broadcast_to(prior_dev[:, :, None], (column_blocks, TILE, shots))
    u = None
    saved = []
    total = None
    for step in range(ITERS):
        ba, halves, whole, rows, others_here = fwd_products(pos, spread, u, ew, check_blocks)
        others, trail = others_forward(rows, check_blocks, n_var, uniform=(step == 0 and (check_blocks * TILE) % shots == 0))
        saved.append((halves, ba, whole, others_here, others, trail))
        if step + 1 < ITERS:
            u, column = fwd_messages(pos, ba, sign_slot, others_here, others, ew, column_blocks)
            total = prior_dev[:, :, None] + checks_total(column, n_chk)
            spread = total

    grad_total = out_cot.reshape(column_blocks, TILE, shots)
    prior_grad = jnp.zeros((column_blocks, TILE), jnp.float32)
    grad_m = None
    acc = None
    for step in reversed(range(ITERS)):
        halves, ba, whole, others_here, others, trail = saved[step]
        prior_grad = prior_grad + jnp.sum(grad_total, axis=2)
        if step + 1 == ITERS:
            acc, grad_ba, grad_here, grad_others, last_column = bwd_messages(
                pos, grad_total, grad_m, ba, sign_slot, others_here, others, ew, acc, column_blocks
            )
            total = prior_dev[:, :, None] + checks_total(last_column, n_chk)
            marginals = total.reshape(column_blocks * TILE, shots)
        else:
            acc, grad_ba, grad_here, grad_others = bwd_messages(
                pos, grad_total, grad_m, ba, sign_slot, others_here, others, ew, acc
            )
        grad_rows = others_backward(trail, grad_others, check_blocks, n_var)
        grad_m, column = bwd_products(
            pos, halves, grad_ba, grad_rows, grad_here, whole, others_here,
            column_blocks, step > 0,
        )
        if step > 0:
            grad_total = checks_total(column, n_chk)
    shot_sums = jnp.sum(column, axis=2)
    if (column_blocks * TILE) % 128 == 0:
        shot_sums = checks_total(shot_sums.reshape(-1, 128), n_chk).reshape(column_blocks, TILE)
    else:
        shot_sums = checks_total(shot_sums, n_chk)
    prior_grad = prior_grad + shot_sums
    weight_grad = jnp.where(edge > 0, jnp.swapaxes(jnp.sum(acc, axis=3), 1, 2), 0.0)
    return (
        marginals,
        weight_grad.reshape(1, 1, slot_total, TILE * TILE),
        prior_grad.reshape(column_blocks * TILE),
    )


def solution(mesh):
    placed = (
        P("chk", "var", None, None),
        P("chk", "var", None, None),
        P("chk", "var"),
        P("chk", "var", None, None),
        P("chk", None),
        P("var"),
        P("var", None),
    )
    return jax.shard_map(
        functools.partial(body, mesh.shape["chk"], mesh.shape["var"]),
        mesh=mesh,
        in_specs=placed,
        out_specs=(P("var", None), P("chk", "var", None, None), P("var")),
        check_vma=False,
    )
```

```python
import functools

import jax
import jax.numpy as jnp
from jax import lax
from jax.experimental import pallas as pl
from jax.sharding import PartitionSpec as P

TILE = 64
ITERS = 2


DAMP = 0.97
EXACT = lax.Precision.HIGHEST
F32 = jnp.float32
UNROLL = 4


def linear_both(values, axis):
    length = values.shape[axis]
    pieces = [lax.slice_in_dim(values, index, index + 1, axis=axis) for index in range(length)]
    ones = jnp.ones_like(pieces[0])
    prefix = [ones]
    for index in range(length - 1):
        prefix.append(prefix[-1] * pieces[index])
    suffix = [ones]
    for index in range(length - 1, 0, -1):
        suffix.append(suffix[-1] * pieces[index])
    suffix = suffix[::-1]
    whole = prefix[-1] * pieces[-1]
    return (jnp.concatenate(prefix, axis=axis), jnp.concatenate(suffix, axis=axis), whole)


def exclusive_both(values, axis):
    length = values.shape[axis]
    if length < 16 or length % 8 != 0:
        return linear_both(values, axis)
    shape = values.shape
    split = values.reshape(shape[:axis] + (length // 8, 8) + shape[axis + 1 :])
    inner_before, inner_after, group_whole = linear_both(split, axis + 1)
    outer_before, outer_after, whole = exclusive_both(group_whole, axis)
    before = (inner_before * outer_before).reshape(shape)
    after = (inner_after * outer_after).reshape(shape)
    whole = whole.reshape(shape[:axis] + (1,) + shape[axis + 1 :])
    return (before, after, whole)


def device_tables(bits, positions, count, check_blocks, column_blocks):
    slot_total = bits.shape[0]
    slots = jnp.arange(slot_total, dtype=jnp.int32)
    live = slots < count
    edge = jnp.where(live[:, None], bits, 0).astype(jnp.float32).reshape(slot_total, TILE, TILE)
    row_hot = (positions[:, 0:1] == jnp.arange(check_blocks, dtype=jnp.int32)[None, :]).astype(
        jnp.float32
    )
    col_hot = (positions[:, 1:2] == jnp.arange(column_blocks, dtype=jnp.int32)[None, :]).astype(
        jnp.float32
    )
    same_row = (positions[:, None, 0] == positions[None, :, 0]) & (slots[:, None] != slots[None, :])
    return (edge, row_hot, col_hot, same_row)


def _spread_row(ref, c, shape):
    return jnp.broadcast_to(ref[0, pl.ds(c, 1), :], shape)


def _row_block(pos_ref, k):
    return pos_ref[2 * k]


def _col_block(pos_ref, k):
    return pos_ref[2 * k + 1]


def _columns(pos_ref, k, slots, n_c):
    return pos_ref[2 * slots + k], 3 * slots + k * n_c


def _loop(count, body, init):
    def group(j, carry):
        for t in range(UNROLL):
            carry = body(UNROLL * j + t, carry)
        return carry

    carry = lax.fori_loop(0, count // UNROLL, group, init)
    return lax.fori_loop(UNROLL * (count // UNROLL), count, body, carry)


def _fwd_products_kernel(has_u, slots, blocks, pos_ref, *refs):
    refs = list(refs)
    spread_ref = refs.pop(0)
    u_ref = refs.pop(0) if has_u else None
    ew_ref = None if has_u else refs.pop(0)
    ba_ref, h_scr, whole_ref, rows_ref, here_ref = refs
    k = pl.program_id(0)
    n_c = ba_ref.shape[1]
    shape = ba_ref.shape[2:]

    count, base = _columns(pos_ref, k, slots, n_c)

    def forward(i, carry):
        c = pos_ref[base + i]
        m = _spread_row(spread_ref, c, shape)
        if has_u:
            u = u_ref[0, c]
            h = jnp.where(u == u, jnp.tanh(0.5 * (m - u)), 1.0)
        else:
            h = jnp.where(ew_ref[0, c] > 0, jnp.tanh(0.5 * m), 1.0)
        h_scr[0, c] = h
        ba_ref[0, c] = carry
        return carry * h

    whole = _loop(count, forward, jnp.ones(shape, F32))
    whole_ref[k] = whole

    def backward(i, carry):
        c = pos_ref[base + count - 1 - i]
        ba_ref[0, c] = ba_ref[0, c] * carry
        return carry * h_scr[0, c]

    _loop(count, backward, jnp.ones(shape, F32))

    @pl.when(k == slots - 1)
    def _():
        wholes = [whole_ref[j] for j in range(slots)]
        rows_of = [_row_block(pos_ref, j) for j in range(slots)]
        for block in range(blocks):
            value = jnp.ones(shape, F32)
            for j in range(slots):
                value = value * jnp.where(rows_of[j] == block, wholes[j], 1.0)
            rows_ref[block] = value
        for j in range(slots):
            value = jnp.ones(shape, F32)
            for other in range(slots):
                if other != j:
                    value = value * jnp.where(rows_of[other] == rows_of[j], wholes[other], 1.0)
            here_ref[j] = value


def _fwd_messages_kernel(slots, pos_ref, ba_ref, sign_ref, here_ref, others_ref, ew_ref, u_ref, col_ref):
    k = pl.program_id(0)
    n_c = ba_ref.shape[1]
    count, base = _columns(pos_ref, k, slots, n_c)

    @pl.when(k == 0)
    def _():
        col_ref[...] = jnp.zeros(col_ref.shape, F32)

    f = sign_ref[k] * here_ref[k] * others_ref[_row_block(pos_ref, k)]
    q = _col_block(pos_ref, k)

    def body(i, carry):
        c = pos_ref[base + i]
        x = ba_ref[0, c] * f
        u = ew_ref[0, c] * jnp.log((1.0 + DAMP * x) / (1.0 - DAMP * x))
        u_ref[0, c] = jnp.where(ew_ref[0, c] > 0, u, jnp.nan)
        col_ref[q, pl.ds(c, 1), :] = col_ref[q, pl.ds(c, 1), :] + jnp.sum(u, axis=0, keepdims=True)
        return carry

    _loop(count, body, 0)


def _bwd_messages_kernel(has_next, has_acc, emit_column, slots, pos_ref, *refs):
    refs = list(refs)
    gsp_ref = refs.pop(0)
    gm_ref = refs.pop(0) if has_next else None
    ba_ref, sign_ref, here_ref, others_ref, ew_ref = refs[:5]
    refs = refs[5:]
    acc_ref = refs.pop(0) if has_acc else None
    gw_ref, gba_ref, ghere_ref, gothers_ref = refs[:4]
    col_ref = refs[4] if emit_column else None
    k = pl.program_id(0)
    n_c = ba_ref.shape[1]
    shape = ba_ref.shape[2:]
    q = _col_block(pos_ref, k)

    @pl.when(k == 0)
    def _():
        gothers_ref[...] = jnp.zeros(gothers_ref.shape, F32)
        if emit_column:
            col_ref[...] = jnp.zeros(col_ref.shape, F32)

    p = _row_block(pos_ref, k)
    sign = sign_ref[k]
    here = here_ref[k]
    others = others_ref[p]
    f = sign * here * others
    count, base = _columns(pos_ref, k, slots, n_c)

    def body(i, total):
        c = pos_ref[base + i]
        gu = _spread_row(gsp_ref, c, shape)
        if has_next:
            gu = gu - gm_ref[0, c]
        ba = ba_ref[0, c]
        x = ba * f
        low = 1.0 - DAMP * x
        high = 1.0 + DAMP * x
        ratio = jnp.log(high / low)
        if emit_column:
            u = ew_ref[0, c] * ratio
            col_ref[q, pl.ds(c, 1), :] = col_ref[q, pl.ds(c, 1), :] + jnp.sum(u, axis=0, keepdims=True)
        gw = gu * ratio
        if has_acc:
            gw = gw + acc_ref[0, c]
        gw_ref[0, c] = gw
        gx = gu * ew_ref[0, c] * ((2.0 * DAMP) / (low * high))
        gba_ref[0, c] = gx * f
        return total + gx * ba

    grad_factor = _loop(count, body, jnp.zeros(shape, F32))
    ghere_ref[k] = grad_factor * sign * others
    gothers_ref[p] = gothers_ref[p] + grad_factor * sign * here


def _bwd_products_kernel(emit_gm, slots, pos_ref, *refs):
    refs = list(refs)
    h_ref, gba_ref, grows_ref, ghere_ref, whole_ref, here_ref = refs[:6]
    refs = refs[6:]
    gm_ref = refs.pop(0) if emit_gm else None
    col_ref, p_scr, q_scr = refs
    k = pl.program_id(0)
    n_c = h_ref.shape[1]
    shape = h_ref.shape[2:]

    @pl.when(k == 0)
    def _():
        col_ref[...] = jnp.zeros(col_ref.shape, F32)

    p = _row_block(pos_ref, k)
    q = _col_block(pos_ref, k)
    rows_of = [_row_block(pos_ref, j) for j in range(slots)]
    gwh = grows_ref[p] * here_ref[k]
    for other in range(slots):
        term = jnp.where(rows_of[other] == p, ghere_ref[other], 0.0)
        for third in range(slots):
            if third != other:
                term = term * jnp.where(
                    (rows_of[third] == p) & (third != k), whole_ref[third], 1.0
                )
        gwh = gwh + jnp.where(other != k, term, 0.0)

    count, base = _columns(pos_ref, k, slots, n_c)

    def forward(i, carry):
        prod, grad = carry
        c = pos_ref[base + i]
        h = h_ref[0, c]
        p_scr[c] = prod
        q_scr[c] = grad
        return (prod * h, grad * h + gba_ref[0, c] * prod)

    ones = jnp.ones(shape, F32)
    zeros = jnp.zeros(shape, F32)
    _loop(count, forward, (ones, zeros))

    def backward(i, carry):
        prod, grad = carry
        c = pos_ref[base + count - 1 - i]
        h = h_ref[0, c]
        before = p_scr[c]
        gh = q_scr[c] * prod + before * (grad + gwh * prod)
        gm = gh * (0.5 * (1.0 - h * h))
        if emit_gm:
            gm_ref[0, c] = gm
        col_ref[q, pl.ds(c, 1), :] = col_ref[q, pl.ds(c, 1), :] + jnp.sum(gm, axis=0, keepdims=True)
        return (prod * h, grad * h + gba_ref[0, c] * prod)

    _loop(count, backward, (ones, zeros))


def _spec(kind, shape):
    if kind == "dense":
        return pl.BlockSpec((1,) + tuple(shape[1:]), lambda k, pos: (k, 0, 0, 0))
    if kind == "column":
        return pl.BlockSpec((1,) + tuple(shape[1:]), lambda k, pos: (pos[2 * k + 1], 0, 0))
    return pl.BlockSpec(tuple(shape), lambda k, pos: (0,) * len(shape))


def _call(kernel, pos, inputs, outputs, scratch=()):
    from jax.experimental.pallas import tpu as pltpu

    dense = [a for kind, a in inputs if kind == "dense"][0]
    grid_spec = pltpu.PrefetchScalarGridSpec(
        num_scalar_prefetch=1,
        grid=(dense.shape[0],),
        in_specs=[_spec(kind, a.shape) for kind, a in inputs],
        out_specs=[_spec(kind, o.shape) for kind, o in outputs],
        scratch_shapes=list(scratch),
    )
    return pl.pallas_call(
        kernel,
        grid_spec=grid_spec,
        out_shape=[o for kind, o in outputs],
    )(pos, *[a for kind, a in inputs])


def _vmem(shape):
    from jax.experimental.pallas import tpu as pltpu

    return pltpu.VMEM(shape, F32)


def fwd_products(pos, spread, u, ew, blocks):
    k, c, r, s = ew.shape
    has_u = u is not None
    inputs = [("column", spread)] + ([("dense", u)] if has_u else [("dense", ew)])
    outs = [
        ("dense", jax.ShapeDtypeStruct(ew.shape, F32)),
        ("dense", jax.ShapeDtypeStruct(ew.shape, F32)),
        ("full", jax.ShapeDtypeStruct((k, r, s), F32)),
        ("full", jax.ShapeDtypeStruct((blocks, r, s), F32)),
        ("full", jax.ShapeDtypeStruct((k, r, s), F32)),
    ]
    return _call(functools.partial(_fwd_products_kernel, has_u, k, blocks), pos, inputs, outs)


def fwd_messages(pos, ba, sign, here, others, ew, col_blocks):
    k, c, r, s = ba.shape
    inputs = [("dense", ba), ("full", sign), ("full", here), ("full", others), ("dense", ew)]
    outs = [
        ("dense", jax.ShapeDtypeStruct(ba.shape, F32)),
        ("full", jax.ShapeDtypeStruct((col_blocks, c, s), F32)),
    ]
    return _call(functools.partial(_fwd_messages_kernel, k), pos, inputs, outs)


def bwd_messages(pos, gsp, gm, ba, sign, here, others, ew, acc, col_blocks=0):
    k, c, r, s = ba.shape
    has_next = gm is not None
    has_acc = acc is not None
    inputs = (
        [("column", gsp)]
        + ([("dense", gm)] if has_next else [])
        + [("dense", ba), ("full", sign), ("full", here), ("full", others), ("dense", ew)]
        + ([("dense", acc)] if has_acc else [])
    )
    outs = [
        ("dense", jax.ShapeDtypeStruct(ba.shape, F32)),
        ("dense", jax.ShapeDtypeStruct(ba.shape, F32)),
        ("full", jax.ShapeDtypeStruct(here.shape, F32)),
        ("full", jax.ShapeDtypeStruct(others.shape, F32)),
    ]
    if col_blocks:
        outs.append(("full", jax.ShapeDtypeStruct((col_blocks, c, s), F32)))
    return _call(
        functools.partial(_bwd_messages_kernel, has_next, has_acc, col_blocks > 0, k), pos, inputs, outs
    )


def bwd_products(pos, h, gba, grows, ghere, whole, here, col_blocks, emit_gm):
    k, c, r, s = h.shape
    inputs = [
        ("dense", h),
        ("dense", gba),
        ("full", grows),
        ("full", ghere),
        ("full", whole),
        ("full", here),
    ]
    outs = ([("dense", jax.ShapeDtypeStruct(h.shape, F32))] if emit_gm else []) + [
        ("full", jax.ShapeDtypeStruct((col_blocks, c, s), F32))
    ]
    results = _call(
        functools.partial(_bwd_products_kernel, emit_gm, k),
        pos,
        inputs,
        outs,
        [_vmem((c, r, s)) for _ in range(2)],
    )
    if emit_gm:
        return results[0], results[1]
    return None, results[0]


def pick(hot, values):
    parts = []
    for k in range(hot.shape[0]):
        value = jnp.zeros_like(values[0])
        for j in range(hot.shape[1]):
            value = value + jnp.where(hot[k, j] > 0, values[j], 0.0)
        parts.append(value)
    return jnp.stack(parts)


def place(hot, values):
    parts = []
    for j in range(hot.shape[1]):
        value = jnp.zeros_like(values[0])
        for k in range(hot.shape[0]):
            value = value + jnp.where(hot[k, j] > 0, values[k], 0.0)
        parts.append(value)
    return jnp.stack(parts)


def combine(whole, row_hot, same_row):
    slots = whole.shape[0]
    blocks = row_hot.shape[1]
    ones = jnp.ones_like(whole[0])
    rows = []
    for block in range(blocks):
        value = ones
        for k in range(slots):
            value = value * jnp.where(row_hot[k, block] > 0, whole[k], 1.0)
        rows.append(value)
    others_here = []
    for k in range(slots):
        value = ones
        for other in range(slots):
            if other != k:
                value = value * jnp.where(same_row[k, other], whole[other], 1.0)
        others_here.append(value)
    return jnp.stack(rows), jnp.stack(others_here)


def _power_of_two(n):
    return n > 1 and (n & (n - 1)) == 0


def _swap(value, axis, n, step):
    perm = [(j, j ^ (1 << step)) for j in range(n)]
    return lax.ppermute(value, axis, perm)


def checks_total(values, n):
    if not _power_of_two(n):
        return lax.psum(values, "chk")
    step = 0
    while (1 << step) < n:
        values = values + _swap(values, "chk", n, step)
        step += 1
    return values


def others_forward(rows, check_blocks, n, uniform=False):
    if not _power_of_two(n):
        return others_gather(rows, check_blocks)
    if uniform:
        shape = rows.shape
        small = rows[:, :, 0].reshape(-1, shape[2])
        others, trail = others_forward(small, check_blocks, n)
        grow = lambda value: jnp.broadcast_to(value.reshape(shape[:2] + (1,)), shape)
        trail = [tuple(grow(value) for value in entry) for entry in trail]
        return grow(others), trail
    full = rows
    excl = jnp.ones_like(rows)
    trail = []
    step = 0
    while (1 << step) < n:
        other = _swap(full, "var", n, step)
        trail.append((full, excl, other))
        excl = excl * other
        full = full * other
        step += 1
    return excl, trail


def others_backward(trail, grads, check_blocks, n):
    if not _power_of_two(n):
        return others_scatter(trail, grads, check_blocks)
    spread = grads
    target = jnp.zeros_like(grads)
    for step, (full, excl, other) in enumerate(trail):
        other_spread = _swap(spread, "var", n, step)
        target = target * other + excl * other_spread
        spread = spread * other + other_spread * full
    return target


def others_gather(rows, check_blocks):
    own = lax.axis_index("var")
    piece = lax.all_gather(rows, "var", axis=0, tiled=True)
    indices = jnp.arange(piece.shape[0], dtype=jnp.int32)
    keep = indices // check_blocks != own
    parts = []
    for block in range(check_blocks):
        pick = (keep & (indices % check_blocks == block))[:, None, None]
        parts.append(jnp.prod(jnp.where(pick, piece, 1.0), axis=0))
    return jnp.stack(parts), piece


def others_scatter(row_piece, grads, check_blocks):
    own = lax.axis_index("var")
    grad_piece = lax.all_gather(grads, "var", axis=0, tiled=True)
    indices = jnp.arange(row_piece.shape[0], dtype=jnp.int32)
    keep = indices // check_blocks != own
    new_sums = []
    for block in range(check_blocks):
        pick = (keep & (indices % check_blocks == block))[:, None, None]
        factors = jnp.where(pick, row_piece, 1.0)
        weights = jnp.where(pick, grad_piece, 0.0)
        before, after, whole = exclusive_both(factors, 0)
        new_sums.append(jnp.sum(weights * before * after, axis=0))
    return jnp.stack(new_sums)


def body(n_chk, n_var, tile_bits, tile_pos, tile_count, edge_weight, syndrome, channel_prior, out_cot):
    slot_total = tile_bits.shape[2]
    shots = syndrome.shape[1]
    check_blocks = syndrome.shape[0] // TILE
    column_blocks = channel_prior.shape[0] // TILE
    edge, row_hot, col_hot, same_row = device_tables(
        tile_bits[0, 0], tile_pos[0, 0], tile_count[0, 0], check_blocks, column_blocks
    )
    weight = edge_weight[0, 0].reshape(slot_total, TILE, TILE)
    edge_t = jnp.swapaxes(edge, 1, 2)
    filled = jnp.any(edge_t > 0, axis=2)
    order = jnp.argsort(jnp.where(filled, 0, 1).astype(jnp.int32), axis=1, stable=True)
    pos = jnp.concatenate(
        [
            tile_pos[0, 0].reshape(slot_total * 2),
            jnp.sum(filled.astype(jnp.int32), axis=1),
            order.astype(jnp.int32).reshape(slot_total * TILE),
        ]
    )
    dense = (slot_total, TILE, TILE, shots)
    ew = jnp.broadcast_to((edge_t * jnp.swapaxes(weight, 1, 2))[..., None], dense)
    sign_dev = (1.0 - 2.0 * syndrome.astype(jnp.float32)).reshape(check_blocks, TILE, shots)
    sign_slot = jnp.einsum("kc,crs->krs", row_hot, sign_dev, precision=EXACT)
    prior_dev = channel_prior.reshape(column_blocks, TILE)
    spread = jnp.broadcast_to(prior_dev[:, :, None], (column_blocks, TILE, shots))
    u = None
    saved = []
    total = None
    for step in range(ITERS):
        ba, halves, whole, rows, others_here = fwd_products(pos, spread, u, ew, check_blocks)
        others, trail = others_forward(rows, check_blocks, n_var, uniform=(step == 0 and (check_blocks * TILE) % shots == 0))
        saved.append((halves, ba, whole, others_here, others, trail))
        if step + 1 < ITERS:
            u, column = fwd_messages(pos, ba, sign_slot, others_here, others, ew, column_blocks)
            total = prior_dev[:, :, None] + checks_total(column, n_chk)
            spread = total

    grad_total = out_cot.reshape(column_blocks, TILE, shots)
    prior_grad = jnp.zeros((column_blocks, TILE), jnp.float32)
    grad_m = None
    acc = None
    for step in reversed(range(ITERS)):
        halves, ba, whole, others_here, others, trail = saved[step]
        prior_grad = prior_grad + jnp.sum(grad_total, axis=2)
        if step + 1 == ITERS:
            acc, grad_ba, grad_here, grad_others, last_column = bwd_messages(
                pos, grad_total, grad_m, ba, sign_slot, others_here, others, ew, acc, column_blocks
            )
            total = prior_dev[:, :, None] + checks_total(last_column, n_chk)
            marginals = total.reshape(column_blocks * TILE, shots)
        else:
            acc, grad_ba, grad_here, grad_others = bwd_messages(
                pos, grad_total, grad_m, ba, sign_slot, others_here, others, ew, acc
            )
        grad_rows = others_backward(trail, grad_others, check_blocks, n_var)
        grad_m, column = bwd_products(
            pos, halves, grad_ba, grad_rows, grad_here, whole, others_here,
            column_blocks, step > 0,
        )
        if step > 0:
            grad_total = checks_total(column, n_chk)
    shot_sums = jnp.sum(column, axis=2)
    if (column_blocks * TILE) % 128 == 0:
        shot_sums = checks_total(shot_sums.reshape(-1, 128), n_chk).reshape(column_blocks, TILE)
    else:
        shot_sums = checks_total(shot_sums, n_chk)
    prior_grad = prior_grad + shot_sums
    weight_grad = jnp.where(edge > 0, jnp.swapaxes(jnp.sum(acc, axis=3), 1, 2), 0.0)
    return (
        marginals,
        weight_grad.reshape(1, 1, slot_total, TILE * TILE),
        prior_grad.reshape(column_blocks * TILE),
    )


def solution(mesh):
    placed = (
        P("chk", "var", None, None),
        P("chk", "var", None, None),
        P("chk", "var"),
        P("chk", "var", None, None),
        P("chk", None),
        P("var"),
        P("var", None),
    )
    return jax.shard_map(
        functools.partial(body, mesh.shape["chk"], mesh.shape["var"]),
        mesh=mesh,
        in_specs=placed,
        out_specs=(P("var", None), P("chk", "var", None, None), P("var")),
        check_vma=False,
    )
```

```python
import functools

import jax
import jax.numpy as jnp
from jax import lax
from jax.experimental import pallas as pl
from jax.sharding import PartitionSpec as P

TILE = 64
ITERS = 2


DAMP = 0.97
EXACT = lax.Precision.HIGHEST
F32 = jnp.float32
UNROLL = 4


def linear_both(values, axis):
    length = values.shape[axis]
    pieces = [lax.slice_in_dim(values, index, index + 1, axis=axis) for index in range(length)]
    ones = jnp.ones_like(pieces[0])
    prefix = [ones]
    for index in range(length - 1):
        prefix.append(prefix[-1] * pieces[index])
    suffix = [ones]
    for index in range(length - 1, 0, -1):
        suffix.append(suffix[-1] * pieces[index])
    suffix = suffix[::-1]
    whole = prefix[-1] * pieces[-1]
    return (jnp.concatenate(prefix, axis=axis), jnp.concatenate(suffix, axis=axis), whole)


def exclusive_both(values, axis):
    length = values.shape[axis]
    if length < 16 or length % 8 != 0:
        return linear_both(values, axis)
    shape = values.shape
    split = values.reshape(shape[:axis] + (length // 8, 8) + shape[axis + 1 :])
    inner_before, inner_after, group_whole = linear_both(split, axis + 1)
    outer_before, outer_after, whole = exclusive_both(group_whole, axis)
    before = (inner_before * outer_before).reshape(shape)
    after = (inner_after * outer_after).reshape(shape)
    whole = whole.reshape(shape[:axis] + (1,) + shape[axis + 1 :])
    return (before, after, whole)


def device_tables(bits, positions, count, check_blocks, column_blocks):
    slot_total = bits.shape[0]
    slots = jnp.arange(slot_total, dtype=jnp.int32)
    live = slots < count
    edge = jnp.where(live[:, None], bits, 0).astype(jnp.float32).reshape(slot_total, TILE, TILE)
    row_hot = (positions[:, 0:1] == jnp.arange(check_blocks, dtype=jnp.int32)[None, :]).astype(
        jnp.float32
    )
    col_hot = (positions[:, 1:2] == jnp.arange(column_blocks, dtype=jnp.int32)[None, :]).astype(
        jnp.float32
    )
    same_row = (positions[:, None, 0] == positions[None, :, 0]) & (slots[:, None] != slots[None, :])
    return (edge, row_hot, col_hot, same_row)


def _spread_row(ref, c, shape):
    return jnp.broadcast_to(ref[0, pl.ds(c, 1), :], shape)


def _row_block(pos_ref, k):
    return pos_ref[2 * k]


def _col_block(pos_ref, k):
    return pos_ref[2 * k + 1]


def _columns(pos_ref, k, slots, n_c):
    return pos_ref[2 * slots + k], 3 * slots + k * n_c


def _loop(count, body, init):
    def group(j, carry):
        for t in range(UNROLL):
            carry = body(UNROLL * j + t, carry)
        return carry

    carry = lax.fori_loop(0, count // UNROLL, group, init)
    return lax.fori_loop(UNROLL * (count // UNROLL), count, body, carry)


def _fwd_products_kernel(has_u, slots, blocks, pos_ref, *refs):
    refs = list(refs)
    spread_ref = refs.pop(0)
    u_ref = refs.pop(0) if has_u else None
    ew_ref, ba_ref, h_scr, whole_ref, rows_ref, here_ref = refs
    k = pl.program_id(0)
    n_c = ew_ref.shape[1]
    shape = ew_ref.shape[2:]

    count, base = _columns(pos_ref, k, slots, n_c)

    def forward(i, carry):
        c = pos_ref[base + i]
        if has_u:
            m = _spread_row(spread_ref, c, shape) - u_ref[0, c]
            h = jnp.where(ew_ref[0, c] > 0, jnp.tanh(0.5 * m), 1.0)
        else:
            t = jnp.broadcast_to(jnp.tanh(0.5 * spread_ref[0, pl.ds(c, 1), :]), shape)
            h = jnp.where(ew_ref[0, c] > 0, t, 1.0)
        h_scr[0, c] = h
        ba_ref[0, c] = carry
        return carry * h

    whole = _loop(count, forward, jnp.ones(shape, F32))
    whole_ref[k] = whole

    def backward(i, carry):
        c = pos_ref[base + count - 1 - i]
        ba_ref[0, c] = ba_ref[0, c] * carry
        return carry * h_scr[0, c]

    _loop(count, backward, jnp.ones(shape, F32))

    @pl.when(k == slots - 1)
    def _():
        wholes = [whole_ref[j] for j in range(slots)]
        rows_of = [_row_block(pos_ref, j) for j in range(slots)]
        for block in range(blocks):
            value = jnp.ones(shape, F32)
            for j in range(slots):
                value = value * jnp.where(rows_of[j] == block, wholes[j], 1.0)
            rows_ref[block] = value
        for j in range(slots):
            value = jnp.ones(shape, F32)
            for other in range(slots):
                if other != j:
                    value = value * jnp.where(rows_of[other] == rows_of[j], wholes[other], 1.0)
            here_ref[j] = value


def _fwd_messages_kernel(slots, pos_ref, ba_ref, sign_ref, here_ref, others_ref, ew_ref, u_ref, col_ref):
    k = pl.program_id(0)
    n_c = ba_ref.shape[1]
    count, base = _columns(pos_ref, k, slots, n_c)

    @pl.when(k == 0)
    def _():
        col_ref[...] = jnp.zeros(col_ref.shape, F32)

    f = sign_ref[k] * here_ref[k] * others_ref[_row_block(pos_ref, k)]
    q = _col_block(pos_ref, k)

    def body(i, carry):
        c = pos_ref[base + i]
        x = ba_ref[0, c] * f
        u = ew_ref[0, c] * jnp.log((1.0 + DAMP * x) / (1.0 - DAMP * x))
        u_ref[0, c] = u
        col_ref[q, pl.ds(c, 1), :] = col_ref[q, pl.ds(c, 1), :] + jnp.sum(u, axis=0, keepdims=True)
        return carry

    _loop(count, body, 0)


def _bwd_messages_kernel(has_next, has_acc, emit_column, slots, pos_ref, *refs):
    refs = list(refs)
    gsp_ref = refs.pop(0)
    gm_ref = refs.pop(0) if has_next else None
    ba_ref, sign_ref, here_ref, others_ref, ew_ref = refs[:5]
    refs = refs[5:]
    acc_ref = refs.pop(0) if has_acc else None
    gw_ref, gba_ref, ghere_ref, gothers_ref = refs[:4]
    col_ref = refs[4] if emit_column else None
    k = pl.program_id(0)
    n_c = ba_ref.shape[1]
    shape = ba_ref.shape[2:]
    q = _col_block(pos_ref, k)

    @pl.when(k == 0)
    def _():
        gothers_ref[...] = jnp.zeros(gothers_ref.shape, F32)
        if emit_column:
            col_ref[...] = jnp.zeros(col_ref.shape, F32)

    p = _row_block(pos_ref, k)
    sign = sign_ref[k]
    here = here_ref[k]
    others = others_ref[p]
    f = sign * here * others
    count, base = _columns(pos_ref, k, slots, n_c)

    def body(i, total):
        c = pos_ref[base + i]
        gu = _spread_row(gsp_ref, c, shape)
        if has_next:
            gu = gu - gm_ref[0, c]
        ba = ba_ref[0, c]
        x = ba * f
        low = 1.0 - DAMP * x
        high = 1.0 + DAMP * x
        ratio = jnp.log(high / low)
        if emit_column:
            u = ew_ref[0, c] * ratio
            col_ref[q, pl.ds(c, 1), :] = col_ref[q, pl.ds(c, 1), :] + jnp.sum(u, axis=0, keepdims=True)
        gw = gu * ratio
        if has_acc:
            gw = gw + acc_ref[0, c]
        gw_ref[0, c] = gw
        gx = gu * ew_ref[0, c] * ((2.0 * DAMP) / (low * high))
        gba_ref[0, c] = gx * f
        return total + gx * ba

    grad_factor = _loop(count, body, jnp.zeros(shape, F32))
    ghere_ref[k] = grad_factor * sign * others
    gothers_ref[p] = gothers_ref[p] + grad_factor * sign * here


def _bwd_products_kernel(emit_gm, slots, pos_ref, *refs):
    refs = list(refs)
    h_ref, gba_ref, grows_ref, ghere_ref, whole_ref, here_ref = refs[:6]
    refs = refs[6:]
    gm_ref = refs.pop(0) if emit_gm else None
    col_ref, p_scr, q_scr = refs
    k = pl.program_id(0)
    n_c = h_ref.shape[1]
    shape = h_ref.shape[2:]

    @pl.when(k == 0)
    def _():
        col_ref[...] = jnp.zeros(col_ref.shape, F32)

    p = _row_block(pos_ref, k)
    q = _col_block(pos_ref, k)
    rows_of = [_row_block(pos_ref, j) for j in range(slots)]
    gwh = grows_ref[p] * here_ref[k]
    for other in range(slots):
        term = jnp.where(rows_of[other] == p, ghere_ref[other], 0.0)
        for third in range(slots):
            if third != other:
                term = term * jnp.where(
                    (rows_of[third] == p) & (third != k), whole_ref[third], 1.0
                )
        gwh = gwh + jnp.where(other != k, term, 0.0)

    count, base = _columns(pos_ref, k, slots, n_c)

    def forward(i, carry):
        prod, grad = carry
        c = pos_ref[base + i]
        h = h_ref[0, c]
        p_scr[c] = prod
        q_scr[c] = grad
        return (prod * h, grad * h + gba_ref[0, c] * prod)

    ones = jnp.ones(shape, F32)
    zeros = jnp.zeros(shape, F32)
    _loop(count, forward, (ones, zeros))

    def backward(i, carry):
        prod, grad = carry
        c = pos_ref[base + count - 1 - i]
        h = h_ref[0, c]
        before = p_scr[c]
        gh = q_scr[c] * prod + before * (grad + gwh * prod)
        gm = gh * (0.5 * (1.0 - h * h))
        if emit_gm:
            gm_ref[0, c] = gm
        col_ref[q, pl.ds(c, 1), :] = col_ref[q, pl.ds(c, 1), :] + jnp.sum(gm, axis=0, keepdims=True)
        return (prod * h, grad * h + gba_ref[0, c] * prod)

    _loop(count, backward, (ones, zeros))


def _spec(kind, shape):
    if kind == "dense":
        return pl.BlockSpec((1,) + tuple(shape[1:]), lambda k, pos: (k, 0, 0, 0))
    if kind == "column":
        return pl.BlockSpec((1,) + tuple(shape[1:]), lambda k, pos: (pos[2 * k + 1], 0, 0))
    return pl.BlockSpec(tuple(shape), lambda k, pos: (0,) * len(shape))


def _call(kernel, pos, inputs, outputs, scratch=()):
    from jax.experimental.pallas import tpu as pltpu

    dense = [a for kind, a in inputs if kind == "dense"][0]
    grid_spec = pltpu.PrefetchScalarGridSpec(
        num_scalar_prefetch=1,
        grid=(dense.shape[0],),
        in_specs=[_spec(kind, a.shape) for kind, a in inputs],
        out_specs=[_spec(kind, o.shape) for kind, o in outputs],
        scratch_shapes=list(scratch),
    )
    return pl.pallas_call(
        kernel,
        grid_spec=grid_spec,
        out_shape=[o for kind, o in outputs],
    )(pos, *[a for kind, a in inputs])


def _vmem(shape):
    from jax.experimental.pallas import tpu as pltpu

    return pltpu.VMEM(shape, F32)


def fwd_products(pos, spread, u, ew, blocks):
    k, c, r, s = ew.shape
    has_u = u is not None
    inputs = [("column", spread)] + ([("dense", u)] if has_u else []) + [("dense", ew)]
    outs = [
        ("dense", jax.ShapeDtypeStruct(ew.shape, F32)),
        ("dense", jax.ShapeDtypeStruct(ew.shape, F32)),
        ("full", jax.ShapeDtypeStruct((k, r, s), F32)),
        ("full", jax.ShapeDtypeStruct((blocks, r, s), F32)),
        ("full", jax.ShapeDtypeStruct((k, r, s), F32)),
    ]
    return _call(functools.partial(_fwd_products_kernel, has_u, k, blocks), pos, inputs, outs)


def fwd_messages(pos, ba, sign, here, others, ew, col_blocks):
    k, c, r, s = ba.shape
    inputs = [("dense", ba), ("full", sign), ("full", here), ("full", others), ("dense", ew)]
    outs = [
        ("dense", jax.ShapeDtypeStruct(ba.shape, F32)),
        ("full", jax.ShapeDtypeStruct((col_blocks, c, s), F32)),
    ]
    return _call(functools.partial(_fwd_messages_kernel, k), pos, inputs, outs)


def bwd_messages(pos, gsp, gm, ba, sign, here, others, ew, acc, col_blocks=0):
    k, c, r, s = ba.shape
    has_next = gm is not None
    has_acc = acc is not None
    inputs = (
        [("column", gsp)]
        + ([("dense", gm)] if has_next else [])
        + [("dense", ba), ("full", sign), ("full", here), ("full", others), ("dense", ew)]
        + ([("dense", acc)] if has_acc else [])
    )
    outs = [
        ("dense", jax.ShapeDtypeStruct(ba.shape, F32)),
        ("dense", jax.ShapeDtypeStruct(ba.shape, F32)),
        ("full", jax.ShapeDtypeStruct(here.shape, F32)),
        ("full", jax.ShapeDtypeStruct(others.shape, F32)),
    ]
    if col_blocks:
        outs.append(("full", jax.ShapeDtypeStruct((col_blocks, c, s), F32)))
    return _call(
        functools.partial(_bwd_messages_kernel, has_next, has_acc, col_blocks > 0, k), pos, inputs, outs
    )


def bwd_products(pos, h, gba, grows, ghere, whole, here, col_blocks, emit_gm):
    k, c, r, s = h.shape
    inputs = [
        ("dense", h),
        ("dense", gba),
        ("full", grows),
        ("full", ghere),
        ("full", whole),
        ("full", here),
    ]
    outs = ([("dense", jax.ShapeDtypeStruct(h.shape, F32))] if emit_gm else []) + [
        ("full", jax.ShapeDtypeStruct((col_blocks, c, s), F32))
    ]
    results = _call(
        functools.partial(_bwd_products_kernel, emit_gm, k),
        pos,
        inputs,
        outs,
        [_vmem((c, r, s)) for _ in range(2)],
    )
    if emit_gm:
        return results[0], results[1]
    return None, results[0]


def pick(hot, values):
    parts = []
    for k in range(hot.shape[0]):
        value = jnp.zeros_like(values[0])
        for j in range(hot.shape[1]):
            value = value + jnp.where(hot[k, j] > 0, values[j], 0.0)
        parts.append(value)
    return jnp.stack(parts)


def place(hot, values):
    parts = []
    for j in range(hot.shape[1]):
        value = jnp.zeros_like(values[0])
        for k in range(hot.shape[0]):
            value = value + jnp.where(hot[k, j] > 0, values[k], 0.0)
        parts.append(value)
    return jnp.stack(parts)


def combine(whole, row_hot, same_row):
    slots = whole.shape[0]
    blocks = row_hot.shape[1]
    ones = jnp.ones_like(whole[0])
    rows = []
    for block in range(blocks):
        value = ones
        for k in range(slots):
            value = value * jnp.where(row_hot[k, block] > 0, whole[k], 1.0)
        rows.append(value)
    others_here = []
    for k in range(slots):
        value = ones
        for other in range(slots):
            if other != k:
                value = value * jnp.where(same_row[k, other], whole[other], 1.0)
        others_here.append(value)
    return jnp.stack(rows), jnp.stack(others_here)


def _power_of_two(n):
    return n > 1 and (n & (n - 1)) == 0


def _swap(value, axis, n, step):
    perm = [(j, j ^ (1 << step)) for j in range(n)]
    return lax.ppermute(value, axis, perm)


def checks_total(values, n):
    if not _power_of_two(n):
        return lax.psum(values, "chk")
    step = 0
    while (1 << step) < n:
        values = values + _swap(values, "chk", n, step)
        step += 1
    return values


def others_forward(rows, check_blocks, n, uniform=False):
    if not _power_of_two(n):
        return others_gather(rows, check_blocks)
    if uniform:
        shape = rows.shape
        small = rows[:, :, 0].reshape(-1, shape[2])
        others, trail = others_forward(small, check_blocks, n)
        grow = lambda value: jnp.broadcast_to(value.reshape(shape[:2] + (1,)), shape)
        trail = [tuple(grow(value) for value in entry) for entry in trail]
        return grow(others), trail
    full = rows
    excl = jnp.ones_like(rows)
    trail = []
    step = 0
    while (1 << step) < n:
        other = _swap(full, "var", n, step)
        trail.append((full, excl, other))
        excl = excl * other
        full = full * other
        step += 1
    return excl, trail


def others_backward(trail, grads, check_blocks, n):
    if not _power_of_two(n):
        return others_scatter(trail, grads, check_blocks)
    spread = grads
    target = jnp.zeros_like(grads)
    for step, (full, excl, other) in enumerate(trail):
        other_spread = _swap(spread, "var", n, step)
        target = target * other + excl * other_spread
        spread = spread * other + other_spread * full
    return target


def others_gather(rows, check_blocks):
    own = lax.axis_index("var")
    piece = lax.all_gather(rows, "var", axis=0, tiled=True)
    indices = jnp.arange(piece.shape[0], dtype=jnp.int32)
    keep = indices // check_blocks != own
    parts = []
    for block in range(check_blocks):
        pick = (keep & (indices % check_blocks == block))[:, None, None]
        parts.append(jnp.prod(jnp.where(pick, piece, 1.0), axis=0))
    return jnp.stack(parts), piece


def others_scatter(row_piece, grads, check_blocks):
    own = lax.axis_index("var")
    grad_piece = lax.all_gather(grads, "var", axis=0, tiled=True)
    indices = jnp.arange(row_piece.shape[0], dtype=jnp.int32)
    keep = indices // check_blocks != own
    new_sums = []
    for block in range(check_blocks):
        pick = (keep & (indices % check_blocks == block))[:, None, None]
        factors = jnp.where(pick, row_piece, 1.0)
        weights = jnp.where(pick, grad_piece, 0.0)
        before, after, whole = exclusive_both(factors, 0)
        new_sums.append(jnp.sum(weights * before * after, axis=0))
    return jnp.stack(new_sums)


def body(n_chk, n_var, tile_bits, tile_pos, tile_count, edge_weight, syndrome, channel_prior, out_cot):
    slot_total = tile_bits.shape[2]
    shots = syndrome.shape[1]
    check_blocks = syndrome.shape[0] // TILE
    column_blocks = channel_prior.shape[0] // TILE
    edge, row_hot, col_hot, same_row = device_tables(
        tile_bits[0, 0], tile_pos[0, 0], tile_count[0, 0], check_blocks, column_blocks
    )
    weight = edge_weight[0, 0].reshape(slot_total, TILE, TILE)
    edge_t = jnp.swapaxes(edge, 1, 2)
    filled = jnp.any(edge_t > 0, axis=2)
    order = jnp.argsort(jnp.where(filled, 0, 1).astype(jnp.int32), axis=1, stable=True)
    pos = jnp.concatenate(
        [
            tile_pos[0, 0].reshape(slot_total * 2),
            jnp.sum(filled.astype(jnp.int32), axis=1),
            order.astype(jnp.int32).reshape(slot_total * TILE),
        ]
    )
    dense = (slot_total, TILE, TILE, shots)
    ew = jnp.broadcast_to((edge_t * jnp.swapaxes(weight, 1, 2))[..., None], dense)
    sign_dev = (1.0 - 2.0 * syndrome.astype(jnp.float32)).reshape(check_blocks, TILE, shots)
    sign_slot = jnp.einsum("kc,crs->krs", row_hot, sign_dev, precision=EXACT)
    prior_dev = channel_prior.reshape(column_blocks, TILE)
    spread = jnp.broadcast_to(prior_dev[:, :, None], (column_blocks, TILE, shots))
    u = None
    saved = []
    total = None
    for step in range(ITERS):
        ba, halves, whole, rows, others_here = fwd_products(pos, spread, u, ew, check_blocks)
        others, trail = others_forward(rows, check_blocks, n_var, uniform=(step == 0 and (check_blocks * TILE) % shots == 0))
        saved.append((halves, ba, whole, others_here, others, trail))
        if step + 1 < ITERS:
            u, column = fwd_messages(pos, ba, sign_slot, others_here, others, ew, column_blocks)
            total = prior_dev[:, :, None] + checks_total(column, n_chk)
            spread = total

    grad_total = out_cot.reshape(column_blocks, TILE, shots)
    prior_grad = jnp.zeros((column_blocks, TILE), jnp.float32)
    grad_m = None
    acc = None
    for step in reversed(range(ITERS)):
        halves, ba, whole, others_here, others, trail = saved[step]
        prior_grad = prior_grad + jnp.sum(grad_total, axis=2)
        if step + 1 == ITERS:
            acc, grad_ba, grad_here, grad_others, last_column = bwd_messages(
                pos, grad_total, grad_m, ba, sign_slot, others_here, others, ew, acc, column_blocks
            )
            total = prior_dev[:, :, None] + checks_total(last_column, n_chk)
            marginals = total.reshape(column_blocks * TILE, shots)
        else:
            acc, grad_ba, grad_here, grad_others = bwd_messages(
                pos, grad_total, grad_m, ba, sign_slot, others_here, others, ew, acc
            )
        grad_rows = others_backward(trail, grad_others, check_blocks, n_var)
        grad_m, column = bwd_products(
            pos, halves, grad_ba, grad_rows, grad_here, whole, others_here,
            column_blocks, step > 0,
        )
        if step > 0:
            grad_total = checks_total(column, n_chk)
    shot_sums = jnp.sum(column, axis=2)
    if (column_blocks * TILE) % 128 == 0:
        shot_sums = checks_total(shot_sums.reshape(-1, 128), n_chk).reshape(column_blocks, TILE)
    else:
        shot_sums = checks_total(shot_sums, n_chk)
    prior_grad = prior_grad + shot_sums
    weight_grad = jnp.where(edge > 0, jnp.swapaxes(jnp.sum(acc, axis=3), 1, 2), 0.0)
    return (
        marginals,
        weight_grad.reshape(1, 1, slot_total, TILE * TILE),
        prior_grad.reshape(column_blocks * TILE),
    )


def solution(mesh):
    placed = (
        P("chk", "var", None, None),
        P("chk", "var", None, None),
        P("chk", "var"),
        P("chk", "var", None, None),
        P("chk", None),
        P("var"),
        P("var", None),
    )
    return jax.shard_map(
        functools.partial(body, mesh.shape["chk"], mesh.shape["var"]),
        mesh=mesh,
        in_specs=placed,
        out_specs=(P("var", None), P("chk", "var", None, None), P("var")),
        check_vma=False,
    )
```

```python
import functools

import jax
import jax.numpy as jnp
from jax import lax
from jax.experimental import pallas as pl
from jax.sharding import PartitionSpec as P

TILE = 64
ITERS = 2


DAMP = 0.97
EXACT = lax.Precision.HIGHEST
F32 = jnp.float32
UNROLL = 4


def linear_both(values, axis):
    length = values.shape[axis]
    pieces = [lax.slice_in_dim(values, index, index + 1, axis=axis) for index in range(length)]
    ones = jnp.ones_like(pieces[0])
    prefix = [ones]
    for index in range(length - 1):
        prefix.append(prefix[-1] * pieces[index])
    suffix = [ones]
    for index in range(length - 1, 0, -1):
        suffix.append(suffix[-1] * pieces[index])
    suffix = suffix[::-1]
    whole = prefix[-1] * pieces[-1]
    return (jnp.concatenate(prefix, axis=axis), jnp.concatenate(suffix, axis=axis), whole)


def exclusive_both(values, axis):
    length = values.shape[axis]
    if length < 16 or length % 8 != 0:
        return linear_both(values, axis)
    shape = values.shape
    split = values.reshape(shape[:axis] + (length // 8, 8) + shape[axis + 1 :])
    inner_before, inner_after, group_whole = linear_both(split, axis + 1)
    outer_before, outer_after, whole = exclusive_both(group_whole, axis)
    before = (inner_before * outer_before).reshape(shape)
    after = (inner_after * outer_after).reshape(shape)
    whole = whole.reshape(shape[:axis] + (1,) + shape[axis + 1 :])
    return (before, after, whole)


def device_tables(bits, positions, count, check_blocks, column_blocks):
    slot_total = bits.shape[0]
    slots = jnp.arange(slot_total, dtype=jnp.int32)
    live = slots < count
    edge = jnp.where(live[:, None], bits, 0).astype(jnp.float32).reshape(slot_total, TILE, TILE)
    row_hot = (positions[:, 0:1] == jnp.arange(check_blocks, dtype=jnp.int32)[None, :]).astype(
        jnp.float32
    )
    col_hot = (positions[:, 1:2] == jnp.arange(column_blocks, dtype=jnp.int32)[None, :]).astype(
        jnp.float32
    )
    same_row = (positions[:, None, 0] == positions[None, :, 0]) & (slots[:, None] != slots[None, :])
    return (edge, row_hot, col_hot, same_row)


def _spread_row(ref, c, shape):
    return jnp.broadcast_to(ref[0, pl.ds(c, 1), :], shape)


def _row_block(pos_ref, k):
    return pos_ref[2 * k]


def _col_block(pos_ref, k):
    return pos_ref[2 * k + 1]


def _columns(pos_ref, k, slots, n_c):
    return pos_ref[2 * slots + k], 3 * slots + k * n_c


def _loop(count, body, init):
    def group(j, carry):
        for t in range(UNROLL):
            carry = body(UNROLL * j + t, carry)
        return carry

    carry = lax.fori_loop(0, count // UNROLL, group, init)
    return lax.fori_loop(UNROLL * (count // UNROLL), count, body, carry)


def _fwd_products_kernel(has_u, slots, blocks, pos_ref, *refs):
    refs = list(refs)
    spread_ref = refs.pop(0)
    u_ref = refs.pop(0) if has_u else None
    ew_ref, ba_ref, h_scr, whole_ref, rows_ref, here_ref = refs
    k = pl.program_id(0)
    n_c = ew_ref.shape[1]
    shape = ew_ref.shape[2:]

    count, base = _columns(pos_ref, k, slots, n_c)

    def forward(i, carry):
        c = pos_ref[base + i]
        m = _spread_row(spread_ref, c, shape)
        if has_u:
            m = m - u_ref[0, c]
        h = jnp.where(ew_ref[0, c] > 0, jnp.tanh(0.5 * m), 1.0)
        h_scr[0, c] = h
        ba_ref[0, c] = carry
        return carry * h

    whole = _loop(count, forward, jnp.ones(shape, F32))
    whole_ref[k] = whole

    def backward(i, carry):
        c = pos_ref[base + count - 1 - i]
        ba_ref[0, c] = ba_ref[0, c] * carry
        return carry * h_scr[0, c]

    _loop(count, backward, jnp.ones(shape, F32))

    @pl.when(k == slots - 1)
    def _():
        wholes = [whole_ref[j] for j in range(slots)]
        rows_of = [_row_block(pos_ref, j) for j in range(slots)]
        for block in range(blocks):
            value = jnp.ones(shape, F32)
            for j in range(slots):
                value = value * jnp.where(rows_of[j] == block, wholes[j], 1.0)
            rows_ref[block] = value
        for j in range(slots):
            value = jnp.ones(shape, F32)
            for other in range(slots):
                if other != j:
                    value = value * jnp.where(rows_of[other] == rows_of[j], wholes[other], 1.0)
            here_ref[j] = value


def _fwd_messages_kernel(slots, pos_ref, ba_ref, sign_ref, here_ref, others_ref, ew_ref, u_ref, col_ref):
    k = pl.program_id(0)
    n_c = ba_ref.shape[1]
    count, base = _columns(pos_ref, k, slots, n_c)

    @pl.when(k == 0)
    def _():
        col_ref[...] = jnp.zeros(col_ref.shape, F32)

    f = sign_ref[k] * here_ref[k] * others_ref[_row_block(pos_ref, k)]
    q = _col_block(pos_ref, k)

    def body(i, carry):
        c = pos_ref[base + i]
        x = ba_ref[0, c] * f
        u = ew_ref[0, c] * jnp.log((1.0 + DAMP * x) / (1.0 - DAMP * x))
        u_ref[0, c] = u
        col_ref[q, pl.ds(c, 1), :] = col_ref[q, pl.ds(c, 1), :] + jnp.sum(u, axis=0, keepdims=True)
        return carry

    _loop(count, body, 0)


def _bwd_messages_kernel(has_next, has_acc, emit_column, slots, pos_ref, *refs):
    refs = list(refs)
    gsp_ref = refs.pop(0)
    gm_ref = refs.pop(0) if has_next else None
    ba_ref, sign_ref, here_ref, others_ref, ew_ref = refs[:5]
    refs = refs[5:]
    acc_ref = refs.pop(0) if has_acc else None
    gw_ref, gba_ref, ghere_ref, gothers_ref = refs[:4]
    col_ref = refs[4] if emit_column else None
    k = pl.program_id(0)
    n_c = ba_ref.shape[1]
    shape = ba_ref.shape[2:]
    q = _col_block(pos_ref, k)

    @pl.when(k == 0)
    def _():
        gothers_ref[...] = jnp.zeros(gothers_ref.shape, F32)
        if emit_column:
            col_ref[...] = jnp.zeros(col_ref.shape, F32)

    p = _row_block(pos_ref, k)
    sign = sign_ref[k]
    here = here_ref[k]
    others = others_ref[p]
    f = sign * here * others
    count, base = _columns(pos_ref, k, slots, n_c)

    def body(i, total):
        c = pos_ref[base + i]
        gu = _spread_row(gsp_ref, c, shape)
        if has_next:
            gu = gu - gm_ref[0, c]
        ba = ba_ref[0, c]
        x = ba * f
        low = 1.0 - DAMP * x
        high = 1.0 + DAMP * x
        ratio = jnp.log(high / low)
        if emit_column:
            u = ew_ref[0, c] * ratio
            col_ref[q, pl.ds(c, 1), :] = col_ref[q, pl.ds(c, 1), :] + jnp.sum(u, axis=0, keepdims=True)
        gw = gu * ratio
        if has_acc:
            gw = gw + acc_ref[0, c]
        gw_ref[0, c] = gw
        gx = gu * ew_ref[0, c] * ((2.0 * DAMP) / (low * high))
        gba_ref[0, c] = gx * f
        return total + gx * ba

    grad_factor = _loop(count, body, jnp.zeros(shape, F32))
    ghere_ref[k] = grad_factor * sign * others
    gothers_ref[p] = gothers_ref[p] + grad_factor * sign * here


def _bwd_products_kernel(emit_gm, slots, pos_ref, *refs):
    refs = list(refs)
    h_ref, gba_ref, grows_ref, ghere_ref, whole_ref, here_ref = refs[:6]
    refs = refs[6:]
    gm_ref = refs.pop(0) if emit_gm else None
    col_ref, p_scr, q_scr = refs
    k = pl.program_id(0)
    n_c = h_ref.shape[1]
    shape = h_ref.shape[2:]

    @pl.when(k == 0)
    def _():
        col_ref[...] = jnp.zeros(col_ref.shape, F32)

    p = _row_block(pos_ref, k)
    q = _col_block(pos_ref, k)
    rows_of = [_row_block(pos_ref, j) for j in range(slots)]
    gwh = grows_ref[p] * here_ref[k]
    for other in range(slots):
        term = jnp.where(rows_of[other] == p, ghere_ref[other], 0.0)
        for third in range(slots):
            if third != other:
                term = term * jnp.where(
                    (rows_of[third] == p) & (third != k), whole_ref[third], 1.0
                )
        gwh = gwh + jnp.where(other != k, term, 0.0)

    count, base = _columns(pos_ref, k, slots, n_c)

    def forward(i, carry):
        prod, grad = carry
        c = pos_ref[base + i]
        h = h_ref[0, c]
        p_scr[c] = prod
        q_scr[c] = grad
        return (prod * h, grad * h + gba_ref[0, c] * prod)

    ones = jnp.ones(shape, F32)
    zeros = jnp.zeros(shape, F32)
    _loop(count, forward, (ones, zeros))

    def backward(i, carry):
        prod, grad = carry
        c = pos_ref[base + count - 1 - i]
        h = h_ref[0, c]
        before = p_scr[c]
        gh = q_scr[c] * prod + before * (grad + gwh * prod)
        gm = gh * (0.5 * (1.0 - h * h))
        if emit_gm:
            gm_ref[0, c] = gm
        col_ref[q, pl.ds(c, 1), :] = col_ref[q, pl.ds(c, 1), :] + jnp.sum(gm, axis=0, keepdims=True)
        return (prod * h, grad * h + gba_ref[0, c] * prod)

    _loop(count, backward, (ones, zeros))


def _spec(kind, shape):
    if kind == "dense":
        return pl.BlockSpec((1,) + tuple(shape[1:]), lambda k, pos: (k, 0, 0, 0))
    if kind == "column":
        return pl.BlockSpec((1,) + tuple(shape[1:]), lambda k, pos: (pos[2 * k + 1], 0, 0))
    return pl.BlockSpec(tuple(shape), lambda k, pos: (0,) * len(shape))


def _call(kernel, pos, inputs, outputs, scratch=()):
    from jax.experimental.pallas import tpu as pltpu

    dense = [a for kind, a in inputs if kind == "dense"][0]
    grid_spec = pltpu.PrefetchScalarGridSpec(
        num_scalar_prefetch=1,
        grid=(dense.shape[0],),
        in_specs=[_spec(kind, a.shape) for kind, a in inputs],
        out_specs=[_spec(kind, o.shape) for kind, o in outputs],
        scratch_shapes=list(scratch),
    )
    return pl.pallas_call(
        kernel,
        grid_spec=grid_spec,
        out_shape=[o for kind, o in outputs],
    )(pos, *[a for kind, a in inputs])


def _vmem(shape):
    from jax.experimental.pallas import tpu as pltpu

    return pltpu.VMEM(shape, F32)


def fwd_products(pos, spread, u, ew, blocks):
    k, c, r, s = ew.shape
    has_u = u is not None
    inputs = [("column", spread)] + ([("dense", u)] if has_u else []) + [("dense", ew)]
    outs = [
        ("dense", jax.ShapeDtypeStruct(ew.shape, F32)),
        ("dense", jax.ShapeDtypeStruct(ew.shape, F32)),
        ("full", jax.ShapeDtypeStruct((k, r, s), F32)),
        ("full", jax.ShapeDtypeStruct((blocks, r, s), F32)),
        ("full", jax.ShapeDtypeStruct((k, r, s), F32)),
    ]
    return _call(functools.partial(_fwd_products_kernel, has_u, k, blocks), pos, inputs, outs)


def fwd_messages(pos, ba, sign, here, others, ew, col_blocks):
    k, c, r, s = ba.shape
    inputs = [("dense", ba), ("full", sign), ("full", here), ("full", others), ("dense", ew)]
    outs = [
        ("dense", jax.ShapeDtypeStruct(ba.shape, F32)),
        ("full", jax.ShapeDtypeStruct((col_blocks, c, s), F32)),
    ]
    return _call(functools.partial(_fwd_messages_kernel, k), pos, inputs, outs)


def bwd_messages(pos, gsp, gm, ba, sign, here, others, ew, acc, col_blocks=0):
    k, c, r, s = ba.shape
    has_next = gm is not None
    has_acc = acc is not None
    inputs = (
        [("column", gsp)]
        + ([("dense", gm)] if has_next else [])
        + [("dense", ba), ("full", sign), ("full", here), ("full", others), ("dense", ew)]
        + ([("dense", acc)] if has_acc else [])
    )
    outs = [
        ("dense", jax.ShapeDtypeStruct(ba.shape, F32)),
        ("dense", jax.ShapeDtypeStruct(ba.shape, F32)),
        ("full", jax.ShapeDtypeStruct(here.shape, F32)),
        ("full", jax.ShapeDtypeStruct(others.shape, F32)),
    ]
    if col_blocks:
        outs.append(("full", jax.ShapeDtypeStruct((col_blocks, c, s), F32)))
    return _call(
        functools.partial(_bwd_messages_kernel, has_next, has_acc, col_blocks > 0, k), pos, inputs, outs
    )


def bwd_products(pos, h, gba, grows, ghere, whole, here, col_blocks, emit_gm):
    k, c, r, s = h.shape
    inputs = [
        ("dense", h),
        ("dense", gba),
        ("full", grows),
        ("full", ghere),
        ("full", whole),
        ("full", here),
    ]
    outs = ([("dense", jax.ShapeDtypeStruct(h.shape, F32))] if emit_gm else []) + [
        ("full", jax.ShapeDtypeStruct((col_blocks, c, s), F32))
    ]
    results = _call(
        functools.partial(_bwd_products_kernel, emit_gm, k),
        pos,
        inputs,
        outs,
        [_vmem((c, r, s)) for _ in range(2)],
    )
    if emit_gm:
        return results[0], results[1]
    return None, results[0]


def pick(hot, values):
    parts = []
    for k in range(hot.shape[0]):
        value = jnp.zeros_like(values[0])
        for j in range(hot.shape[1]):
            value = value + jnp.where(hot[k, j] > 0, values[j], 0.0)
        parts.append(value)
    return jnp.stack(parts)


def place(hot, values):
    parts = []
    for j in range(hot.shape[1]):
        value = jnp.zeros_like(values[0])
        for k in range(hot.shape[0]):
            value = value + jnp.where(hot[k, j] > 0, values[k], 0.0)
        parts.append(value)
    return jnp.stack(parts)


def combine(whole, row_hot, same_row):
    slots = whole.shape[0]
    blocks = row_hot.shape[1]
    ones = jnp.ones_like(whole[0])
    rows = []
    for block in range(blocks):
        value = ones
        for k in range(slots):
            value = value * jnp.where(row_hot[k, block] > 0, whole[k], 1.0)
        rows.append(value)
    others_here = []
    for k in range(slots):
        value = ones
        for other in range(slots):
            if other != k:
                value = value * jnp.where(same_row[k, other], whole[other], 1.0)
        others_here.append(value)
    return jnp.stack(rows), jnp.stack(others_here)


def _power_of_two(n):
    return n > 1 and (n & (n - 1)) == 0


def _swap(value, axis, n, step):
    perm = [(j, j ^ (1 << step)) for j in range(n)]
    return lax.ppermute(value, axis, perm)


def checks_total(values, n):
    if not _power_of_two(n):
        return lax.psum(values, "chk")
    step = 0
    while (1 << step) < n:
        values = values + _swap(values, "chk", n, step)
        step += 1
    return values


def others_forward(rows, check_blocks, n, uniform=False):
    if not _power_of_two(n):
        return others_gather(rows, check_blocks)
    if uniform:
        shape = rows.shape
        small = rows[:, :, 0].reshape(-1, shape[2])
        others, trail = others_forward(small, check_blocks, n)
        grow = lambda value: jnp.broadcast_to(value.reshape(shape[:2] + (1,)), shape)
        trail = [tuple(grow(value) for value in entry) for entry in trail]
        return grow(others), trail
    full = rows
    excl = jnp.ones_like(rows)
    trail = []
    step = 0
    while (1 << step) < n:
        other = _swap(full, "var", n, step)
        trail.append((full, excl, other))
        excl = excl * other
        full = full * other
        step += 1
    return excl, trail


def others_backward(trail, grads, check_blocks, n):
    if not _power_of_two(n):
        return others_scatter(trail, grads, check_blocks)
    spread = grads
    target = jnp.zeros_like(grads)
    for step, (full, excl, other) in enumerate(trail):
        other_spread = _swap(spread, "var", n, step)
        target = target * other + excl * other_spread
        spread = spread * other + other_spread * full
    return target


def others_gather(rows, check_blocks):
    own = lax.axis_index("var")
    piece = lax.all_gather(rows, "var", axis=0, tiled=True)
    indices = jnp.arange(piece.shape[0], dtype=jnp.int32)
    keep = indices // check_blocks != own
    parts = []
    for block in range(check_blocks):
        pick = (keep & (indices % check_blocks == block))[:, None, None]
        parts.append(jnp.prod(jnp.where(pick, piece, 1.0), axis=0))
    return jnp.stack(parts), piece


def others_scatter(row_piece, grads, check_blocks):
    own = lax.axis_index("var")
    grad_piece = lax.all_gather(grads, "var", axis=0, tiled=True)
    indices = jnp.arange(row_piece.shape[0], dtype=jnp.int32)
    keep = indices // check_blocks != own
    new_sums = []
    for block in range(check_blocks):
        pick = (keep & (indices % check_blocks == block))[:, None, None]
        factors = jnp.where(pick, row_piece, 1.0)
        weights = jnp.where(pick, grad_piece, 0.0)
        before, after, whole = exclusive_both(factors, 0)
        new_sums.append(jnp.sum(weights * before * after, axis=0))
    return jnp.stack(new_sums)


def body(n_chk, n_var, tile_bits, tile_pos, tile_count, edge_weight, syndrome, channel_prior, out_cot):
    slot_total = tile_bits.shape[2]
    shots = syndrome.shape[1]
    check_blocks = syndrome.shape[0] // TILE
    column_blocks = channel_prior.shape[0] // TILE
    edge, row_hot, col_hot, same_row = device_tables(
        tile_bits[0, 0], tile_pos[0, 0], tile_count[0, 0], check_blocks, column_blocks
    )
    weight = edge_weight[0, 0].reshape(slot_total, TILE, TILE)
    edge_t = jnp.swapaxes(edge, 1, 2)
    filled = jnp.any(edge_t > 0, axis=2)
    order = jnp.argsort(jnp.where(filled, 0, 1).astype(jnp.int32), axis=1, stable=True)
    pos = jnp.concatenate(
        [
            tile_pos[0, 0].reshape(slot_total * 2),
            jnp.sum(filled.astype(jnp.int32), axis=1),
            order.astype(jnp.int32).reshape(slot_total * TILE),
        ]
    )
    dense = (slot_total, TILE, TILE, shots)
    ew = jnp.broadcast_to((edge_t * jnp.swapaxes(weight, 1, 2))[..., None], dense)
    sign_dev = (1.0 - 2.0 * syndrome.astype(jnp.float32)).reshape(check_blocks, TILE, shots)
    sign_slot = pick(row_hot, sign_dev)
    prior_dev = channel_prior.reshape(column_blocks, TILE)
    spread = jnp.broadcast_to(prior_dev[:, :, None], (column_blocks, TILE, shots))
    u = None
    saved = []
    total = None
    for step in range(ITERS):
        ba, halves, whole, rows, others_here = fwd_products(pos, spread, u, ew, check_blocks)
        others, trail = others_forward(rows, check_blocks, n_var, uniform=(step == 0 and (check_blocks * TILE) % shots == 0))
        saved.append((halves, ba, whole, others_here, others, trail))
        if step + 1 < ITERS:
            u, column = fwd_messages(pos, ba, sign_slot, others_here, others, ew, column_blocks)
            total = prior_dev[:, :, None] + checks_total(column, n_chk)
            spread = total

    grad_total = out_cot.reshape(column_blocks, TILE, shots)
    prior_grad = jnp.zeros((column_blocks, TILE), jnp.float32)
    grad_m = None
    acc = None
    for step in reversed(range(ITERS)):
        halves, ba, whole, others_here, others, trail = saved[step]
        prior_grad = prior_grad + jnp.sum(grad_total, axis=2)
        if step + 1 == ITERS:
            acc, grad_ba, grad_here, grad_others, last_column = bwd_messages(
                pos, grad_total, grad_m, ba, sign_slot, others_here, others, ew, acc, column_blocks
            )
            total = prior_dev[:, :, None] + checks_total(last_column, n_chk)
            marginals = total.reshape(column_blocks * TILE, shots)
        else:
            acc, grad_ba, grad_here, grad_others = bwd_messages(
                pos, grad_total, grad_m, ba, sign_slot, others_here, others, ew, acc
            )
        grad_rows = others_backward(trail, grad_others, check_blocks, n_var)
        grad_m, column = bwd_products(
            pos, halves, grad_ba, grad_rows, grad_here, whole, others_here,
            column_blocks, step > 0,
        )
        if step > 0:
            grad_total = checks_total(column, n_chk)
    shot_sums = jnp.sum(column, axis=2)
    if (column_blocks * TILE) % 128 == 0:
        shot_sums = checks_total(shot_sums.reshape(-1, 128), n_chk).reshape(column_blocks, TILE)
    else:
        shot_sums = checks_total(shot_sums, n_chk)
    prior_grad = prior_grad + shot_sums
    weight_grad = jnp.where(edge > 0, jnp.swapaxes(jnp.sum(acc, axis=3), 1, 2), 0.0)
    return (
        marginals,
        weight_grad.reshape(1, 1, slot_total, TILE * TILE),
        prior_grad.reshape(column_blocks * TILE),
    )


def solution(mesh):
    placed = (
        P("chk", "var", None, None),
        P("chk", "var", None, None),
        P("chk", "var"),
        P("chk", "var", None, None),
        P("chk", None),
        P("var"),
        P("var", None),
    )
    return jax.shard_map(
        functools.partial(body, mesh.shape["chk"], mesh.shape["var"]),
        mesh=mesh,
        in_specs=placed,
        out_specs=(P("var", None), P("chk", "var", None, None), P("var")),
        check_vma=False,
    )
```

```python
import functools

import jax
import jax.numpy as jnp
from jax import lax
from jax.experimental import pallas as pl
from jax.sharding import PartitionSpec as P

TILE = 64
ITERS = 2


DAMP = 0.97
EXACT = lax.Precision.HIGHEST
F32 = jnp.float32
UNROLL = 4


def linear_both(values, axis):
    length = values.shape[axis]
    pieces = [lax.slice_in_dim(values, index, index + 1, axis=axis) for index in range(length)]
    ones = jnp.ones_like(pieces[0])
    prefix = [ones]
    for index in range(length - 1):
        prefix.append(prefix[-1] * pieces[index])
    suffix = [ones]
    for index in range(length - 1, 0, -1):
        suffix.append(suffix[-1] * pieces[index])
    suffix = suffix[::-1]
    whole = prefix[-1] * pieces[-1]
    return (jnp.concatenate(prefix, axis=axis), jnp.concatenate(suffix, axis=axis), whole)


def exclusive_both(values, axis):
    length = values.shape[axis]
    if length < 16 or length % 8 != 0:
        return linear_both(values, axis)
    shape = values.shape
    split = values.reshape(shape[:axis] + (length // 8, 8) + shape[axis + 1 :])
    inner_before, inner_after, group_whole = linear_both(split, axis + 1)
    outer_before, outer_after, whole = exclusive_both(group_whole, axis)
    before = (inner_before * outer_before).reshape(shape)
    after = (inner_after * outer_after).reshape(shape)
    whole = whole.reshape(shape[:axis] + (1,) + shape[axis + 1 :])
    return (before, after, whole)


def device_tables(bits, positions, count, check_blocks, column_blocks):
    slot_total = bits.shape[0]
    slots = jnp.arange(slot_total, dtype=jnp.int32)
    live = slots < count
    edge = jnp.where(live[:, None], bits, 0).astype(jnp.float32).reshape(slot_total, TILE, TILE)
    row_hot = (positions[:, 0:1] == jnp.arange(check_blocks, dtype=jnp.int32)[None, :]).astype(
        jnp.float32
    )
    col_hot = (positions[:, 1:2] == jnp.arange(column_blocks, dtype=jnp.int32)[None, :]).astype(
        jnp.float32
    )
    same_row = (positions[:, None, 0] == positions[None, :, 0]) & (slots[:, None] != slots[None, :])
    return (edge, row_hot, col_hot, same_row)


def _spread_row(ref, c, shape):
    return jnp.broadcast_to(ref[0, pl.ds(c, 1), :], shape)


def _row_block(pos_ref, k):
    return pos_ref[2 * k]


def _col_block(pos_ref, k):
    return pos_ref[2 * k + 1]


def _columns(pos_ref, k, slots, n_c):
    return pos_ref[2 * slots + k], 3 * slots + k * n_c


def _loop(count, body, init):
    def group(j, carry):
        for t in range(UNROLL):
            carry = body(UNROLL * j + t, carry)
        return carry

    carry = lax.fori_loop(0, count // UNROLL, group, init)
    return lax.fori_loop(UNROLL * (count // UNROLL), count, body, carry)


def _fwd_products_kernel(has_u, slots, blocks, pos_ref, *refs):
    refs = list(refs)
    spread_ref = refs.pop(0)
    u_ref = refs.pop(0) if has_u else None
    ew_ref, ba_ref, h_scr, whole_ref, rows_ref, here_ref = refs
    k = pl.program_id(0)
    n_c = ew_ref.shape[1]
    shape = ew_ref.shape[2:]

    count, base = _columns(pos_ref, k, slots, n_c)

    def forward(i, carry):
        c = pos_ref[base + i]
        m = _spread_row(spread_ref, c, shape)
        if has_u:
            m = m - u_ref[0, c]
        h = jnp.where(ew_ref[0, c] > 0, jnp.tanh(0.5 * m), 1.0)
        h_scr[0, c] = h
        ba_ref[0, c] = carry
        return carry * h

    whole = _loop(count, forward, jnp.ones(shape, F32))
    whole_ref[k] = whole

    def backward(i, carry):
        c = pos_ref[base + count - 1 - i]
        ba_ref[0, c] = ba_ref[0, c] * carry
        return carry * h_scr[0, c]

    _loop(count, backward, jnp.ones(shape, F32))

    @pl.when(k == slots - 1)
    def _():
        wholes = [whole_ref[j] for j in range(slots)]
        rows_of = [_row_block(pos_ref, j) for j in range(slots)]
        for block in range(blocks):
            value = jnp.ones(shape, F32)
            for j in range(slots):
                value = value * jnp.where(rows_of[j] == block, wholes[j], 1.0)
            rows_ref[block] = value
        for j in range(slots):
            value = jnp.ones(shape, F32)
            for other in range(slots):
                if other != j:
                    value = value * jnp.where(rows_of[other] == rows_of[j], wholes[other], 1.0)
            here_ref[j] = value


def _fwd_messages_kernel(
    slots, pos_ref, ba_ref, sign_ref, here_ref, others_ref, ew_ref, u_ref, col_ref, cs_scr
):
    k = pl.program_id(0)
    n_c = ba_ref.shape[1]
    count, base = _columns(pos_ref, k, slots, n_c)

    @pl.when(k == 0)
    def _():
        col_ref[...] = jnp.zeros(col_ref.shape, F32)

    f = sign_ref[k] * here_ref[k] * others_ref[_row_block(pos_ref, k)]
    q = _col_block(pos_ref, k)

    def body(i, carry):
        c = pos_ref[base + i]
        x = ba_ref[0, c] * f
        u = ew_ref[0, c] * jnp.log((1.0 + DAMP * x) / (1.0 - DAMP * x))
        u_ref[0, c] = u
        cs_scr[pl.ds(c, 1), :] = jnp.sum(u, axis=0, keepdims=True)
        return carry

    cs_scr[...] = jnp.zeros(cs_scr.shape, F32)
    _loop(count, body, 0)
    col_ref[q] = col_ref[q] + cs_scr[...]


def _bwd_messages_kernel(has_next, has_acc, emit_column, slots, pos_ref, *refs):
    refs = list(refs)
    gsp_ref = refs.pop(0)
    gm_ref = refs.pop(0) if has_next else None
    ba_ref, sign_ref, here_ref, others_ref, ew_ref = refs[:5]
    refs = refs[5:]
    acc_ref = refs.pop(0) if has_acc else None
    gw_ref, gba_ref, ghere_ref, gothers_ref = refs[:4]
    col_ref = refs[4] if emit_column else None
    cs_scr = refs[5] if emit_column else None
    k = pl.program_id(0)
    n_c = ba_ref.shape[1]
    shape = ba_ref.shape[2:]
    q = _col_block(pos_ref, k)

    @pl.when(k == 0)
    def _():
        gothers_ref[...] = jnp.zeros(gothers_ref.shape, F32)
        if emit_column:
            col_ref[...] = jnp.zeros(col_ref.shape, F32)

    p = _row_block(pos_ref, k)
    sign = sign_ref[k]
    here = here_ref[k]
    others = others_ref[p]
    f = sign * here * others
    count, base = _columns(pos_ref, k, slots, n_c)

    def body(i, total):
        c = pos_ref[base + i]
        gu = _spread_row(gsp_ref, c, shape)
        if has_next:
            gu = gu - gm_ref[0, c]
        ba = ba_ref[0, c]
        x = ba * f
        low = 1.0 - DAMP * x
        high = 1.0 + DAMP * x
        ratio = jnp.log(high / low)
        if emit_column:
            u = ew_ref[0, c] * ratio
            cs_scr[pl.ds(c, 1), :] = jnp.sum(u, axis=0, keepdims=True)
        gw = gu * ratio
        if has_acc:
            gw = gw + acc_ref[0, c]
        gw_ref[0, c] = gw
        gx = gu * ew_ref[0, c] * ((2.0 * DAMP) / (low * high))
        gba_ref[0, c] = gx * f
        return total + gx * ba

    if emit_column:
        cs_scr[...] = jnp.zeros(cs_scr.shape, F32)
    grad_factor = _loop(count, body, jnp.zeros(shape, F32))
    if emit_column:
        col_ref[q] = col_ref[q] + cs_scr[...]
    ghere_ref[k] = grad_factor * sign * others
    gothers_ref[p] = gothers_ref[p] + grad_factor * sign * here


def _bwd_products_kernel(emit_gm, slots, pos_ref, *refs):
    refs = list(refs)
    h_ref, gba_ref, grows_ref, ghere_ref, whole_ref, here_ref = refs[:6]
    refs = refs[6:]
    gm_ref = refs.pop(0) if emit_gm else None
    col_ref, p_scr, q_scr, cs_scr = refs
    k = pl.program_id(0)
    n_c = h_ref.shape[1]
    shape = h_ref.shape[2:]

    @pl.when(k == 0)
    def _():
        col_ref[...] = jnp.zeros(col_ref.shape, F32)

    p = _row_block(pos_ref, k)
    q = _col_block(pos_ref, k)
    rows_of = [_row_block(pos_ref, j) for j in range(slots)]
    gwh = grows_ref[p] * here_ref[k]
    for other in range(slots):
        term = jnp.where(rows_of[other] == p, ghere_ref[other], 0.0)
        for third in range(slots):
            if third != other:
                term = term * jnp.where(
                    (rows_of[third] == p) & (third != k), whole_ref[third], 1.0
                )
        gwh = gwh + jnp.where(other != k, term, 0.0)

    count, base = _columns(pos_ref, k, slots, n_c)

    def forward(i, carry):
        prod, grad = carry
        c = pos_ref[base + i]
        h = h_ref[0, c]
        p_scr[c] = prod
        q_scr[c] = grad
        return (prod * h, grad * h + gba_ref[0, c] * prod)

    ones = jnp.ones(shape, F32)
    zeros = jnp.zeros(shape, F32)
    _loop(count, forward, (ones, zeros))

    def backward(i, carry):
        prod, grad = carry
        c = pos_ref[base + count - 1 - i]
        h = h_ref[0, c]
        before = p_scr[c]
        gh = q_scr[c] * prod + before * (grad + gwh * prod)
        gm = gh * (0.5 * (1.0 - h * h))
        if emit_gm:
            gm_ref[0, c] = gm
        cs_scr[pl.ds(c, 1), :] = jnp.sum(gm, axis=0, keepdims=True)
        return (prod * h, grad * h + gba_ref[0, c] * prod)

    cs_scr[...] = jnp.zeros(cs_scr.shape, F32)
    _loop(count, backward, (ones, zeros))
    col_ref[q] = col_ref[q] + cs_scr[...]


def _spec(kind, shape):
    if kind == "dense":
        return pl.BlockSpec((1,) + tuple(shape[1:]), lambda k, pos: (k, 0, 0, 0))
    if kind == "column":
        return pl.BlockSpec((1,) + tuple(shape[1:]), lambda k, pos: (pos[2 * k + 1], 0, 0))
    return pl.BlockSpec(tuple(shape), lambda k, pos: (0,) * len(shape))


def _call(kernel, pos, inputs, outputs, scratch=()):
    from jax.experimental.pallas import tpu as pltpu

    dense = [a for kind, a in inputs if kind == "dense"][0]
    grid_spec = pltpu.PrefetchScalarGridSpec(
        num_scalar_prefetch=1,
        grid=(dense.shape[0],),
        in_specs=[_spec(kind, a.shape) for kind, a in inputs],
        out_specs=[_spec(kind, o.shape) for kind, o in outputs],
        scratch_shapes=list(scratch),
    )
    return pl.pallas_call(
        kernel,
        grid_spec=grid_spec,
        out_shape=[o for kind, o in outputs],
    )(pos, *[a for kind, a in inputs])


def _vmem(shape):
    from jax.experimental.pallas import tpu as pltpu

    return pltpu.VMEM(shape, F32)


def fwd_products(pos, spread, u, ew, blocks):
    k, c, r, s = ew.shape
    has_u = u is not None
    inputs = [("column", spread)] + ([("dense", u)] if has_u else []) + [("dense", ew)]
    outs = [
        ("dense", jax.ShapeDtypeStruct(ew.shape, F32)),
        ("dense", jax.ShapeDtypeStruct(ew.shape, F32)),
        ("full", jax.ShapeDtypeStruct((k, r, s), F32)),
        ("full", jax.ShapeDtypeStruct((blocks, r, s), F32)),
        ("full", jax.ShapeDtypeStruct((k, r, s), F32)),
    ]
    return _call(functools.partial(_fwd_products_kernel, has_u, k, blocks), pos, inputs, outs)


def fwd_messages(pos, ba, sign, here, others, ew, col_blocks):
    k, c, r, s = ba.shape
    inputs = [("dense", ba), ("full", sign), ("full", here), ("full", others), ("dense", ew)]
    outs = [
        ("dense", jax.ShapeDtypeStruct(ba.shape, F32)),
        ("full", jax.ShapeDtypeStruct((col_blocks, c, s), F32)),
    ]
    return _call(functools.partial(_fwd_messages_kernel, k), pos, inputs, outs, [_vmem((c, s))])


def bwd_messages(pos, gsp, gm, ba, sign, here, others, ew, acc, col_blocks=0):
    k, c, r, s = ba.shape
    has_next = gm is not None
    has_acc = acc is not None
    inputs = (
        [("column", gsp)]
        + ([("dense", gm)] if has_next else [])
        + [("dense", ba), ("full", sign), ("full", here), ("full", others), ("dense", ew)]
        + ([("dense", acc)] if has_acc else [])
    )
    outs = [
        ("dense", jax.ShapeDtypeStruct(ba.shape, F32)),
        ("dense", jax.ShapeDtypeStruct(ba.shape, F32)),
        ("full", jax.ShapeDtypeStruct(here.shape, F32)),
        ("full", jax.ShapeDtypeStruct(others.shape, F32)),
    ]
    if col_blocks:
        outs.append(("full", jax.ShapeDtypeStruct((col_blocks, c, s), F32)))
    return _call(
        functools.partial(_bwd_messages_kernel, has_next, has_acc, col_blocks > 0, k),
        pos,
        inputs,
        outs,
        [_vmem((c, s))] if col_blocks else [],
    )


def bwd_products(pos, h, gba, grows, ghere, whole, here, col_blocks, emit_gm):
    k, c, r, s = h.shape
    inputs = [
        ("dense", h),
        ("dense", gba),
        ("full", grows),
        ("full", ghere),
        ("full", whole),
        ("full", here),
    ]
    outs = ([("dense", jax.ShapeDtypeStruct(h.shape, F32))] if emit_gm else []) + [
        ("full", jax.ShapeDtypeStruct((col_blocks, c, s), F32))
    ]
    results = _call(
        functools.partial(_bwd_products_kernel, emit_gm, k),
        pos,
        inputs,
        outs,
        [_vmem((c, r, s)) for _ in range(2)] + [_vmem((c, s))],
    )
    if emit_gm:
        return results[0], results[1]
    return None, results[0]


def pick(hot, values):
    parts = []
    for k in range(hot.shape[0]):
        value = jnp.zeros_like(values[0])
        for j in range(hot.shape[1]):
            value = value + jnp.where(hot[k, j] > 0, values[j], 0.0)
        parts.append(value)
    return jnp.stack(parts)


def place(hot, values):
    parts = []
    for j in range(hot.shape[1]):
        value = jnp.zeros_like(values[0])
        for k in range(hot.shape[0]):
            value = value + jnp.where(hot[k, j] > 0, values[k], 0.0)
        parts.append(value)
    return jnp.stack(parts)


def combine(whole, row_hot, same_row):
    slots = whole.shape[0]
    blocks = row_hot.shape[1]
    ones = jnp.ones_like(whole[0])
    rows = []
    for block in range(blocks):
        value = ones
        for k in range(slots):
            value = value * jnp.where(row_hot[k, block] > 0, whole[k], 1.0)
        rows.append(value)
    others_here = []
    for k in range(slots):
        value = ones
        for other in range(slots):
            if other != k:
                value = value * jnp.where(same_row[k, other], whole[other], 1.0)
        others_here.append(value)
    return jnp.stack(rows), jnp.stack(others_here)


def _power_of_two(n):
    return n > 1 and (n & (n - 1)) == 0


def _swap(value, axis, n, step):
    perm = [(j, j ^ (1 << step)) for j in range(n)]
    return lax.ppermute(value, axis, perm)


def checks_total(values, n):
    if not _power_of_two(n):
        return lax.psum(values, "chk")
    step = 0
    while (1 << step) < n:
        values = values + _swap(values, "chk", n, step)
        step += 1
    return values


def others_forward(rows, check_blocks, n, uniform=False):
    if not _power_of_two(n):
        return others_gather(rows, check_blocks)
    if uniform:
        shape = rows.shape
        small = rows[:, :, 0].reshape(-1, shape[2])
        others, trail = others_forward(small, check_blocks, n)
        grow = lambda value: jnp.broadcast_to(value.reshape(shape[:2] + (1,)), shape)
        trail = [tuple(grow(value) for value in entry) for entry in trail]
        return grow(others), trail
    full = rows
    excl = jnp.ones_like(rows)
    trail = []
    step = 0
    while (1 << step) < n:
        other = _swap(full, "var", n, step)
        trail.append((full, excl, other))
        excl = excl * other
        full = full * other
        step += 1
    return excl, trail


def others_backward(trail, grads, check_blocks, n):
    if not _power_of_two(n):
        return others_scatter(trail, grads, check_blocks)
    spread = grads
    target = jnp.zeros_like(grads)
    for step, (full, excl, other) in enumerate(trail):
        other_spread = _swap(spread, "var", n, step)
        target = target * other + excl * other_spread
        spread = spread * other + other_spread * full
    return target


def others_gather(rows, check_blocks):
    own = lax.axis_index("var")
    piece = lax.all_gather(rows, "var", axis=0, tiled=True)
    indices = jnp.arange(piece.shape[0], dtype=jnp.int32)
    keep = indices // check_blocks != own
    parts = []
    for block in range(check_blocks):
        pick = (keep & (indices % check_blocks == block))[:, None, None]
        parts.append(jnp.prod(jnp.where(pick, piece, 1.0), axis=0))
    return jnp.stack(parts), piece


def others_scatter(row_piece, grads, check_blocks):
    own = lax.axis_index("var")
    grad_piece = lax.all_gather(grads, "var", axis=0, tiled=True)
    indices = jnp.arange(row_piece.shape[0], dtype=jnp.int32)
    keep = indices // check_blocks != own
    new_sums = []
    for block in range(check_blocks):
        pick = (keep & (indices % check_blocks == block))[:, None, None]
        factors = jnp.where(pick, row_piece, 1.0)
        weights = jnp.where(pick, grad_piece, 0.0)
        before, after, whole = exclusive_both(factors, 0)
        new_sums.append(jnp.sum(weights * before * after, axis=0))
    return jnp.stack(new_sums)


def body(n_chk, n_var, tile_bits, tile_pos, tile_count, edge_weight, syndrome, channel_prior, out_cot):
    slot_total = tile_bits.shape[2]
    shots = syndrome.shape[1]
    check_blocks = syndrome.shape[0] // TILE
    column_blocks = channel_prior.shape[0] // TILE
    edge, row_hot, col_hot, same_row = device_tables(
        tile_bits[0, 0], tile_pos[0, 0], tile_count[0, 0], check_blocks, column_blocks
    )
    weight = edge_weight[0, 0].reshape(slot_total, TILE, TILE)
    edge_t = jnp.swapaxes(edge, 1, 2)
    filled = jnp.any(edge_t > 0, axis=2)
    order = jnp.argsort(jnp.where(filled, 0, 1).astype(jnp.int32), axis=1, stable=True)
    pos = jnp.concatenate(
        [
            tile_pos[0, 0].reshape(slot_total * 2),
            jnp.sum(filled.astype(jnp.int32), axis=1),
            order.astype(jnp.int32).reshape(slot_total * TILE),
        ]
    )
    dense = (slot_total, TILE, TILE, shots)
    ew = jnp.broadcast_to((edge_t * jnp.swapaxes(weight, 1, 2))[..., None], dense)
    sign_dev = (1.0 - 2.0 * syndrome.astype(jnp.float32)).reshape(check_blocks, TILE, shots)
    sign_slot = jnp.einsum("kc,crs->krs", row_hot, sign_dev, precision=EXACT)
    prior_dev = channel_prior.reshape(column_blocks, TILE)
    spread = jnp.broadcast_to(prior_dev[:, :, None], (column_blocks, TILE, shots))
    u = None
    saved = []
    total = None
    for step in range(ITERS):
        ba, halves, whole, rows, others_here = fwd_products(pos, spread, u, ew, check_blocks)
        others, trail = others_forward(rows, check_blocks, n_var, uniform=(step == 0 and (check_blocks * TILE) % shots == 0))
        saved.append((halves, ba, whole, others_here, others, trail))
        if step + 1 < ITERS:
            u, column = fwd_messages(pos, ba, sign_slot, others_here, others, ew, column_blocks)
            total = prior_dev[:, :, None] + checks_total(column, n_chk)
            spread = total

    grad_total = out_cot.reshape(column_blocks, TILE, shots)
    prior_grad = jnp.zeros((column_blocks, TILE), jnp.float32)
    grad_m = None
    acc = None
    for step in reversed(range(ITERS)):
        halves, ba, whole, others_here, others, trail = saved[step]
        prior_grad = prior_grad + jnp.sum(grad_total, axis=2)
        if step + 1 == ITERS:
            acc, grad_ba, grad_here, grad_others, last_column = bwd_messages(
                pos, grad_total, grad_m, ba, sign_slot, others_here, others, ew, acc, column_blocks
            )
            total = prior_dev[:, :, None] + checks_total(last_column, n_chk)
            marginals = total.reshape(column_blocks * TILE, shots)
        else:
            acc, grad_ba, grad_here, grad_others = bwd_messages(
                pos, grad_total, grad_m, ba, sign_slot, others_here, others, ew, acc
            )
        grad_rows = others_backward(trail, grad_others, check_blocks, n_var)
        grad_m, column = bwd_products(
            pos, halves, grad_ba, grad_rows, grad_here, whole, others_here,
            column_blocks, step > 0,
        )
        if step > 0:
            grad_total = checks_total(column, n_chk)
    shot_sums = jnp.sum(column, axis=2)
    if (column_blocks * TILE) % 128 == 0:
        shot_sums = checks_total(shot_sums.reshape(-1, 128), n_chk).reshape(column_blocks, TILE)
    else:
        shot_sums = checks_total(shot_sums, n_chk)
    prior_grad = prior_grad + shot_sums
    weight_grad = jnp.where(edge > 0, jnp.swapaxes(jnp.sum(acc, axis=3), 1, 2), 0.0)
    return (
        marginals,
        weight_grad.reshape(1, 1, slot_total, TILE * TILE),
        prior_grad.reshape(column_blocks * TILE),
    )


def solution(mesh):
    placed = (
        P("chk", "var", None, None),
        P("chk", "var", None, None),
        P("chk", "var"),
        P("chk", "var", None, None),
        P("chk", None),
        P("var"),
        P("var", None),
    )
    return jax.shard_map(
        functools.partial(body, mesh.shape["chk"], mesh.shape["var"]),
        mesh=mesh,
        in_specs=placed,
        out_specs=(P("var", None), P("chk", "var", None, None), P("var")),
        check_vma=False,
    )
```

```python
import functools

import jax
import jax.numpy as jnp
from jax import lax
from jax.experimental import pallas as pl
from jax.sharding import PartitionSpec as P

TILE = 64
ITERS = 2


DAMP = 0.97
EXACT = lax.Precision.HIGHEST
F32 = jnp.float32
UNROLL = 4


def linear_both(values, axis):
    length = values.shape[axis]
    pieces = [lax.slice_in_dim(values, index, index + 1, axis=axis) for index in range(length)]
    ones = jnp.ones_like(pieces[0])
    prefix = [ones]
    for index in range(length - 1):
        prefix.append(prefix[-1] * pieces[index])
    suffix = [ones]
    for index in range(length - 1, 0, -1):
        suffix.append(suffix[-1] * pieces[index])
    suffix = suffix[::-1]
    whole = prefix[-1] * pieces[-1]
    return (jnp.concatenate(prefix, axis=axis), jnp.concatenate(suffix, axis=axis), whole)


def exclusive_both(values, axis):
    length = values.shape[axis]
    if length < 16 or length % 8 != 0:
        return linear_both(values, axis)
    shape = values.shape
    split = values.reshape(shape[:axis] + (length // 8, 8) + shape[axis + 1 :])
    inner_before, inner_after, group_whole = linear_both(split, axis + 1)
    outer_before, outer_after, whole = exclusive_both(group_whole, axis)
    before = (inner_before * outer_before).reshape(shape)
    after = (inner_after * outer_after).reshape(shape)
    whole = whole.reshape(shape[:axis] + (1,) + shape[axis + 1 :])
    return (before, after, whole)


def device_tables(bits, positions, count, check_blocks, column_blocks):
    slot_total = bits.shape[0]
    slots = jnp.arange(slot_total, dtype=jnp.int32)
    live = slots < count
    edge = jnp.where(live[:, None], bits, 0).astype(jnp.float32).reshape(slot_total, TILE, TILE)
    row_hot = (positions[:, 0:1] == jnp.arange(check_blocks, dtype=jnp.int32)[None, :]).astype(
        jnp.float32
    )
    col_hot = (positions[:, 1:2] == jnp.arange(column_blocks, dtype=jnp.int32)[None, :]).astype(
        jnp.float32
    )
    same_row = (positions[:, None, 0] == positions[None, :, 0]) & (slots[:, None] != slots[None, :])
    return (edge, row_hot, col_hot, same_row)


def _spread_row(ref, c, shape):
    return jnp.broadcast_to(ref[0, pl.ds(c, 1), :], shape)


def _row_block(pos_ref, k):
    return pos_ref[2 * k]


def _col_block(pos_ref, k):
    return pos_ref[2 * k + 1]


def _columns(pos_ref, k, slots, n_c):
    return pos_ref[2 * slots + k], 3 * slots + k * n_c


def _loop(count, body, init):
    def group(j, carry):
        for t in range(UNROLL):
            carry = body(UNROLL * j + t, carry)
        return carry

    carry = lax.fori_loop(0, count // UNROLL, group, init)
    return lax.fori_loop(UNROLL * (count // UNROLL), count, body, carry)


def _fwd_products_kernel(has_u, slots, blocks, pos_ref, *refs):
    refs = list(refs)
    spread_ref = refs.pop(0)
    u_ref = refs.pop(0) if has_u else None
    ew_ref, ba_ref, h_scr, whole_ref, rows_ref, here_ref = refs
    k = pl.program_id(0)
    n_c = ew_ref.shape[1]
    shape = ew_ref.shape[2:]

    count, base = _columns(pos_ref, k, slots, n_c)

    def forward(i, carry):
        c = pos_ref[base + i]
        m = _spread_row(spread_ref, c, shape)
        if has_u:
            m = m - u_ref[0, c]
        h = jnp.where(ew_ref[0, c] > 0, jnp.tanh(0.5 * m), 1.0)
        h_scr[0, c] = h
        ba_ref[0, c] = carry
        return carry * h

    whole = _loop(count, forward, jnp.ones(shape, F32))
    whole_ref[k] = whole

    def backward(i, carry):
        c = pos_ref[base + count - 1 - i]
        ba_ref[0, c] = ba_ref[0, c] * carry
        return carry * h_scr[0, c]

    _loop(count, backward, jnp.ones(shape, F32))

    @pl.when(k == slots - 1)
    def _():
        wholes = [whole_ref[j] for j in range(slots)]
        rows_of = [_row_block(pos_ref, j) for j in range(slots)]
        for block in range(blocks):
            value = jnp.ones(shape, F32)
            for j in range(slots):
                value = value * jnp.where(rows_of[j] == block, wholes[j], 1.0)
            rows_ref[block] = value
        for j in range(slots):
            value = jnp.ones(shape, F32)
            for other in range(slots):
                if other != j:
                    value = value * jnp.where(rows_of[other] == rows_of[j], wholes[other], 1.0)
            here_ref[j] = value


def _fwd_messages_kernel(slots, pos_ref, ba_ref, sign_ref, here_ref, others_ref, ew_ref, u_ref, col_ref):
    k = pl.program_id(0)
    n_c = ba_ref.shape[1]
    count, base = _columns(pos_ref, k, slots, n_c)

    @pl.when(k == 0)
    def _():
        col_ref[...] = jnp.zeros(col_ref.shape, F32)

    f = sign_ref[k] * here_ref[k] * others_ref[_row_block(pos_ref, k)]
    q = _col_block(pos_ref, k)

    def body(i, carry):
        c = pos_ref[base + i]
        x = ba_ref[0, c] * f
        u = ew_ref[0, c] * jnp.log((1.0 + DAMP * x) / (1.0 - DAMP * x))
        u_ref[0, c] = u
        col_ref[q, pl.ds(c, 1), :] = col_ref[q, pl.ds(c, 1), :] + jnp.sum(u, axis=0, keepdims=True)
        return carry

    _loop(count, body, 0)


def _bwd_messages_kernel(has_next, has_acc, emit_column, slots, pos_ref, *refs):
    refs = list(refs)
    gsp_ref = refs.pop(0)
    gm_ref = refs.pop(0) if has_next else None
    ba_ref, sign_ref, here_ref, others_ref, ew_ref = refs[:5]
    refs = refs[5:]
    acc_ref = refs.pop(0) if has_acc else None
    gw_ref, gba_ref, ghere_ref, gothers_ref = refs[:4]
    col_ref = refs[4] if emit_column else None
    k = pl.program_id(0)
    n_c = ba_ref.shape[1]
    shape = ba_ref.shape[2:]
    q = _col_block(pos_ref, k)

    @pl.when(k == 0)
    def _():
        gothers_ref[...] = jnp.zeros(gothers_ref.shape, F32)
        if emit_column:
            col_ref[...] = jnp.zeros(col_ref.shape, F32)

    p = _row_block(pos_ref, k)
    sign = sign_ref[k]
    here = here_ref[k]
    others = others_ref[p]
    f = sign * here * others
    count, base = _columns(pos_ref, k, slots, n_c)

    def body(i, total):
        c = pos_ref[base + i]
        gu = _spread_row(gsp_ref, c, shape)
        if has_next:
            gu = gu - gm_ref[0, c]
        ba = ba_ref[0, c]
        x = ba * f
        low = 1.0 - DAMP * x
        high = 1.0 + DAMP * x
        inverse = 1.0 / (low * high)
        ratio = jnp.log(high * high * inverse)
        if emit_column:
            u = ew_ref[0, c] * ratio
            col_ref[q, pl.ds(c, 1), :] = col_ref[q, pl.ds(c, 1), :] + jnp.sum(u, axis=0, keepdims=True)
        gw = gu * ratio
        if has_acc:
            gw = gw + acc_ref[0, c]
        gw_ref[0, c] = gw
        gx = gu * ew_ref[0, c] * ((2.0 * DAMP) * inverse)
        gba_ref[0, c] = gx * f
        return total + gx * ba

    grad_factor = _loop(count, body, jnp.zeros(shape, F32))
    ghere_ref[k] = grad_factor * sign * others
    gothers_ref[p] = gothers_ref[p] + grad_factor * sign * here


def _bwd_products_kernel(emit_gm, slots, pos_ref, *refs):
    refs = list(refs)
    h_ref, gba_ref, grows_ref, ghere_ref, whole_ref, here_ref = refs[:6]
    refs = refs[6:]
    gm_ref = refs.pop(0) if emit_gm else None
    col_ref, p_scr, q_scr = refs
    k = pl.program_id(0)
    n_c = h_ref.shape[1]
    shape = h_ref.shape[2:]

    @pl.when(k == 0)
    def _():
        col_ref[...] = jnp.zeros(col_ref.shape, F32)

    p = _row_block(pos_ref, k)
    q = _col_block(pos_ref, k)
    rows_of = [_row_block(pos_ref, j) for j in range(slots)]
    gwh = grows_ref[p] * here_ref[k]
    for other in range(slots):
        term = jnp.where(rows_of[other] == p, ghere_ref[other], 0.0)
        for third in range(slots):
            if third != other:
                term = term * jnp.where(
                    (rows_of[third] == p) & (third != k), whole_ref[third], 1.0
                )
        gwh = gwh + jnp.where(other != k, term, 0.0)

    count, base = _columns(pos_ref, k, slots, n_c)

    def forward(i, carry):
        prod, grad = carry
        c = pos_ref[base + i]
        h = h_ref[0, c]
        p_scr[c] = prod
        q_scr[c] = grad
        return (prod * h, grad * h + gba_ref[0, c] * prod)

    ones = jnp.ones(shape, F32)
    zeros = jnp.zeros(shape, F32)
    _loop(count, forward, (ones, zeros))

    def backward(i, carry):
        prod, grad = carry
        c = pos_ref[base + count - 1 - i]
        h = h_ref[0, c]
        before = p_scr[c]
        gh = q_scr[c] * prod + before * (grad + gwh * prod)
        gm = gh * (0.5 * (1.0 - h * h))
        if emit_gm:
            gm_ref[0, c] = gm
        col_ref[q, pl.ds(c, 1), :] = col_ref[q, pl.ds(c, 1), :] + jnp.sum(gm, axis=0, keepdims=True)
        return (prod * h, grad * h + gba_ref[0, c] * prod)

    _loop(count, backward, (ones, zeros))


def _spec(kind, shape):
    if kind == "dense":
        return pl.BlockSpec((1,) + tuple(shape[1:]), lambda k, pos: (k, 0, 0, 0))
    if kind == "column":
        return pl.BlockSpec((1,) + tuple(shape[1:]), lambda k, pos: (pos[2 * k + 1], 0, 0))
    return pl.BlockSpec(tuple(shape), lambda k, pos: (0,) * len(shape))


def _call(kernel, pos, inputs, outputs, scratch=()):
    from jax.experimental.pallas import tpu as pltpu

    dense = [a for kind, a in inputs if kind == "dense"][0]
    grid_spec = pltpu.PrefetchScalarGridSpec(
        num_scalar_prefetch=1,
        grid=(dense.shape[0],),
        in_specs=[_spec(kind, a.shape) for kind, a in inputs],
        out_specs=[_spec(kind, o.shape) for kind, o in outputs],
        scratch_shapes=list(scratch),
    )
    return pl.pallas_call(
        kernel,
        grid_spec=grid_spec,
        out_shape=[o for kind, o in outputs],
    )(pos, *[a for kind, a in inputs])


def _vmem(shape):
    from jax.experimental.pallas import tpu as pltpu

    return pltpu.VMEM(shape, F32)


def fwd_products(pos, spread, u, ew, blocks):
    k, c, r, s = ew.shape
    has_u = u is not None
    inputs = [("column", spread)] + ([("dense", u)] if has_u else []) + [("dense", ew)]
    outs = [
        ("dense", jax.ShapeDtypeStruct(ew.shape, F32)),
        ("dense", jax.ShapeDtypeStruct(ew.shape, F32)),
        ("full", jax.ShapeDtypeStruct((k, r, s), F32)),
        ("full", jax.ShapeDtypeStruct((blocks, r, s), F32)),
        ("full", jax.ShapeDtypeStruct((k, r, s), F32)),
    ]
    return _call(functools.partial(_fwd_products_kernel, has_u, k, blocks), pos, inputs, outs)


def fwd_messages(pos, ba, sign, here, others, ew, col_blocks):
    k, c, r, s = ba.shape
    inputs = [("dense", ba), ("full", sign), ("full", here), ("full", others), ("dense", ew)]
    outs = [
        ("dense", jax.ShapeDtypeStruct(ba.shape, F32)),
        ("full", jax.ShapeDtypeStruct((col_blocks, c, s), F32)),
    ]
    return _call(functools.partial(_fwd_messages_kernel, k), pos, inputs, outs)


def bwd_messages(pos, gsp, gm, ba, sign, here, others, ew, acc, col_blocks=0):
    k, c, r, s = ba.shape
    has_next = gm is not None
    has_acc = acc is not None
    inputs = (
        [("column", gsp)]
        + ([("dense", gm)] if has_next else [])
        + [("dense", ba), ("full", sign), ("full", here), ("full", others), ("dense", ew)]
        + ([("dense", acc)] if has_acc else [])
    )
    outs = [
        ("dense", jax.ShapeDtypeStruct(ba.shape, F32)),
        ("dense", jax.ShapeDtypeStruct(ba.shape, F32)),
        ("full", jax.ShapeDtypeStruct(here.shape, F32)),
        ("full", jax.ShapeDtypeStruct(others.shape, F32)),
    ]
    if col_blocks:
        outs.append(("full", jax.ShapeDtypeStruct((col_blocks, c, s), F32)))
    return _call(
        functools.partial(_bwd_messages_kernel, has_next, has_acc, col_blocks > 0, k), pos, inputs, outs
    )


def bwd_products(pos, h, gba, grows, ghere, whole, here, col_blocks, emit_gm):
    k, c, r, s = h.shape
    inputs = [
        ("dense", h),
        ("dense", gba),
        ("full", grows),
        ("full", ghere),
        ("full", whole),
        ("full", here),
    ]
    outs = ([("dense", jax.ShapeDtypeStruct(h.shape, F32))] if emit_gm else []) + [
        ("full", jax.ShapeDtypeStruct((col_blocks, c, s), F32))
    ]
    results = _call(
        functools.partial(_bwd_products_kernel, emit_gm, k),
        pos,
        inputs,
        outs,
        [_vmem((c, r, s)) for _ in range(2)],
    )
    if emit_gm:
        return results[0], results[1]
    return None, results[0]


def pick(hot, values):
    parts = []
    for k in range(hot.shape[0]):
        value = jnp.zeros_like(values[0])
        for j in range(hot.shape[1]):
            value = value + jnp.where(hot[k, j] > 0, values[j], 0.0)
        parts.append(value)
    return jnp.stack(parts)


def place(hot, values):
    parts = []
    for j in range(hot.shape[1]):
        value = jnp.zeros_like(values[0])
        for k in range(hot.shape[0]):
            value = value + jnp.where(hot[k, j] > 0, values[k], 0.0)
        parts.append(value)
    return jnp.stack(parts)


def combine(whole, row_hot, same_row):
    slots = whole.shape[0]
    blocks = row_hot.shape[1]
    ones = jnp.ones_like(whole[0])
    rows = []
    for block in range(blocks):
        value = ones
        for k in range(slots):
            value = value * jnp.where(row_hot[k, block] > 0, whole[k], 1.0)
        rows.append(value)
    others_here = []
    for k in range(slots):
        value = ones
        for other in range(slots):
            if other != k:
                value = value * jnp.where(same_row[k, other], whole[other], 1.0)
        others_here.append(value)
    return jnp.stack(rows), jnp.stack(others_here)


def _power_of_two(n):
    return n > 1 and (n & (n - 1)) == 0


def _swap(value, axis, n, step):
    perm = [(j, j ^ (1 << step)) for j in range(n)]
    return lax.ppermute(value, axis, perm)


def checks_total(values, n):
    if not _power_of_two(n):
        return lax.psum(values, "chk")
    step = 0
    while (1 << step) < n:
        values = values + _swap(values, "chk", n, step)
        step += 1
    return values


def others_forward(rows, check_blocks, n, uniform=False):
    if not _power_of_two(n):
        return others_gather(rows, check_blocks)
    if uniform:
        shape = rows.shape
        small = rows[:, :, 0].reshape(-1, shape[2])
        others, trail = others_forward(small, check_blocks, n)
        grow = lambda value: jnp.broadcast_to(value.reshape(shape[:2] + (1,)), shape)
        trail = [tuple(grow(value) for value in entry) for entry in trail]
        return grow(others), trail
    full = rows
    excl = jnp.ones_like(rows)
    trail = []
    step = 0
    while (1 << step) < n:
        other = _swap(full, "var", n, step)
        trail.append((full, excl, other))
        excl = excl * other
        full = full * other
        step += 1
    return excl, trail


def others_backward(trail, grads, check_blocks, n):
    if not _power_of_two(n):
        return others_scatter(trail, grads, check_blocks)
    spread = grads
    target = jnp.zeros_like(grads)
    for step, (full, excl, other) in enumerate(trail):
        other_spread = _swap(spread, "var", n, step)
        target = target * other + excl * other_spread
        spread = spread * other + other_spread * full
    return target


def others_gather(rows, check_blocks):
    own = lax.axis_index("var")
    piece = lax.all_gather(rows, "var", axis=0, tiled=True)
    indices = jnp.arange(piece.shape[0], dtype=jnp.int32)
    keep = indices // check_blocks != own
    parts = []
    for block in range(check_blocks):
        pick = (keep & (indices % check_blocks == block))[:, None, None]
        parts.append(jnp.prod(jnp.where(pick, piece, 1.0), axis=0))
    return jnp.stack(parts), piece


def others_scatter(row_piece, grads, check_blocks):
    own = lax.axis_index("var")
    grad_piece = lax.all_gather(grads, "var", axis=0, tiled=True)
    indices = jnp.arange(row_piece.shape[0], dtype=jnp.int32)
    keep = indices // check_blocks != own
    new_sums = []
    for block in range(check_blocks):
        pick = (keep & (indices % check_blocks == block))[:, None, None]
        factors = jnp.where(pick, row_piece, 1.0)
        weights = jnp.where(pick, grad_piece, 0.0)
        before, after, whole = exclusive_both(factors, 0)
        new_sums.append(jnp.sum(weights * before * after, axis=0))
    return jnp.stack(new_sums)


def body(n_chk, n_var, tile_bits, tile_pos, tile_count, edge_weight, syndrome, channel_prior, out_cot):
    slot_total = tile_bits.shape[2]
    shots = syndrome.shape[1]
    check_blocks = syndrome.shape[0] // TILE
    column_blocks = channel_prior.shape[0] // TILE
    edge, row_hot, col_hot, same_row = device_tables(
        tile_bits[0, 0], tile_pos[0, 0], tile_count[0, 0], check_blocks, column_blocks
    )
    weight = edge_weight[0, 0].reshape(slot_total, TILE, TILE)
    edge_t = jnp.swapaxes(edge, 1, 2)
    filled = jnp.any(edge_t > 0, axis=2)
    order = jnp.argsort(jnp.where(filled, 0, 1).astype(jnp.int32), axis=1, stable=True)
    pos = jnp.concatenate(
        [
            tile_pos[0, 0].reshape(slot_total * 2),
            jnp.sum(filled.astype(jnp.int32), axis=1),
            order.astype(jnp.int32).reshape(slot_total * TILE),
        ]
    )
    dense = (slot_total, TILE, TILE, shots)
    ew = jnp.broadcast_to((edge_t * jnp.swapaxes(weight, 1, 2))[..., None], dense)
    sign_dev = (1.0 - 2.0 * syndrome.astype(jnp.float32)).reshape(check_blocks, TILE, shots)
    sign_slot = jnp.einsum("kc,crs->krs", row_hot, sign_dev, precision=EXACT)
    prior_dev = channel_prior.reshape(column_blocks, TILE)
    spread = jnp.broadcast_to(prior_dev[:, :, None], (column_blocks, TILE, shots))
    u = None
    saved = []
    total = None
    for step in range(ITERS):
        ba, halves, whole, rows, others_here = fwd_products(pos, spread, u, ew, check_blocks)
        others, trail = others_forward(rows, check_blocks, n_var, uniform=(step == 0 and (check_blocks * TILE) % shots == 0))
        saved.append((halves, ba, whole, others_here, others, trail))
        if step + 1 < ITERS:
            u, column = fwd_messages(pos, ba, sign_slot, others_here, others, ew, column_blocks)
            total = prior_dev[:, :, None] + checks_total(column, n_chk)
            spread = total

    grad_total = out_cot.reshape(column_blocks, TILE, shots)
    prior_grad = jnp.zeros((column_blocks, TILE), jnp.float32)
    grad_m = None
    acc = None
    for step in reversed(range(ITERS)):
        halves, ba, whole, others_here, others, trail = saved[step]
        prior_grad = prior_grad + jnp.sum(grad_total, axis=2)
        if step + 1 == ITERS:
            acc, grad_ba, grad_here, grad_others, last_column = bwd_messages(
                pos, grad_total, grad_m, ba, sign_slot, others_here, others, ew, acc, column_blocks
            )
            total = prior_dev[:, :, None] + checks_total(last_column, n_chk)
            marginals = total.reshape(column_blocks * TILE, shots)
        else:
            acc, grad_ba, grad_here, grad_others = bwd_messages(
                pos, grad_total, grad_m, ba, sign_slot, others_here, others, ew, acc
            )
        grad_rows = others_backward(trail, grad_others, check_blocks, n_var)
        grad_m, column = bwd_products(
            pos, halves, grad_ba, grad_rows, grad_here, whole, others_here,
            column_blocks, step > 0,
        )
        if step > 0:
            grad_total = checks_total(column, n_chk)
    shot_sums = jnp.sum(column, axis=2)
    if (column_blocks * TILE) % 128 == 0:
        shot_sums = checks_total(shot_sums.reshape(-1, 128), n_chk).reshape(column_blocks, TILE)
    else:
        shot_sums = checks_total(shot_sums, n_chk)
    prior_grad = prior_grad + shot_sums
    weight_grad = jnp.where(edge > 0, jnp.swapaxes(jnp.sum(acc, axis=3), 1, 2), 0.0)
    return (
        marginals,
        weight_grad.reshape(1, 1, slot_total, TILE * TILE),
        prior_grad.reshape(column_blocks * TILE),
    )


def solution(mesh):
    placed = (
        P("chk", "var", None, None),
        P("chk", "var", None, None),
        P("chk", "var"),
        P("chk", "var", None, None),
        P("chk", None),
        P("var"),
        P("var", None),
    )
    return jax.shard_map(
        functools.partial(body, mesh.shape["chk"], mesh.shape["var"]),
        mesh=mesh,
        in_specs=placed,
        out_specs=(P("var", None), P("chk", "var", None, None), P("var")),
        check_vma=False,
    )
```
